128 devices in a mesh: phi: 16 (over z_hi, y, core), band: 8 (over z_lo, x).
Axes of the slice: x: 4, y: 4, z: 4 (z_hi: 2, z_lo: 2; z = z_hi * 2 + z_lo), core: 2. Of those that a mesh axis runs over, the one named last changes fastest.
Arguments:
- density: float32 [256, 128, 256], P('phi', 'band'), may hold values from 0.5 to 2
- velocity: float32 [3, 256, 128, 256], P(None, 'phi', 'band'), may hold values from -3 to 3
- magnetic_vector: float32 [3, 256, 128, 256], P(None, 'phi', 'band'), may hold values from -3 to 3
- pressure: float32 [256, 128, 256], P('phi', 'band'), may hold values from 0.2 to 2
- fluid_courant_number: float32 [], replicated, may hold values from 0.3 to 0.6
- cosmic_ray_density: float32 [64, 256, 128, 128], P('band', 'phi'), may hold values from 0.3 to 3
- diffusion_per_bin: float32 [64], replicated, may hold values from 0.15 to 0.5
- super_step_scale: float32 [], replicated, may hold values from 2 to 4
Outputs:
- fluid_state: float32 [8, 256, 128, 256], P(None, 'phi', 'band')
- cosmic_ray_next: float32 [64, 256, 128, 128], P('band', 'phi')
The draws below stay inside these ranges and needn't reach their ends.
All inputs are finite; a program needn't handle non-finite values.
Results may differ from the reference program's by a relative error of at most 0.00125.
Values may be sent and summed in bfloat16 or wider, within the bound.
No kernel may reach another device: no remote copies, remote signals or barrier semaphores. Data moves between devices by JAX's collectives and lax.ppermute only.
A program may use at most 256 MiB of HBM per device.

```python
import math
import jax
import jax.numpy as jnp
from jax import lax

RADIAL_CELLS = 256
OUTER_SHELLS = 128
MOMENTUM_BINS = 64
AZIMUTH_CELLS = 256
COLAT_CELLS = 128


def draw_magnetic_vector(key, part):
    transverse_key, strength_key, polarity_key = jax.random.split(key, 3)
    transverse = jnp.clip(0.35 * jax.random.normal(transverse_key, (2, AZIMUTH_CELLS, COLAT_CELLS, RADIAL_CELLS), jnp.float32), -1.2, 1.2)
    strength = jax.random.uniform(strength_key, (AZIMUTH_CELLS, COLAT_CELLS, RADIAL_CELLS), jnp.float32, 1.2, 2.8)
    polarity = 2.0 * jax.random.randint(polarity_key, (AZIMUTH_CELLS, COLAT_CELLS, RADIAL_CELLS), 0, 2).astype(jnp.float32) - 1.0
    return jnp.concatenate([transverse, (polarity * strength)[None]], axis=0)


def block_levels(key, shape, pieces, low, top_value):
    def one(axis_at, parts):
        steps = jax.random.uniform(jax.random.fold_in(jax.random.fold_in(key, 6), axis_at), (parts,), jnp.float32, low / len(pieces), top_value / len(pieces))
        return jnp.repeat(jnp.exp(steps), shape[axis_at] // parts).reshape((-1,) + (1,) * (len(shape) - axis_at - 1))

    gain = one(*pieces[0])
    for cut in pieces[1:]:
        gain = gain * one(*cut)
    return gain


def scatter_about(stream_key, dims, width, limit, pieces=(), kind=jnp.bfloat16):
    entries = jax.random.normal(stream_key, dims, jnp.float32) * width
    if len(pieces) > 0:
        entries = block_levels(stream_key, dims, pieces, -0.22, 0.18) * entries
    return jnp.clip(entries, min=-limit, max=limit).astype(kind)


def setup_inputs(seed: int = 0) -> dict:
    key_list = jax.random.split(jax.random.key(seed), 9)
    return {
        "density": jnp.clip(jnp.exp(math.log(2.0) - 1.3862944 * jax.random.uniform(key_list[0], (AZIMUTH_CELLS, COLAT_CELLS, RADIAL_CELLS), jnp.float32) ** block_levels(key_list[0], (AZIMUTH_CELLS, COLAT_CELLS, RADIAL_CELLS), ((0, 16), (1, 8)), -0.2, 0.2)), 0.5, 2.0),
        "velocity": scatter_about(key_list[1], (3, AZIMUTH_CELLS, COLAT_CELLS, RADIAL_CELLS), 0.5, 3.0, ((1, 16), (2, 8)), jnp.float32),
        "magnetic_vector": draw_magnetic_vector(jax.random.fold_in(key_list[8], 71), 0),
        "pressure": jnp.clip(jnp.exp(math.log(2.0) - 2.3025851 * jax.random.uniform(key_list[3], (AZIMUTH_CELLS, COLAT_CELLS, RADIAL_CELLS), jnp.float32) ** block_levels(key_list[3], (AZIMUTH_CELLS, COLAT_CELLS, RADIAL_CELLS), ((0, 16), (1, 8)), -0.2, 0.2)), 0.2, 2.0),
        "fluid_courant_number": jnp.clip(jax.random.uniform(key_list[4], (), jnp.float32, 0.3, 0.6), 0.3, 0.6),
        "cosmic_ray_density": jnp.clip(jnp.exp(math.log(3.0) - 2.3025851 * jax.random.uniform(key_list[5], (MOMENTUM_BINS, AZIMUTH_CELLS, COLAT_CELLS, OUTER_SHELLS), jnp.float32) ** block_levels(key_list[5], (MOMENTUM_BINS, AZIMUTH_CELLS, COLAT_CELLS, OUTER_SHELLS), ((0, 8), (1, 16)), -0.2, 0.2)), 0.3, 3.0),
        "diffusion_per_bin": jnp.clip(jnp.exp(jax.random.uniform(key_list[6], (MOMENTUM_BINS,), jnp.float32, math.log(0.15), math.log(0.5))), 0.15, 0.5),
        "super_step_scale": jnp.clip(jax.random.uniform(key_list[7], (), jnp.float32, 2.0, 4.0), 2.0, 4.0),
    }


ADIABATIC = 5.0 / 3.0
INNER_RADIUS = 0.1
R_RATIO = 30.0
COLAT_LOW = math.pi / 6.0
COLAT_SPAN = 2.0 * math.pi / 3.0
P_RATIO = 1000.0
K_RATIO = 0.1
B_FLOOR = 0.1
V_BOUND = 3.0
B_BOUND = 3.0
P_HIGH = 2.0
RHO_LOW = 0.5
KAPPA_HIGH = 0.5

def grid_steps(n_radial, n_colat, n_azim, n_bins):
    return (math.log(R_RATIO) / n_radial, COLAT_SPAN / n_colat, 2.0 * math.pi / n_azim, math.log(P_RATIO) / n_bins)

def rate_limits(n_radial, n_shells, n_colat, n_azim, n_bins):
    radial_spacing, colatitude_spacing, azimuth_spacing, step_m = grid_steps(n_radial, n_colat, n_azim, n_bins)
    sine_lower = math.sin(COLAT_LOW + 0.5 * colatitude_spacing)
    fluid_radius = INNER_RADIUS * math.exp(0.5 * radial_spacing)
    fastest_limit = V_BOUND + math.sqrt((ADIABATIC * P_HIGH + 3.0 * B_BOUND ** 2) / RHO_LOW)
    fluid_rate = fastest_limit * (1.0 / (fluid_radius * radial_spacing) + 1.0 / (fluid_radius * colatitude_spacing) + 1.0 / (fluid_radius * sine_lower * azimuth_spacing))
    shell_low = INNER_RADIUS * math.exp(radial_spacing * (n_radial - n_shells + 0.5))
    inv_r = 1.0 / (shell_low * radial_spacing)
    inv_t = 1.0 / (shell_low * colatitude_spacing)
    inv_p = 1.0 / (shell_low * sine_lower * azimuth_spacing)
    cosmic_ray_rate = 2.0 * KAPPA_HIGH * (inv_r ** 2 + inv_t ** 2 + inv_p ** 2) + V_BOUND * (inv_r + inv_t + inv_p) + V_BOUND * (inv_r + inv_t + inv_p + 4.0 / shell_low) / (3.0 * step_m)
    return (fluid_rate, cosmic_ray_rate)

def shell_radii(start_index, cell_count, n_radial):
    cell_index = jnp.arange(cell_count, dtype=jnp.float32) + (start_index + 0.5)
    return INNER_RADIUS * jnp.exp(math.log(R_RATIO) / n_radial * cell_index)

def colatitudes(start_index, cell_count, n_colat):
    cell_index = jnp.arange(cell_count, dtype=jnp.float32) + 0.5
    return COLAT_LOW + COLAT_SPAN * (cell_index + start_index) / n_colat

def rounded(values):
    return lax.optimization_barrier(values.astype(jnp.bfloat16)).astype(jnp.float32)

def conserved(primitive):
    density = primitive[0]
    velocity = primitive[1:4]
    magnetic_vector = primitive[4:7]
    pressure = primitive[7]
    energy = pressure / (ADIABATIC - 1.0) + 0.5 * density * lax.optimization_barrier(jnp.sum(velocity * velocity, axis=0)) + 0.5 * lax.optimization_barrier(jnp.sum(magnetic_vector * magnetic_vector, axis=0))
    return jnp.concatenate([density[None], density[None] * velocity, magnetic_vector, energy[None]], axis=0)

def face_terms(primitive, cell_state, normal):
    density = primitive[0]
    velocity = primitive[1:4]
    magnetic_vector = primitive[4:7]
    pressure = primitive[7]
    v_normal = velocity[normal]
    b_normal = magnetic_vector[normal]
    magnetic = 0.5 * lax.optimization_barrier(jnp.sum(magnetic_vector * magnetic_vector, axis=0))
    total_p = pressure + magnetic
    momentum = [density * velocity[k] * v_normal - magnetic_vector[k] * b_normal for k in range(3)]
    momentum[normal] = momentum[normal] + total_p
    induction = [v_normal * magnetic_vector[k] - b_normal * velocity[k] for k in range(3)]
    energy_flux = (cell_state[7] + total_p) * v_normal - b_normal * lax.optimization_barrier(jnp.sum(velocity * magnetic_vector, axis=0))
    fluxes = jnp.stack([density * v_normal] + momentum + induction + [energy_flux], axis=0)
    speeds = jnp.abs(v_normal) + jnp.sqrt((ADIABATIC * pressure + 2.0 * magnetic) / density)
    return (fluxes, speeds)

def rusanov(primitive, cell_state, normal, along_axis, spacing):
    fluxes, speeds = face_terms(primitive, cell_state, normal)
    length = speeds.shape[along_axis]
    wave_speed = jnp.maximum(lax.slice_in_dim(speeds, 0, length - 1, axis=along_axis), lax.slice_in_dim(speeds, 1, length, axis=along_axis))
    flux_low = lax.slice_in_dim(fluxes, 0, length - 1, axis=along_axis + 1)
    flux_high = lax.slice_in_dim(fluxes, 1, length, axis=along_axis + 1)
    state_low = lax.slice_in_dim(cell_state, 0, length - 1, axis=along_axis + 1)
    state_high = lax.slice_in_dim(cell_state, 1, length, axis=along_axis + 1)
    face_flux = 0.5 * (flux_low + flux_high) - 0.5 * wave_speed[None] * (state_high - state_low)
    upper = lax.slice_in_dim(face_flux, 1, length - 1, axis=along_axis + 1)
    lower = lax.slice_in_dim(face_flux, 0, length - 2, axis=along_axis + 1)
    return (upper - lower) / spacing

def fluid_update(padded_array, radius_values, colatitude_mesh, timestep_length, mesh_spacing):
    ghosted = jnp.pad(padded_array, ((0, 0), (0, 0), (0, 0), (1, 1)), mode='edge')
    cell_state = conserved(ghosted)
    width_r = radius_values * mesh_spacing[0]
    width_t = radius_values * mesh_spacing[1]
    width_p = jnp.sin(colatitude_mesh)[:, None] * radius_values * mesh_spacing[2]
    radial = rusanov(ghosted[:, 1:-1, 1:-1, :], cell_state[:, 1:-1, 1:-1, :], 0, 2, width_r)
    polar = rusanov(ghosted[:, 1:-1, :, 1:-1], cell_state[:, 1:-1, :, 1:-1], 1, 1, width_t)
    azimuthal = rusanov(ghosted[:, :, 1:-1, 1:-1], cell_state[:, :, 1:-1, 1:-1], 2, 0, width_p)
    return cell_state[:, 1:-1, 1:-1, 1:-1] - timestep_length * (radial + polar + azimuthal)

def divergence(radial_pad, polar_pad, azim_pad, radius_values, colatitude_mesh, mesh_spacing):
    sin_colat = jnp.sin(colatitude_mesh)[:, None]
    cotangent = (jnp.cos(colatitude_mesh) / jnp.sin(colatitude_mesh))[:, None]
    radial_mid = radial_pad[:, :, 1:-1]
    polar_mid = polar_pad[:, 1:-1, :]
    d_radial = (radial_pad[:, :, 2:] - radial_pad[:, :, :-2]) / (2.0 * radius_values * mesh_spacing[0])
    d_polar = (polar_pad[:, 2:, :] - polar_pad[:, :-2, :]) / (2.0 * radius_values * mesh_spacing[1])
    d_azim = (azim_pad[2:] - azim_pad[:-2]) / (2.0 * radius_values * sin_colat * mesh_spacing[2])
    return d_radial + 2.0 * radial_mid / radius_values + d_polar + cotangent * polar_mid / radius_values + d_azim

def transport_coefficients(wind_vel, mag_wind, spread, radius_values, colatitude_mesh, mesh_spacing):
    width_r = radius_values * mesh_spacing[0]
    width_t = radius_values * mesh_spacing[1]
    width_p = jnp.sin(colatitude_mesh)[:, None] * radius_values * mesh_spacing[2]
    widths = (width_r, width_t, width_p)
    mag_sq = lax.optimization_barrier(jnp.sum(mag_wind * mag_wind, axis=0)) + B_FLOOR
    b_share = K_RATIO + (1.0 - K_RATIO) * mag_wind * mag_wind / mag_sq
    coef_list = [b_share[k] / (widths[k] * widths[k]) for k in range(3)]
    up_list = [jnp.maximum(wind_vel[k], 0.0) / widths[k] for k in range(3)]
    down_list = [jnp.minimum(wind_vel[k], 0.0) / widths[k] for k in range(3)]
    drift_rate = spread / 3.0
    return (coef_list, up_list, down_list, jnp.maximum(drift_rate, 0.0), jnp.minimum(drift_rate, 0.0))

def transport_rate(extended, coef_set, kappa_col, step_m):
    coef_list, up_list, down_list, drift_up, drift_down = coef_set
    center = extended[1:-1, 1:-1, 1:-1, 1:-1]
    low_cells = (extended[1:-1, 1:-1, 1:-1, :-2], extended[1:-1, 1:-1, :-2, 1:-1], extended[1:-1, :-2, 1:-1, 1:-1])
    high_cells = (extended[1:-1, 1:-1, 1:-1, 2:], extended[1:-1, 1:-1, 2:, 1:-1], extended[1:-1, 2:, 1:-1, 1:-1])
    curvature = coef_list[0] * (high_cells[0] - 2.0 * center + low_cells[0])
    curvature = curvature + coef_list[1] * (high_cells[1] - 2.0 * center + low_cells[1])
    curvature = curvature + coef_list[2] * (high_cells[2] - 2.0 * center + low_cells[2])
    diffusion = kappa_col[:, None, None, None] * curvature
    advection = up_list[0] * (center - low_cells[0]) + down_list[0] * (high_cells[0] - center)
    advection = advection + up_list[1] * (center - low_cells[1]) + down_list[1] * (high_cells[1] - center)
    advection = advection + up_list[2] * (center - low_cells[2]) + down_list[2] * (high_cells[2] - center)
    bin_low = extended[:-2, 1:-1, 1:-1, 1:-1]
    bin_high = extended[2:, 1:-1, 1:-1, 1:-1]
    momentum = (drift_up * (bin_high - center) + drift_down * (center - bin_low)) / step_m
    return diffusion - advection + momentum

def full_pad(values):
    extended = jnp.pad(values, ((1, 1), (0, 0), (1, 1), (1, 1)), mode='edge')
    return jnp.pad(extended, ((0, 0), (1, 1), (0, 0), (0, 0)), mode='wrap')

def reference(density, velocity, magnetic_vector, pressure, fluid_courant_number, cosmic_ray_density, diffusion_per_bin, super_step_scale):
    mesh_spacing = grid_steps(RADIAL_CELLS, COLAT_CELLS, AZIMUTH_CELLS, MOMENTUM_BINS)
    fluid_rate, cosmic_ray_rate = rate_limits(RADIAL_CELLS, OUTER_SHELLS, COLAT_CELLS, AZIMUTH_CELLS, MOMENTUM_BINS)
    primitive = jnp.concatenate([density[None], velocity, magnetic_vector, pressure[None]], axis=0)
    padded_array = jnp.pad(primitive, ((0, 0), (1, 1), (0, 0), (0, 0)), mode='wrap')
    padded_array = jnp.pad(padded_array, ((0, 0), (0, 0), (1, 1), (0, 0)), mode='edge')
    radius_full = shell_radii(0, RADIAL_CELLS, RADIAL_CELLS)
    colatitude_full = colatitudes(0, COLAT_CELLS, COLAT_CELLS)
    fluid_state = fluid_update(padded_array, radius_full, colatitude_full, fluid_courant_number / fluid_rate, mesh_spacing)
    first_shell = RADIAL_CELLS - OUTER_SHELLS
    wind_vel = rounded(velocity[:, :, :, first_shell:])
    mag_wind = rounded(magnetic_vector[:, :, :, first_shell:])
    radius_sh = shell_radii(first_shell, OUTER_SHELLS, RADIAL_CELLS)
    radial_pad = jnp.pad(wind_vel[0], ((0, 0), (0, 0), (1, 1)), mode='edge')
    polar_pad = jnp.pad(wind_vel[1], ((0, 0), (1, 1), (0, 0)), mode='edge')
    azim_pad = jnp.pad(wind_vel[2], ((1, 1), (0, 0), (0, 0)), mode='wrap')
    spread = rounded(divergence(radial_pad, polar_pad, azim_pad, radius_sh, colatitude_full, mesh_spacing))
    coef_set = transport_coefficients(wind_vel, mag_wind, spread, radius_sh, colatitude_full, mesh_spacing)
    sts_step = super_step_scale / cosmic_ray_rate
    first_section = cosmic_ray_density + sts_step / 3.0 * transport_rate(full_pad(cosmic_ray_density), coef_set, diffusion_per_bin, mesh_spacing[3])
    cosmic_ray_next = 1.5 * first_section - 0.5 * cosmic_ray_density + sts_step / 2.0 * transport_rate(full_pad(first_section), coef_set, diffusion_per_bin, mesh_spacing[3])
    return (fluid_state, cosmic_ray_next)
```

```python
import functools
import math

import jax
import jax.numpy as jnp
from jax import lax
from jax.experimental import pallas as pl
from jax.experimental.pallas import tpu as pltpu
from jax.sharding import PartitionSpec as P

ADIABATIC = 5.0 / 3.0
INNER_RADIUS = 0.1
R_RATIO = 30.0
COLAT_LOW = math.pi / 6.0
COLAT_SPAN = 2.0 * math.pi / 3.0
P_RATIO = 1000.0
K_RATIO = 0.1
B_FLOOR = 0.1
V_BOUND = 3.0
B_BOUND = 3.0
P_HIGH = 2.0
RHO_LOW = 0.5
KAPPA_HIGH = 0.5


def padded(value, sides, width):
    for axis, dim in sides:
        size, length = (lax.axis_size(axis), value.shape[dim])
        up = [(i, (i + 1) % size) for i in range(size)]
        down = [(j, i) for i, j in up]
        last = lax.slice_in_dim(value, length - width, length, axis=dim)
        leading = lax.slice_in_dim(value, 0, width, axis=dim)
        before = lax.ppermute(last, axis, up)
        after = lax.ppermute(leading, axis, down)
        value = jnp.concatenate([before, value, after], axis=dim)
    return value


def grid_steps(n_radial, n_colat, n_azim, n_bins):
    return (
        math.log(R_RATIO) / n_radial,
        COLAT_SPAN / n_colat,
        2.0 * math.pi / n_azim,
        math.log(P_RATIO) / n_bins,
    )


def rate_limits(n_radial, n_shells, n_colat, n_azim, n_bins):
    radial_spacing, colatitude_spacing, azimuth_spacing, step_m = grid_steps(
        n_radial, n_colat, n_azim, n_bins
    )
    sine_lower = math.sin(COLAT_LOW + 0.5 * colatitude_spacing)
    fluid_radius = INNER_RADIUS * math.exp(0.5 * radial_spacing)
    fastest_limit = V_BOUND + math.sqrt((ADIABATIC * P_HIGH + 3.0 * B_BOUND**2) / RHO_LOW)
    fluid_rate = fastest_limit * (
        1.0 / (fluid_radius * radial_spacing)
        + 1.0 / (fluid_radius * colatitude_spacing)
        + 1.0 / (fluid_radius * sine_lower * azimuth_spacing)
    )
    shell_low = INNER_RADIUS * math.exp(radial_spacing * (n_radial - n_shells + 0.5))
    inv_r = 1.0 / (shell_low * radial_spacing)
    inv_t = 1.0 / (shell_low * colatitude_spacing)
    inv_p = 1.0 / (shell_low * sine_lower * azimuth_spacing)
    cosmic_ray_rate = (
        2.0 * KAPPA_HIGH * (inv_r**2 + inv_t**2 + inv_p**2)
        + V_BOUND * (inv_r + inv_t + inv_p)
        + V_BOUND * (inv_r + inv_t + inv_p + 4.0 / shell_low) / (3.0 * step_m)
    )
    return (fluid_rate, cosmic_ray_rate)


def shell_radii(start_index, cell_count, n_radial):
    cell_index = jnp.arange(cell_count, dtype=jnp.float32) + (start_index + 0.5)
    return INNER_RADIUS * jnp.exp(math.log(R_RATIO) / n_radial * cell_index)


def colatitudes(start_index, cell_count, n_colat):
    cell_index = jnp.arange(cell_count, dtype=jnp.float32) + 0.5
    return COLAT_LOW + COLAT_SPAN * (cell_index + start_index) / n_colat


def edge_fix(values, along_axis, depth, band_pos, axis_count):
    extent = values.shape[along_axis]
    low_ghost = lax.slice_in_dim(values, 0, depth, axis=along_axis)
    high_ghost = lax.slice_in_dim(values, extent - depth, extent, axis=along_axis)
    first_own = lax.slice_in_dim(values, depth, depth + 1, axis=along_axis)
    last_own = lax.slice_in_dim(values, extent - depth - 1, extent - depth, axis=along_axis)
    low_rim = jnp.where(band_pos == 0, first_own, low_ghost)
    high_rim = jnp.where(band_pos == axis_count - 1, last_own, high_ghost)
    middle = lax.slice_in_dim(values, depth, extent - depth, axis=along_axis)
    return jnp.concatenate([low_rim, middle, high_rim], axis=along_axis)


def conserved(primitive):
    density = primitive[0]
    velocity = primitive[1:4]
    magnetic_vector = primitive[4:7]
    pressure = primitive[7]
    energy = (
        pressure / (ADIABATIC - 1.0)
        + 0.5 * density * jnp.sum(velocity * velocity, axis=0)
        + 0.5 * jnp.sum(magnetic_vector * magnetic_vector, axis=0)
    )
    return jnp.concatenate(
        [density[None], density[None] * velocity, magnetic_vector, energy[None]], axis=0
    )


def face_terms(primitive, cell_state, normal):
    density = primitive[0]
    velocity = primitive[1:4]
    magnetic_vector = primitive[4:7]
    pressure = primitive[7]
    v_normal = velocity[normal]
    b_normal = magnetic_vector[normal]
    magnetic = 0.5 * jnp.sum(magnetic_vector * magnetic_vector, axis=0)
    total_p = pressure + magnetic
    momentum = [density * velocity[k] * v_normal - magnetic_vector[k] * b_normal for k in range(3)]
    momentum[normal] = momentum[normal] + total_p
    induction = [v_normal * magnetic_vector[k] - b_normal * velocity[k] for k in range(3)]
    energy_flux = (cell_state[7] + total_p) * v_normal - b_normal * jnp.sum(
        velocity * magnetic_vector, axis=0
    )
    fluxes = jnp.stack([density * v_normal] + momentum + induction + [energy_flux], axis=0)
    speeds = jnp.abs(v_normal) + jnp.sqrt((ADIABATIC * pressure + 2.0 * magnetic) / density)
    return (fluxes, speeds)


def rusanov(primitive, cell_state, normal, along_axis, spacing):
    fluxes, speeds = face_terms(primitive, cell_state, normal)
    length = speeds.shape[along_axis]
    wave_speed = jnp.maximum(
        lax.slice_in_dim(speeds, 0, length - 1, axis=along_axis),
        lax.slice_in_dim(speeds, 1, length, axis=along_axis),
    )
    flux_low = lax.slice_in_dim(fluxes, 0, length - 1, axis=along_axis + 1)
    flux_high = lax.slice_in_dim(fluxes, 1, length, axis=along_axis + 1)
    state_low = lax.slice_in_dim(cell_state, 0, length - 1, axis=along_axis + 1)
    state_high = lax.slice_in_dim(cell_state, 1, length, axis=along_axis + 1)
    face_flux = 0.5 * (flux_low + flux_high) - 0.5 * wave_speed[None] * (state_high - state_low)
    upper = lax.slice_in_dim(face_flux, 1, length - 1, axis=along_axis + 1)
    lower = lax.slice_in_dim(face_flux, 0, length - 2, axis=along_axis + 1)
    return (upper - lower) / spacing


def fluid_update(padded_array, radius_values, colatitude_mesh, timestep_length, mesh_spacing):
    ghosted = jnp.pad(padded_array, ((0, 0), (0, 0), (0, 0), (1, 1)), mode="edge")
    cell_state = conserved(ghosted)
    width_r = radius_values * mesh_spacing[0]
    width_t = radius_values * mesh_spacing[1]
    width_p = jnp.sin(colatitude_mesh)[:, None] * radius_values * mesh_spacing[2]
    radial = rusanov(ghosted[:, 1:-1, 1:-1, :], cell_state[:, 1:-1, 1:-1, :], 0, 2, width_r)
    polar = rusanov(ghosted[:, 1:-1, :, 1:-1], cell_state[:, 1:-1, :, 1:-1], 1, 1, width_t)
    azimuthal = rusanov(ghosted[:, :, 1:-1, 1:-1], cell_state[:, :, 1:-1, 1:-1], 2, 0, width_p)
    return cell_state[:, 1:-1, 1:-1, 1:-1] - timestep_length * (radial + polar + azimuthal)


def divergence(radial_pad, polar_pad, azim_pad, radius_values, colatitude_mesh, mesh_spacing):
    sin_colat = jnp.sin(colatitude_mesh)[:, None]
    cotangent = (jnp.cos(colatitude_mesh) / jnp.sin(colatitude_mesh))[:, None]
    radial_mid = radial_pad[:, :, 1:-1]
    polar_mid = polar_pad[:, 1:-1, :]
    d_radial = (radial_pad[:, :, 2:] - radial_pad[:, :, :-2]) / (
        2.0 * radius_values * mesh_spacing[0]
    )
    d_polar = (polar_pad[:, 2:, :] - polar_pad[:, :-2, :]) / (2.0 * radius_values * mesh_spacing[1])
    d_azim = (azim_pad[2:] - azim_pad[:-2]) / (2.0 * radius_values * sin_colat * mesh_spacing[2])
    return (
        d_radial
        + 2.0 * radial_mid / radius_values
        + d_polar
        + cotangent * polar_mid / radius_values
        + d_azim
    )


def transport_coefficients(
    wind_vel, mag_wind, spread, radius_values, colatitude_mesh, mesh_spacing
):
    width_r = radius_values * mesh_spacing[0]
    width_t = radius_values * mesh_spacing[1]
    width_p = jnp.sin(colatitude_mesh)[:, None] * radius_values * mesh_spacing[2]
    widths = (width_r, width_t, width_p)
    mag_sq = jnp.sum(mag_wind * mag_wind, axis=0) + B_FLOOR
    b_share = K_RATIO + (1.0 - K_RATIO) * mag_wind * mag_wind / mag_sq
    coef_list = [b_share[k] / (widths[k] * widths[k]) for k in range(3)]
    up_list = [jnp.maximum(wind_vel[k], 0.0) / widths[k] for k in range(3)]
    down_list = [jnp.minimum(wind_vel[k], 0.0) / widths[k] for k in range(3)]
    drift_rate = spread / 3.0
    return (
        coef_list,
        up_list,
        down_list,
        jnp.maximum(drift_rate, 0.0),
        jnp.minimum(drift_rate, 0.0),
    )


def transport_rate(extended, coef_set, kappa_col, step_m):
    coef_list, up_list, down_list, drift_up, drift_down = coef_set
    center = extended[1:-1, 1:-1, 1:-1, 1:-1]
    low_cells = (
        extended[1:-1, 1:-1, 1:-1, :-2],
        extended[1:-1, 1:-1, :-2, 1:-1],
        extended[1:-1, :-2, 1:-1, 1:-1],
    )
    high_cells = (
        extended[1:-1, 1:-1, 1:-1, 2:],
        extended[1:-1, 1:-1, 2:, 1:-1],
        extended[1:-1, 2:, 1:-1, 1:-1],
    )
    curvature = coef_list[0] * (high_cells[0] - 2.0 * center + low_cells[0])
    curvature = curvature + coef_list[1] * (high_cells[1] - 2.0 * center + low_cells[1])
    curvature = curvature + coef_list[2] * (high_cells[2] - 2.0 * center + low_cells[2])
    diffusion = kappa_col[:, None, None, None] * curvature
    advection = up_list[0] * (center - low_cells[0]) + down_list[0] * (high_cells[0] - center)
    advection = (
        advection + up_list[1] * (center - low_cells[1]) + down_list[1] * (high_cells[1] - center)
    )
    advection = (
        advection + up_list[2] * (center - low_cells[2]) + down_list[2] * (high_cells[2] - center)
    )
    bin_low = extended[:-2, 1:-1, 1:-1, 1:-1]
    bin_high = extended[2:, 1:-1, 1:-1, 1:-1]
    momentum = (drift_up * (bin_high - center) + drift_down * (center - bin_low)) / step_m
    return diffusion - advection + momentum


ROWS = 16


def _vec(shape, scalar):
    return jnp.full(shape, scalar, jnp.int32)


def section_kernel(scal_ref, kappa_ref, g_ref, gp_ref, gn_ref, azlo_ref, azhi_ref,
                   binlo_ref, binhi_ref, coef_ref, *rest, second):
    if second:
        f0_ref, out_ref = rest
    else:
        (out_ref,) = rest
    step = pl.program_id(0)
    last_step = pl.num_programs(0) - 1
    bins, _, colat, shells = g_ref.shape
    shape = (ROWS, shells)
    row = lax.broadcasted_iota(jnp.int32, shape, 0)
    lane = lax.broadcasted_iota(jnp.int32, shape, 1)
    first_az = _vec(shape, step) == 0
    last_az = _vec(shape, step) == last_step
    scale = scal_ref[0]

    def per_bin(k, carry):
        kap = kappa_ref[k]
        k_low = jnp.maximum(k - 1, 0)
        k_high = jnp.minimum(k + 1, bins - 1)
        first_bin = _vec(shape, k) == 0
        last_bin = _vec(shape, k) == bins - 1
        for r0 in range(0, colat, ROWS):
            rows = slice(r0, r0 + ROWS)
            center = g_ref[k, 0, rows, :]
            if r0 == 0:
                low_t = jnp.where(row == 0, center, pltpu.roll(center, 1, 0))
            else:
                low_t = g_ref[k, 0, r0 - 1:r0 - 1 + ROWS, :]
            if r0 + ROWS == colat:
                high_t = jnp.where(row == ROWS - 1, center, pltpu.roll(center, ROWS - 1, 0))
            else:
                high_t = g_ref[k, 0, r0 + 1:r0 + 1 + ROWS, :]
            low_r = jnp.where(lane == 0, center, pltpu.roll(center, 1, 1))
            high_r = jnp.where(lane == shells - 1, center, pltpu.roll(center, shells - 1, 1))
            low_p = jnp.where(first_az, azlo_ref[k, 0, rows, :], gp_ref[k, 0, rows, :])
            high_p = jnp.where(last_az, azhi_ref[k, 0, rows, :], gn_ref[k, 0, rows, :])
            low_b = jnp.where(first_bin, binlo_ref[0, 0, rows, :], g_ref[k_low, 0, rows, :])
            high_b = jnp.where(last_bin, binhi_ref[0, 0, rows, :], g_ref[k_high, 0, rows, :])
            twice = 2.0 * center
            curvature = coef_ref[0, 0, rows, :] * (high_r - twice + low_r)
            curvature = curvature + coef_ref[1, 0, rows, :] * (high_t - twice + low_t)
            curvature = curvature + coef_ref[2, 0, rows, :] * (high_p - twice + low_p)
            w_r = coef_ref[3, 0, rows, :]
            w_t = coef_ref[4, 0, rows, :]
            w_p = coef_ref[5, 0, rows, :]
            advection = jnp.maximum(w_r, 0.0) * (center - low_r) + jnp.minimum(w_r, 0.0) * (high_r - center)
            advection = advection + jnp.maximum(w_t, 0.0) * (center - low_t) + jnp.minimum(w_t, 0.0) * (high_t - center)
            advection = advection + jnp.maximum(w_p, 0.0) * (center - low_p) + jnp.minimum(w_p, 0.0) * (high_p - center)
            drift = coef_ref[6, 0, rows, :]
            momentum = jnp.maximum(drift, 0.0) * (high_b - center) + jnp.minimum(drift, 0.0) * (center - low_b)
            rate = kap * curvature - advection + momentum
            if second:
                value = 1.5 * center - 0.5 * f0_ref[k, 0, rows, :] + scale * rate
            else:
                value = center + scale * rate
            out_ref[k, 0, rows, :] = value
        return carry

    lax.fori_loop(0, bins, per_bin, 0)


def section_call(scal, kappa, g, az_low, az_high, bin_low, bin_high, coefs, f0=None, interpret=False):
    bins, azim, colat, shells = g.shape
    block = (bins, 1, colat, shells)
    plane = (1, 1, colat, shells)
    smem = pl.BlockSpec(memory_space=pltpu.SMEM)
    in_specs = [
        smem,
        smem,
        pl.BlockSpec(block, lambda a: (0, a, 0, 0)),
        pl.BlockSpec(block, lambda a: (0, jnp.maximum(a - 1, 0), 0, 0)),
        pl.BlockSpec(block, lambda a: (0, jnp.minimum(a + 1, azim - 1), 0, 0)),
        pl.BlockSpec(block, lambda a: (0, 0, 0, 0)),
        pl.BlockSpec(block, lambda a: (0, 0, 0, 0)),
        pl.BlockSpec(plane, lambda a: (0, a, 0, 0)),
        pl.BlockSpec(plane, lambda a: (0, a, 0, 0)),
        pl.BlockSpec((coefs.shape[0], 1, colat, shells), lambda a: (0, a, 0, 0)),
    ]
    args = [scal, kappa, g, g, g, az_low, az_high, bin_low, bin_high, coefs]
    if f0 is not None:
        in_specs.append(pl.BlockSpec(block, lambda a: (0, a, 0, 0)))
        args.append(f0)
    return pl.pallas_call(
        functools.partial(section_kernel, second=f0 is not None),
        grid=(azim,),
        in_specs=in_specs,
        out_specs=pl.BlockSpec(block, lambda a: (0, a, 0, 0)),
        out_shape=jax.ShapeDtypeStruct(g.shape, jnp.float32),
        compiler_params=pltpu.CompilerParams(dimension_semantics=("arbitrary",)),
        interpret=interpret,
    )(*args)


def neighbours(value, axis, dim):
    size = lax.axis_size(axis)
    up = [(i, (i + 1) % size) for i in range(size)]
    down = [(j, i) for i, j in up]
    length = value.shape[dim]
    last = lax.slice_in_dim(value, length - 1, length, axis=dim).astype(jnp.bfloat16)
    leading = lax.slice_in_dim(value, 0, 1, axis=dim).astype(jnp.bfloat16)
    before = lax.ppermute(last, axis, up).astype(value.dtype)
    after = lax.ppermute(leading, axis, down).astype(value.dtype)
    return before, after


def section_halos(values, band_pos, band_count):
    az_low, az_high = neighbours(values, "phi", 1)
    bin_low, bin_high = neighbours(values, "band", 0)
    bins = values.shape[0]
    bin_low = jnp.where(band_pos == 0, values[0:1], bin_low)
    bin_high = jnp.where(band_pos == band_count - 1, values[bins - 1:bins], bin_high)
    return az_low, az_high, bin_low, bin_high


def body(
    density,
    velocity,
    magnetic_vector,
    pressure,
    fluid_courant_number,
    cosmic_ray_density,
    diffusion_per_bin,
    super_step_scale,
):
    azim_dev = density.shape[0]
    colat_dev = density.shape[1]
    radial_cell_count = density.shape[2]
    band_count = lax.axis_size("band")
    phi_count = lax.axis_size("phi")
    colatitude_count = colat_dev * band_count
    azimuth_cell_count = azim_dev * phi_count
    bin_dev = cosmic_ray_density.shape[0]
    momentum_bin_count = bin_dev * band_count
    outer_shell_count = cosmic_ray_density.shape[3]
    band_pos = lax.axis_index("band")
    mesh_spacing = grid_steps(
        radial_cell_count, colatitude_count, azimuth_cell_count, momentum_bin_count
    )
    fluid_rate, cosmic_ray_rate = rate_limits(
        radial_cell_count,
        outer_shell_count,
        colatitude_count,
        azimuth_cell_count,
        momentum_bin_count,
    )
    primitive = jnp.concatenate([density[None], velocity, magnetic_vector, pressure[None]], axis=0)
    padded_array = padded(primitive, (("phi", 1), ("band", 2)), 1)
    padded_array = edge_fix(padded_array, 2, 1, band_pos, band_count)
    radius_full = shell_radii(0, radial_cell_count, radial_cell_count)
    colatitude_local = colatitudes(band_pos * colat_dev, colat_dev, colatitude_count)
    fluid_state = fluid_update(
        padded_array, radius_full, colatitude_local, fluid_courant_number / fluid_rate, mesh_spacing
    )
    first_shell = radial_cell_count - outer_shell_count
    radius_sh = shell_radii(first_shell, outer_shell_count, radial_cell_count)
    colatitude_full = colatitudes(0, colatitude_count, colatitude_count)
    own_fields = jnp.concatenate(
        [velocity[:, :, :, first_shell:], magnetic_vector[:, :, :, first_shell:]], axis=0
    ).astype(jnp.bfloat16)
    wind_half = lax.all_gather(own_fields, "band", axis=2, tiled=True)
    wind_vel = wind_half[0:3].astype(jnp.float32)
    azim_pad = padded(wind_half[2], (("phi", 0),), 1).astype(jnp.float32)
    radial_pad = jnp.pad(wind_vel[0], ((0, 0), (0, 0), (1, 1)), mode="edge")
    polar_pad = jnp.pad(wind_vel[1], ((0, 0), (1, 1), (0, 0)), mode="edge")
    spread_half = divergence(
        radial_pad, polar_pad, azim_pad, radius_sh, colatitude_full, mesh_spacing
    ).astype(jnp.bfloat16)
    kappa_here = lax.dynamic_slice_in_dim(diffusion_per_bin, band_pos * bin_dev, bin_dev)
    sts_step = super_step_scale / cosmic_ray_rate
    coef_set = transport_coefficients(
        wind_half[0:3].astype(jnp.float32),
        wind_half[3:6].astype(jnp.float32),
        spread_half.astype(jnp.float32),
        radius_sh,
        colatitude_full,
        mesh_spacing,
    )

    coef_list, up_list, down_list, drift_up, drift_down = coef_set
    widths = (
        radius_sh * mesh_spacing[0],
        radius_sh * mesh_spacing[1],
        jnp.sin(colatitude_full)[:, None] * radius_sh * mesh_spacing[2],
    )
    drift = spread_half.astype(jnp.float32) / 3.0 / mesh_spacing[3]
    coefs = jnp.stack(
        list(coef_list) + [wind_vel[n] / widths[n] for n in range(3)] + [drift], axis=0
    )
    scal1 = jnp.reshape(sts_step / 3.0, (1,)).astype(jnp.float32)
    scal2 = jnp.reshape(sts_step / 2.0, (1,)).astype(jnp.float32)
    first_section = section_call(
        scal1, kappa_here, cosmic_ray_density,
        *section_halos(cosmic_ray_density, band_pos, band_count), coefs
    )
    cosmic_ray_next = section_call(
        scal2, kappa_here, first_section,
        *section_halos(first_section, band_pos, band_count), coefs, cosmic_ray_density
    )
    return (fluid_state, cosmic_ray_next)


def solution(mesh):
    placed = (
        P("phi", "band", None),
        P(None, "phi", "band", None),
        P(None, "phi", "band", None),
        P("phi", "band", None),
        P(),
        P("band", "phi", None, None),
        P(),
        P(),
    )
    return jax.shard_map(
        body,
        mesh=mesh,
        in_specs=placed,
        out_specs=(P(None, "phi", "band", None), P("band", "phi", None, None)),
        check_vma=False,
    )
```

```python
import functools
import math

import jax
import jax.numpy as jnp
from jax import lax
from jax.experimental import pallas as pl
from jax.experimental.pallas import tpu as pltpu
from jax.sharding import PartitionSpec as P

ADIABATIC = 5.0 / 3.0
INNER_RADIUS = 0.1
R_RATIO = 30.0
COLAT_LOW = math.pi / 6.0
COLAT_SPAN = 2.0 * math.pi / 3.0
P_RATIO = 1000.0
K_RATIO = 0.1
B_FLOOR = 0.1
V_BOUND = 3.0
B_BOUND = 3.0
P_HIGH = 2.0
RHO_LOW = 0.5
KAPPA_HIGH = 0.5


def padded(value, sides, width):
    for axis, dim in sides:
        size, length = (lax.axis_size(axis), value.shape[dim])
        up = [(i, (i + 1) % size) for i in range(size)]
        down = [(j, i) for i, j in up]
        last = lax.slice_in_dim(value, length - width, length, axis=dim)
        leading = lax.slice_in_dim(value, 0, width, axis=dim)
        before = lax.ppermute(last, axis, up)
        after = lax.ppermute(leading, axis, down)
        value = jnp.concatenate([before, value, after], axis=dim)
    return value


def grid_steps(n_radial, n_colat, n_azim, n_bins):
    return (
        math.log(R_RATIO) / n_radial,
        COLAT_SPAN / n_colat,
        2.0 * math.pi / n_azim,
        math.log(P_RATIO) / n_bins,
    )


def rate_limits(n_radial, n_shells, n_colat, n_azim, n_bins):
    radial_spacing, colatitude_spacing, azimuth_spacing, step_m = grid_steps(
        n_radial, n_colat, n_azim, n_bins
    )
    sine_lower = math.sin(COLAT_LOW + 0.5 * colatitude_spacing)
    fluid_radius = INNER_RADIUS * math.exp(0.5 * radial_spacing)
    fastest_limit = V_BOUND + math.sqrt((ADIABATIC * P_HIGH + 3.0 * B_BOUND**2) / RHO_LOW)
    fluid_rate = fastest_limit * (
        1.0 / (fluid_radius * radial_spacing)
        + 1.0 / (fluid_radius * colatitude_spacing)
        + 1.0 / (fluid_radius * sine_lower * azimuth_spacing)
    )
    shell_low = INNER_RADIUS * math.exp(radial_spacing * (n_radial - n_shells + 0.5))
    inv_r = 1.0 / (shell_low * radial_spacing)
    inv_t = 1.0 / (shell_low * colatitude_spacing)
    inv_p = 1.0 / (shell_low * sine_lower * azimuth_spacing)
    cosmic_ray_rate = (
        2.0 * KAPPA_HIGH * (inv_r**2 + inv_t**2 + inv_p**2)
        + V_BOUND * (inv_r + inv_t + inv_p)
        + V_BOUND * (inv_r + inv_t + inv_p + 4.0 / shell_low) / (3.0 * step_m)
    )
    return (fluid_rate, cosmic_ray_rate)


def shell_radii(start_index, cell_count, n_radial):
    cell_index = jnp.arange(cell_count, dtype=jnp.float32) + (start_index + 0.5)
    return INNER_RADIUS * jnp.exp(math.log(R_RATIO) / n_radial * cell_index)


def colatitudes(start_index, cell_count, n_colat):
    cell_index = jnp.arange(cell_count, dtype=jnp.float32) + 0.5
    return COLAT_LOW + COLAT_SPAN * (cell_index + start_index) / n_colat


def edge_fix(values, along_axis, depth, band_pos, axis_count):
    extent = values.shape[along_axis]
    low_ghost = lax.slice_in_dim(values, 0, depth, axis=along_axis)
    high_ghost = lax.slice_in_dim(values, extent - depth, extent, axis=along_axis)
    first_own = lax.slice_in_dim(values, depth, depth + 1, axis=along_axis)
    last_own = lax.slice_in_dim(values, extent - depth - 1, extent - depth, axis=along_axis)
    low_rim = jnp.where(band_pos == 0, first_own, low_ghost)
    high_rim = jnp.where(band_pos == axis_count - 1, last_own, high_ghost)
    middle = lax.slice_in_dim(values, depth, extent - depth, axis=along_axis)
    return jnp.concatenate([low_rim, middle, high_rim], axis=along_axis)


def conserved(primitive):
    density = primitive[0]
    velocity = primitive[1:4]
    magnetic_vector = primitive[4:7]
    pressure = primitive[7]
    energy = (
        pressure / (ADIABATIC - 1.0)
        + 0.5 * density * jnp.sum(velocity * velocity, axis=0)
        + 0.5 * jnp.sum(magnetic_vector * magnetic_vector, axis=0)
    )
    return jnp.concatenate(
        [density[None], density[None] * velocity, magnetic_vector, energy[None]], axis=0
    )


def face_terms(primitive, cell_state, normal):
    density = primitive[0]
    velocity = primitive[1:4]
    magnetic_vector = primitive[4:7]
    pressure = primitive[7]
    v_normal = velocity[normal]
    b_normal = magnetic_vector[normal]
    magnetic = 0.5 * jnp.sum(magnetic_vector * magnetic_vector, axis=0)
    total_p = pressure + magnetic
    momentum = [density * velocity[k] * v_normal - magnetic_vector[k] * b_normal for k in range(3)]
    momentum[normal] = momentum[normal] + total_p
    induction = [v_normal * magnetic_vector[k] - b_normal * velocity[k] for k in range(3)]
    energy_flux = (cell_state[7] + total_p) * v_normal - b_normal * jnp.sum(
        velocity * magnetic_vector, axis=0
    )
    fluxes = jnp.stack([density * v_normal] + momentum + induction + [energy_flux], axis=0)
    speeds = jnp.abs(v_normal) + jnp.sqrt((ADIABATIC * pressure + 2.0 * magnetic) / density)
    return (fluxes, speeds)


def rusanov(primitive, cell_state, normal, along_axis, spacing):
    fluxes, speeds = face_terms(primitive, cell_state, normal)
    length = speeds.shape[along_axis]
    wave_speed = jnp.maximum(
        lax.slice_in_dim(speeds, 0, length - 1, axis=along_axis),
        lax.slice_in_dim(speeds, 1, length, axis=along_axis),
    )
    flux_low = lax.slice_in_dim(fluxes, 0, length - 1, axis=along_axis + 1)
    flux_high = lax.slice_in_dim(fluxes, 1, length, axis=along_axis + 1)
    state_low = lax.slice_in_dim(cell_state, 0, length - 1, axis=along_axis + 1)
    state_high = lax.slice_in_dim(cell_state, 1, length, axis=along_axis + 1)
    face_flux = 0.5 * (flux_low + flux_high) - 0.5 * wave_speed[None] * (state_high - state_low)
    upper = lax.slice_in_dim(face_flux, 1, length - 1, axis=along_axis + 1)
    lower = lax.slice_in_dim(face_flux, 0, length - 2, axis=along_axis + 1)
    return (upper - lower) / spacing


def fluid_update(padded_array, radius_values, colatitude_mesh, timestep_length, mesh_spacing):
    ghosted = jnp.pad(padded_array, ((0, 0), (0, 0), (0, 0), (1, 1)), mode="edge")
    cell_state = conserved(ghosted)
    width_r = radius_values * mesh_spacing[0]
    width_t = radius_values * mesh_spacing[1]
    width_p = jnp.sin(colatitude_mesh)[:, None] * radius_values * mesh_spacing[2]
    radial = rusanov(ghosted[:, 1:-1, 1:-1, :], cell_state[:, 1:-1, 1:-1, :], 0, 2, width_r)
    polar = rusanov(ghosted[:, 1:-1, :, 1:-1], cell_state[:, 1:-1, :, 1:-1], 1, 1, width_t)
    azimuthal = rusanov(ghosted[:, :, 1:-1, 1:-1], cell_state[:, :, 1:-1, 1:-1], 2, 0, width_p)
    return cell_state[:, 1:-1, 1:-1, 1:-1] - timestep_length * (radial + polar + azimuthal)


def divergence(radial_pad, polar_pad, azim_pad, radius_values, colatitude_mesh, mesh_spacing):
    sin_colat = jnp.sin(colatitude_mesh)[:, None]
    cotangent = (jnp.cos(colatitude_mesh) / jnp.sin(colatitude_mesh))[:, None]
    radial_mid = radial_pad[:, :, 1:-1]
    polar_mid = polar_pad[:, 1:-1, :]
    d_radial = (radial_pad[:, :, 2:] - radial_pad[:, :, :-2]) / (
        2.0 * radius_values * mesh_spacing[0]
    )
    d_polar = (polar_pad[:, 2:, :] - polar_pad[:, :-2, :]) / (2.0 * radius_values * mesh_spacing[1])
    d_azim = (azim_pad[2:] - azim_pad[:-2]) / (2.0 * radius_values * sin_colat * mesh_spacing[2])
    return (
        d_radial
        + 2.0 * radial_mid / radius_values
        + d_polar
        + cotangent * polar_mid / radius_values
        + d_azim
    )


def transport_coefficients(
    wind_vel, mag_wind, spread, radius_values, colatitude_mesh, mesh_spacing
):
    width_r = radius_values * mesh_spacing[0]
    width_t = radius_values * mesh_spacing[1]
    width_p = jnp.sin(colatitude_mesh)[:, None] * radius_values * mesh_spacing[2]
    widths = (width_r, width_t, width_p)
    mag_sq = jnp.sum(mag_wind * mag_wind, axis=0) + B_FLOOR
    b_share = K_RATIO + (1.0 - K_RATIO) * mag_wind * mag_wind / mag_sq
    coef_list = [b_share[k] / (widths[k] * widths[k]) for k in range(3)]
    up_list = [jnp.maximum(wind_vel[k], 0.0) / widths[k] for k in range(3)]
    down_list = [jnp.minimum(wind_vel[k], 0.0) / widths[k] for k in range(3)]
    drift_rate = spread / 3.0
    return (
        coef_list,
        up_list,
        down_list,
        jnp.maximum(drift_rate, 0.0),
        jnp.minimum(drift_rate, 0.0),
    )


def transport_rate(extended, coef_set, kappa_col, step_m):
    coef_list, up_list, down_list, drift_up, drift_down = coef_set
    center = extended[1:-1, 1:-1, 1:-1, 1:-1]
    low_cells = (
        extended[1:-1, 1:-1, 1:-1, :-2],
        extended[1:-1, 1:-1, :-2, 1:-1],
        extended[1:-1, :-2, 1:-1, 1:-1],
    )
    high_cells = (
        extended[1:-1, 1:-1, 1:-1, 2:],
        extended[1:-1, 1:-1, 2:, 1:-1],
        extended[1:-1, 2:, 1:-1, 1:-1],
    )
    curvature = coef_list[0] * (high_cells[0] - 2.0 * center + low_cells[0])
    curvature = curvature + coef_list[1] * (high_cells[1] - 2.0 * center + low_cells[1])
    curvature = curvature + coef_list[2] * (high_cells[2] - 2.0 * center + low_cells[2])
    diffusion = kappa_col[:, None, None, None] * curvature
    advection = up_list[0] * (center - low_cells[0]) + down_list[0] * (high_cells[0] - center)
    advection = (
        advection + up_list[1] * (center - low_cells[1]) + down_list[1] * (high_cells[1] - center)
    )
    advection = (
        advection + up_list[2] * (center - low_cells[2]) + down_list[2] * (high_cells[2] - center)
    )
    bin_low = extended[:-2, 1:-1, 1:-1, 1:-1]
    bin_high = extended[2:, 1:-1, 1:-1, 1:-1]
    momentum = (drift_up * (bin_high - center) + drift_down * (center - bin_low)) / step_m
    return diffusion - advection + momentum


ROWS = 16


def _vec(shape, scalar):
    return jnp.full(shape, scalar, jnp.int32)


def section_kernel(scal_ref, kappa_ref, g_ref, gp_ref, gn_ref, azlo_ref, azhi_ref,
                   binlo_ref, binhi_ref, coef_ref, *rest, second):
    if second:
        f0_ref, out_ref = rest
    else:
        (out_ref,) = rest
    step = pl.program_id(0)
    last_step = pl.num_programs(0) - 1
    bins, _, colat, shells = g_ref.shape
    shape = (ROWS, shells)
    row = lax.broadcasted_iota(jnp.int32, shape, 0)
    lane = lax.broadcasted_iota(jnp.int32, shape, 1)
    first_az = _vec(shape, step) == 0
    last_az = _vec(shape, step) == last_step
    scale = scal_ref[0]

    def per_bin(k, carry):
        kap = kappa_ref[k]
        k_low = jnp.maximum(k - 1, 0)
        k_high = jnp.minimum(k + 1, bins - 1)
        first_bin = _vec(shape, k) == 0
        last_bin = _vec(shape, k) == bins - 1
        for r0 in range(0, colat, ROWS):
            rows = slice(r0, r0 + ROWS)
            center = g_ref[k, 0, rows, :]
            if r0 == 0:
                low_t = jnp.where(row == 0, center, pltpu.roll(center, 1, 0))
            else:
                low_t = g_ref[k, 0, r0 - 1:r0 - 1 + ROWS, :]
            if r0 + ROWS == colat:
                high_t = jnp.where(row == ROWS - 1, center, pltpu.roll(center, ROWS - 1, 0))
            else:
                high_t = g_ref[k, 0, r0 + 1:r0 + 1 + ROWS, :]
            low_r = jnp.where(lane == 0, center, pltpu.roll(center, 1, 1))
            high_r = jnp.where(lane == shells - 1, center, pltpu.roll(center, shells - 1, 1))
            low_p = jnp.where(first_az, azlo_ref[k, 0, rows, :], gp_ref[k, 0, rows, :])
            high_p = jnp.where(last_az, azhi_ref[k, 0, rows, :], gn_ref[k, 0, rows, :])
            low_b = jnp.where(first_bin, binlo_ref[0, 0, rows, :], g_ref[k_low, 0, rows, :])
            high_b = jnp.where(last_bin, binhi_ref[0, 0, rows, :], g_ref[k_high, 0, rows, :])
            twice = 2.0 * center
            curvature = coef_ref[0, 0, rows, :] * (high_r - twice + low_r)
            curvature = curvature + coef_ref[1, 0, rows, :] * (high_t - twice + low_t)
            curvature = curvature + coef_ref[2, 0, rows, :] * (high_p - twice + low_p)
            w_r = coef_ref[3, 0, rows, :]
            w_t = coef_ref[4, 0, rows, :]
            w_p = coef_ref[5, 0, rows, :]
            advection = jnp.maximum(w_r, 0.0) * (center - low_r) + jnp.minimum(w_r, 0.0) * (high_r - center)
            advection = advection + jnp.maximum(w_t, 0.0) * (center - low_t) + jnp.minimum(w_t, 0.0) * (high_t - center)
            advection = advection + jnp.maximum(w_p, 0.0) * (center - low_p) + jnp.minimum(w_p, 0.0) * (high_p - center)
            drift = coef_ref[6, 0, rows, :]
            momentum = jnp.maximum(drift, 0.0) * (high_b - center) + jnp.minimum(drift, 0.0) * (center - low_b)
            rate = kap * curvature - advection + momentum
            if second:
                value = 1.5 * center - 0.5 * f0_ref[k, 0, rows, :] + scale * rate
            else:
                value = center + scale * rate
            out_ref[k, 0, rows, :] = value
        return carry

    lax.fori_loop(0, bins, per_bin, 0)


def section_call(scal, kappa, g, az_low, az_high, bin_low, bin_high, coefs, f0=None, interpret=False):
    bins, azim, colat, shells = g.shape
    block = (bins, 1, colat, shells)
    plane = (1, 1, colat, shells)
    smem = pl.BlockSpec(memory_space=pltpu.SMEM)
    in_specs = [
        smem,
        smem,
        pl.BlockSpec(block, lambda a: (0, a, 0, 0)),
        pl.BlockSpec(block, lambda a: (0, jnp.maximum(a - 1, 0), 0, 0)),
        pl.BlockSpec(block, lambda a: (0, jnp.minimum(a + 1, azim - 1), 0, 0)),
        pl.BlockSpec(block, lambda a: (0, 0, 0, 0)),
        pl.BlockSpec(block, lambda a: (0, 0, 0, 0)),
        pl.BlockSpec(plane, lambda a: (0, a, 0, 0)),
        pl.BlockSpec(plane, lambda a: (0, a, 0, 0)),
        pl.BlockSpec((coefs.shape[0], 1, colat, shells), lambda a: (0, a, 0, 0)),
    ]
    args = [scal, kappa, g, g, g, az_low, az_high, bin_low, bin_high, coefs]
    if f0 is not None:
        in_specs.append(pl.BlockSpec(block, lambda a: (0, a, 0, 0)))
        args.append(f0)
    return pl.pallas_call(
        functools.partial(section_kernel, second=f0 is not None),
        grid=(azim,),
        in_specs=in_specs,
        out_specs=pl.BlockSpec(block, lambda a: (0, a, 0, 0)),
        out_shape=jax.ShapeDtypeStruct(g.shape, jnp.float32),
        compiler_params=pltpu.CompilerParams(dimension_semantics=("arbitrary",)),
        interpret=interpret,
    )(*args)


def cell_state(q):
    rho, v, b, p = q[0], q[1:4], q[4:7], q[7]
    vv = v[0] * v[0] + v[1] * v[1] + v[2] * v[2]
    bb = b[0] * b[0] + b[1] * b[1] + b[2] * b[2]
    energy = p / (ADIABATIC - 1.0) + 0.5 * rho * vv + 0.5 * bb
    return [rho, rho * v[0], rho * v[1], rho * v[2], b[0], b[1], b[2], energy]


def cell_flux(q, u, normal):
    rho, v, b, p = q[0], q[1:4], q[4:7], q[7]
    vn, bn = v[normal], b[normal]
    magnetic = 0.5 * (b[0] * b[0] + b[1] * b[1] + b[2] * b[2])
    total_p = p + magnetic
    momentum = [rho * v[k] * vn - b[k] * bn for k in range(3)]
    momentum[normal] = momentum[normal] + total_p
    induction = [vn * b[k] - bn * v[k] for k in range(3)]
    energy = (u[7] + total_p) * vn - bn * (v[0] * b[0] + v[1] * b[1] + v[2] * b[2])
    speed = jnp.abs(vn) + jnp.sqrt((ADIABATIC * p + 2.0 * magnetic) / rho)
    return [rho * vn] + momentum + induction + [energy], speed


def face_flux(f_low, s_low, u_low, f_high, s_high, u_high):
    wave = jnp.maximum(s_low, s_high)
    return [0.5 * (f_low[c] + f_high[c]) - 0.5 * wave * (u_high[c] - u_low[c]) for c in range(8)]


def mhd_kernel(dt_ref, rho_c, v_c, b_c, p_c, rho_m, v_m, b_m, p_m, rho_p, v_p, b_p, p_p,
               azlo_ref, azhi_ref, clo_ref, chi_ref, wr_ref, wt_ref, wp_ref, out_ref):
    step = pl.program_id(0)
    last_step = pl.num_programs(0) - 1

    def prim(rho_ref, v_ref, b_ref, p_ref):
        return [rho_ref[0], v_ref[0, 0], v_ref[1, 0], v_ref[2, 0],
                b_ref[0, 0], b_ref[1, 0], b_ref[2, 0], p_ref[0]]

    q = prim(rho_c, v_c, b_c, p_c)
    shape = q[0].shape
    nrow, nlane = shape
    row = lax.broadcasted_iota(jnp.int32, shape, 0)
    lane = lax.broadcasted_iota(jnp.int32, shape, 1)
    first_az = _vec(shape, step) == 0
    last_az = _vec(shape, step) == last_step
    q_m = prim(rho_m, v_m, b_m, p_m)
    q_p = prim(rho_p, v_p, b_p, p_p)
    q_m = [jnp.where(first_az, azlo_ref[c, 0], q_m[c]) for c in range(8)]
    q_p = [jnp.where(last_az, azhi_ref[c, 0], q_p[c]) for c in range(8)]
    u = cell_state(q)
    dt = dt_ref[0]

    def lane_next(x):
        return jnp.where(lane == nlane - 1, x, pltpu.roll(x, nlane - 1, 1))

    f, s = cell_flux(q, u, 0)
    high = face_flux(f, s, u, [lane_next(x) for x in f], lane_next(s), [lane_next(x) for x in u])
    low = [jnp.where(lane == 0, f[c], pltpu.roll(high[c], 1, 1)) for c in range(8)]
    width_r = wr_ref[...]
    radial = [(high[c] - low[c]) / width_r for c in range(8)]

    q_l = [clo_ref[c, 0] for c in range(8)]
    q_h = [chi_ref[c, 0] for c in range(8)]
    u_l = cell_state(q_l)
    u_h = cell_state(q_h)
    f, s = cell_flux(q, u, 1)
    f_l, s_l = cell_flux(q_l, u_l, 1)
    f_h, s_h = cell_flux(q_h, u_h, 1)

    def row_next(x, h):
        return jnp.where(row == nrow - 1, jnp.broadcast_to(h, shape), pltpu.roll(x, nrow - 1, 0))

    high = face_flux(f, s, u, [row_next(f[c], f_h[c]) for c in range(8)], row_next(s, s_h),
                     [row_next(u[c], u_h[c]) for c in range(8)])
    first = face_flux(f_l, s_l, u_l, f, s, u)
    low = [jnp.where(row == 0, first[c], pltpu.roll(high[c], 1, 0)) for c in range(8)]
    width_t = wt_ref[...]
    polar = [(high[c] - low[c]) / width_t for c in range(8)]

    u_m = cell_state(q_m)
    u_p = cell_state(q_p)
    f, s = cell_flux(q, u, 2)
    f_m, s_m = cell_flux(q_m, u_m, 2)
    f_p, s_p = cell_flux(q_p, u_p, 2)
    high = face_flux(f, s, u, f_p, s_p, u_p)
    low = face_flux(f_m, s_m, u_m, f, s, u)
    width_p = wp_ref[...]
    for c in range(8):
        azimuthal = (high[c] - low[c]) / width_p
        out_ref[c, 0] = u[c] - dt * (radial[c] + polar[c] + azimuthal)


def mhd_call(dt, density, velocity, magnetic_vector, pressure, az_low, az_high,
             colat_low, colat_high, width_r, width_t, width_p):
    azim, colat, radial = density.shape
    scalar_block = (1, colat, radial)
    vector_block = (3, 1, colat, radial)

    def clamp_low(a):
        return jnp.maximum(a - 1, 0)

    def clamp_high(a):
        return jnp.minimum(a + 1, azim - 1)

    in_specs = [pl.BlockSpec(memory_space=pltpu.SMEM)]
    for pick in (lambda a: a, clamp_low, clamp_high):
        in_specs += [
            pl.BlockSpec(scalar_block, lambda a, pick=pick: (pick(a), 0, 0)),
            pl.BlockSpec(vector_block, lambda a, pick=pick: (0, pick(a), 0, 0)),
            pl.BlockSpec(vector_block, lambda a, pick=pick: (0, pick(a), 0, 0)),
            pl.BlockSpec(scalar_block, lambda a, pick=pick: (pick(a), 0, 0)),
        ]
    in_specs += [
        pl.BlockSpec((8, 1, colat, radial), lambda a: (0, 0, 0, 0)),
        pl.BlockSpec((8, 1, colat, radial), lambda a: (0, 0, 0, 0)),
        pl.BlockSpec((8, 1, 1, radial), lambda a: (0, a, 0, 0)),
        pl.BlockSpec((8, 1, 1, radial), lambda a: (0, a, 0, 0)),
        pl.BlockSpec((1, radial), lambda a: (0, 0)),
        pl.BlockSpec((1, radial), lambda a: (0, 0)),
        pl.BlockSpec((colat, radial), lambda a: (0, 0)),
    ]
    fields = (density, velocity, magnetic_vector, pressure)
    return pl.pallas_call(
        mhd_kernel,
        grid=(azim,),
        in_specs=in_specs,
        out_specs=pl.BlockSpec((8, 1, colat, radial), lambda a: (0, a, 0, 0)),
        out_shape=jax.ShapeDtypeStruct((8, azim, colat, radial), jnp.float32),
        compiler_params=pltpu.CompilerParams(dimension_semantics=("arbitrary",)),
    )(dt, *fields, *fields, *fields, az_low, az_high, colat_low, colat_high,
      width_r, width_t, width_p)


def mhd_halos(density, velocity, magnetic_vector, pressure, band_pos, band_count):
    fields = [density, velocity[0], velocity[1], velocity[2],
              magnetic_vector[0], magnetic_vector[1], magnetic_vector[2], pressure]
    azim, colat = density.shape[0], density.shape[1]
    az_first = jnp.stack([x[0:1] for x in fields])
    az_last = jnp.stack([x[azim - 1:azim] for x in fields])
    c_first = jnp.stack([x[:, 0:1] for x in fields])
    c_last = jnp.stack([x[:, colat - 1:colat] for x in fields])
    phi_size = lax.axis_size("phi")
    up = [(i, (i + 1) % phi_size) for i in range(phi_size)]
    down = [(j, i) for i, j in up]
    az_low = lax.ppermute(az_last, "phi", up)
    az_high = lax.ppermute(az_first, "phi", down)
    up = [(i, (i + 1) % band_count) for i in range(band_count)]
    down = [(j, i) for i, j in up]
    c_low = lax.ppermute(c_last, "band", up)
    c_high = lax.ppermute(c_first, "band", down)
    c_low = jnp.where(band_pos == 0, c_first, c_low)
    c_high = jnp.where(band_pos == band_count - 1, c_last, c_high)
    return az_low, az_high, c_low, c_high


def neighbours(value, axis, dim):
    size = lax.axis_size(axis)
    up = [(i, (i + 1) % size) for i in range(size)]
    down = [(j, i) for i, j in up]
    length = value.shape[dim]
    last = lax.slice_in_dim(value, length - 1, length, axis=dim).astype(jnp.bfloat16)
    leading = lax.slice_in_dim(value, 0, 1, axis=dim).astype(jnp.bfloat16)
    before = lax.ppermute(last, axis, up).astype(value.dtype)
    after = lax.ppermute(leading, axis, down).astype(value.dtype)
    return before, after


def section_halos(values, band_pos, band_count):
    az_low, az_high = neighbours(values, "phi", 1)
    bin_low, bin_high = neighbours(values, "band", 0)
    bins = values.shape[0]
    bin_low = jnp.where(band_pos == 0, values[0:1], bin_low)
    bin_high = jnp.where(band_pos == band_count - 1, values[bins - 1:bins], bin_high)
    return az_low, az_high, bin_low, bin_high


def body(
    density,
    velocity,
    magnetic_vector,
    pressure,
    fluid_courant_number,
    cosmic_ray_density,
    diffusion_per_bin,
    super_step_scale,
):
    azim_dev = density.shape[0]
    colat_dev = density.shape[1]
    radial_cell_count = density.shape[2]
    band_count = lax.axis_size("band")
    phi_count = lax.axis_size("phi")
    colatitude_count = colat_dev * band_count
    azimuth_cell_count = azim_dev * phi_count
    bin_dev = cosmic_ray_density.shape[0]
    momentum_bin_count = bin_dev * band_count
    outer_shell_count = cosmic_ray_density.shape[3]
    band_pos = lax.axis_index("band")
    mesh_spacing = grid_steps(
        radial_cell_count, colatitude_count, azimuth_cell_count, momentum_bin_count
    )
    fluid_rate, cosmic_ray_rate = rate_limits(
        radial_cell_count,
        outer_shell_count,
        colatitude_count,
        azimuth_cell_count,
        momentum_bin_count,
    )
    radius_full = shell_radii(0, radial_cell_count, radial_cell_count)
    colatitude_local = colatitudes(band_pos * colat_dev, colat_dev, colatitude_count)
    dt = jnp.reshape(fluid_courant_number / fluid_rate, (1,)).astype(jnp.float32)
    fluid_state = mhd_call(
        dt, density, velocity, magnetic_vector, pressure,
        *mhd_halos(density, velocity, magnetic_vector, pressure, band_pos, band_count),
        (radius_full * mesh_spacing[0])[None],
        (radius_full * mesh_spacing[1])[None],
        jnp.sin(colatitude_local)[:, None] * radius_full * mesh_spacing[2],
    )
    first_shell = radial_cell_count - outer_shell_count
    radius_sh = shell_radii(first_shell, outer_shell_count, radial_cell_count)
    colatitude_full = colatitudes(0, colatitude_count, colatitude_count)
    own_fields = jnp.concatenate(
        [velocity[:, :, :, first_shell:], magnetic_vector[:, :, :, first_shell:]], axis=0
    ).astype(jnp.bfloat16)
    wind_half = lax.all_gather(own_fields, "band", axis=2, tiled=True)
    wind_vel = wind_half[0:3].astype(jnp.float32)
    azim_pad = padded(wind_half[2], (("phi", 0),), 1).astype(jnp.float32)
    radial_pad = jnp.pad(wind_vel[0], ((0, 0), (0, 0), (1, 1)), mode="edge")
    polar_pad = jnp.pad(wind_vel[1], ((0, 0), (1, 1), (0, 0)), mode="edge")
    spread_half = divergence(
        radial_pad, polar_pad, azim_pad, radius_sh, colatitude_full, mesh_spacing
    ).astype(jnp.bfloat16)
    kappa_here = lax.dynamic_slice_in_dim(diffusion_per_bin, band_pos * bin_dev, bin_dev)
    sts_step = super_step_scale / cosmic_ray_rate
    coef_set = transport_coefficients(
        wind_half[0:3].astype(jnp.float32),
        wind_half[3:6].astype(jnp.float32),
        spread_half.astype(jnp.float32),
        radius_sh,
        colatitude_full,
        mesh_spacing,
    )

    coef_list, up_list, down_list, drift_up, drift_down = coef_set
    widths = (
        radius_sh * mesh_spacing[0],
        radius_sh * mesh_spacing[1],
        jnp.sin(colatitude_full)[:, None] * radius_sh * mesh_spacing[2],
    )
    drift = spread_half.astype(jnp.float32) / 3.0 / mesh_spacing[3]
    coefs = jnp.stack(
        list(coef_list) + [wind_vel[n] / widths[n] for n in range(3)] + [drift], axis=0
    )
    scal1 = jnp.reshape(sts_step / 3.0, (1,)).astype(jnp.float32)
    scal2 = jnp.reshape(sts_step / 2.0, (1,)).astype(jnp.float32)
    first_section = section_call(
        scal1, kappa_here, cosmic_ray_density,
        *section_halos(cosmic_ray_density, band_pos, band_count), coefs
    )
    cosmic_ray_next = section_call(
        scal2, kappa_here, first_section,
        *section_halos(first_section, band_pos, band_count), coefs, cosmic_ray_density
    )
    return (fluid_state, cosmic_ray_next)


def solution(mesh):
    placed = (
        P("phi", "band", None),
        P(None, "phi", "band", None),
        P(None, "phi", "band", None),
        P("phi", "band", None),
        P(),
        P("band", "phi", None, None),
        P(),
        P(),
    )
    return jax.shard_map(
        body,
        mesh=mesh,
        in_specs=placed,
        out_specs=(P(None, "phi", "band", None), P("band", "phi", None, None)),
        check_vma=False,
    )
```

```python
import functools
import math

import jax
import jax.numpy as jnp
from jax import lax
from jax.experimental import pallas as pl
from jax.experimental.pallas import tpu as pltpu
from jax.sharding import PartitionSpec as P

ADIABATIC = 5.0 / 3.0
INNER_RADIUS = 0.1
R_RATIO = 30.0
COLAT_LOW = math.pi / 6.0
COLAT_SPAN = 2.0 * math.pi / 3.0
P_RATIO = 1000.0
K_RATIO = 0.1
B_FLOOR = 0.1
V_BOUND = 3.0
B_BOUND = 3.0
P_HIGH = 2.0
RHO_LOW = 0.5
KAPPA_HIGH = 0.5


def padded(value, sides, width):
    for axis, dim in sides:
        size, length = (lax.axis_size(axis), value.shape[dim])
        up = [(i, (i + 1) % size) for i in range(size)]
        down = [(j, i) for i, j in up]
        last = lax.slice_in_dim(value, length - width, length, axis=dim)
        leading = lax.slice_in_dim(value, 0, width, axis=dim)
        before = lax.ppermute(last, axis, up)
        after = lax.ppermute(leading, axis, down)
        value = jnp.concatenate([before, value, after], axis=dim)
    return value


def grid_steps(n_radial, n_colat, n_azim, n_bins):
    return (
        math.log(R_RATIO) / n_radial,
        COLAT_SPAN / n_colat,
        2.0 * math.pi / n_azim,
        math.log(P_RATIO) / n_bins,
    )


def rate_limits(n_radial, n_shells, n_colat, n_azim, n_bins):
    radial_spacing, colatitude_spacing, azimuth_spacing, step_m = grid_steps(
        n_radial, n_colat, n_azim, n_bins
    )
    sine_lower = math.sin(COLAT_LOW + 0.5 * colatitude_spacing)
    fluid_radius = INNER_RADIUS * math.exp(0.5 * radial_spacing)
    fastest_limit = V_BOUND + math.sqrt((ADIABATIC * P_HIGH + 3.0 * B_BOUND**2) / RHO_LOW)
    fluid_rate = fastest_limit * (
        1.0 / (fluid_radius * radial_spacing)
        + 1.0 / (fluid_radius * colatitude_spacing)
        + 1.0 / (fluid_radius * sine_lower * azimuth_spacing)
    )
    shell_low = INNER_RADIUS * math.exp(radial_spacing * (n_radial - n_shells + 0.5))
    inv_r = 1.0 / (shell_low * radial_spacing)
    inv_t = 1.0 / (shell_low * colatitude_spacing)
    inv_p = 1.0 / (shell_low * sine_lower * azimuth_spacing)
    cosmic_ray_rate = (
        2.0 * KAPPA_HIGH * (inv_r**2 + inv_t**2 + inv_p**2)
        + V_BOUND * (inv_r + inv_t + inv_p)
        + V_BOUND * (inv_r + inv_t + inv_p + 4.0 / shell_low) / (3.0 * step_m)
    )
    return (fluid_rate, cosmic_ray_rate)


def shell_radii(start_index, cell_count, n_radial):
    cell_index = jnp.arange(cell_count, dtype=jnp.float32) + (start_index + 0.5)
    return INNER_RADIUS * jnp.exp(math.log(R_RATIO) / n_radial * cell_index)


def colatitudes(start_index, cell_count, n_colat):
    cell_index = jnp.arange(cell_count, dtype=jnp.float32) + 0.5
    return COLAT_LOW + COLAT_SPAN * (cell_index + start_index) / n_colat


def edge_fix(values, along_axis, depth, band_pos, axis_count):
    extent = values.shape[along_axis]
    low_ghost = lax.slice_in_dim(values, 0, depth, axis=along_axis)
    high_ghost = lax.slice_in_dim(values, extent - depth, extent, axis=along_axis)
    first_own = lax.slice_in_dim(values, depth, depth + 1, axis=along_axis)
    last_own = lax.slice_in_dim(values, extent - depth - 1, extent - depth, axis=along_axis)
    low_rim = jnp.where(band_pos == 0, first_own, low_ghost)
    high_rim = jnp.where(band_pos == axis_count - 1, last_own, high_ghost)
    middle = lax.slice_in_dim(values, depth, extent - depth, axis=along_axis)
    return jnp.concatenate([low_rim, middle, high_rim], axis=along_axis)


def conserved(primitive):
    density = primitive[0]
    velocity = primitive[1:4]
    magnetic_vector = primitive[4:7]
    pressure = primitive[7]
    energy = (
        pressure / (ADIABATIC - 1.0)
        + 0.5 * density * jnp.sum(velocity * velocity, axis=0)
        + 0.5 * jnp.sum(magnetic_vector * magnetic_vector, axis=0)
    )
    return jnp.concatenate(
        [density[None], density[None] * velocity, magnetic_vector, energy[None]], axis=0
    )


def face_terms(primitive, cell_state, normal):
    density = primitive[0]
    velocity = primitive[1:4]
    magnetic_vector = primitive[4:7]
    pressure = primitive[7]
    v_normal = velocity[normal]
    b_normal = magnetic_vector[normal]
    magnetic = 0.5 * jnp.sum(magnetic_vector * magnetic_vector, axis=0)
    total_p = pressure + magnetic
    momentum = [density * velocity[k] * v_normal - magnetic_vector[k] * b_normal for k in range(3)]
    momentum[normal] = momentum[normal] + total_p
    induction = [v_normal * magnetic_vector[k] - b_normal * velocity[k] for k in range(3)]
    energy_flux = (cell_state[7] + total_p) * v_normal - b_normal * jnp.sum(
        velocity * magnetic_vector, axis=0
    )
    fluxes = jnp.stack([density * v_normal] + momentum + induction + [energy_flux], axis=0)
    speeds = jnp.abs(v_normal) + jnp.sqrt((ADIABATIC * pressure + 2.0 * magnetic) / density)
    return (fluxes, speeds)


def rusanov(primitive, cell_state, normal, along_axis, spacing):
    fluxes, speeds = face_terms(primitive, cell_state, normal)
    length = speeds.shape[along_axis]
    wave_speed = jnp.maximum(
        lax.slice_in_dim(speeds, 0, length - 1, axis=along_axis),
        lax.slice_in_dim(speeds, 1, length, axis=along_axis),
    )
    flux_low = lax.slice_in_dim(fluxes, 0, length - 1, axis=along_axis + 1)
    flux_high = lax.slice_in_dim(fluxes, 1, length, axis=along_axis + 1)
    state_low = lax.slice_in_dim(cell_state, 0, length - 1, axis=along_axis + 1)
    state_high = lax.slice_in_dim(cell_state, 1, length, axis=along_axis + 1)
    face_flux = 0.5 * (flux_low + flux_high) - 0.5 * wave_speed[None] * (state_high - state_low)
    upper = lax.slice_in_dim(face_flux, 1, length - 1, axis=along_axis + 1)
    lower = lax.slice_in_dim(face_flux, 0, length - 2, axis=along_axis + 1)
    return (upper - lower) / spacing


def fluid_update(padded_array, radius_values, colatitude_mesh, timestep_length, mesh_spacing):
    ghosted = jnp.pad(padded_array, ((0, 0), (0, 0), (0, 0), (1, 1)), mode="edge")
    cell_state = conserved(ghosted)
    width_r = radius_values * mesh_spacing[0]
    width_t = radius_values * mesh_spacing[1]
    width_p = jnp.sin(colatitude_mesh)[:, None] * radius_values * mesh_spacing[2]
    radial = rusanov(ghosted[:, 1:-1, 1:-1, :], cell_state[:, 1:-1, 1:-1, :], 0, 2, width_r)
    polar = rusanov(ghosted[:, 1:-1, :, 1:-1], cell_state[:, 1:-1, :, 1:-1], 1, 1, width_t)
    azimuthal = rusanov(ghosted[:, :, 1:-1, 1:-1], cell_state[:, :, 1:-1, 1:-1], 2, 0, width_p)
    return cell_state[:, 1:-1, 1:-1, 1:-1] - timestep_length * (radial + polar + azimuthal)


def divergence(radial_pad, polar_pad, azim_pad, radius_values, colatitude_mesh, mesh_spacing):
    sin_colat = jnp.sin(colatitude_mesh)[:, None]
    cotangent = (jnp.cos(colatitude_mesh) / jnp.sin(colatitude_mesh))[:, None]
    radial_mid = radial_pad[:, :, 1:-1]
    polar_mid = polar_pad[:, 1:-1, :]
    d_radial = (radial_pad[:, :, 2:] - radial_pad[:, :, :-2]) / (
        2.0 * radius_values * mesh_spacing[0]
    )
    d_polar = (polar_pad[:, 2:, :] - polar_pad[:, :-2, :]) / (2.0 * radius_values * mesh_spacing[1])
    d_azim = (azim_pad[2:] - azim_pad[:-2]) / (2.0 * radius_values * sin_colat * mesh_spacing[2])
    return (
        d_radial
        + 2.0 * radial_mid / radius_values
        + d_polar
        + cotangent * polar_mid / radius_values
        + d_azim
    )


def transport_coefficients(
    wind_vel, mag_wind, spread, radius_values, colatitude_mesh, mesh_spacing
):
    width_r = radius_values * mesh_spacing[0]
    width_t = radius_values * mesh_spacing[1]
    width_p = jnp.sin(colatitude_mesh)[:, None] * radius_values * mesh_spacing[2]
    widths = (width_r, width_t, width_p)
    mag_sq = jnp.sum(mag_wind * mag_wind, axis=0) + B_FLOOR
    b_share = K_RATIO + (1.0 - K_RATIO) * mag_wind * mag_wind / mag_sq
    coef_list = [b_share[k] / (widths[k] * widths[k]) for k in range(3)]
    up_list = [jnp.maximum(wind_vel[k], 0.0) / widths[k] for k in range(3)]
    down_list = [jnp.minimum(wind_vel[k], 0.0) / widths[k] for k in range(3)]
    drift_rate = spread / 3.0
    return (
        coef_list,
        up_list,
        down_list,
        jnp.maximum(drift_rate, 0.0),
        jnp.minimum(drift_rate, 0.0),
    )


def transport_rate(extended, coef_set, kappa_col, step_m):
    coef_list, up_list, down_list, drift_up, drift_down = coef_set
    center = extended[1:-1, 1:-1, 1:-1, 1:-1]
    low_cells = (
        extended[1:-1, 1:-1, 1:-1, :-2],
        extended[1:-1, 1:-1, :-2, 1:-1],
        extended[1:-1, :-2, 1:-1, 1:-1],
    )
    high_cells = (
        extended[1:-1, 1:-1, 1:-1, 2:],
        extended[1:-1, 1:-1, 2:, 1:-1],
        extended[1:-1, 2:, 1:-1, 1:-1],
    )
    curvature = coef_list[0] * (high_cells[0] - 2.0 * center + low_cells[0])
    curvature = curvature + coef_list[1] * (high_cells[1] - 2.0 * center + low_cells[1])
    curvature = curvature + coef_list[2] * (high_cells[2] - 2.0 * center + low_cells[2])
    diffusion = kappa_col[:, None, None, None] * curvature
    advection = up_list[0] * (center - low_cells[0]) + down_list[0] * (high_cells[0] - center)
    advection = (
        advection + up_list[1] * (center - low_cells[1]) + down_list[1] * (high_cells[1] - center)
    )
    advection = (
        advection + up_list[2] * (center - low_cells[2]) + down_list[2] * (high_cells[2] - center)
    )
    bin_low = extended[:-2, 1:-1, 1:-1, 1:-1]
    bin_high = extended[2:, 1:-1, 1:-1, 1:-1]
    momentum = (drift_up * (bin_high - center) + drift_down * (center - bin_low)) / step_m
    return diffusion - advection + momentum


ROWS = 16


def _vec(shape, scalar):
    return jnp.full(shape, scalar, jnp.int32)


def section_kernel(scal_ref, flag_ref, kappa_ref, g_ref, gp_ref, gn_ref, azlo_ref, azhi_ref,
                   binlo_ref, binhi_ref, coef_ref, *rest, second):
    if second:
        f0_ref, out_ref = rest
    else:
        out_ref, az_first_ref, az_last_ref, bin_first_ref, bin_last_ref = rest
    step = pl.program_id(0)
    last_step = pl.num_programs(0) - 1
    bins, planes, colat, shells = g_ref.shape
    shape = (ROWS, shells)
    row = lax.broadcasted_iota(jnp.int32, shape, 0)
    lane = lax.broadcasted_iota(jnp.int32, shape, 1)
    first_az = _vec(shape, step) == 0
    last_az = _vec(shape, step) == last_step
    band_first = _vec(shape, flag_ref[0]) == 1
    band_last = _vec(shape, flag_ref[1]) == 1
    scale = scal_ref[0]

    def chunk(k, i, r0, kap, edge):
        rows = slice(r0, r0 + ROWS)
        center = g_ref[k, i, rows, :]
        if r0 == 0:
            low_t = jnp.where(row == 0, center, pltpu.roll(center, 1, 0))
        else:
            low_t = g_ref[k, i, r0 - 1:r0 - 1 + ROWS, :]
        if r0 + ROWS == colat:
            high_t = jnp.where(row == ROWS - 1, center, pltpu.roll(center, ROWS - 1, 0))
        else:
            high_t = g_ref[k, i, r0 + 1:r0 + 1 + ROWS, :]
        low_r = jnp.where(lane == 0, center, pltpu.roll(center, 1, 1))
        high_r = jnp.where(lane == shells - 1, center, pltpu.roll(center, shells - 1, 1))
        if i == 0:
            low_p = jnp.where(first_az, azlo_ref[k, 0, rows, :].astype(jnp.float32), gp_ref[k, 0, rows, :])
        else:
            low_p = g_ref[k, i - 1, rows, :]
        if i == planes - 1:
            high_p = jnp.where(last_az, azhi_ref[k, 0, rows, :].astype(jnp.float32), gn_ref[k, 0, rows, :])
        else:
            high_p = g_ref[k, i + 1, rows, :]
        if edge == "low":
            low_b = jnp.where(band_first, center, binlo_ref[0, i, rows, :].astype(jnp.float32))
        else:
            low_b = g_ref[k - 1, i, rows, :]
        if edge == "high":
            high_b = jnp.where(band_last, center, binhi_ref[0, i, rows, :].astype(jnp.float32))
        else:
            high_b = g_ref[k + 1, i, rows, :]
        d_lo = (center - low_r, center - low_t, center - low_p)
        d_hi = (high_r - center, high_t - center, high_p - center)
        curvature = coef_ref[0, i, rows, :] * (d_hi[0] - d_lo[0])
        curvature = curvature + coef_ref[1, i, rows, :] * (d_hi[1] - d_lo[1])
        curvature = curvature + coef_ref[2, i, rows, :] * (d_hi[2] - d_lo[2])
        advection = coef_ref[3, i, rows, :] * d_lo[0] + coef_ref[6, i, rows, :] * d_hi[0]
        advection = advection + coef_ref[4, i, rows, :] * d_lo[1] + coef_ref[7, i, rows, :] * d_hi[1]
        advection = advection + coef_ref[5, i, rows, :] * d_lo[2] + coef_ref[8, i, rows, :] * d_hi[2]
        momentum = coef_ref[9, i, rows, :] * (high_b - center) + coef_ref[10, i, rows, :] * (center - low_b)
        rate = kap * curvature - advection + momentum
        if second:
            value = 1.5 * center - 0.5 * f0_ref[k, i, rows, :] + scale * rate
        else:
            value = center + scale * rate
        out_ref[k, i, rows, :] = value
        if not second:
            half = value.astype(jnp.bfloat16)
            if i == 0:
                @pl.when(step == 0)
                def _():
                    az_first_ref[k, 0, rows, :] = half
            if i == planes - 1:
                @pl.when(step == last_step)
                def _():
                    az_last_ref[k, 0, rows, :] = half
            if edge == "low":
                bin_first_ref[0, i, rows, :] = half
            if edge == "high":
                bin_last_ref[0, i, rows, :] = half

    def all_rows(k, edge):
        kap = kappa_ref[k]
        for i in range(planes):
            for r0 in range(0, colat, ROWS):
                chunk(k, i, r0, kap, edge)

    all_rows(0, "low")

    def middle(k, carry):
        all_rows(k, None)
        return carry

    lax.fori_loop(1, bins - 1, middle, 0)
    all_rows(bins - 1, "high")


PLANES = 2


def section_call(scal, flags, kappa, g, az_low, az_high, bin_low, bin_high, coefs, f0=None):
    bins, azim, colat, shells = g.shape
    block = (bins, PLANES, colat, shells)
    plane = (bins, 1, colat, shells)
    bin_block = (1, PLANES, colat, shells)
    smem = pl.BlockSpec(memory_space=pltpu.SMEM)
    in_specs = [
        smem,
        smem,
        smem,
        pl.BlockSpec(block, lambda a: (0, a, 0, 0)),
        pl.BlockSpec(plane, lambda a: (0, jnp.maximum(a * PLANES - 1, 0), 0, 0)),
        pl.BlockSpec(plane, lambda a: (0, jnp.minimum(a * PLANES + PLANES, azim - 1), 0, 0)),
        pl.BlockSpec(plane, lambda a: (0, 0, 0, 0)),
        pl.BlockSpec(plane, lambda a: (0, 0, 0, 0)),
        pl.BlockSpec(bin_block, lambda a: (0, a, 0, 0)),
        pl.BlockSpec(bin_block, lambda a: (0, a, 0, 0)),
        pl.BlockSpec((coefs.shape[0], PLANES, colat, shells), lambda a: (0, a, 0, 0)),
    ]
    args = [scal, flags, kappa, g, g, g, az_low, az_high, bin_low, bin_high, coefs]
    out_specs = pl.BlockSpec(block, lambda a: (0, a, 0, 0))
    out_shape = jax.ShapeDtypeStruct(g.shape, jnp.float32)
    if f0 is not None:
        in_specs.append(pl.BlockSpec(block, lambda a: (0, a, 0, 0)))
        args.append(f0)
    else:
        out_specs = [
            out_specs,
            pl.BlockSpec(plane, lambda a: (0, 0, 0, 0)),
            pl.BlockSpec(plane, lambda a: (0, 0, 0, 0)),
            pl.BlockSpec(bin_block, lambda a: (0, a, 0, 0)),
            pl.BlockSpec(bin_block, lambda a: (0, a, 0, 0)),
        ]
        half_plane = jax.ShapeDtypeStruct((bins, 1, colat, shells), jnp.bfloat16)
        half_bin = jax.ShapeDtypeStruct((1, azim, colat, shells), jnp.bfloat16)
        out_shape = [out_shape, half_plane, half_plane, half_bin, half_bin]
    return pl.pallas_call(
        functools.partial(section_kernel, second=f0 is not None),
        grid=(azim // PLANES,),
        in_specs=in_specs,
        out_specs=out_specs,
        out_shape=out_shape,
        compiler_params=pltpu.CompilerParams(dimension_semantics=("arbitrary",)),
    )(*args)


def exchange(first, last, axis):
    size = lax.axis_size(axis)
    up = [(i, (i + 1) % size) for i in range(size)]
    down = [(j, i) for i, j in up]
    return lax.ppermute(last, axis, up), lax.ppermute(first, axis, down)


def cell_state(q):
    rho, v, b, p = q[0], q[1:4], q[4:7], q[7]
    vv = v[0] * v[0] + v[1] * v[1] + v[2] * v[2]
    bb = b[0] * b[0] + b[1] * b[1] + b[2] * b[2]
    energy = p / (ADIABATIC - 1.0) + 0.5 * rho * vv + 0.5 * bb
    return [rho, rho * v[0], rho * v[1], rho * v[2], b[0], b[1], b[2], energy]


def cell_flux(q, u, normal):
    rho, v, b, p = q[0], q[1:4], q[4:7], q[7]
    vn, bn = v[normal], b[normal]
    magnetic = 0.5 * (b[0] * b[0] + b[1] * b[1] + b[2] * b[2])
    total_p = p + magnetic
    momentum = [rho * v[k] * vn - b[k] * bn for k in range(3)]
    momentum[normal] = momentum[normal] + total_p
    induction = [vn * b[k] - bn * v[k] for k in range(3)]
    energy = (u[7] + total_p) * vn - bn * (v[0] * b[0] + v[1] * b[1] + v[2] * b[2])
    speed = jnp.abs(vn) + jnp.sqrt((ADIABATIC * p + 2.0 * magnetic) / rho)
    return [rho * vn] + momentum + induction + [energy], speed


def face_flux(f_low, s_low, u_low, f_high, s_high, u_high):
    wave = jnp.maximum(s_low, s_high)
    return [0.5 * (f_low[c] + f_high[c]) - 0.5 * wave * (u_high[c] - u_low[c]) for c in range(8)]


def mhd_kernel(dt_ref, rho_c, v_c, b_c, p_c, rho_m, v_m, b_m, p_m, rho_p, v_p, b_p, p_p,
               azlo_ref, azhi_ref, clo_ref, chi_ref, wr_ref, wt_ref, wp_ref, out_ref):
    step = pl.program_id(0)
    last_step = pl.num_programs(0) - 1

    def prim(rho_ref, v_ref, b_ref, p_ref):
        return [rho_ref[0], v_ref[0, 0], v_ref[1, 0], v_ref[2, 0],
                b_ref[0, 0], b_ref[1, 0], b_ref[2, 0], p_ref[0]]

    q = prim(rho_c, v_c, b_c, p_c)
    shape = q[0].shape
    nrow, nlane = shape
    row = lax.broadcasted_iota(jnp.int32, shape, 0)
    lane = lax.broadcasted_iota(jnp.int32, shape, 1)
    first_az = _vec(shape, step) == 0
    last_az = _vec(shape, step) == last_step
    q_m = prim(rho_m, v_m, b_m, p_m)
    q_p = prim(rho_p, v_p, b_p, p_p)
    q_m = [jnp.where(first_az, azlo_ref[c, 0], q_m[c]) for c in range(8)]
    q_p = [jnp.where(last_az, azhi_ref[c, 0], q_p[c]) for c in range(8)]
    u = cell_state(q)
    dt = dt_ref[0]

    def lane_next(x):
        return jnp.where(lane == nlane - 1, x, pltpu.roll(x, nlane - 1, 1))

    f, s = cell_flux(q, u, 0)
    high = face_flux(f, s, u, [lane_next(x) for x in f], lane_next(s), [lane_next(x) for x in u])
    low = [jnp.where(lane == 0, f[c], pltpu.roll(high[c], 1, 1)) for c in range(8)]
    width_r = wr_ref[...]
    radial = [(high[c] - low[c]) / width_r for c in range(8)]

    q_l = [clo_ref[c, 0] for c in range(8)]
    q_h = [chi_ref[c, 0] for c in range(8)]
    u_l = cell_state(q_l)
    u_h = cell_state(q_h)
    f, s = cell_flux(q, u, 1)
    f_l, s_l = cell_flux(q_l, u_l, 1)
    f_h, s_h = cell_flux(q_h, u_h, 1)

    def row_next(x, h):
        return jnp.where(row == nrow - 1, jnp.broadcast_to(h, shape), pltpu.roll(x, nrow - 1, 0))

    high = face_flux(f, s, u, [row_next(f[c], f_h[c]) for c in range(8)], row_next(s, s_h),
                     [row_next(u[c], u_h[c]) for c in range(8)])
    first = face_flux(f_l, s_l, u_l, f, s, u)
    low = [jnp.where(row == 0, first[c], pltpu.roll(high[c], 1, 0)) for c in range(8)]
    width_t = wt_ref[...]
    polar = [(high[c] - low[c]) / width_t for c in range(8)]

    u_m = cell_state(q_m)
    u_p = cell_state(q_p)
    f, s = cell_flux(q, u, 2)
    f_m, s_m = cell_flux(q_m, u_m, 2)
    f_p, s_p = cell_flux(q_p, u_p, 2)
    high = face_flux(f, s, u, f_p, s_p, u_p)
    low = face_flux(f_m, s_m, u_m, f, s, u)
    width_p = wp_ref[...]
    for c in range(8):
        azimuthal = (high[c] - low[c]) / width_p
        out_ref[c, 0] = u[c] - dt * (radial[c] + polar[c] + azimuthal)


def mhd_call(dt, density, velocity, magnetic_vector, pressure, az_low, az_high,
             colat_low, colat_high, width_r, width_t, width_p):
    azim, colat, radial = density.shape
    scalar_block = (1, colat, radial)
    vector_block = (3, 1, colat, radial)

    def clamp_low(a):
        return jnp.maximum(a - 1, 0)

    def clamp_high(a):
        return jnp.minimum(a + 1, azim - 1)

    in_specs = [pl.BlockSpec(memory_space=pltpu.SMEM)]
    for pick in (lambda a: a, clamp_low, clamp_high):
        in_specs += [
            pl.BlockSpec(scalar_block, lambda a, pick=pick: (pick(a), 0, 0)),
            pl.BlockSpec(vector_block, lambda a, pick=pick: (0, pick(a), 0, 0)),
            pl.BlockSpec(vector_block, lambda a, pick=pick: (0, pick(a), 0, 0)),
            pl.BlockSpec(scalar_block, lambda a, pick=pick: (pick(a), 0, 0)),
        ]
    in_specs += [
        pl.BlockSpec((8, 1, colat, radial), lambda a: (0, 0, 0, 0)),
        pl.BlockSpec((8, 1, colat, radial), lambda a: (0, 0, 0, 0)),
        pl.BlockSpec((8, 1, 1, radial), lambda a: (0, a, 0, 0)),
        pl.BlockSpec((8, 1, 1, radial), lambda a: (0, a, 0, 0)),
        pl.BlockSpec((1, radial), lambda a: (0, 0)),
        pl.BlockSpec((1, radial), lambda a: (0, 0)),
        pl.BlockSpec((colat, radial), lambda a: (0, 0)),
    ]
    fields = (density, velocity, magnetic_vector, pressure)
    return pl.pallas_call(
        mhd_kernel,
        grid=(azim,),
        in_specs=in_specs,
        out_specs=pl.BlockSpec((8, 1, colat, radial), lambda a: (0, a, 0, 0)),
        out_shape=jax.ShapeDtypeStruct((8, azim, colat, radial), jnp.float32),
        compiler_params=pltpu.CompilerParams(dimension_semantics=("arbitrary",)),
    )(dt, *fields, *fields, *fields, az_low, az_high, colat_low, colat_high,
      width_r, width_t, width_p)


def mhd_halos(density, velocity, magnetic_vector, pressure, band_pos, band_count):
    fields = [density, velocity[0], velocity[1], velocity[2],
              magnetic_vector[0], magnetic_vector[1], magnetic_vector[2], pressure]
    azim, colat = density.shape[0], density.shape[1]
    az_first = jnp.stack([x[0:1] for x in fields])
    az_last = jnp.stack([x[azim - 1:azim] for x in fields])
    c_first = jnp.stack([x[:, 0:1] for x in fields])
    c_last = jnp.stack([x[:, colat - 1:colat] for x in fields])
    phi_size = lax.axis_size("phi")
    up = [(i, (i + 1) % phi_size) for i in range(phi_size)]
    down = [(j, i) for i, j in up]
    az_low = lax.ppermute(az_last, "phi", up)
    az_high = lax.ppermute(az_first, "phi", down)
    up = [(i, (i + 1) % band_count) for i in range(band_count)]
    down = [(j, i) for i, j in up]
    c_low = lax.ppermute(c_last, "band", up)
    c_high = lax.ppermute(c_first, "band", down)
    c_low = jnp.where(band_pos == 0, c_first, c_low)
    c_high = jnp.where(band_pos == band_count - 1, c_last, c_high)
    return az_low, az_high, c_low, c_high


def body(
    density,
    velocity,
    magnetic_vector,
    pressure,
    fluid_courant_number,
    cosmic_ray_density,
    diffusion_per_bin,
    super_step_scale,
):
    azim_dev = density.shape[0]
    colat_dev = density.shape[1]
    radial_cell_count = density.shape[2]
    band_count = lax.axis_size("band")
    phi_count = lax.axis_size("phi")
    colatitude_count = colat_dev * band_count
    azimuth_cell_count = azim_dev * phi_count
    bin_dev = cosmic_ray_density.shape[0]
    momentum_bin_count = bin_dev * band_count
    outer_shell_count = cosmic_ray_density.shape[3]
    band_pos = lax.axis_index("band")
    mesh_spacing = grid_steps(
        radial_cell_count, colatitude_count, azimuth_cell_count, momentum_bin_count
    )
    fluid_rate, cosmic_ray_rate = rate_limits(
        radial_cell_count,
        outer_shell_count,
        colatitude_count,
        azimuth_cell_count,
        momentum_bin_count,
    )
    radius_full = shell_radii(0, radial_cell_count, radial_cell_count)
    colatitude_local = colatitudes(band_pos * colat_dev, colat_dev, colatitude_count)
    dt = jnp.reshape(fluid_courant_number / fluid_rate, (1,)).astype(jnp.float32)
    fluid_state = mhd_call(
        dt, density, velocity, magnetic_vector, pressure,
        *mhd_halos(density, velocity, magnetic_vector, pressure, band_pos, band_count),
        (radius_full * mesh_spacing[0])[None],
        (radius_full * mesh_spacing[1])[None],
        jnp.sin(colatitude_local)[:, None] * radius_full * mesh_spacing[2],
    )
    first_shell = radial_cell_count - outer_shell_count
    radius_sh = shell_radii(first_shell, outer_shell_count, radial_cell_count)
    colatitude_full = colatitudes(0, colatitude_count, colatitude_count)
    own_fields = jnp.concatenate(
        [velocity[:, :, :, first_shell:], magnetic_vector[:, :, :, first_shell:]], axis=0
    ).astype(jnp.bfloat16)
    wind_half = lax.all_gather(own_fields, "band", axis=2, tiled=True)
    fluid_state, wind_half = lax.optimization_barrier((fluid_state, wind_half))
    wind_vel = wind_half[0:3].astype(jnp.float32)
    azim_pad = padded(wind_half[2], (("phi", 0),), 1).astype(jnp.float32)
    radial_pad = jnp.pad(wind_vel[0], ((0, 0), (0, 0), (1, 1)), mode="edge")
    polar_pad = jnp.pad(wind_vel[1], ((0, 0), (1, 1), (0, 0)), mode="edge")
    spread_half = divergence(
        radial_pad, polar_pad, azim_pad, radius_sh, colatitude_full, mesh_spacing
    ).astype(jnp.bfloat16)
    kappa_here = lax.dynamic_slice_in_dim(diffusion_per_bin, band_pos * bin_dev, bin_dev)
    sts_step = super_step_scale / cosmic_ray_rate
    coef_set = transport_coefficients(
        wind_half[0:3].astype(jnp.float32),
        wind_half[3:6].astype(jnp.float32),
        spread_half.astype(jnp.float32),
        radius_sh,
        colatitude_full,
        mesh_spacing,
    )

    coef_list, up_list, down_list, drift_up, drift_down = coef_set
    coefs = jnp.stack(
        list(coef_list) + list(up_list) + list(down_list)
        + [drift_up / mesh_spacing[3], drift_down / mesh_spacing[3]],
        axis=0,
    )
    scal1 = jnp.reshape(sts_step / 3.0, (1,)).astype(jnp.float32)
    scal2 = jnp.reshape(sts_step / 2.0, (1,)).astype(jnp.float32)
    flags = jnp.stack([band_pos == 0, band_pos == band_count - 1]).astype(jnp.int32)
    bins = cosmic_ray_density.shape[0]
    edges = (
        cosmic_ray_density[:, 0:1],
        cosmic_ray_density[:, azim_dev - 1:azim_dev],
        cosmic_ray_density[0:1],
        cosmic_ray_density[bins - 1:bins],
    )
    edges = [x.astype(jnp.bfloat16) for x in lax.optimization_barrier(edges)]
    az_low, az_high = exchange(edges[0], edges[1], "phi")
    bin_low, bin_high = exchange(edges[2], edges[3], "band")
    first_section, *edges = section_call(
        scal1, flags, kappa_here, cosmic_ray_density, az_low, az_high, bin_low, bin_high, coefs
    )
    az_low, az_high = exchange(edges[0], edges[1], "phi")
    bin_low, bin_high = exchange(edges[2], edges[3], "band")
    cosmic_ray_next = section_call(
        scal2, flags, kappa_here, first_section, az_low, az_high, bin_low, bin_high, coefs,
        cosmic_ray_density,
    )
    return (fluid_state, cosmic_ray_next)


def solution(mesh):
    placed = (
        P("phi", "band", None),
        P(None, "phi", "band", None),
        P(None, "phi", "band", None),
        P("phi", "band", None),
        P(),
        P("band", "phi", None, None),
        P(),
        P(),
    )
    return jax.shard_map(
        body,
        mesh=mesh,
        in_specs=placed,
        out_specs=(P(None, "phi", "band", None), P("band", "phi", None, None)),
        check_vma=False,
    )
```

```python
import functools
import math

import jax
import jax.numpy as jnp
from jax import lax
from jax.experimental import pallas as pl
from jax.experimental.pallas import tpu as pltpu
from jax.sharding import PartitionSpec as P

ADIABATIC = 5.0 / 3.0
INNER_RADIUS = 0.1
R_RATIO = 30.0
COLAT_LOW = math.pi / 6.0
COLAT_SPAN = 2.0 * math.pi / 3.0
P_RATIO = 1000.0
K_RATIO = 0.1
B_FLOOR = 0.1
V_BOUND = 3.0
B_BOUND = 3.0
P_HIGH = 2.0
RHO_LOW = 0.5
KAPPA_HIGH = 0.5


def padded(value, sides, width):
    for axis, dim in sides:
        size, length = (lax.axis_size(axis), value.shape[dim])
        up = [(i, (i + 1) % size) for i in range(size)]
        down = [(j, i) for i, j in up]
        last = lax.slice_in_dim(value, length - width, length, axis=dim)
        leading = lax.slice_in_dim(value, 0, width, axis=dim)
        before = lax.ppermute(last, axis, up)
        after = lax.ppermute(leading, axis, down)
        value = jnp.concatenate([before, value, after], axis=dim)
    return value


def grid_steps(n_radial, n_colat, n_azim, n_bins):
    return (
        math.log(R_RATIO) / n_radial,
        COLAT_SPAN / n_colat,
        2.0 * math.pi / n_azim,
        math.log(P_RATIO) / n_bins,
    )


def rate_limits(n_radial, n_shells, n_colat, n_azim, n_bins):
    radial_spacing, colatitude_spacing, azimuth_spacing, step_m = grid_steps(
        n_radial, n_colat, n_azim, n_bins
    )
    sine_lower = math.sin(COLAT_LOW + 0.5 * colatitude_spacing)
    fluid_radius = INNER_RADIUS * math.exp(0.5 * radial_spacing)
    fastest_limit = V_BOUND + math.sqrt((ADIABATIC * P_HIGH + 3.0 * B_BOUND**2) / RHO_LOW)
    fluid_rate = fastest_limit * (
        1.0 / (fluid_radius * radial_spacing)
        + 1.0 / (fluid_radius * colatitude_spacing)
        + 1.0 / (fluid_radius * sine_lower * azimuth_spacing)
    )
    shell_low = INNER_RADIUS * math.exp(radial_spacing * (n_radial - n_shells + 0.5))
    inv_r = 1.0 / (shell_low * radial_spacing)
    inv_t = 1.0 / (shell_low * colatitude_spacing)
    inv_p = 1.0 / (shell_low * sine_lower * azimuth_spacing)
    cosmic_ray_rate = (
        2.0 * KAPPA_HIGH * (inv_r**2 + inv_t**2 + inv_p**2)
        + V_BOUND * (inv_r + inv_t + inv_p)
        + V_BOUND * (inv_r + inv_t + inv_p + 4.0 / shell_low) / (3.0 * step_m)
    )
    return (fluid_rate, cosmic_ray_rate)


def shell_radii(start_index, cell_count, n_radial):
    cell_index = jnp.arange(cell_count, dtype=jnp.float32) + (start_index + 0.5)
    return INNER_RADIUS * jnp.exp(math.log(R_RATIO) / n_radial * cell_index)


def colatitudes(start_index, cell_count, n_colat):
    cell_index = jnp.arange(cell_count, dtype=jnp.float32) + 0.5
    return COLAT_LOW + COLAT_SPAN * (cell_index + start_index) / n_colat


def edge_fix(values, along_axis, depth, band_pos, axis_count):
    extent = values.shape[along_axis]
    low_ghost = lax.slice_in_dim(values, 0, depth, axis=along_axis)
    high_ghost = lax.slice_in_dim(values, extent - depth, extent, axis=along_axis)
    first_own = lax.slice_in_dim(values, depth, depth + 1, axis=along_axis)
    last_own = lax.slice_in_dim(values, extent - depth - 1, extent - depth, axis=along_axis)
    low_rim = jnp.where(band_pos == 0, first_own, low_ghost)
    high_rim = jnp.where(band_pos == axis_count - 1, last_own, high_ghost)
    middle = lax.slice_in_dim(values, depth, extent - depth, axis=along_axis)
    return jnp.concatenate([low_rim, middle, high_rim], axis=along_axis)


def conserved(primitive):
    density = primitive[0]
    velocity = primitive[1:4]
    magnetic_vector = primitive[4:7]
    pressure = primitive[7]
    energy = (
        pressure / (ADIABATIC - 1.0)
        + 0.5 * density * jnp.sum(velocity * velocity, axis=0)
        + 0.5 * jnp.sum(magnetic_vector * magnetic_vector, axis=0)
    )
    return jnp.concatenate(
        [density[None], density[None] * velocity, magnetic_vector, energy[None]], axis=0
    )


def face_terms(primitive, cell_state, normal):
    density = primitive[0]
    velocity = primitive[1:4]
    magnetic_vector = primitive[4:7]
    pressure = primitive[7]
    v_normal = velocity[normal]
    b_normal = magnetic_vector[normal]
    magnetic = 0.5 * jnp.sum(magnetic_vector * magnetic_vector, axis=0)
    total_p = pressure + magnetic
    momentum = [density * velocity[k] * v_normal - magnetic_vector[k] * b_normal for k in range(3)]
    momentum[normal] = momentum[normal] + total_p
    induction = [v_normal * magnetic_vector[k] - b_normal * velocity[k] for k in range(3)]
    energy_flux = (cell_state[7] + total_p) * v_normal - b_normal * jnp.sum(
        velocity * magnetic_vector, axis=0
    )
    fluxes = jnp.stack([density * v_normal] + momentum + induction + [energy_flux], axis=0)
    speeds = jnp.abs(v_normal) + jnp.sqrt((ADIABATIC * pressure + 2.0 * magnetic) / density)
    return (fluxes, speeds)


def rusanov(primitive, cell_state, normal, along_axis, spacing):
    fluxes, speeds = face_terms(primitive, cell_state, normal)
    length = speeds.shape[along_axis]
    wave_speed = jnp.maximum(
        lax.slice_in_dim(speeds, 0, length - 1, axis=along_axis),
        lax.slice_in_dim(speeds, 1, length, axis=along_axis),
    )
    flux_low = lax.slice_in_dim(fluxes, 0, length - 1, axis=along_axis + 1)
    flux_high = lax.slice_in_dim(fluxes, 1, length, axis=along_axis + 1)
    state_low = lax.slice_in_dim(cell_state, 0, length - 1, axis=along_axis + 1)
    state_high = lax.slice_in_dim(cell_state, 1, length, axis=along_axis + 1)
    face_flux = 0.5 * (flux_low + flux_high) - 0.5 * wave_speed[None] * (state_high - state_low)
    upper = lax.slice_in_dim(face_flux, 1, length - 1, axis=along_axis + 1)
    lower = lax.slice_in_dim(face_flux, 0, length - 2, axis=along_axis + 1)
    return (upper - lower) / spacing


def fluid_update(padded_array, radius_values, colatitude_mesh, timestep_length, mesh_spacing):
    ghosted = jnp.pad(padded_array, ((0, 0), (0, 0), (0, 0), (1, 1)), mode="edge")
    cell_state = conserved(ghosted)
    width_r = radius_values * mesh_spacing[0]
    width_t = radius_values * mesh_spacing[1]
    width_p = jnp.sin(colatitude_mesh)[:, None] * radius_values * mesh_spacing[2]
    radial = rusanov(ghosted[:, 1:-1, 1:-1, :], cell_state[:, 1:-1, 1:-1, :], 0, 2, width_r)
    polar = rusanov(ghosted[:, 1:-1, :, 1:-1], cell_state[:, 1:-1, :, 1:-1], 1, 1, width_t)
    azimuthal = rusanov(ghosted[:, :, 1:-1, 1:-1], cell_state[:, :, 1:-1, 1:-1], 2, 0, width_p)
    return cell_state[:, 1:-1, 1:-1, 1:-1] - timestep_length * (radial + polar + azimuthal)


def divergence(radial_pad, polar_pad, azim_pad, radius_values, colatitude_mesh, mesh_spacing):
    sin_colat = jnp.sin(colatitude_mesh)[:, None]
    cotangent = (jnp.cos(colatitude_mesh) / jnp.sin(colatitude_mesh))[:, None]
    radial_mid = radial_pad[:, :, 1:-1]
    polar_mid = polar_pad[:, 1:-1, :]
    d_radial = (radial_pad[:, :, 2:] - radial_pad[:, :, :-2]) / (
        2.0 * radius_values * mesh_spacing[0]
    )
    d_polar = (polar_pad[:, 2:, :] - polar_pad[:, :-2, :]) / (2.0 * radius_values * mesh_spacing[1])
    d_azim = (azim_pad[2:] - azim_pad[:-2]) / (2.0 * radius_values * sin_colat * mesh_spacing[2])
    return (
        d_radial
        + 2.0 * radial_mid / radius_values
        + d_polar
        + cotangent * polar_mid / radius_values
        + d_azim
    )


def transport_coefficients(
    wind_vel, mag_wind, spread, radius_values, colatitude_mesh, mesh_spacing
):
    width_r = radius_values * mesh_spacing[0]
    width_t = radius_values * mesh_spacing[1]
    width_p = jnp.sin(colatitude_mesh)[:, None] * radius_values * mesh_spacing[2]
    widths = (width_r, width_t, width_p)
    mag_sq = jnp.sum(mag_wind * mag_wind, axis=0) + B_FLOOR
    b_share = K_RATIO + (1.0 - K_RATIO) * mag_wind * mag_wind / mag_sq
    coef_list = [b_share[k] / (widths[k] * widths[k]) for k in range(3)]
    up_list = [jnp.maximum(wind_vel[k], 0.0) / widths[k] for k in range(3)]
    down_list = [jnp.minimum(wind_vel[k], 0.0) / widths[k] for k in range(3)]
    drift_rate = spread / 3.0
    return (
        coef_list,
        up_list,
        down_list,
        jnp.maximum(drift_rate, 0.0),
        jnp.minimum(drift_rate, 0.0),
    )


def transport_rate(extended, coef_set, kappa_col, step_m):
    coef_list, up_list, down_list, drift_up, drift_down = coef_set
    center = extended[1:-1, 1:-1, 1:-1, 1:-1]
    low_cells = (
        extended[1:-1, 1:-1, 1:-1, :-2],
        extended[1:-1, 1:-1, :-2, 1:-1],
        extended[1:-1, :-2, 1:-1, 1:-1],
    )
    high_cells = (
        extended[1:-1, 1:-1, 1:-1, 2:],
        extended[1:-1, 1:-1, 2:, 1:-1],
        extended[1:-1, 2:, 1:-1, 1:-1],
    )
    curvature = coef_list[0] * (high_cells[0] - 2.0 * center + low_cells[0])
    curvature = curvature + coef_list[1] * (high_cells[1] - 2.0 * center + low_cells[1])
    curvature = curvature + coef_list[2] * (high_cells[2] - 2.0 * center + low_cells[2])
    diffusion = kappa_col[:, None, None, None] * curvature
    advection = up_list[0] * (center - low_cells[0]) + down_list[0] * (high_cells[0] - center)
    advection = (
        advection + up_list[1] * (center - low_cells[1]) + down_list[1] * (high_cells[1] - center)
    )
    advection = (
        advection + up_list[2] * (center - low_cells[2]) + down_list[2] * (high_cells[2] - center)
    )
    bin_low = extended[:-2, 1:-1, 1:-1, 1:-1]
    bin_high = extended[2:, 1:-1, 1:-1, 1:-1]
    momentum = (drift_up * (bin_high - center) + drift_down * (center - bin_low)) / step_m
    return diffusion - advection + momentum


ROWS = 16


def _vec(shape, scalar):
    return jnp.full(shape, scalar, jnp.int32)


def section_kernel(scal_ref, flag_ref, kappa_ref, g_ref, gp_ref, gn_ref, azlo_ref, azhi_ref,
                   binlo_ref, binhi_ref, coef_ref, *rest, second):
    if second:
        f0_ref, out_ref = rest
    else:
        out_ref, az_first_ref, az_last_ref, bin_first_ref, bin_last_ref = rest
    step = pl.program_id(0)
    last_step = pl.num_programs(0) - 1
    bins, planes, colat, shells = g_ref.shape
    shape = (ROWS, shells)
    row = lax.broadcasted_iota(jnp.int32, shape, 0)
    lane = lax.broadcasted_iota(jnp.int32, shape, 1)
    first_az = _vec(shape, step) == 0
    last_az = _vec(shape, step) == last_step
    band_first = _vec(shape, flag_ref[0]) == 1
    band_last = _vec(shape, flag_ref[1]) == 1
    scale = scal_ref[0]

    def chunk(k, i, r0, kap, edge):
        rows = slice(r0, r0 + ROWS)
        center = g_ref[k, i, rows, :]
        if r0 == 0:
            low_t = jnp.where(row == 0, center, pltpu.roll(center, 1, 0))
        else:
            low_t = g_ref[k, i, r0 - 1:r0 - 1 + ROWS, :]
        if r0 + ROWS == colat:
            high_t = jnp.where(row == ROWS - 1, center, pltpu.roll(center, ROWS - 1, 0))
        else:
            high_t = g_ref[k, i, r0 + 1:r0 + 1 + ROWS, :]
        low_r = jnp.where(lane == 0, center, pltpu.roll(center, 1, 1))
        high_r = jnp.where(lane == shells - 1, center, pltpu.roll(center, shells - 1, 1))
        if i == 0:
            low_p = jnp.where(first_az, azlo_ref[k, 0, rows, :].astype(jnp.float32), gp_ref[k, 0, rows, :])
        else:
            low_p = g_ref[k, i - 1, rows, :]
        if i == planes - 1:
            high_p = jnp.where(last_az, azhi_ref[k, 0, rows, :].astype(jnp.float32), gn_ref[k, 0, rows, :])
        else:
            high_p = g_ref[k, i + 1, rows, :]
        if edge == "low":
            low_b = jnp.where(band_first, center, binlo_ref[0, i, rows, :].astype(jnp.float32))
        else:
            low_b = g_ref[k - 1, i, rows, :]
        if edge == "high":
            high_b = jnp.where(band_last, center, binhi_ref[0, i, rows, :].astype(jnp.float32))
        else:
            high_b = g_ref[k + 1, i, rows, :]
        d_lo = (center - low_r, center - low_t, center - low_p)
        d_hi = (high_r - center, high_t - center, high_p - center)
        curvature = coef_ref[0, i, rows, :] * (d_hi[0] - d_lo[0])
        curvature = curvature + coef_ref[1, i, rows, :] * (d_hi[1] - d_lo[1])
        curvature = curvature + coef_ref[2, i, rows, :] * (d_hi[2] - d_lo[2])
        advection = coef_ref[3, i, rows, :] * d_lo[0] + coef_ref[6, i, rows, :] * d_hi[0]
        advection = advection + coef_ref[4, i, rows, :] * d_lo[1] + coef_ref[7, i, rows, :] * d_hi[1]
        advection = advection + coef_ref[5, i, rows, :] * d_lo[2] + coef_ref[8, i, rows, :] * d_hi[2]
        momentum = coef_ref[9, i, rows, :] * (high_b - center) + coef_ref[10, i, rows, :] * (center - low_b)
        rate = kap * curvature - advection + momentum
        if second:
            value = 1.5 * center - 0.5 * f0_ref[k, i, rows, :] + scale * rate
        else:
            value = center + scale * rate
        out_ref[k, i, rows, :] = value
        if not second:
            half = value.astype(jnp.bfloat16)
            if i == 0:
                az_first_ref[k, 0, rows, :] = half
            if i == planes - 1:
                az_last_ref[k, 0, rows, :] = half
            if edge == "low":
                bin_first_ref[0, i, rows, :] = half
            if edge == "high":
                bin_last_ref[0, i, rows, :] = half

    def all_rows(k, edge):
        kap = kappa_ref[k]
        for i in range(planes):
            for r0 in range(0, colat, ROWS):
                chunk(k, i, r0, kap, edge)

    all_rows(0, "low")

    def middle(k, carry):
        all_rows(k, None)
        return carry

    lax.fori_loop(1, bins - 1, middle, 0)
    all_rows(bins - 1, "high")


PLANES = 2


def section_call(scal, flags, kappa, g, az_low, az_high, bin_low, bin_high, coefs, f0=None):
    bins, azim, colat, shells = g.shape
    block = (bins, PLANES, colat, shells)
    plane = (bins, 1, colat, shells)
    bin_block = (1, PLANES, colat, shells)
    smem = pl.BlockSpec(memory_space=pltpu.SMEM)
    in_specs = [
        smem,
        smem,
        smem,
        pl.BlockSpec(block, lambda a: (0, a, 0, 0)),
        pl.BlockSpec(plane, lambda a: (0, jnp.maximum(a * PLANES - 1, 0), 0, 0)),
        pl.BlockSpec(plane, lambda a: (0, jnp.minimum(a * PLANES + PLANES, azim - 1), 0, 0)),
        pl.BlockSpec(plane, lambda a: (0, 0, 0, 0)),
        pl.BlockSpec(plane, lambda a: (0, 0, 0, 0)),
        pl.BlockSpec(bin_block, lambda a: (0, a, 0, 0)),
        pl.BlockSpec(bin_block, lambda a: (0, a, 0, 0)),
        pl.BlockSpec((coefs.shape[0], PLANES, colat, shells), lambda a: (0, a, 0, 0)),
    ]
    args = [scal, flags, kappa, g, g, g, az_low, az_high, bin_low, bin_high, coefs]
    out_specs = pl.BlockSpec(block, lambda a: (0, a, 0, 0))
    out_shape = jax.ShapeDtypeStruct(g.shape, jnp.float32)
    if f0 is not None:
        in_specs.append(pl.BlockSpec(block, lambda a: (0, a, 0, 0)))
        args.append(f0)
    else:
        out_specs = [
            out_specs,
            pl.BlockSpec(plane, lambda a: (0, a, 0, 0)),
            pl.BlockSpec(plane, lambda a: (0, a, 0, 0)),
            pl.BlockSpec(bin_block, lambda a: (0, a, 0, 0)),
            pl.BlockSpec(bin_block, lambda a: (0, a, 0, 0)),
        ]
        half_plane = jax.ShapeDtypeStruct((bins, azim // PLANES, colat, shells), jnp.bfloat16)
        half_bin = jax.ShapeDtypeStruct((1, azim, colat, shells), jnp.bfloat16)
        out_shape = [out_shape, half_plane, half_plane, half_bin, half_bin]
    return pl.pallas_call(
        functools.partial(section_kernel, second=f0 is not None),
        grid=(azim // PLANES,),
        in_specs=in_specs,
        out_specs=out_specs,
        out_shape=out_shape,
        compiler_params=pltpu.CompilerParams(dimension_semantics=("arbitrary",)),
    )(*args)


def exchange(first, last, axis):
    size = lax.axis_size(axis)
    up = [(i, (i + 1) % size) for i in range(size)]
    down = [(j, i) for i, j in up]
    return lax.ppermute(last, axis, up), lax.ppermute(first, axis, down)


def cell_state(q):
    rho, v, b, p = q[0], q[1:4], q[4:7], q[7]
    vv = v[0] * v[0] + v[1] * v[1] + v[2] * v[2]
    bb = b[0] * b[0] + b[1] * b[1] + b[2] * b[2]
    energy = p / (ADIABATIC - 1.0) + 0.5 * rho * vv + 0.5 * bb
    return [rho, rho * v[0], rho * v[1], rho * v[2], b[0], b[1], b[2], energy]


def cell_flux(q, u, normal):
    rho, v, b, p = q[0], q[1:4], q[4:7], q[7]
    vn, bn = v[normal], b[normal]
    magnetic = 0.5 * (b[0] * b[0] + b[1] * b[1] + b[2] * b[2])
    total_p = p + magnetic
    momentum = [rho * v[k] * vn - b[k] * bn for k in range(3)]
    momentum[normal] = momentum[normal] + total_p
    induction = [vn * b[k] - bn * v[k] for k in range(3)]
    energy = (u[7] + total_p) * vn - bn * (v[0] * b[0] + v[1] * b[1] + v[2] * b[2])
    speed = jnp.abs(vn) + jnp.sqrt((ADIABATIC * p + 2.0 * magnetic) / rho)
    return [rho * vn] + momentum + induction + [energy], speed


def face_flux(f_low, s_low, u_low, f_high, s_high, u_high):
    wave = jnp.maximum(s_low, s_high)
    return [0.5 * (f_low[c] + f_high[c]) - 0.5 * wave * (u_high[c] - u_low[c]) for c in range(8)]


def mhd_kernel(dt_ref, rho_c, v_c, b_c, p_c, rho_m, v_m, b_m, p_m, rho_p, v_p, b_p, p_p,
               azlo_ref, azhi_ref, clo_ref, chi_ref, wr_ref, wt_ref, wp_ref, out_ref):
    step = pl.program_id(0)
    last_step = pl.num_programs(0) - 1

    def prim(rho_ref, v_ref, b_ref, p_ref):
        return [rho_ref[0], v_ref[0, 0], v_ref[1, 0], v_ref[2, 0],
                b_ref[0, 0], b_ref[1, 0], b_ref[2, 0], p_ref[0]]

    q = prim(rho_c, v_c, b_c, p_c)
    shape = q[0].shape
    nrow, nlane = shape
    row = lax.broadcasted_iota(jnp.int32, shape, 0)
    lane = lax.broadcasted_iota(jnp.int32, shape, 1)
    first_az = _vec(shape, step) == 0
    last_az = _vec(shape, step) == last_step
    q_m = prim(rho_m, v_m, b_m, p_m)
    q_p = prim(rho_p, v_p, b_p, p_p)
    q_m = [jnp.where(first_az, azlo_ref[c, 0], q_m[c]) for c in range(8)]
    q_p = [jnp.where(last_az, azhi_ref[c, 0], q_p[c]) for c in range(8)]
    u = cell_state(q)
    dt = dt_ref[0]

    def lane_next(x):
        return jnp.where(lane == nlane - 1, x, pltpu.roll(x, nlane - 1, 1))

    f, s = cell_flux(q, u, 0)
    high = face_flux(f, s, u, [lane_next(x) for x in f], lane_next(s), [lane_next(x) for x in u])
    low = [jnp.where(lane == 0, f[c], pltpu.roll(high[c], 1, 1)) for c in range(8)]
    width_r = wr_ref[...]
    radial = [(high[c] - low[c]) / width_r for c in range(8)]

    q_l = [clo_ref[c, 0] for c in range(8)]
    q_h = [chi_ref[c, 0] for c in range(8)]
    u_l = cell_state(q_l)
    u_h = cell_state(q_h)
    f, s = cell_flux(q, u, 1)
    f_l, s_l = cell_flux(q_l, u_l, 1)
    f_h, s_h = cell_flux(q_h, u_h, 1)

    def row_next(x, h):
        return jnp.where(row == nrow - 1, jnp.broadcast_to(h, shape), pltpu.roll(x, nrow - 1, 0))

    high = face_flux(f, s, u, [row_next(f[c], f_h[c]) for c in range(8)], row_next(s, s_h),
                     [row_next(u[c], u_h[c]) for c in range(8)])
    first = face_flux(f_l, s_l, u_l, f, s, u)
    low = [jnp.where(row == 0, first[c], pltpu.roll(high[c], 1, 0)) for c in range(8)]
    width_t = wt_ref[...]
    polar = [(high[c] - low[c]) / width_t for c in range(8)]

    u_m = cell_state(q_m)
    u_p = cell_state(q_p)
    f, s = cell_flux(q, u, 2)
    f_m, s_m = cell_flux(q_m, u_m, 2)
    f_p, s_p = cell_flux(q_p, u_p, 2)
    high = face_flux(f, s, u, f_p, s_p, u_p)
    low = face_flux(f_m, s_m, u_m, f, s, u)
    width_p = wp_ref[...]
    for c in range(8):
        azimuthal = (high[c] - low[c]) / width_p
        out_ref[c, 0] = u[c] - dt * (radial[c] + polar[c] + azimuthal)


def mhd_call(dt, density, velocity, magnetic_vector, pressure, az_low, az_high,
             colat_low, colat_high, width_r, width_t, width_p):
    azim, colat, radial = density.shape
    scalar_block = (1, colat, radial)
    vector_block = (3, 1, colat, radial)

    def clamp_low(a):
        return jnp.maximum(a - 1, 0)

    def clamp_high(a):
        return jnp.minimum(a + 1, azim - 1)

    in_specs = [pl.BlockSpec(memory_space=pltpu.SMEM)]
    for pick in (lambda a: a, clamp_low, clamp_high):
        in_specs += [
            pl.BlockSpec(scalar_block, lambda a, pick=pick: (pick(a), 0, 0)),
            pl.BlockSpec(vector_block, lambda a, pick=pick: (0, pick(a), 0, 0)),
            pl.BlockSpec(vector_block, lambda a, pick=pick: (0, pick(a), 0, 0)),
            pl.BlockSpec(scalar_block, lambda a, pick=pick: (pick(a), 0, 0)),
        ]
    in_specs += [
        pl.BlockSpec((8, 1, colat, radial), lambda a: (0, 0, 0, 0)),
        pl.BlockSpec((8, 1, colat, radial), lambda a: (0, 0, 0, 0)),
        pl.BlockSpec((8, 1, 1, radial), lambda a: (0, a, 0, 0)),
        pl.BlockSpec((8, 1, 1, radial), lambda a: (0, a, 0, 0)),
        pl.BlockSpec((1, radial), lambda a: (0, 0)),
        pl.BlockSpec((1, radial), lambda a: (0, 0)),
        pl.BlockSpec((colat, radial), lambda a: (0, 0)),
    ]
    fields = (density, velocity, magnetic_vector, pressure)
    return pl.pallas_call(
        mhd_kernel,
        grid=(azim,),
        in_specs=in_specs,
        out_specs=pl.BlockSpec((8, 1, colat, radial), lambda a: (0, a, 0, 0)),
        out_shape=jax.ShapeDtypeStruct((8, azim, colat, radial), jnp.float32),
        compiler_params=pltpu.CompilerParams(dimension_semantics=("arbitrary",)),
    )(dt, *fields, *fields, *fields, az_low, az_high, colat_low, colat_high,
      width_r, width_t, width_p)


def mhd_halos(density, velocity, magnetic_vector, pressure, band_pos, band_count):
    fields = [density, velocity[0], velocity[1], velocity[2],
              magnetic_vector[0], magnetic_vector[1], magnetic_vector[2], pressure]
    azim, colat = density.shape[0], density.shape[1]
    az_first = jnp.stack([x[0:1] for x in fields])
    az_last = jnp.stack([x[azim - 1:azim] for x in fields])
    c_first = jnp.stack([x[:, 0:1] for x in fields])
    c_last = jnp.stack([x[:, colat - 1:colat] for x in fields])
    phi_size = lax.axis_size("phi")
    up = [(i, (i + 1) % phi_size) for i in range(phi_size)]
    down = [(j, i) for i, j in up]
    az_low = lax.ppermute(az_last, "phi", up)
    az_high = lax.ppermute(az_first, "phi", down)
    up = [(i, (i + 1) % band_count) for i in range(band_count)]
    down = [(j, i) for i, j in up]
    c_low = lax.ppermute(c_last, "band", up)
    c_high = lax.ppermute(c_first, "band", down)
    c_low = jnp.where(band_pos == 0, c_first, c_low)
    c_high = jnp.where(band_pos == band_count - 1, c_last, c_high)
    return az_low, az_high, c_low, c_high


def body(
    density,
    velocity,
    magnetic_vector,
    pressure,
    fluid_courant_number,
    cosmic_ray_density,
    diffusion_per_bin,
    super_step_scale,
):
    azim_dev = density.shape[0]
    colat_dev = density.shape[1]
    radial_cell_count = density.shape[2]
    band_count = lax.axis_size("band")
    phi_count = lax.axis_size("phi")
    colatitude_count = colat_dev * band_count
    azimuth_cell_count = azim_dev * phi_count
    bin_dev = cosmic_ray_density.shape[0]
    momentum_bin_count = bin_dev * band_count
    outer_shell_count = cosmic_ray_density.shape[3]
    band_pos = lax.axis_index("band")
    mesh_spacing = grid_steps(
        radial_cell_count, colatitude_count, azimuth_cell_count, momentum_bin_count
    )
    fluid_rate, cosmic_ray_rate = rate_limits(
        radial_cell_count,
        outer_shell_count,
        colatitude_count,
        azimuth_cell_count,
        momentum_bin_count,
    )
    radius_full = shell_radii(0, radial_cell_count, radial_cell_count)
    colatitude_local = colatitudes(band_pos * colat_dev, colat_dev, colatitude_count)
    dt = jnp.reshape(fluid_courant_number / fluid_rate, (1,)).astype(jnp.float32)
    fluid_state = mhd_call(
        dt, density, velocity, magnetic_vector, pressure,
        *mhd_halos(density, velocity, magnetic_vector, pressure, band_pos, band_count),
        (radius_full * mesh_spacing[0])[None],
        (radius_full * mesh_spacing[1])[None],
        jnp.sin(colatitude_local)[:, None] * radius_full * mesh_spacing[2],
    )
    first_shell = radial_cell_count - outer_shell_count
    radius_sh = shell_radii(first_shell, outer_shell_count, radial_cell_count)
    colatitude_full = colatitudes(0, colatitude_count, colatitude_count)
    own_fields = jnp.concatenate(
        [velocity[:, :, :, first_shell:], magnetic_vector[:, :, :, first_shell:]], axis=0
    ).astype(jnp.bfloat16)
    wind_half = lax.all_gather(own_fields, "band", axis=0)
    wind_half = jnp.transpose(wind_half, (1, 2, 0, 3, 4)).reshape(
        own_fields.shape[0], azim_dev, colatitude_count, outer_shell_count
    )
    fluid_state, wind_half = lax.optimization_barrier((fluid_state, wind_half))
    wind_vel = wind_half[0:3].astype(jnp.float32)
    azim_pad = padded(wind_half[2], (("phi", 0),), 1).astype(jnp.float32)
    radial_pad = jnp.pad(wind_vel[0], ((0, 0), (0, 0), (1, 1)), mode="edge")
    polar_pad = jnp.pad(wind_vel[1], ((0, 0), (1, 1), (0, 0)), mode="edge")
    spread_half = divergence(
        radial_pad, polar_pad, azim_pad, radius_sh, colatitude_full, mesh_spacing
    ).astype(jnp.bfloat16)
    kappa_here = lax.dynamic_slice_in_dim(diffusion_per_bin, band_pos * bin_dev, bin_dev)
    sts_step = super_step_scale / cosmic_ray_rate
    coef_set = transport_coefficients(
        wind_half[0:3].astype(jnp.float32),
        wind_half[3:6].astype(jnp.float32),
        spread_half.astype(jnp.float32),
        radius_sh,
        colatitude_full,
        mesh_spacing,
    )

    coef_list, up_list, down_list, drift_up, drift_down = coef_set
    coefs = jnp.stack(
        list(coef_list) + list(up_list) + list(down_list)
        + [drift_up / mesh_spacing[3], drift_down / mesh_spacing[3]],
        axis=0,
    )
    scal1 = jnp.reshape(sts_step / 3.0, (1,)).astype(jnp.float32)
    scal2 = jnp.reshape(sts_step / 2.0, (1,)).astype(jnp.float32)
    flags = jnp.stack([band_pos == 0, band_pos == band_count - 1]).astype(jnp.int32)
    bins = cosmic_ray_density.shape[0]
    edges = (
        cosmic_ray_density[:, 0:1],
        cosmic_ray_density[:, azim_dev - 1:azim_dev],
        cosmic_ray_density[0:1],
        cosmic_ray_density[bins - 1:bins],
    )
    edges = [x.astype(jnp.bfloat16) for x in lax.optimization_barrier(edges)]
    az_low, az_high = exchange(edges[0], edges[1], "phi")
    bin_low, bin_high = exchange(edges[2], edges[3], "band")
    first_section, *edges = section_call(
        scal1, flags, kappa_here, cosmic_ray_density, az_low, az_high, bin_low, bin_high, coefs
    )
    steps = edges[0].shape[1]
    az_low, az_high = exchange(edges[0][:, 0:1], edges[1][:, steps - 1:steps], "phi")
    bin_low, bin_high = exchange(edges[2], edges[3], "band")
    cosmic_ray_next = section_call(
        scal2, flags, kappa_here, first_section, az_low, az_high, bin_low, bin_high, coefs,
        cosmic_ray_density,
    )
    return (fluid_state, cosmic_ray_next)


def solution(mesh):
    placed = (
        P("phi", "band", None),
        P(None, "phi", "band", None),
        P(None, "phi", "band", None),
        P("phi", "band", None),
        P(),
        P("band", "phi", None, None),
        P(),
        P(),
    )
    return jax.shard_map(
        body,
        mesh=mesh,
        in_specs=placed,
        out_specs=(P(None, "phi", "band", None), P("band", "phi", None, None)),
        check_vma=False,
    )
```

```python
import functools
import math

import jax
import jax.numpy as jnp
from jax import lax
from jax.experimental import pallas as pl
from jax.experimental.pallas import tpu as pltpu
from jax.sharding import PartitionSpec as P

ADIABATIC = 5.0 / 3.0
INNER_RADIUS = 0.1
R_RATIO = 30.0
COLAT_LOW = math.pi / 6.0
COLAT_SPAN = 2.0 * math.pi / 3.0
P_RATIO = 1000.0
K_RATIO = 0.1
B_FLOOR = 0.1
V_BOUND = 3.0
B_BOUND = 3.0
P_HIGH = 2.0
RHO_LOW = 0.5
KAPPA_HIGH = 0.5


def padded(value, sides, width):
    for axis, dim in sides:
        size, length = (lax.axis_size(axis), value.shape[dim])
        up = [(i, (i + 1) % size) for i in range(size)]
        down = [(j, i) for i, j in up]
        last = lax.slice_in_dim(value, length - width, length, axis=dim)
        leading = lax.slice_in_dim(value, 0, width, axis=dim)
        before = lax.ppermute(last, axis, up)
        after = lax.ppermute(leading, axis, down)
        value = jnp.concatenate([before, value, after], axis=dim)
    return value


def grid_steps(n_radial, n_colat, n_azim, n_bins):
    return (
        math.log(R_RATIO) / n_radial,
        COLAT_SPAN / n_colat,
        2.0 * math.pi / n_azim,
        math.log(P_RATIO) / n_bins,
    )


def rate_limits(n_radial, n_shells, n_colat, n_azim, n_bins):
    radial_spacing, colatitude_spacing, azimuth_spacing, step_m = grid_steps(
        n_radial, n_colat, n_azim, n_bins
    )
    sine_lower = math.sin(COLAT_LOW + 0.5 * colatitude_spacing)
    fluid_radius = INNER_RADIUS * math.exp(0.5 * radial_spacing)
    fastest_limit = V_BOUND + math.sqrt((ADIABATIC * P_HIGH + 3.0 * B_BOUND**2) / RHO_LOW)
    fluid_rate = fastest_limit * (
        1.0 / (fluid_radius * radial_spacing)
        + 1.0 / (fluid_radius * colatitude_spacing)
        + 1.0 / (fluid_radius * sine_lower * azimuth_spacing)
    )
    shell_low = INNER_RADIUS * math.exp(radial_spacing * (n_radial - n_shells + 0.5))
    inv_r = 1.0 / (shell_low * radial_spacing)
    inv_t = 1.0 / (shell_low * colatitude_spacing)
    inv_p = 1.0 / (shell_low * sine_lower * azimuth_spacing)
    cosmic_ray_rate = (
        2.0 * KAPPA_HIGH * (inv_r**2 + inv_t**2 + inv_p**2)
        + V_BOUND * (inv_r + inv_t + inv_p)
        + V_BOUND * (inv_r + inv_t + inv_p + 4.0 / shell_low) / (3.0 * step_m)
    )
    return (fluid_rate, cosmic_ray_rate)


def shell_radii(start_index, cell_count, n_radial):
    cell_index = jnp.arange(cell_count, dtype=jnp.float32) + (start_index + 0.5)
    return INNER_RADIUS * jnp.exp(math.log(R_RATIO) / n_radial * cell_index)


def colatitudes(start_index, cell_count, n_colat):
    cell_index = jnp.arange(cell_count, dtype=jnp.float32) + 0.5
    return COLAT_LOW + COLAT_SPAN * (cell_index + start_index) / n_colat


def edge_fix(values, along_axis, depth, band_pos, axis_count):
    extent = values.shape[along_axis]
    low_ghost = lax.slice_in_dim(values, 0, depth, axis=along_axis)
    high_ghost = lax.slice_in_dim(values, extent - depth, extent, axis=along_axis)
    first_own = lax.slice_in_dim(values, depth, depth + 1, axis=along_axis)
    last_own = lax.slice_in_dim(values, extent - depth - 1, extent - depth, axis=along_axis)
    low_rim = jnp.where(band_pos == 0, first_own, low_ghost)
    high_rim = jnp.where(band_pos == axis_count - 1, last_own, high_ghost)
    middle = lax.slice_in_dim(values, depth, extent - depth, axis=along_axis)
    return jnp.concatenate([low_rim, middle, high_rim], axis=along_axis)


def conserved(primitive):
    density = primitive[0]
    velocity = primitive[1:4]
    magnetic_vector = primitive[4:7]
    pressure = primitive[7]
    energy = (
        pressure / (ADIABATIC - 1.0)
        + 0.5 * density * jnp.sum(velocity * velocity, axis=0)
        + 0.5 * jnp.sum(magnetic_vector * magnetic_vector, axis=0)
    )
    return jnp.concatenate(
        [density[None], density[None] * velocity, magnetic_vector, energy[None]], axis=0
    )


def face_terms(primitive, cell_state, normal):
    density = primitive[0]
    velocity = primitive[1:4]
    magnetic_vector = primitive[4:7]
    pressure = primitive[7]
    v_normal = velocity[normal]
    b_normal = magnetic_vector[normal]
    magnetic = 0.5 * jnp.sum(magnetic_vector * magnetic_vector, axis=0)
    total_p = pressure + magnetic
    momentum = [density * velocity[k] * v_normal - magnetic_vector[k] * b_normal for k in range(3)]
    momentum[normal] = momentum[normal] + total_p
    induction = [v_normal * magnetic_vector[k] - b_normal * velocity[k] for k in range(3)]
    energy_flux = (cell_state[7] + total_p) * v_normal - b_normal * jnp.sum(
        velocity * magnetic_vector, axis=0
    )
    fluxes = jnp.stack([density * v_normal] + momentum + induction + [energy_flux], axis=0)
    speeds = jnp.abs(v_normal) + jnp.sqrt((ADIABATIC * pressure + 2.0 * magnetic) / density)
    return (fluxes, speeds)


def rusanov(primitive, cell_state, normal, along_axis, spacing):
    fluxes, speeds = face_terms(primitive, cell_state, normal)
    length = speeds.shape[along_axis]
    wave_speed = jnp.maximum(
        lax.slice_in_dim(speeds, 0, length - 1, axis=along_axis),
        lax.slice_in_dim(speeds, 1, length, axis=along_axis),
    )
    flux_low = lax.slice_in_dim(fluxes, 0, length - 1, axis=along_axis + 1)
    flux_high = lax.slice_in_dim(fluxes, 1, length, axis=along_axis + 1)
    state_low = lax.slice_in_dim(cell_state, 0, length - 1, axis=along_axis + 1)
    state_high = lax.slice_in_dim(cell_state, 1, length, axis=along_axis + 1)
    face_flux = 0.5 * (flux_low + flux_high) - 0.5 * wave_speed[None] * (state_high - state_low)
    upper = lax.slice_in_dim(face_flux, 1, length - 1, axis=along_axis + 1)
    lower = lax.slice_in_dim(face_flux, 0, length - 2, axis=along_axis + 1)
    return (upper - lower) / spacing


def fluid_update(padded_array, radius_values, colatitude_mesh, timestep_length, mesh_spacing):
    ghosted = jnp.pad(padded_array, ((0, 0), (0, 0), (0, 0), (1, 1)), mode="edge")
    cell_state = conserved(ghosted)
    width_r = radius_values * mesh_spacing[0]
    width_t = radius_values * mesh_spacing[1]
    width_p = jnp.sin(colatitude_mesh)[:, None] * radius_values * mesh_spacing[2]
    radial = rusanov(ghosted[:, 1:-1, 1:-1, :], cell_state[:, 1:-1, 1:-1, :], 0, 2, width_r)
    polar = rusanov(ghosted[:, 1:-1, :, 1:-1], cell_state[:, 1:-1, :, 1:-1], 1, 1, width_t)
    azimuthal = rusanov(ghosted[:, :, 1:-1, 1:-1], cell_state[:, :, 1:-1, 1:-1], 2, 0, width_p)
    return cell_state[:, 1:-1, 1:-1, 1:-1] - timestep_length * (radial + polar + azimuthal)


def divergence(radial_pad, polar_pad, azim_pad, radius_values, colatitude_mesh, mesh_spacing):
    sin_colat = jnp.sin(colatitude_mesh)[:, None]
    cotangent = (jnp.cos(colatitude_mesh) / jnp.sin(colatitude_mesh))[:, None]
    radial_mid = radial_pad[:, :, 1:-1]
    polar_mid = polar_pad[:, 1:-1, :]
    d_radial = (radial_pad[:, :, 2:] - radial_pad[:, :, :-2]) / (
        2.0 * radius_values * mesh_spacing[0]
    )
    d_polar = (polar_pad[:, 2:, :] - polar_pad[:, :-2, :]) / (2.0 * radius_values * mesh_spacing[1])
    d_azim = (azim_pad[2:] - azim_pad[:-2]) / (2.0 * radius_values * sin_colat * mesh_spacing[2])
    return (
        d_radial
        + 2.0 * radial_mid / radius_values
        + d_polar
        + cotangent * polar_mid / radius_values
        + d_azim
    )


def transport_coefficients(
    wind_vel, mag_wind, spread, radius_values, colatitude_mesh, mesh_spacing
):
    width_r = radius_values * mesh_spacing[0]
    width_t = radius_values * mesh_spacing[1]
    width_p = jnp.sin(colatitude_mesh)[:, None] * radius_values * mesh_spacing[2]
    widths = (width_r, width_t, width_p)
    mag_sq = jnp.sum(mag_wind * mag_wind, axis=0) + B_FLOOR
    b_share = K_RATIO + (1.0 - K_RATIO) * mag_wind * mag_wind / mag_sq
    coef_list = [b_share[k] / (widths[k] * widths[k]) for k in range(3)]
    up_list = [jnp.maximum(wind_vel[k], 0.0) / widths[k] for k in range(3)]
    down_list = [jnp.minimum(wind_vel[k], 0.0) / widths[k] for k in range(3)]
    drift_rate = spread / 3.0
    return (
        coef_list,
        up_list,
        down_list,
        jnp.maximum(drift_rate, 0.0),
        jnp.minimum(drift_rate, 0.0),
    )


def transport_rate(extended, coef_set, kappa_col, step_m):
    coef_list, up_list, down_list, drift_up, drift_down = coef_set
    center = extended[1:-1, 1:-1, 1:-1, 1:-1]
    low_cells = (
        extended[1:-1, 1:-1, 1:-1, :-2],
        extended[1:-1, 1:-1, :-2, 1:-1],
        extended[1:-1, :-2, 1:-1, 1:-1],
    )
    high_cells = (
        extended[1:-1, 1:-1, 1:-1, 2:],
        extended[1:-1, 1:-1, 2:, 1:-1],
        extended[1:-1, 2:, 1:-1, 1:-1],
    )
    curvature = coef_list[0] * (high_cells[0] - 2.0 * center + low_cells[0])
    curvature = curvature + coef_list[1] * (high_cells[1] - 2.0 * center + low_cells[1])
    curvature = curvature + coef_list[2] * (high_cells[2] - 2.0 * center + low_cells[2])
    diffusion = kappa_col[:, None, None, None] * curvature
    advection = up_list[0] * (center - low_cells[0]) + down_list[0] * (high_cells[0] - center)
    advection = (
        advection + up_list[1] * (center - low_cells[1]) + down_list[1] * (high_cells[1] - center)
    )
    advection = (
        advection + up_list[2] * (center - low_cells[2]) + down_list[2] * (high_cells[2] - center)
    )
    bin_low = extended[:-2, 1:-1, 1:-1, 1:-1]
    bin_high = extended[2:, 1:-1, 1:-1, 1:-1]
    momentum = (drift_up * (bin_high - center) + drift_down * (center - bin_low)) / step_m
    return diffusion - advection + momentum


ROWS = 16


def _vec(shape, scalar):
    return jnp.full(shape, scalar, jnp.int32)


def section_kernel(scal_ref, flag_ref, kappa_ref, g_ref, gp_ref, gn_ref, azlo_ref, azhi_ref,
                   binlo_ref, binhi_ref, coef_ref, *rest, second):
    if second:
        f0_ref, out_ref = rest
    else:
        out_ref, az_first_ref, az_last_ref, bin_first_ref, bin_last_ref = rest
    step = pl.program_id(0)
    last_step = pl.num_programs(0) - 1
    bins, planes, colat, shells = g_ref.shape
    shape = (ROWS, shells)
    row = lax.broadcasted_iota(jnp.int32, shape, 0)
    lane = lax.broadcasted_iota(jnp.int32, shape, 1)
    first_az = _vec(shape, step) == 0
    last_az = _vec(shape, step) == last_step
    band_first = _vec(shape, flag_ref[0]) == 1
    band_last = _vec(shape, flag_ref[1]) == 1
    scale = scal_ref[0]

    def chunk(k, i, r0, kap, edge):
        rows = slice(r0, r0 + ROWS)
        center = g_ref[k, i, rows, :]
        if r0 == 0:
            low_t = jnp.where(row == 0, center, pltpu.roll(center, 1, 0))
        else:
            low_t = g_ref[k, i, r0 - 1:r0 - 1 + ROWS, :]
        if r0 + ROWS == colat:
            high_t = jnp.where(row == ROWS - 1, center, pltpu.roll(center, ROWS - 1, 0))
        else:
            high_t = g_ref[k, i, r0 + 1:r0 + 1 + ROWS, :]
        low_r = jnp.where(lane == 0, center, pltpu.roll(center, 1, 1))
        high_r = jnp.where(lane == shells - 1, center, pltpu.roll(center, shells - 1, 1))
        if i == 0:
            low_p = jnp.where(first_az, azlo_ref[k, 0, rows, :].astype(jnp.float32), gp_ref[k, 0, rows, :])
        else:
            low_p = g_ref[k, i - 1, rows, :]
        if i == planes - 1:
            high_p = jnp.where(last_az, azhi_ref[k, 0, rows, :].astype(jnp.float32), gn_ref[k, 0, rows, :])
        else:
            high_p = g_ref[k, i + 1, rows, :]
        if edge == "low":
            low_b = jnp.where(band_first, center, binlo_ref[0, i, rows, :].astype(jnp.float32))
        else:
            low_b = g_ref[k - 1, i, rows, :]
        if edge == "high":
            high_b = jnp.where(band_last, center, binhi_ref[0, i, rows, :].astype(jnp.float32))
        else:
            high_b = g_ref[k + 1, i, rows, :]
        d_lo = (center - low_r, center - low_t, center - low_p)
        d_hi = (high_r - center, high_t - center, high_p - center)
        curvature = coef_ref[0, i, rows, :] * (d_hi[0] - d_lo[0])
        curvature = curvature + coef_ref[1, i, rows, :] * (d_hi[1] - d_lo[1])
        curvature = curvature + coef_ref[2, i, rows, :] * (d_hi[2] - d_lo[2])
        advection = coef_ref[3, i, rows, :] * d_lo[0] + coef_ref[6, i, rows, :] * d_hi[0]
        advection = advection + coef_ref[4, i, rows, :] * d_lo[1] + coef_ref[7, i, rows, :] * d_hi[1]
        advection = advection + coef_ref[5, i, rows, :] * d_lo[2] + coef_ref[8, i, rows, :] * d_hi[2]
        momentum = coef_ref[9, i, rows, :] * (high_b - center) + coef_ref[10, i, rows, :] * (center - low_b)
        rate = kap * curvature - advection + momentum
        if second:
            value = 1.5 * center - 0.5 * f0_ref[k, i, rows, :] + scale * rate
        else:
            value = center + scale * rate
        out_ref[k, i, rows, :] = value
        if not second:
            half = value.astype(jnp.bfloat16)
            if i == 0:
                az_first_ref[k, 0, rows, :] = half
            if i == planes - 1:
                az_last_ref[k, 0, rows, :] = half
            if edge == "low":
                bin_first_ref[0, i, rows, :] = half
            if edge == "high":
                bin_last_ref[0, i, rows, :] = half

    def all_rows(k, edge):
        kap = kappa_ref[k]
        for i in range(planes):
            for r0 in range(0, colat, ROWS):
                chunk(k, i, r0, kap, edge)

    all_rows(0, "low")

    def middle(k, carry):
        all_rows(k, None)
        return carry

    lax.fori_loop(1, bins - 1, middle, 0)
    all_rows(bins - 1, "high")


PLANES = 2


def section_call(scal, flags, kappa, g, az_low, az_high, bin_low, bin_high, coefs, f0=None):
    bins, azim, colat, shells = g.shape
    block = (bins, PLANES, colat, shells)
    plane = (bins, 1, colat, shells)
    bin_block = (1, PLANES, colat, shells)
    smem = pl.BlockSpec(memory_space=pltpu.SMEM)
    in_specs = [
        smem,
        smem,
        smem,
        pl.BlockSpec(block, lambda a: (0, a, 0, 0)),
        pl.BlockSpec(plane, lambda a: (0, jnp.maximum(a * PLANES - 1, 0), 0, 0)),
        pl.BlockSpec(plane, lambda a: (0, jnp.minimum(a * PLANES + PLANES, azim - 1), 0, 0)),
        pl.BlockSpec(plane, lambda a: (0, 0, 0, 0)),
        pl.BlockSpec(plane, lambda a: (0, 0, 0, 0)),
        pl.BlockSpec(bin_block, lambda a: (0, a, 0, 0)),
        pl.BlockSpec(bin_block, lambda a: (0, a, 0, 0)),
        pl.BlockSpec((coefs.shape[0], PLANES, colat, shells), lambda a: (0, a, 0, 0)),
    ]
    args = [scal, flags, kappa, g, g, g, az_low, az_high, bin_low, bin_high, coefs]
    out_specs = pl.BlockSpec(block, lambda a: (0, a, 0, 0))
    out_shape = jax.ShapeDtypeStruct(g.shape, jnp.float32)
    if f0 is not None:
        in_specs.append(pl.BlockSpec(block, lambda a: (0, a, 0, 0)))
        args.append(f0)
    else:
        out_specs = [
            out_specs,
            pl.BlockSpec(plane, lambda a: (0, a, 0, 0)),
            pl.BlockSpec(plane, lambda a: (0, a, 0, 0)),
            pl.BlockSpec(bin_block, lambda a: (0, a, 0, 0)),
            pl.BlockSpec(bin_block, lambda a: (0, a, 0, 0)),
        ]
        half_plane = jax.ShapeDtypeStruct((bins, azim // PLANES, colat, shells), jnp.bfloat16)
        half_bin = jax.ShapeDtypeStruct((1, azim, colat, shells), jnp.bfloat16)
        out_shape = [out_shape, half_plane, half_plane, half_bin, half_bin]
    return pl.pallas_call(
        functools.partial(section_kernel, second=f0 is not None),
        grid=(azim // PLANES,),
        in_specs=in_specs,
        out_specs=out_specs,
        out_shape=out_shape,
        compiler_params=pltpu.CompilerParams(dimension_semantics=("arbitrary",)),
    )(*args)


def exchange(first, last, axis):
    size = lax.axis_size(axis)
    up = [(i, (i + 1) % size) for i in range(size)]
    down = [(j, i) for i, j in up]
    return lax.ppermute(last, axis, up), lax.ppermute(first, axis, down)


def cell_state(q):
    rho, v, b, p = q[0], q[1:4], q[4:7], q[7]
    vv = v[0] * v[0] + v[1] * v[1] + v[2] * v[2]
    bb = b[0] * b[0] + b[1] * b[1] + b[2] * b[2]
    energy = p / (ADIABATIC - 1.0) + 0.5 * rho * vv + 0.5 * bb
    return [rho, rho * v[0], rho * v[1], rho * v[2], b[0], b[1], b[2], energy]


def cell_flux(q, u, normal):
    rho, v, b, p = q[0], q[1:4], q[4:7], q[7]
    vn, bn = v[normal], b[normal]
    magnetic = 0.5 * (b[0] * b[0] + b[1] * b[1] + b[2] * b[2])
    total_p = p + magnetic
    momentum = [rho * v[k] * vn - b[k] * bn for k in range(3)]
    momentum[normal] = momentum[normal] + total_p
    induction = [vn * b[k] - bn * v[k] for k in range(3)]
    energy = (u[7] + total_p) * vn - bn * (v[0] * b[0] + v[1] * b[1] + v[2] * b[2])
    speed = jnp.abs(vn) + jnp.sqrt((ADIABATIC * p + 2.0 * magnetic) / rho)
    return [rho * vn] + momentum + induction + [energy], speed


def face_flux(f_low, s_low, u_low, f_high, s_high, u_high):
    wave = jnp.maximum(s_low, s_high)
    return [0.5 * (f_low[c] + f_high[c]) - 0.5 * wave * (u_high[c] - u_low[c]) for c in range(8)]


def mhd_kernel(dt_ref, rho_c, v_c, b_c, p_c, rho_m, v_m, b_m, p_m, rho_p, v_p, b_p, p_p,
               azlo_ref, azhi_ref, clo_ref, chi_ref, wr_ref, wt_ref, wp_ref, out_ref):
    step = pl.program_id(0)
    last_step = pl.num_programs(0) - 1

    def prim(rho_ref, v_ref, b_ref, p_ref):
        return [rho_ref[0], v_ref[0, 0], v_ref[1, 0], v_ref[2, 0],
                b_ref[0, 0], b_ref[1, 0], b_ref[2, 0], p_ref[0]]

    q = prim(rho_c, v_c, b_c, p_c)
    shape = q[0].shape
    nrow, nlane = shape
    row = lax.broadcasted_iota(jnp.int32, shape, 0)
    lane = lax.broadcasted_iota(jnp.int32, shape, 1)
    first_az = _vec(shape, step) == 0
    last_az = _vec(shape, step) == last_step
    q_m = prim(rho_m, v_m, b_m, p_m)
    q_p = prim(rho_p, v_p, b_p, p_p)
    q_m = [jnp.where(first_az, azlo_ref[c, 0], q_m[c]) for c in range(8)]
    q_p = [jnp.where(last_az, azhi_ref[c, 0], q_p[c]) for c in range(8)]
    u = cell_state(q)
    dt = dt_ref[0]

    def lane_next(x):
        return jnp.where(lane == nlane - 1, x, pltpu.roll(x, nlane - 1, 1))

    f, s = cell_flux(q, u, 0)
    high = face_flux(f, s, u, [lane_next(x) for x in f], lane_next(s), [lane_next(x) for x in u])
    low = [jnp.where(lane == 0, f[c], pltpu.roll(high[c], 1, 1)) for c in range(8)]
    width_r = wr_ref[...]
    radial = [(high[c] - low[c]) / width_r for c in range(8)]

    q_l = [clo_ref[c, 0] for c in range(8)]
    q_h = [chi_ref[c, 0] for c in range(8)]
    u_l = cell_state(q_l)
    u_h = cell_state(q_h)
    f, s = cell_flux(q, u, 1)
    f_l, s_l = cell_flux(q_l, u_l, 1)
    f_h, s_h = cell_flux(q_h, u_h, 1)

    def row_next(x, h):
        return jnp.where(row == nrow - 1, jnp.broadcast_to(h, shape), pltpu.roll(x, nrow - 1, 0))

    high = face_flux(f, s, u, [row_next(f[c], f_h[c]) for c in range(8)], row_next(s, s_h),
                     [row_next(u[c], u_h[c]) for c in range(8)])
    first = face_flux(f_l, s_l, u_l, f, s, u)
    low = [jnp.where(row == 0, first[c], pltpu.roll(high[c], 1, 0)) for c in range(8)]
    width_t = wt_ref[...]
    polar = [(high[c] - low[c]) / width_t for c in range(8)]

    u_m = cell_state(q_m)
    u_p = cell_state(q_p)
    f, s = cell_flux(q, u, 2)
    f_m, s_m = cell_flux(q_m, u_m, 2)
    f_p, s_p = cell_flux(q_p, u_p, 2)
    high = face_flux(f, s, u, f_p, s_p, u_p)
    low = face_flux(f_m, s_m, u_m, f, s, u)
    width_p = wp_ref[...]
    for c in range(8):
        azimuthal = (high[c] - low[c]) / width_p
        out_ref[c, 0] = u[c] - dt * (radial[c] + polar[c] + azimuthal)


def mhd_call(dt, density, velocity, magnetic_vector, pressure, az_low, az_high,
             colat_low, colat_high, width_r, width_t, width_p):
    azim, colat, radial = density.shape
    scalar_block = (1, colat, radial)
    vector_block = (3, 1, colat, radial)

    def clamp_low(a):
        return jnp.maximum(a - 1, 0)

    def clamp_high(a):
        return jnp.minimum(a + 1, azim - 1)

    in_specs = [pl.BlockSpec(memory_space=pltpu.SMEM)]
    for pick in (lambda a: a, clamp_low, clamp_high):
        in_specs += [
            pl.BlockSpec(scalar_block, lambda a, pick=pick: (pick(a), 0, 0)),
            pl.BlockSpec(vector_block, lambda a, pick=pick: (0, pick(a), 0, 0)),
            pl.BlockSpec(vector_block, lambda a, pick=pick: (0, pick(a), 0, 0)),
            pl.BlockSpec(scalar_block, lambda a, pick=pick: (pick(a), 0, 0)),
        ]
    in_specs += [
        pl.BlockSpec((8, 1, colat, radial), lambda a: (0, 0, 0, 0)),
        pl.BlockSpec((8, 1, colat, radial), lambda a: (0, 0, 0, 0)),
        pl.BlockSpec((8, 1, 1, radial), lambda a: (0, a, 0, 0)),
        pl.BlockSpec((8, 1, 1, radial), lambda a: (0, a, 0, 0)),
        pl.BlockSpec((1, radial), lambda a: (0, 0)),
        pl.BlockSpec((1, radial), lambda a: (0, 0)),
        pl.BlockSpec((colat, radial), lambda a: (0, 0)),
    ]
    fields = (density, velocity, magnetic_vector, pressure)
    return pl.pallas_call(
        mhd_kernel,
        grid=(azim,),
        in_specs=in_specs,
        out_specs=pl.BlockSpec((8, 1, colat, radial), lambda a: (0, a, 0, 0)),
        out_shape=jax.ShapeDtypeStruct((8, azim, colat, radial), jnp.float32),
        compiler_params=pltpu.CompilerParams(dimension_semantics=("arbitrary",)),
    )(dt, *fields, *fields, *fields, az_low, az_high, colat_low, colat_high,
      width_r, width_t, width_p)


def mhd_halos(density, velocity, magnetic_vector, pressure, band_pos, band_count):
    fields = [density, velocity[0], velocity[1], velocity[2],
              magnetic_vector[0], magnetic_vector[1], magnetic_vector[2], pressure]
    azim, colat = density.shape[0], density.shape[1]
    az_first = jnp.stack([x[0:1] for x in fields])
    az_last = jnp.stack([x[azim - 1:azim] for x in fields])
    c_first = jnp.stack([x[:, 0:1] for x in fields])
    c_last = jnp.stack([x[:, colat - 1:colat] for x in fields])
    phi_size = lax.axis_size("phi")
    up = [(i, (i + 1) % phi_size) for i in range(phi_size)]
    down = [(j, i) for i, j in up]
    az_low = lax.ppermute(az_last, "phi", up)
    az_high = lax.ppermute(az_first, "phi", down)
    up = [(i, (i + 1) % band_count) for i in range(band_count)]
    down = [(j, i) for i, j in up]
    c_low = lax.ppermute(c_last, "band", up)
    c_high = lax.ppermute(c_first, "band", down)
    c_low = jnp.where(band_pos == 0, c_first, c_low)
    c_high = jnp.where(band_pos == band_count - 1, c_last, c_high)
    return az_low, az_high, c_low, c_high


def body(
    density,
    velocity,
    magnetic_vector,
    pressure,
    fluid_courant_number,
    cosmic_ray_density,
    diffusion_per_bin,
    super_step_scale,
):
    azim_dev = density.shape[0]
    colat_dev = density.shape[1]
    radial_cell_count = density.shape[2]
    band_count = lax.axis_size("band")
    phi_count = lax.axis_size("phi")
    colatitude_count = colat_dev * band_count
    azimuth_cell_count = azim_dev * phi_count
    bin_dev = cosmic_ray_density.shape[0]
    momentum_bin_count = bin_dev * band_count
    outer_shell_count = cosmic_ray_density.shape[3]
    band_pos = lax.axis_index("band")
    mesh_spacing = grid_steps(
        radial_cell_count, colatitude_count, azimuth_cell_count, momentum_bin_count
    )
    fluid_rate, cosmic_ray_rate = rate_limits(
        radial_cell_count,
        outer_shell_count,
        colatitude_count,
        azimuth_cell_count,
        momentum_bin_count,
    )
    radius_full = shell_radii(0, radial_cell_count, radial_cell_count)
    colatitude_local = colatitudes(band_pos * colat_dev, colat_dev, colatitude_count)
    dt = jnp.reshape(fluid_courant_number / fluid_rate, (1,)).astype(jnp.float32)
    fluid_state = mhd_call(
        dt, density, velocity, magnetic_vector, pressure,
        *mhd_halos(density, velocity, magnetic_vector, pressure, band_pos, band_count),
        (radius_full * mesh_spacing[0])[None],
        (radius_full * mesh_spacing[1])[None],
        jnp.sin(colatitude_local)[:, None] * radius_full * mesh_spacing[2],
    )
    first_shell = radial_cell_count - outer_shell_count
    radius_sh = shell_radii(first_shell, outer_shell_count, radial_cell_count)
    colatitude_full = colatitudes(0, colatitude_count, colatitude_count)
    own_fields = jnp.concatenate(
        [velocity[:, :, :, first_shell:], magnetic_vector[:, :, :, first_shell:]], axis=0
    ).astype(jnp.bfloat16)
    wind_half = jnp.zeros(
        (own_fields.shape[0], azim_dev, colatitude_count, outer_shell_count), jnp.bfloat16
    )
    wind_half = lax.dynamic_update_slice(wind_half, own_fields, (0, 0, band_pos * colat_dev, 0))
    for shift in range(1, band_count):
        pairs = [(i, (i + shift) % band_count) for i in range(band_count)]
        piece = lax.ppermute(own_fields, "band", pairs)
        source = (band_pos + band_count - shift) % band_count
        wind_half = lax.dynamic_update_slice(wind_half, piece, (0, 0, source * colat_dev, 0))
    fluid_state, wind_half = lax.optimization_barrier((fluid_state, wind_half))
    wind_vel = wind_half[0:3].astype(jnp.float32)
    azim_pad = padded(wind_half[2], (("phi", 0),), 1).astype(jnp.float32)
    radial_pad = jnp.pad(wind_vel[0], ((0, 0), (0, 0), (1, 1)), mode="edge")
    polar_pad = jnp.pad(wind_vel[1], ((0, 0), (1, 1), (0, 0)), mode="edge")
    spread_half = divergence(
        radial_pad, polar_pad, azim_pad, radius_sh, colatitude_full, mesh_spacing
    ).astype(jnp.bfloat16)
    kappa_here = lax.dynamic_slice_in_dim(diffusion_per_bin, band_pos * bin_dev, bin_dev)
    sts_step = super_step_scale / cosmic_ray_rate
    coef_set = transport_coefficients(
        wind_half[0:3].astype(jnp.float32),
        wind_half[3:6].astype(jnp.float32),
        spread_half.astype(jnp.float32),
        radius_sh,
        colatitude_full,
        mesh_spacing,
    )

    coef_list, up_list, down_list, drift_up, drift_down = coef_set
    coefs = jnp.stack(
        list(coef_list) + list(up_list) + list(down_list)
        + [drift_up / mesh_spacing[3], drift_down / mesh_spacing[3]],
        axis=0,
    )
    scal1 = jnp.reshape(sts_step / 3.0, (1,)).astype(jnp.float32)
    scal2 = jnp.reshape(sts_step / 2.0, (1,)).astype(jnp.float32)
    flags = jnp.stack([band_pos == 0, band_pos == band_count - 1]).astype(jnp.int32)
    bins = cosmic_ray_density.shape[0]
    edges = (
        cosmic_ray_density[:, 0:1],
        cosmic_ray_density[:, azim_dev - 1:azim_dev],
        cosmic_ray_density[0:1],
        cosmic_ray_density[bins - 1:bins],
    )
    edges = [x.astype(jnp.bfloat16) for x in lax.optimization_barrier(edges)]
    az_low, az_high = exchange(edges[0], edges[1], "phi")
    bin_low, bin_high = exchange(edges[2], edges[3], "band")
    first_section, *edges = section_call(
        scal1, flags, kappa_here, cosmic_ray_density, az_low, az_high, bin_low, bin_high, coefs
    )
    steps = edges[0].shape[1]
    az_low, az_high = exchange(edges[0][:, 0:1], edges[1][:, steps - 1:steps], "phi")
    bin_low, bin_high = exchange(edges[2], edges[3], "band")
    cosmic_ray_next = section_call(
        scal2, flags, kappa_here, first_section, az_low, az_high, bin_low, bin_high, coefs,
        cosmic_ray_density,
    )
    return (fluid_state, cosmic_ray_next)


def solution(mesh):
    placed = (
        P("phi", "band", None),
        P(None, "phi", "band", None),
        P(None, "phi", "band", None),
        P("phi", "band", None),
        P(),
        P("band", "phi", None, None),
        P(),
        P(),
    )
    return jax.shard_map(
        body,
        mesh=mesh,
        in_specs=placed,
        out_specs=(P(None, "phi", "band", None), P("band", "phi", None, None)),
        check_vma=False,
    )
```

```python
import functools
import math

import jax
import jax.numpy as jnp
from jax import lax
from jax.experimental import pallas as pl
from jax.experimental.pallas import tpu as pltpu
from jax.sharding import PartitionSpec as P

ADIABATIC = 5.0 / 3.0
INNER_RADIUS = 0.1
R_RATIO = 30.0
COLAT_LOW = math.pi / 6.0
COLAT_SPAN = 2.0 * math.pi / 3.0
P_RATIO = 1000.0
K_RATIO = 0.1
B_FLOOR = 0.1
V_BOUND = 3.0
B_BOUND = 3.0
P_HIGH = 2.0
RHO_LOW = 0.5
KAPPA_HIGH = 0.5


def padded(value, sides, width):
    for axis, dim in sides:
        size, length = (lax.axis_size(axis), value.shape[dim])
        up = [(i, (i + 1) % size) for i in range(size)]
        down = [(j, i) for i, j in up]
        last = lax.slice_in_dim(value, length - width, length, axis=dim)
        leading = lax.slice_in_dim(value, 0, width, axis=dim)
        before = lax.ppermute(last, axis, up)
        after = lax.ppermute(leading, axis, down)
        value = jnp.concatenate([before, value, after], axis=dim)
    return value


def grid_steps(n_radial, n_colat, n_azim, n_bins):
    return (
        math.log(R_RATIO) / n_radial,
        COLAT_SPAN / n_colat,
        2.0 * math.pi / n_azim,
        math.log(P_RATIO) / n_bins,
    )


def rate_limits(n_radial, n_shells, n_colat, n_azim, n_bins):
    radial_spacing, colatitude_spacing, azimuth_spacing, step_m = grid_steps(
        n_radial, n_colat, n_azim, n_bins
    )
    sine_lower = math.sin(COLAT_LOW + 0.5 * colatitude_spacing)
    fluid_radius = INNER_RADIUS * math.exp(0.5 * radial_spacing)
    fastest_limit = V_BOUND + math.sqrt((ADIABATIC * P_HIGH + 3.0 * B_BOUND**2) / RHO_LOW)
    fluid_rate = fastest_limit * (
        1.0 / (fluid_radius * radial_spacing)
        + 1.0 / (fluid_radius * colatitude_spacing)
        + 1.0 / (fluid_radius * sine_lower * azimuth_spacing)
    )
    shell_low = INNER_RADIUS * math.exp(radial_spacing * (n_radial - n_shells + 0.5))
    inv_r = 1.0 / (shell_low * radial_spacing)
    inv_t = 1.0 / (shell_low * colatitude_spacing)
    inv_p = 1.0 / (shell_low * sine_lower * azimuth_spacing)
    cosmic_ray_rate = (
        2.0 * KAPPA_HIGH * (inv_r**2 + inv_t**2 + inv_p**2)
        + V_BOUND * (inv_r + inv_t + inv_p)
        + V_BOUND * (inv_r + inv_t + inv_p + 4.0 / shell_low) / (3.0 * step_m)
    )
    return (fluid_rate, cosmic_ray_rate)


def shell_radii(start_index, cell_count, n_radial):
    cell_index = jnp.arange(cell_count, dtype=jnp.float32) + (start_index + 0.5)
    return INNER_RADIUS * jnp.exp(math.log(R_RATIO) / n_radial * cell_index)


def colatitudes(start_index, cell_count, n_colat):
    cell_index = jnp.arange(cell_count, dtype=jnp.float32) + 0.5
    return COLAT_LOW + COLAT_SPAN * (cell_index + start_index) / n_colat


def edge_fix(values, along_axis, depth, band_pos, axis_count):
    extent = values.shape[along_axis]
    low_ghost = lax.slice_in_dim(values, 0, depth, axis=along_axis)
    high_ghost = lax.slice_in_dim(values, extent - depth, extent, axis=along_axis)
    first_own = lax.slice_in_dim(values, depth, depth + 1, axis=along_axis)
    last_own = lax.slice_in_dim(values, extent - depth - 1, extent - depth, axis=along_axis)
    low_rim = jnp.where(band_pos == 0, first_own, low_ghost)
    high_rim = jnp.where(band_pos == axis_count - 1, last_own, high_ghost)
    middle = lax.slice_in_dim(values, depth, extent - depth, axis=along_axis)
    return jnp.concatenate([low_rim, middle, high_rim], axis=along_axis)


def conserved(primitive):
    density = primitive[0]
    velocity = primitive[1:4]
    magnetic_vector = primitive[4:7]
    pressure = primitive[7]
    energy = (
        pressure / (ADIABATIC - 1.0)
        + 0.5 * density * jnp.sum(velocity * velocity, axis=0)
        + 0.5 * jnp.sum(magnetic_vector * magnetic_vector, axis=0)
    )
    return jnp.concatenate(
        [density[None], density[None] * velocity, magnetic_vector, energy[None]], axis=0
    )


def face_terms(primitive, cell_state, normal):
    density = primitive[0]
    velocity = primitive[1:4]
    magnetic_vector = primitive[4:7]
    pressure = primitive[7]
    v_normal = velocity[normal]
    b_normal = magnetic_vector[normal]
    magnetic = 0.5 * jnp.sum(magnetic_vector * magnetic_vector, axis=0)
    total_p = pressure + magnetic
    momentum = [density * velocity[k] * v_normal - magnetic_vector[k] * b_normal for k in range(3)]
    momentum[normal] = momentum[normal] + total_p
    induction = [v_normal * magnetic_vector[k] - b_normal * velocity[k] for k in range(3)]
    energy_flux = (cell_state[7] + total_p) * v_normal - b_normal * jnp.sum(
        velocity * magnetic_vector, axis=0
    )
    fluxes = jnp.stack([density * v_normal] + momentum + induction + [energy_flux], axis=0)
    speeds = jnp.abs(v_normal) + jnp.sqrt((ADIABATIC * pressure + 2.0 * magnetic) / density)
    return (fluxes, speeds)


def rusanov(primitive, cell_state, normal, along_axis, spacing):
    fluxes, speeds = face_terms(primitive, cell_state, normal)
    length = speeds.shape[along_axis]
    wave_speed = jnp.maximum(
        lax.slice_in_dim(speeds, 0, length - 1, axis=along_axis),
        lax.slice_in_dim(speeds, 1, length, axis=along_axis),
    )
    flux_low = lax.slice_in_dim(fluxes, 0, length - 1, axis=along_axis + 1)
    flux_high = lax.slice_in_dim(fluxes, 1, length, axis=along_axis + 1)
    state_low = lax.slice_in_dim(cell_state, 0, length - 1, axis=along_axis + 1)
    state_high = lax.slice_in_dim(cell_state, 1, length, axis=along_axis + 1)
    face_flux = 0.5 * (flux_low + flux_high) - 0.5 * wave_speed[None] * (state_high - state_low)
    upper = lax.slice_in_dim(face_flux, 1, length - 1, axis=along_axis + 1)
    lower = lax.slice_in_dim(face_flux, 0, length - 2, axis=along_axis + 1)
    return (upper - lower) / spacing


def fluid_update(padded_array, radius_values, colatitude_mesh, timestep_length, mesh_spacing):
    ghosted = jnp.pad(padded_array, ((0, 0), (0, 0), (0, 0), (1, 1)), mode="edge")
    cell_state = conserved(ghosted)
    width_r = radius_values * mesh_spacing[0]
    width_t = radius_values * mesh_spacing[1]
    width_p = jnp.sin(colatitude_mesh)[:, None] * radius_values * mesh_spacing[2]
    radial = rusanov(ghosted[:, 1:-1, 1:-1, :], cell_state[:, 1:-1, 1:-1, :], 0, 2, width_r)
    polar = rusanov(ghosted[:, 1:-1, :, 1:-1], cell_state[:, 1:-1, :, 1:-1], 1, 1, width_t)
    azimuthal = rusanov(ghosted[:, :, 1:-1, 1:-1], cell_state[:, :, 1:-1, 1:-1], 2, 0, width_p)
    return cell_state[:, 1:-1, 1:-1, 1:-1] - timestep_length * (radial + polar + azimuthal)


def divergence(radial_pad, polar_pad, azim_pad, radius_values, colatitude_mesh, mesh_spacing):
    sin_colat = jnp.sin(colatitude_mesh)[:, None]
    cotangent = (jnp.cos(colatitude_mesh) / jnp.sin(colatitude_mesh))[:, None]
    radial_mid = radial_pad[:, :, 1:-1]
    polar_mid = polar_pad[:, 1:-1, :]
    d_radial = (radial_pad[:, :, 2:] - radial_pad[:, :, :-2]) / (
        2.0 * radius_values * mesh_spacing[0]
    )
    d_polar = (polar_pad[:, 2:, :] - polar_pad[:, :-2, :]) / (2.0 * radius_values * mesh_spacing[1])
    d_azim = (azim_pad[2:] - azim_pad[:-2]) / (2.0 * radius_values * sin_colat * mesh_spacing[2])
    return (
        d_radial
        + 2.0 * radial_mid / radius_values
        + d_polar
        + cotangent * polar_mid / radius_values
        + d_azim
    )


def transport_coefficients(
    wind_vel, mag_wind, spread, radius_values, colatitude_mesh, mesh_spacing
):
    width_r = radius_values * mesh_spacing[0]
    width_t = radius_values * mesh_spacing[1]
    width_p = jnp.sin(colatitude_mesh)[:, None] * radius_values * mesh_spacing[2]
    widths = (width_r, width_t, width_p)
    mag_sq = jnp.sum(mag_wind * mag_wind, axis=0) + B_FLOOR
    b_share = K_RATIO + (1.0 - K_RATIO) * mag_wind * mag_wind / mag_sq
    coef_list = [b_share[k] / (widths[k] * widths[k]) for k in range(3)]
    up_list = [jnp.maximum(wind_vel[k], 0.0) / widths[k] for k in range(3)]
    down_list = [jnp.minimum(wind_vel[k], 0.0) / widths[k] for k in range(3)]
    drift_rate = spread / 3.0
    return (
        coef_list,
        up_list,
        down_list,
        jnp.maximum(drift_rate, 0.0),
        jnp.minimum(drift_rate, 0.0),
    )


def transport_rate(extended, coef_set, kappa_col, step_m):
    coef_list, up_list, down_list, drift_up, drift_down = coef_set
    center = extended[1:-1, 1:-1, 1:-1, 1:-1]
    low_cells = (
        extended[1:-1, 1:-1, 1:-1, :-2],
        extended[1:-1, 1:-1, :-2, 1:-1],
        extended[1:-1, :-2, 1:-1, 1:-1],
    )
    high_cells = (
        extended[1:-1, 1:-1, 1:-1, 2:],
        extended[1:-1, 1:-1, 2:, 1:-1],
        extended[1:-1, 2:, 1:-1, 1:-1],
    )
    curvature = coef_list[0] * (high_cells[0] - 2.0 * center + low_cells[0])
    curvature = curvature + coef_list[1] * (high_cells[1] - 2.0 * center + low_cells[1])
    curvature = curvature + coef_list[2] * (high_cells[2] - 2.0 * center + low_cells[2])
    diffusion = kappa_col[:, None, None, None] * curvature
    advection = up_list[0] * (center - low_cells[0]) + down_list[0] * (high_cells[0] - center)
    advection = (
        advection + up_list[1] * (center - low_cells[1]) + down_list[1] * (high_cells[1] - center)
    )
    advection = (
        advection + up_list[2] * (center - low_cells[2]) + down_list[2] * (high_cells[2] - center)
    )
    bin_low = extended[:-2, 1:-1, 1:-1, 1:-1]
    bin_high = extended[2:, 1:-1, 1:-1, 1:-1]
    momentum = (drift_up * (bin_high - center) + drift_down * (center - bin_low)) / step_m
    return diffusion - advection + momentum


ROWS = 16


def _vec(shape, scalar):
    return jnp.full(shape, scalar, jnp.int32)


def section_kernel(scal_ref, flag_ref, kappa_ref, g_ref, gp_ref, gn_ref, azlo_ref, azhi_ref,
                   binlo_ref, binhi_ref, coef_ref, *rest, second):
    if second:
        f0_ref, out_ref = rest
    else:
        out_ref, az_first_ref, az_last_ref, bin_first_ref, bin_last_ref = rest
    step = pl.program_id(0)
    last_step = pl.num_programs(0) - 1
    bins, planes, colat, shells = g_ref.shape
    shape = (ROWS, shells)
    row = lax.broadcasted_iota(jnp.int32, shape, 0)
    lane = lax.broadcasted_iota(jnp.int32, shape, 1)
    first_az = _vec(shape, step) == 0
    last_az = _vec(shape, step) == last_step
    band_first = _vec(shape, flag_ref[0]) == 1
    band_last = _vec(shape, flag_ref[1]) == 1
    scale = scal_ref[0]

    def chunk(k, i, r0, kap, edge):
        rows = slice(r0, r0 + ROWS)
        center = g_ref[k, i, rows, :]
        if r0 == 0:
            low_t = jnp.where(row == 0, center, pltpu.roll(center, 1, 0))
        else:
            low_t = g_ref[k, i, r0 - 1:r0 - 1 + ROWS, :]
        if r0 + ROWS == colat:
            high_t = jnp.where(row == ROWS - 1, center, pltpu.roll(center, ROWS - 1, 0))
        else:
            high_t = g_ref[k, i, r0 + 1:r0 + 1 + ROWS, :]
        low_r = jnp.where(lane == 0, center, pltpu.roll(center, 1, 1))
        high_r = jnp.where(lane == shells - 1, center, pltpu.roll(center, shells - 1, 1))
        if i == 0:
            low_p = jnp.where(first_az, azlo_ref[k, 0, rows, :].astype(jnp.float32), gp_ref[k, 0, rows, :])
        else:
            low_p = g_ref[k, i - 1, rows, :]
        if i == planes - 1:
            high_p = jnp.where(last_az, azhi_ref[k, 0, rows, :].astype(jnp.float32), gn_ref[k, 0, rows, :])
        else:
            high_p = g_ref[k, i + 1, rows, :]
        if edge == "low":
            low_b = jnp.where(band_first, center, binlo_ref[0, i, rows, :].astype(jnp.float32))
        else:
            low_b = g_ref[k - 1, i, rows, :]
        if edge == "high":
            high_b = jnp.where(band_last, center, binhi_ref[0, i, rows, :].astype(jnp.float32))
        else:
            high_b = g_ref[k + 1, i, rows, :]
        d_lo = (center - low_r, center - low_t, center - low_p)
        d_hi = (high_r - center, high_t - center, high_p - center)
        curvature = coef_ref[0, i, rows, :] * (d_hi[0] - d_lo[0])
        curvature = curvature + coef_ref[1, i, rows, :] * (d_hi[1] - d_lo[1])
        curvature = curvature + coef_ref[2, i, rows, :] * (d_hi[2] - d_lo[2])
        advection = coef_ref[3, i, rows, :] * d_lo[0] + coef_ref[6, i, rows, :] * d_hi[0]
        advection = advection + coef_ref[4, i, rows, :] * d_lo[1] + coef_ref[7, i, rows, :] * d_hi[1]
        advection = advection + coef_ref[5, i, rows, :] * d_lo[2] + coef_ref[8, i, rows, :] * d_hi[2]
        momentum = coef_ref[9, i, rows, :] * (high_b - center) + coef_ref[10, i, rows, :] * (center - low_b)
        rate = kap * curvature - advection + momentum
        if second:
            value = 1.5 * center - 0.5 * f0_ref[k, i, rows, :] + scale * rate
        else:
            value = center + scale * rate
        out_ref[k, i, rows, :] = value
        if not second:
            half = value.astype(jnp.bfloat16)
            if i == 0:
                az_first_ref[k, 0, rows, :] = half
            if i == planes - 1:
                az_last_ref[k, 0, rows, :] = half
            if edge == "low":
                bin_first_ref[0, i, rows, :] = half
            if edge == "high":
                bin_last_ref[0, i, rows, :] = half

    def all_rows(k, edge):
        kap = kappa_ref[k]
        for i in range(planes):
            for r0 in range(0, colat, ROWS):
                chunk(k, i, r0, kap, edge)

    all_rows(0, "low")

    def middle(k, carry):
        all_rows(k, None)
        return carry

    lax.fori_loop(1, bins - 1, middle, 0)
    all_rows(bins - 1, "high")


PLANES = 2


def section_call(scal, flags, kappa, g, az_low, az_high, bin_low, bin_high, coefs, f0=None):
    bins, azim, colat, shells = g.shape
    block = (bins, PLANES, colat, shells)
    plane = (bins, 1, colat, shells)
    bin_block = (1, PLANES, colat, shells)
    smem = pl.BlockSpec(memory_space=pltpu.SMEM)
    in_specs = [
        smem,
        smem,
        smem,
        pl.BlockSpec(block, lambda a: (0, a, 0, 0)),
        pl.BlockSpec(plane, lambda a: (0, jnp.maximum(a * PLANES - 1, 0), 0, 0)),
        pl.BlockSpec(plane, lambda a: (0, jnp.minimum(a * PLANES + PLANES, azim - 1), 0, 0)),
        pl.BlockSpec(plane, lambda a: (0, 0, 0, 0)),
        pl.BlockSpec(plane, lambda a: (0, 0, 0, 0)),
        pl.BlockSpec(bin_block, lambda a: (0, a, 0, 0)),
        pl.BlockSpec(bin_block, lambda a: (0, a, 0, 0)),
        pl.BlockSpec((coefs.shape[0], PLANES, colat, shells), lambda a: (0, a, 0, 0)),
    ]
    args = [scal, flags, kappa, g, g, g, az_low, az_high, bin_low, bin_high, coefs]
    out_specs = pl.BlockSpec(block, lambda a: (0, a, 0, 0))
    out_shape = jax.ShapeDtypeStruct(g.shape, jnp.float32)
    if f0 is not None:
        in_specs.append(pl.BlockSpec(block, lambda a: (0, a, 0, 0)))
        args.append(f0)
    else:
        out_specs = [
            out_specs,
            pl.BlockSpec(plane, lambda a: (0, a, 0, 0)),
            pl.BlockSpec(plane, lambda a: (0, a, 0, 0)),
            pl.BlockSpec(bin_block, lambda a: (0, a, 0, 0)),
            pl.BlockSpec(bin_block, lambda a: (0, a, 0, 0)),
        ]
        half_plane = jax.ShapeDtypeStruct((bins, azim // PLANES, colat, shells), jnp.bfloat16)
        half_bin = jax.ShapeDtypeStruct((1, azim, colat, shells), jnp.bfloat16)
        out_shape = [out_shape, half_plane, half_plane, half_bin, half_bin]
    return pl.pallas_call(
        functools.partial(section_kernel, second=f0 is not None),
        grid=(azim // PLANES,),
        in_specs=in_specs,
        out_specs=out_specs,
        out_shape=out_shape,
        compiler_params=pltpu.CompilerParams(dimension_semantics=("arbitrary",)),
    )(*args)


def exchange(first, last, axis):
    size = lax.axis_size(axis)
    up = [(i, (i + 1) % size) for i in range(size)]
    down = [(j, i) for i, j in up]
    return lax.ppermute(last, axis, up), lax.ppermute(first, axis, down)


def cell_state(q):
    rho, v, b, p = q[0], q[1:4], q[4:7], q[7]
    vv = v[0] * v[0] + v[1] * v[1] + v[2] * v[2]
    bb = b[0] * b[0] + b[1] * b[1] + b[2] * b[2]
    energy = p / (ADIABATIC - 1.0) + 0.5 * rho * vv + 0.5 * bb
    return [rho, rho * v[0], rho * v[1], rho * v[2], b[0], b[1], b[2], energy]


def cell_flux(q, u, normal):
    rho, v, b, p = q[0], q[1:4], q[4:7], q[7]
    vn, bn = v[normal], b[normal]
    magnetic = 0.5 * (b[0] * b[0] + b[1] * b[1] + b[2] * b[2])
    total_p = p + magnetic
    momentum = [rho * v[k] * vn - b[k] * bn for k in range(3)]
    momentum[normal] = momentum[normal] + total_p
    induction = [vn * b[k] - bn * v[k] for k in range(3)]
    energy = (u[7] + total_p) * vn - bn * (v[0] * b[0] + v[1] * b[1] + v[2] * b[2])
    speed = jnp.abs(vn) + jnp.sqrt((ADIABATIC * p + 2.0 * magnetic) / rho)
    return [rho * vn] + momentum + induction + [energy], speed


def face_flux(f_low, s_low, u_low, f_high, s_high, u_high):
    wave = jnp.maximum(s_low, s_high)
    return [0.5 * (f_low[c] + f_high[c]) - 0.5 * wave * (u_high[c] - u_low[c]) for c in range(8)]


def mhd_kernel(dt_ref, rho_c, v_c, b_c, p_c, rho_m, v_m, b_m, p_m, rho_p, v_p, b_p, p_p,
               azlo_ref, azhi_ref, clo_ref, chi_ref, wr_ref, wt_ref, wp_ref, *rest, offset, last_step):
    out_ref = rest[-1]
    step = pl.program_id(0) + offset

    def prim(rho_ref, v_ref, b_ref, p_ref):
        return [rho_ref[0], v_ref[0, 0], v_ref[1, 0], v_ref[2, 0],
                b_ref[0, 0], b_ref[1, 0], b_ref[2, 0], p_ref[0]]

    q = prim(rho_c, v_c, b_c, p_c)
    shape = q[0].shape
    nrow, nlane = shape
    row = lax.broadcasted_iota(jnp.int32, shape, 0)
    lane = lax.broadcasted_iota(jnp.int32, shape, 1)
    first_az = _vec(shape, step) == 0
    last_az = _vec(shape, step) == last_step
    q_m = prim(rho_m, v_m, b_m, p_m)
    q_p = prim(rho_p, v_p, b_p, p_p)
    q_m = [jnp.where(first_az, azlo_ref[c, 0], q_m[c]) for c in range(8)]
    q_p = [jnp.where(last_az, azhi_ref[c, 0], q_p[c]) for c in range(8)]
    u = cell_state(q)
    dt = dt_ref[0]

    def lane_next(x):
        return jnp.where(lane == nlane - 1, x, pltpu.roll(x, nlane - 1, 1))

    f, s = cell_flux(q, u, 0)
    high = face_flux(f, s, u, [lane_next(x) for x in f], lane_next(s), [lane_next(x) for x in u])
    low = [jnp.where(lane == 0, f[c], pltpu.roll(high[c], 1, 1)) for c in range(8)]
    width_r = wr_ref[...]
    radial = [(high[c] - low[c]) / width_r for c in range(8)]

    q_l = [clo_ref[c, 0] for c in range(8)]
    q_h = [chi_ref[c, 0] for c in range(8)]
    u_l = cell_state(q_l)
    u_h = cell_state(q_h)
    f, s = cell_flux(q, u, 1)
    f_l, s_l = cell_flux(q_l, u_l, 1)
    f_h, s_h = cell_flux(q_h, u_h, 1)

    def row_next(x, h):
        return jnp.where(row == nrow - 1, jnp.broadcast_to(h, shape), pltpu.roll(x, nrow - 1, 0))

    high = face_flux(f, s, u, [row_next(f[c], f_h[c]) for c in range(8)], row_next(s, s_h),
                     [row_next(u[c], u_h[c]) for c in range(8)])
    first = face_flux(f_l, s_l, u_l, f, s, u)
    low = [jnp.where(row == 0, first[c], pltpu.roll(high[c], 1, 0)) for c in range(8)]
    width_t = wt_ref[...]
    polar = [(high[c] - low[c]) / width_t for c in range(8)]

    u_m = cell_state(q_m)
    u_p = cell_state(q_p)
    f, s = cell_flux(q, u, 2)
    f_m, s_m = cell_flux(q_m, u_m, 2)
    f_p, s_p = cell_flux(q_p, u_p, 2)
    high = face_flux(f, s, u, f_p, s_p, u_p)
    low = face_flux(f_m, s_m, u_m, f, s, u)
    width_p = wp_ref[...]
    for c in range(8):
        azimuthal = (high[c] - low[c]) / width_p
        out_ref[c, 0] = u[c] - dt * (radial[c] + polar[c] + azimuthal)


def mhd_call(dt, density, velocity, magnetic_vector, pressure, az_low, az_high,
             colat_low, colat_high, width_r, width_t, width_p, offset, count, previous=None):
    azim, colat, radial = density.shape
    scalar_block = (1, colat, radial)
    vector_block = (3, 1, colat, radial)

    def own(a):
        return a + offset

    def clamp_low(a):
        return jnp.maximum(a + offset - 1, 0)

    def clamp_high(a):
        return jnp.minimum(a + offset + 1, azim - 1)

    in_specs = [pl.BlockSpec(memory_space=pltpu.SMEM)]
    for pick in (own, clamp_low, clamp_high):
        in_specs += [
            pl.BlockSpec(scalar_block, lambda a, pick=pick: (pick(a), 0, 0)),
            pl.BlockSpec(vector_block, lambda a, pick=pick: (0, pick(a), 0, 0)),
            pl.BlockSpec(vector_block, lambda a, pick=pick: (0, pick(a), 0, 0)),
            pl.BlockSpec(scalar_block, lambda a, pick=pick: (pick(a), 0, 0)),
        ]
    in_specs += [
        pl.BlockSpec((8, 1, colat, radial), lambda a: (0, 0, 0, 0)),
        pl.BlockSpec((8, 1, colat, radial), lambda a: (0, 0, 0, 0)),
        pl.BlockSpec((8, 1, 1, radial), lambda a: (0, a + offset, 0, 0)),
        pl.BlockSpec((8, 1, 1, radial), lambda a: (0, a + offset, 0, 0)),
        pl.BlockSpec((1, radial), lambda a: (0, 0)),
        pl.BlockSpec((1, radial), lambda a: (0, 0)),
        pl.BlockSpec((colat, radial), lambda a: (0, 0)),
    ]
    fields = (density, velocity, magnetic_vector, pressure)
    args = [dt, *fields, *fields, *fields, az_low, az_high, colat_low, colat_high,
            width_r, width_t, width_p]
    aliases = {}
    if previous is not None:
        in_specs.append(pl.BlockSpec(memory_space=pl.ANY))
        aliases = {len(args): 0}
        args.append(previous)
    return pl.pallas_call(
        functools.partial(mhd_kernel, offset=offset, last_step=azim - 1),
        grid=(count,),
        in_specs=in_specs,
        out_specs=pl.BlockSpec((8, 1, colat, radial), lambda a: (0, a + offset, 0, 0)),
        out_shape=jax.ShapeDtypeStruct((8, azim, colat, radial), jnp.float32),
        input_output_aliases=aliases,
        compiler_params=pltpu.CompilerParams(dimension_semantics=("arbitrary",)),
    )(*args)


def mhd_halos(density, velocity, magnetic_vector, pressure, band_pos, band_count):
    fields = [density, velocity[0], velocity[1], velocity[2],
              magnetic_vector[0], magnetic_vector[1], magnetic_vector[2], pressure]
    azim, colat = density.shape[0], density.shape[1]
    az_first = jnp.stack([x[0:1] for x in fields])
    az_last = jnp.stack([x[azim - 1:azim] for x in fields])
    c_first = jnp.stack([x[:, 0:1] for x in fields])
    c_last = jnp.stack([x[:, colat - 1:colat] for x in fields])
    phi_size = lax.axis_size("phi")
    up = [(i, (i + 1) % phi_size) for i in range(phi_size)]
    down = [(j, i) for i, j in up]
    az_low = lax.ppermute(az_last, "phi", up)
    az_high = lax.ppermute(az_first, "phi", down)
    up = [(i, (i + 1) % band_count) for i in range(band_count)]
    down = [(j, i) for i, j in up]
    c_low = lax.ppermute(c_last, "band", up)
    c_high = lax.ppermute(c_first, "band", down)
    c_low = jnp.where(band_pos == 0, c_first, c_low)
    c_high = jnp.where(band_pos == band_count - 1, c_last, c_high)
    return az_low, az_high, c_low, c_high


def body(
    density,
    velocity,
    magnetic_vector,
    pressure,
    fluid_courant_number,
    cosmic_ray_density,
    diffusion_per_bin,
    super_step_scale,
):
    azim_dev = density.shape[0]
    colat_dev = density.shape[1]
    radial_cell_count = density.shape[2]
    band_count = lax.axis_size("band")
    phi_count = lax.axis_size("phi")
    colatitude_count = colat_dev * band_count
    azimuth_cell_count = azim_dev * phi_count
    bin_dev = cosmic_ray_density.shape[0]
    momentum_bin_count = bin_dev * band_count
    outer_shell_count = cosmic_ray_density.shape[3]
    band_pos = lax.axis_index("band")
    mesh_spacing = grid_steps(
        radial_cell_count, colatitude_count, azimuth_cell_count, momentum_bin_count
    )
    fluid_rate, cosmic_ray_rate = rate_limits(
        radial_cell_count,
        outer_shell_count,
        colatitude_count,
        azimuth_cell_count,
        momentum_bin_count,
    )
    radius_full = shell_radii(0, radial_cell_count, radial_cell_count)
    colatitude_local = colatitudes(band_pos * colat_dev, colat_dev, colatitude_count)
    dt = jnp.reshape(fluid_courant_number / fluid_rate, (1,)).astype(jnp.float32)
    mhd_args = (
        dt, density, velocity, magnetic_vector, pressure,
        *mhd_halos(density, velocity, magnetic_vector, pressure, band_pos, band_count),
        (radius_full * mesh_spacing[0])[None],
        (radius_full * mesh_spacing[1])[None],
        jnp.sin(colatitude_local)[:, None] * radius_full * mesh_spacing[2],
    )
    first_planes = azim_dev // 2
    fluid_state = mhd_call(*mhd_args, 0, first_planes)
    first_shell = radial_cell_count - outer_shell_count
    radius_sh = shell_radii(first_shell, outer_shell_count, radial_cell_count)
    colatitude_full = colatitudes(0, colatitude_count, colatitude_count)
    own_fields = jnp.concatenate(
        [velocity[:, :, :, first_shell:], magnetic_vector[:, :, :, first_shell:]], axis=0
    ).astype(jnp.bfloat16)
    wind_half = lax.all_gather(own_fields, "band", axis=0)
    wind_half = jnp.transpose(wind_half, (1, 2, 0, 3, 4)).reshape(
        own_fields.shape[0], azim_dev, colatitude_count, outer_shell_count
    )
    fluid_state, wind_half = lax.optimization_barrier((fluid_state, wind_half))
    wind_vel = wind_half[0:3].astype(jnp.float32)
    azim_pad = padded(wind_half[2], (("phi", 0),), 1).astype(jnp.float32)
    radial_pad = jnp.pad(wind_vel[0], ((0, 0), (0, 0), (1, 1)), mode="edge")
    polar_pad = jnp.pad(wind_vel[1], ((0, 0), (1, 1), (0, 0)), mode="edge")
    spread_half = divergence(
        radial_pad, polar_pad, azim_pad, radius_sh, colatitude_full, mesh_spacing
    ).astype(jnp.bfloat16)
    kappa_here = lax.dynamic_slice_in_dim(diffusion_per_bin, band_pos * bin_dev, bin_dev)
    sts_step = super_step_scale / cosmic_ray_rate
    coef_set = transport_coefficients(
        wind_half[0:3].astype(jnp.float32),
        wind_half[3:6].astype(jnp.float32),
        spread_half.astype(jnp.float32),
        radius_sh,
        colatitude_full,
        mesh_spacing,
    )

    coef_list, up_list, down_list, drift_up, drift_down = coef_set
    coefs = jnp.stack(
        list(coef_list) + list(up_list) + list(down_list)
        + [drift_up / mesh_spacing[3], drift_down / mesh_spacing[3]],
        axis=0,
    )
    scal1 = jnp.reshape(sts_step / 3.0, (1,)).astype(jnp.float32)
    scal2 = jnp.reshape(sts_step / 2.0, (1,)).astype(jnp.float32)
    flags = jnp.stack([band_pos == 0, band_pos == band_count - 1]).astype(jnp.int32)
    bins = cosmic_ray_density.shape[0]
    edges = (
        cosmic_ray_density[:, 0:1],
        cosmic_ray_density[:, azim_dev - 1:azim_dev],
        cosmic_ray_density[0:1],
        cosmic_ray_density[bins - 1:bins],
    )
    edges = [x.astype(jnp.bfloat16) for x in lax.optimization_barrier(edges)]
    az_low, az_high = exchange(edges[0], edges[1], "phi")
    bin_low, bin_high = exchange(edges[2], edges[3], "band")
    first_section, *edges = section_call(
        scal1, flags, kappa_here, cosmic_ray_density, az_low, az_high, bin_low, bin_high, coefs
    )
    steps = edges[0].shape[1]
    az_low, az_high = exchange(edges[0][:, 0:1], edges[1][:, steps - 1:steps], "phi")
    bin_low, bin_high = exchange(edges[2], edges[3], "band")
    fluid_state, first_section = lax.optimization_barrier((fluid_state, first_section))
    fluid_state = mhd_call(
        *mhd_args, first_planes, azim_dev - first_planes, previous=fluid_state
    )
    fluid_state, az_low, az_high, bin_low, bin_high = lax.optimization_barrier(
        (fluid_state, az_low, az_high, bin_low, bin_high)
    )
    cosmic_ray_next = section_call(
        scal2, flags, kappa_here, first_section, az_low, az_high, bin_low, bin_high, coefs,
        cosmic_ray_density,
    )
    return (fluid_state, cosmic_ray_next)


def solution(mesh):
    placed = (
        P("phi", "band", None),
        P(None, "phi", "band", None),
        P(None, "phi", "band", None),
        P("phi", "band", None),
        P(),
        P("band", "phi", None, None),
        P(),
        P(),
    )
    return jax.shard_map(
        body,
        mesh=mesh,
        in_specs=placed,
        out_specs=(P(None, "phi", "band", None), P("band", "phi", None, None)),
        check_vma=False,
    )
```

```python
import functools
import math

import jax
import jax.numpy as jnp
from jax import lax
from jax.experimental import pallas as pl
from jax.experimental.pallas import tpu as pltpu
from jax.sharding import PartitionSpec as P

ADIABATIC = 5.0 / 3.0
INNER_RADIUS = 0.1
R_RATIO = 30.0
COLAT_LOW = math.pi / 6.0
COLAT_SPAN = 2.0 * math.pi / 3.0
P_RATIO = 1000.0
K_RATIO = 0.1
B_FLOOR = 0.1
V_BOUND = 3.0
B_BOUND = 3.0
P_HIGH = 2.0
RHO_LOW = 0.5
KAPPA_HIGH = 0.5


def padded(value, sides, width):
    for axis, dim in sides:
        size, length = (lax.axis_size(axis), value.shape[dim])
        up = [(i, (i + 1) % size) for i in range(size)]
        down = [(j, i) for i, j in up]
        last = lax.slice_in_dim(value, length - width, length, axis=dim)
        leading = lax.slice_in_dim(value, 0, width, axis=dim)
        before = lax.ppermute(last, axis, up)
        after = lax.ppermute(leading, axis, down)
        value = jnp.concatenate([before, value, after], axis=dim)
    return value


def grid_steps(n_radial, n_colat, n_azim, n_bins):
    return (
        math.log(R_RATIO) / n_radial,
        COLAT_SPAN / n_colat,
        2.0 * math.pi / n_azim,
        math.log(P_RATIO) / n_bins,
    )


def rate_limits(n_radial, n_shells, n_colat, n_azim, n_bins):
    radial_spacing, colatitude_spacing, azimuth_spacing, step_m = grid_steps(
        n_radial, n_colat, n_azim, n_bins
    )
    sine_lower = math.sin(COLAT_LOW + 0.5 * colatitude_spacing)
    fluid_radius = INNER_RADIUS * math.exp(0.5 * radial_spacing)
    fastest_limit = V_BOUND + math.sqrt((ADIABATIC * P_HIGH + 3.0 * B_BOUND**2) / RHO_LOW)
    fluid_rate = fastest_limit * (
        1.0 / (fluid_radius * radial_spacing)
        + 1.0 / (fluid_radius * colatitude_spacing)
        + 1.0 / (fluid_radius * sine_lower * azimuth_spacing)
    )
    shell_low = INNER_RADIUS * math.exp(radial_spacing * (n_radial - n_shells + 0.5))
    inv_r = 1.0 / (shell_low * radial_spacing)
    inv_t = 1.0 / (shell_low * colatitude_spacing)
    inv_p = 1.0 / (shell_low * sine_lower * azimuth_spacing)
    cosmic_ray_rate = (
        2.0 * KAPPA_HIGH * (inv_r**2 + inv_t**2 + inv_p**2)
        + V_BOUND * (inv_r + inv_t + inv_p)
        + V_BOUND * (inv_r + inv_t + inv_p + 4.0 / shell_low) / (3.0 * step_m)
    )
    return (fluid_rate, cosmic_ray_rate)


def shell_radii(start_index, cell_count, n_radial):
    cell_index = jnp.arange(cell_count, dtype=jnp.float32) + (start_index + 0.5)
    return INNER_RADIUS * jnp.exp(math.log(R_RATIO) / n_radial * cell_index)


def colatitudes(start_index, cell_count, n_colat):
    cell_index = jnp.arange(cell_count, dtype=jnp.float32) + 0.5
    return COLAT_LOW + COLAT_SPAN * (cell_index + start_index) / n_colat


def edge_fix(values, along_axis, depth, band_pos, axis_count):
    extent = values.shape[along_axis]
    low_ghost = lax.slice_in_dim(values, 0, depth, axis=along_axis)
    high_ghost = lax.slice_in_dim(values, extent - depth, extent, axis=along_axis)
    first_own = lax.slice_in_dim(values, depth, depth + 1, axis=along_axis)
    last_own = lax.slice_in_dim(values, extent - depth - 1, extent - depth, axis=along_axis)
    low_rim = jnp.where(band_pos == 0, first_own, low_ghost)
    high_rim = jnp.where(band_pos == axis_count - 1, last_own, high_ghost)
    middle = lax.slice_in_dim(values, depth, extent - depth, axis=along_axis)
    return jnp.concatenate([low_rim, middle, high_rim], axis=along_axis)


def conserved(primitive):
    density = primitive[0]
    velocity = primitive[1:4]
    magnetic_vector = primitive[4:7]
    pressure = primitive[7]
    energy = (
        pressure / (ADIABATIC - 1.0)
        + 0.5 * density * jnp.sum(velocity * velocity, axis=0)
        + 0.5 * jnp.sum(magnetic_vector * magnetic_vector, axis=0)
    )
    return jnp.concatenate(
        [density[None], density[None] * velocity, magnetic_vector, energy[None]], axis=0
    )


def face_terms(primitive, cell_state, normal):
    density = primitive[0]
    velocity = primitive[1:4]
    magnetic_vector = primitive[4:7]
    pressure = primitive[7]
    v_normal = velocity[normal]
    b_normal = magnetic_vector[normal]
    magnetic = 0.5 * jnp.sum(magnetic_vector * magnetic_vector, axis=0)
    total_p = pressure + magnetic
    momentum = [density * velocity[k] * v_normal - magnetic_vector[k] * b_normal for k in range(3)]
    momentum[normal] = momentum[normal] + total_p
    induction = [v_normal * magnetic_vector[k] - b_normal * velocity[k] for k in range(3)]
    energy_flux = (cell_state[7] + total_p) * v_normal - b_normal * jnp.sum(
        velocity * magnetic_vector, axis=0
    )
    fluxes = jnp.stack([density * v_normal] + momentum + induction + [energy_flux], axis=0)
    speeds = jnp.abs(v_normal) + jnp.sqrt((ADIABATIC * pressure + 2.0 * magnetic) / density)
    return (fluxes, speeds)


def rusanov(primitive, cell_state, normal, along_axis, spacing):
    fluxes, speeds = face_terms(primitive, cell_state, normal)
    length = speeds.shape[along_axis]
    wave_speed = jnp.maximum(
        lax.slice_in_dim(speeds, 0, length - 1, axis=along_axis),
        lax.slice_in_dim(speeds, 1, length, axis=along_axis),
    )
    flux_low = lax.slice_in_dim(fluxes, 0, length - 1, axis=along_axis + 1)
    flux_high = lax.slice_in_dim(fluxes, 1, length, axis=along_axis + 1)
    state_low = lax.slice_in_dim(cell_state, 0, length - 1, axis=along_axis + 1)
    state_high = lax.slice_in_dim(cell_state, 1, length, axis=along_axis + 1)
    face_flux = 0.5 * (flux_low + flux_high) - 0.5 * wave_speed[None] * (state_high - state_low)
    upper = lax.slice_in_dim(face_flux, 1, length - 1, axis=along_axis + 1)
    lower = lax.slice_in_dim(face_flux, 0, length - 2, axis=along_axis + 1)
    return (upper - lower) / spacing


def fluid_update(padded_array, radius_values, colatitude_mesh, timestep_length, mesh_spacing):
    ghosted = jnp.pad(padded_array, ((0, 0), (0, 0), (0, 0), (1, 1)), mode="edge")
    cell_state = conserved(ghosted)
    width_r = radius_values * mesh_spacing[0]
    width_t = radius_values * mesh_spacing[1]
    width_p = jnp.sin(colatitude_mesh)[:, None] * radius_values * mesh_spacing[2]
    radial = rusanov(ghosted[:, 1:-1, 1:-1, :], cell_state[:, 1:-1, 1:-1, :], 0, 2, width_r)
    polar = rusanov(ghosted[:, 1:-1, :, 1:-1], cell_state[:, 1:-1, :, 1:-1], 1, 1, width_t)
    azimuthal = rusanov(ghosted[:, :, 1:-1, 1:-1], cell_state[:, :, 1:-1, 1:-1], 2, 0, width_p)
    return cell_state[:, 1:-1, 1:-1, 1:-1] - timestep_length * (radial + polar + azimuthal)


def divergence(radial_pad, polar_pad, azim_pad, radius_values, colatitude_mesh, mesh_spacing):
    sin_colat = jnp.sin(colatitude_mesh)[:, None]
    cotangent = (jnp.cos(colatitude_mesh) / jnp.sin(colatitude_mesh))[:, None]
    radial_mid = radial_pad[:, :, 1:-1]
    polar_mid = polar_pad[:, 1:-1, :]
    d_radial = (radial_pad[:, :, 2:] - radial_pad[:, :, :-2]) / (
        2.0 * radius_values * mesh_spacing[0]
    )
    d_polar = (polar_pad[:, 2:, :] - polar_pad[:, :-2, :]) / (2.0 * radius_values * mesh_spacing[1])
    d_azim = (azim_pad[2:] - azim_pad[:-2]) / (2.0 * radius_values * sin_colat * mesh_spacing[2])
    return (
        d_radial
        + 2.0 * radial_mid / radius_values
        + d_polar
        + cotangent * polar_mid / radius_values
        + d_azim
    )


def transport_coefficients(
    wind_vel, mag_wind, spread, radius_values, colatitude_mesh, mesh_spacing
):
    width_r = radius_values * mesh_spacing[0]
    width_t = radius_values * mesh_spacing[1]
    width_p = jnp.sin(colatitude_mesh)[:, None] * radius_values * mesh_spacing[2]
    widths = (width_r, width_t, width_p)
    mag_sq = jnp.sum(mag_wind * mag_wind, axis=0) + B_FLOOR
    b_share = K_RATIO + (1.0 - K_RATIO) * mag_wind * mag_wind / mag_sq
    coef_list = [b_share[k] / (widths[k] * widths[k]) for k in range(3)]
    up_list = [jnp.maximum(wind_vel[k], 0.0) / widths[k] for k in range(3)]
    down_list = [jnp.minimum(wind_vel[k], 0.0) / widths[k] for k in range(3)]
    drift_rate = spread / 3.0
    return (
        coef_list,
        up_list,
        down_list,
        jnp.maximum(drift_rate, 0.0),
        jnp.minimum(drift_rate, 0.0),
    )


def transport_rate(extended, coef_set, kappa_col, step_m):
    coef_list, up_list, down_list, drift_up, drift_down = coef_set
    center = extended[1:-1, 1:-1, 1:-1, 1:-1]
    low_cells = (
        extended[1:-1, 1:-1, 1:-1, :-2],
        extended[1:-1, 1:-1, :-2, 1:-1],
        extended[1:-1, :-2, 1:-1, 1:-1],
    )
    high_cells = (
        extended[1:-1, 1:-1, 1:-1, 2:],
        extended[1:-1, 1:-1, 2:, 1:-1],
        extended[1:-1, 2:, 1:-1, 1:-1],
    )
    curvature = coef_list[0] * (high_cells[0] - 2.0 * center + low_cells[0])
    curvature = curvature + coef_list[1] * (high_cells[1] - 2.0 * center + low_cells[1])
    curvature = curvature + coef_list[2] * (high_cells[2] - 2.0 * center + low_cells[2])
    diffusion = kappa_col[:, None, None, None] * curvature
    advection = up_list[0] * (center - low_cells[0]) + down_list[0] * (high_cells[0] - center)
    advection = (
        advection + up_list[1] * (center - low_cells[1]) + down_list[1] * (high_cells[1] - center)
    )
    advection = (
        advection + up_list[2] * (center - low_cells[2]) + down_list[2] * (high_cells[2] - center)
    )
    bin_low = extended[:-2, 1:-1, 1:-1, 1:-1]
    bin_high = extended[2:, 1:-1, 1:-1, 1:-1]
    momentum = (drift_up * (bin_high - center) + drift_down * (center - bin_low)) / step_m
    return diffusion - advection + momentum


ROWS = 16


def _vec(shape, scalar):
    return jnp.full(shape, scalar, jnp.int32)


def section_kernel(scal_ref, flag_ref, kappa_ref, g_ref, gp_ref, gn_ref, azlo_ref, azhi_ref,
                   binlo_ref, binhi_ref, coef_ref, *rest, second):
    if second:
        f0_ref, out_ref = rest
    else:
        out_ref, az_first_ref, az_last_ref, bin_first_ref, bin_last_ref = rest
    step = pl.program_id(0)
    last_step = pl.num_programs(0) - 1
    bins, planes, colat, shells = g_ref.shape
    shape = (ROWS, shells)
    row = lax.broadcasted_iota(jnp.int32, shape, 0)
    lane = lax.broadcasted_iota(jnp.int32, shape, 1)
    first_az = _vec(shape, step) == 0
    last_az = _vec(shape, step) == last_step
    band_first = _vec(shape, flag_ref[0]) == 1
    band_last = _vec(shape, flag_ref[1]) == 1
    scale = scal_ref[0]

    def chunk(k, i, r0, kap, edge):
        rows = slice(r0, r0 + ROWS)
        center = g_ref[k, i, rows, :]
        if r0 == 0:
            low_t = jnp.where(row == 0, center, pltpu.roll(center, 1, 0))
        else:
            low_t = g_ref[k, i, r0 - 1:r0 - 1 + ROWS, :]
        if r0 + ROWS == colat:
            high_t = jnp.where(row == ROWS - 1, center, pltpu.roll(center, ROWS - 1, 0))
        else:
            high_t = g_ref[k, i, r0 + 1:r0 + 1 + ROWS, :]
        low_r = jnp.where(lane == 0, center, pltpu.roll(center, 1, 1))
        high_r = jnp.where(lane == shells - 1, center, pltpu.roll(center, shells - 1, 1))
        if i == 0:
            low_p = jnp.where(first_az, azlo_ref[k, 0, rows, :].astype(jnp.float32), gp_ref[k, 0, rows, :])
        else:
            low_p = g_ref[k, i - 1, rows, :]
        if i == planes - 1:
            high_p = jnp.where(last_az, azhi_ref[k, 0, rows, :].astype(jnp.float32), gn_ref[k, 0, rows, :])
        else:
            high_p = g_ref[k, i + 1, rows, :]
        if edge == "low":
            low_b = jnp.where(band_first, center, binlo_ref[0, i, rows, :].astype(jnp.float32))
        else:
            low_b = g_ref[k - 1, i, rows, :]
        if edge == "high":
            high_b = jnp.where(band_last, center, binhi_ref[0, i, rows, :].astype(jnp.float32))
        else:
            high_b = g_ref[k + 1, i, rows, :]
        d_lo = (center - low_r, center - low_t, center - low_p)
        d_hi = (high_r - center, high_t - center, high_p - center)
        curvature = coef_ref[0, i, rows, :] * (d_hi[0] - d_lo[0])
        curvature = curvature + coef_ref[1, i, rows, :] * (d_hi[1] - d_lo[1])
        curvature = curvature + coef_ref[2, i, rows, :] * (d_hi[2] - d_lo[2])
        advection = coef_ref[3, i, rows, :] * d_lo[0] + coef_ref[6, i, rows, :] * d_hi[0]
        advection = advection + coef_ref[4, i, rows, :] * d_lo[1] + coef_ref[7, i, rows, :] * d_hi[1]
        advection = advection + coef_ref[5, i, rows, :] * d_lo[2] + coef_ref[8, i, rows, :] * d_hi[2]
        momentum = coef_ref[9, i, rows, :] * (high_b - center) + coef_ref[10, i, rows, :] * (center - low_b)
        rate = kap * curvature - advection + momentum
        if second:
            value = 1.5 * center - 0.5 * f0_ref[k, i, rows, :] + scale * rate
        else:
            value = center + scale * rate
        out_ref[k, i, rows, :] = value
        if not second:
            half = value.astype(jnp.bfloat16)
            if i == 0:
                az_first_ref[k, 0, rows, :] = half
            if i == planes - 1:
                az_last_ref[k, 0, rows, :] = half
            if edge == "low":
                bin_first_ref[0, i, rows, :] = half
            if edge == "high":
                bin_last_ref[0, i, rows, :] = half

    def all_rows(k, edge):
        kap = kappa_ref[k]
        for i in range(planes):
            for r0 in range(0, colat, ROWS):
                chunk(k, i, r0, kap, edge)

    all_rows(0, "low")

    def middle(k, carry):
        all_rows(k, None)
        return carry

    lax.fori_loop(1, bins - 1, middle, 0)
    all_rows(bins - 1, "high")


PLANES = 2


def section_call(scal, flags, kappa, g, az_low, az_high, bin_low, bin_high, coefs, f0=None):
    bins, azim, colat, shells = g.shape
    block = (bins, PLANES, colat, shells)
    plane = (bins, 1, colat, shells)
    bin_block = (1, PLANES, colat, shells)
    smem = pl.BlockSpec(memory_space=pltpu.SMEM)
    in_specs = [
        smem,
        smem,
        smem,
        pl.BlockSpec(block, lambda a: (0, a, 0, 0)),
        pl.BlockSpec(plane, lambda a: (0, jnp.maximum(a * PLANES - 1, 0), 0, 0)),
        pl.BlockSpec(plane, lambda a: (0, jnp.minimum(a * PLANES + PLANES, azim - 1), 0, 0)),
        pl.BlockSpec(plane, lambda a: (0, 0, 0, 0)),
        pl.BlockSpec(plane, lambda a: (0, 0, 0, 0)),
        pl.BlockSpec(bin_block, lambda a: (0, a, 0, 0)),
        pl.BlockSpec(bin_block, lambda a: (0, a, 0, 0)),
        pl.BlockSpec((coefs.shape[0], PLANES, colat, shells), lambda a: (0, a, 0, 0)),
    ]
    args = [scal, flags, kappa, g, g, g, az_low, az_high, bin_low, bin_high, coefs]
    out_specs = pl.BlockSpec(block, lambda a: (0, a, 0, 0))
    out_shape = jax.ShapeDtypeStruct(g.shape, jnp.float32)
    if f0 is not None:
        in_specs.append(pl.BlockSpec(block, lambda a: (0, a, 0, 0)))
        args.append(f0)
    else:
        out_specs = [
            out_specs,
            pl.BlockSpec(plane, lambda a: (0, a, 0, 0)),
            pl.BlockSpec(plane, lambda a: (0, a, 0, 0)),
            pl.BlockSpec(bin_block, lambda a: (0, a, 0, 0)),
            pl.BlockSpec(bin_block, lambda a: (0, a, 0, 0)),
        ]
        half_plane = jax.ShapeDtypeStruct((bins, azim // PLANES, colat, shells), jnp.bfloat16)
        half_bin = jax.ShapeDtypeStruct((1, azim, colat, shells), jnp.bfloat16)
        out_shape = [out_shape, half_plane, half_plane, half_bin, half_bin]
    return pl.pallas_call(
        functools.partial(section_kernel, second=f0 is not None),
        grid=(azim // PLANES,),
        in_specs=in_specs,
        out_specs=out_specs,
        out_shape=out_shape,
        compiler_params=pltpu.CompilerParams(dimension_semantics=("arbitrary",)),
    )(*args)


def exchange(first, last, axis):
    size = lax.axis_size(axis)
    up = [(i, (i + 1) % size) for i in range(size)]
    down = [(j, i) for i, j in up]
    return lax.ppermute(last, axis, up), lax.ppermute(first, axis, down)


def cell_state(q):
    rho, v, b, p = q[0], q[1:4], q[4:7], q[7]
    vv = v[0] * v[0] + v[1] * v[1] + v[2] * v[2]
    bb = b[0] * b[0] + b[1] * b[1] + b[2] * b[2]
    energy = p / (ADIABATIC - 1.0) + 0.5 * rho * vv + 0.5 * bb
    return [rho, rho * v[0], rho * v[1], rho * v[2], b[0], b[1], b[2], energy]


def cell_flux(q, u, normal):
    rho, v, b, p = q[0], q[1:4], q[4:7], q[7]
    vn, bn = v[normal], b[normal]
    magnetic = 0.5 * (b[0] * b[0] + b[1] * b[1] + b[2] * b[2])
    total_p = p + magnetic
    momentum = [rho * v[k] * vn - b[k] * bn for k in range(3)]
    momentum[normal] = momentum[normal] + total_p
    induction = [vn * b[k] - bn * v[k] for k in range(3)]
    energy = (u[7] + total_p) * vn - bn * (v[0] * b[0] + v[1] * b[1] + v[2] * b[2])
    speed = jnp.abs(vn) + jnp.sqrt((ADIABATIC * p + 2.0 * magnetic) / rho)
    return [rho * vn] + momentum + induction + [energy], speed


def face_flux(f_low, s_low, u_low, f_high, s_high, u_high):
    wave = jnp.maximum(s_low, s_high)
    return [0.5 * (f_low[c] + f_high[c]) - 0.5 * wave * (u_high[c] - u_low[c]) for c in range(8)]


def mhd_kernel(dt_ref, rho_c, v_c, b_c, p_c, rho_m, v_m, b_m, p_m, rho_p, v_p, b_p, p_p,
               azlo_ref, azhi_ref, clo_ref, chi_ref, wr_ref, wt_ref, wp_ref, *rest, offset, last_step):
    out_ref = rest[-1]
    step = pl.program_id(0) + offset

    def prim(rho_ref, v_ref, b_ref, p_ref):
        return [rho_ref[0], v_ref[0, 0], v_ref[1, 0], v_ref[2, 0],
                b_ref[0, 0], b_ref[1, 0], b_ref[2, 0], p_ref[0]]

    q = prim(rho_c, v_c, b_c, p_c)
    shape = q[0].shape
    nrow, nlane = shape
    row = lax.broadcasted_iota(jnp.int32, shape, 0)
    lane = lax.broadcasted_iota(jnp.int32, shape, 1)
    first_az = _vec(shape, step) == 0
    last_az = _vec(shape, step) == last_step
    q_m = prim(rho_m, v_m, b_m, p_m)
    q_p = prim(rho_p, v_p, b_p, p_p)
    q_m = [jnp.where(first_az, azlo_ref[c, 0], q_m[c]) for c in range(8)]
    q_p = [jnp.where(last_az, azhi_ref[c, 0], q_p[c]) for c in range(8)]
    u = cell_state(q)
    dt = dt_ref[0]

    def lane_next(x):
        return jnp.where(lane == nlane - 1, x, pltpu.roll(x, nlane - 1, 1))

    f, s = cell_flux(q, u, 0)
    high = face_flux(f, s, u, [lane_next(x) for x in f], lane_next(s), [lane_next(x) for x in u])
    low = [jnp.where(lane == 0, f[c], pltpu.roll(high[c], 1, 1)) for c in range(8)]
    width_r = wr_ref[...]
    radial = [(high[c] - low[c]) / width_r for c in range(8)]

    q_l = [clo_ref[c, 0] for c in range(8)]
    q_h = [chi_ref[c, 0] for c in range(8)]
    u_l = cell_state(q_l)
    u_h = cell_state(q_h)
    f, s = cell_flux(q, u, 1)
    f_l, s_l = cell_flux(q_l, u_l, 1)
    f_h, s_h = cell_flux(q_h, u_h, 1)

    def row_next(x, h):
        return jnp.where(row == nrow - 1, jnp.broadcast_to(h, shape), pltpu.roll(x, nrow - 1, 0))

    high = face_flux(f, s, u, [row_next(f[c], f_h[c]) for c in range(8)], row_next(s, s_h),
                     [row_next(u[c], u_h[c]) for c in range(8)])
    first = face_flux(f_l, s_l, u_l, f, s, u)
    low = [jnp.where(row == 0, first[c], pltpu.roll(high[c], 1, 0)) for c in range(8)]
    width_t = wt_ref[...]
    polar = [(high[c] - low[c]) / width_t for c in range(8)]

    u_m = cell_state(q_m)
    u_p = cell_state(q_p)
    f, s = cell_flux(q, u, 2)
    f_m, s_m = cell_flux(q_m, u_m, 2)
    f_p, s_p = cell_flux(q_p, u_p, 2)
    high = face_flux(f, s, u, f_p, s_p, u_p)
    low = face_flux(f_m, s_m, u_m, f, s, u)
    width_p = wp_ref[...]
    for c in range(8):
        azimuthal = (high[c] - low[c]) / width_p
        out_ref[c, 0] = u[c] - dt * (radial[c] + polar[c] + azimuthal)


def mhd_call(dt, density, velocity, magnetic_vector, pressure, az_low, az_high,
             colat_low, colat_high, width_r, width_t, width_p, offset, count, previous=None):
    azim, colat, radial = density.shape
    scalar_block = (1, colat, radial)
    vector_block = (3, 1, colat, radial)

    def own(a):
        return a + offset

    def clamp_low(a):
        return jnp.maximum(a + offset - 1, 0)

    def clamp_high(a):
        return jnp.minimum(a + offset + 1, azim - 1)

    in_specs = [pl.BlockSpec(memory_space=pltpu.SMEM)]
    for pick in (own, clamp_low, clamp_high):
        in_specs += [
            pl.BlockSpec(scalar_block, lambda a, pick=pick: (pick(a), 0, 0)),
            pl.BlockSpec(vector_block, lambda a, pick=pick: (0, pick(a), 0, 0)),
            pl.BlockSpec(vector_block, lambda a, pick=pick: (0, pick(a), 0, 0)),
            pl.BlockSpec(scalar_block, lambda a, pick=pick: (pick(a), 0, 0)),
        ]
    in_specs += [
        pl.BlockSpec((8, 1, colat, radial), lambda a: (0, 0, 0, 0)),
        pl.BlockSpec((8, 1, colat, radial), lambda a: (0, 0, 0, 0)),
        pl.BlockSpec((8, 1, 1, radial), lambda a: (0, a + offset, 0, 0)),
        pl.BlockSpec((8, 1, 1, radial), lambda a: (0, a + offset, 0, 0)),
        pl.BlockSpec((1, radial), lambda a: (0, 0)),
        pl.BlockSpec((1, radial), lambda a: (0, 0)),
        pl.BlockSpec((colat, radial), lambda a: (0, 0)),
    ]
    fields = (density, velocity, magnetic_vector, pressure)
    args = [dt, *fields, *fields, *fields, az_low, az_high, colat_low, colat_high,
            width_r, width_t, width_p]
    aliases = {}
    if previous is not None:
        in_specs.append(pl.BlockSpec(memory_space=pl.ANY))
        aliases = {len(args): 0}
        args.append(previous)
    return pl.pallas_call(
        functools.partial(mhd_kernel, offset=offset, last_step=azim - 1),
        grid=(count,),
        in_specs=in_specs,
        out_specs=pl.BlockSpec((8, 1, colat, radial), lambda a: (0, a + offset, 0, 0)),
        out_shape=jax.ShapeDtypeStruct((8, azim, colat, radial), jnp.float32),
        input_output_aliases=aliases,
        compiler_params=pltpu.CompilerParams(dimension_semantics=("arbitrary",)),
    )(*args)


def mhd_halos(density, velocity, magnetic_vector, pressure, band_pos, band_count):
    fields = [density, velocity[0], velocity[1], velocity[2],
              magnetic_vector[0], magnetic_vector[1], magnetic_vector[2], pressure]
    azim, colat = density.shape[0], density.shape[1]
    az_first = jnp.stack([x[0:1] for x in fields])
    az_last = jnp.stack([x[azim - 1:azim] for x in fields])
    c_first = jnp.stack([x[:, 0:1] for x in fields])
    c_last = jnp.stack([x[:, colat - 1:colat] for x in fields])
    phi_size = lax.axis_size("phi")
    up = [(i, (i + 1) % phi_size) for i in range(phi_size)]
    down = [(j, i) for i, j in up]
    az_low = lax.ppermute(az_last, "phi", up)
    az_high = lax.ppermute(az_first, "phi", down)
    up = [(i, (i + 1) % band_count) for i in range(band_count)]
    down = [(j, i) for i, j in up]
    c_low = lax.ppermute(c_last, "band", up)
    c_high = lax.ppermute(c_first, "band", down)
    c_low = jnp.where(band_pos == 0, c_first, c_low)
    c_high = jnp.where(band_pos == band_count - 1, c_last, c_high)
    return az_low, az_high, c_low, c_high


def body(
    density,
    velocity,
    magnetic_vector,
    pressure,
    fluid_courant_number,
    cosmic_ray_density,
    diffusion_per_bin,
    super_step_scale,
):
    azim_dev = density.shape[0]
    colat_dev = density.shape[1]
    radial_cell_count = density.shape[2]
    band_count = lax.axis_size("band")
    phi_count = lax.axis_size("phi")
    colatitude_count = colat_dev * band_count
    azimuth_cell_count = azim_dev * phi_count
    bin_dev = cosmic_ray_density.shape[0]
    momentum_bin_count = bin_dev * band_count
    outer_shell_count = cosmic_ray_density.shape[3]
    band_pos = lax.axis_index("band")
    mesh_spacing = grid_steps(
        radial_cell_count, colatitude_count, azimuth_cell_count, momentum_bin_count
    )
    fluid_rate, cosmic_ray_rate = rate_limits(
        radial_cell_count,
        outer_shell_count,
        colatitude_count,
        azimuth_cell_count,
        momentum_bin_count,
    )
    radius_full = shell_radii(0, radial_cell_count, radial_cell_count)
    colatitude_local = colatitudes(band_pos * colat_dev, colat_dev, colatitude_count)
    dt = jnp.reshape(fluid_courant_number / fluid_rate, (1,)).astype(jnp.float32)
    mhd_args = (
        dt, density, velocity, magnetic_vector, pressure,
        *mhd_halos(density, velocity, magnetic_vector, pressure, band_pos, band_count),
        (radius_full * mesh_spacing[0])[None],
        (radius_full * mesh_spacing[1])[None],
        jnp.sin(colatitude_local)[:, None] * radius_full * mesh_spacing[2],
    )
    first_planes = azim_dev // 2
    fluid_state = mhd_call(*mhd_args, 0, first_planes)
    first_shell = radial_cell_count - outer_shell_count
    radius_sh = shell_radii(first_shell, outer_shell_count, radial_cell_count)
    colatitude_full = colatitudes(0, colatitude_count, colatitude_count)
    own_fields = jnp.concatenate(
        [velocity[:, :, :, first_shell:], magnetic_vector[:, :, :, first_shell:]], axis=0
    ).astype(jnp.bfloat16)
    wind_half = jnp.broadcast_to(own_fields[None], (band_count,) + own_fields.shape)
    wind_half = lax.all_to_all(wind_half, "band", 0, 0, tiled=True)
    wind_half = jnp.transpose(wind_half, (1, 2, 0, 3, 4)).reshape(
        own_fields.shape[0], azim_dev, colatitude_count, outer_shell_count
    )
    fluid_state, wind_half = lax.optimization_barrier((fluid_state, wind_half))
    wind_vel = wind_half[0:3].astype(jnp.float32)
    azim_pad = padded(wind_half[2], (("phi", 0),), 1).astype(jnp.float32)
    radial_pad = jnp.pad(wind_vel[0], ((0, 0), (0, 0), (1, 1)), mode="edge")
    polar_pad = jnp.pad(wind_vel[1], ((0, 0), (1, 1), (0, 0)), mode="edge")
    spread_half = divergence(
        radial_pad, polar_pad, azim_pad, radius_sh, colatitude_full, mesh_spacing
    ).astype(jnp.bfloat16)
    kappa_here = lax.dynamic_slice_in_dim(diffusion_per_bin, band_pos * bin_dev, bin_dev)
    sts_step = super_step_scale / cosmic_ray_rate
    coef_set = transport_coefficients(
        wind_half[0:3].astype(jnp.float32),
        wind_half[3:6].astype(jnp.float32),
        spread_half.astype(jnp.float32),
        radius_sh,
        colatitude_full,
        mesh_spacing,
    )

    coef_list, up_list, down_list, drift_up, drift_down = coef_set
    coefs = jnp.stack(
        list(coef_list) + list(up_list) + list(down_list)
        + [drift_up / mesh_spacing[3], drift_down / mesh_spacing[3]],
        axis=0,
    )
    scal1 = jnp.reshape(sts_step / 3.0, (1,)).astype(jnp.float32)
    scal2 = jnp.reshape(sts_step / 2.0, (1,)).astype(jnp.float32)
    flags = jnp.stack([band_pos == 0, band_pos == band_count - 1]).astype(jnp.int32)
    bins = cosmic_ray_density.shape[0]
    edges = (
        cosmic_ray_density[:, 0:1],
        cosmic_ray_density[:, azim_dev - 1:azim_dev],
        cosmic_ray_density[0:1],
        cosmic_ray_density[bins - 1:bins],
    )
    edges = [x.astype(jnp.bfloat16) for x in lax.optimization_barrier(edges)]
    az_low, az_high = exchange(edges[0], edges[1], "phi")
    bin_low, bin_high = exchange(edges[2], edges[3], "band")
    first_section, *edges = section_call(
        scal1, flags, kappa_here, cosmic_ray_density, az_low, az_high, bin_low, bin_high, coefs
    )
    steps = edges[0].shape[1]
    az_low, az_high = exchange(edges[0][:, 0:1], edges[1][:, steps - 1:steps], "phi")
    bin_low, bin_high = exchange(edges[2], edges[3], "band")
    fluid_state, first_section = lax.optimization_barrier((fluid_state, first_section))
    fluid_state = mhd_call(
        *mhd_args, first_planes, azim_dev - first_planes, previous=fluid_state
    )
    fluid_state, az_low, az_high, bin_low, bin_high = lax.optimization_barrier(
        (fluid_state, az_low, az_high, bin_low, bin_high)
    )
    cosmic_ray_next = section_call(
        scal2, flags, kappa_here, first_section, az_low, az_high, bin_low, bin_high, coefs,
        cosmic_ray_density,
    )
    return (fluid_state, cosmic_ray_next)


def solution(mesh):
    placed = (
        P("phi", "band", None),
        P(None, "phi", "band", None),
        P(None, "phi", "band", None),
        P("phi", "band", None),
        P(),
        P("band", "phi", None, None),
        P(),
        P(),
    )
    return jax.shard_map(
        body,
        mesh=mesh,
        in_specs=placed,
        out_specs=(P(None, "phi", "band", None), P("band", "phi", None, None)),
        check_vma=False,
    )
```

```python
import functools
import math

import jax
import jax.numpy as jnp
from jax import lax
from jax.experimental import pallas as pl
from jax.experimental.pallas import tpu as pltpu
from jax.sharding import PartitionSpec as P

ADIABATIC = 5.0 / 3.0
INNER_RADIUS = 0.1
R_RATIO = 30.0
COLAT_LOW = math.pi / 6.0
COLAT_SPAN = 2.0 * math.pi / 3.0
P_RATIO = 1000.0
K_RATIO = 0.1
B_FLOOR = 0.1
V_BOUND = 3.0
B_BOUND = 3.0
P_HIGH = 2.0
RHO_LOW = 0.5
KAPPA_HIGH = 0.5


def padded(value, sides, width):
    for axis, dim in sides:
        size, length = (lax.axis_size(axis), value.shape[dim])
        up = [(i, (i + 1) % size) for i in range(size)]
        down = [(j, i) for i, j in up]
        last = lax.slice_in_dim(value, length - width, length, axis=dim)
        leading = lax.slice_in_dim(value, 0, width, axis=dim)
        before = lax.ppermute(last, axis, up)
        after = lax.ppermute(leading, axis, down)
        value = jnp.concatenate([before, value, after], axis=dim)
    return value


def grid_steps(n_radial, n_colat, n_azim, n_bins):
    return (
        math.log(R_RATIO) / n_radial,
        COLAT_SPAN / n_colat,
        2.0 * math.pi / n_azim,
        math.log(P_RATIO) / n_bins,
    )


def rate_limits(n_radial, n_shells, n_colat, n_azim, n_bins):
    radial_spacing, colatitude_spacing, azimuth_spacing, step_m = grid_steps(
        n_radial, n_colat, n_azim, n_bins
    )
    sine_lower = math.sin(COLAT_LOW + 0.5 * colatitude_spacing)
    fluid_radius = INNER_RADIUS * math.exp(0.5 * radial_spacing)
    fastest_limit = V_BOUND + math.sqrt((ADIABATIC * P_HIGH + 3.0 * B_BOUND**2) / RHO_LOW)
    fluid_rate = fastest_limit * (
        1.0 / (fluid_radius * radial_spacing)
        + 1.0 / (fluid_radius * colatitude_spacing)
        + 1.0 / (fluid_radius * sine_lower * azimuth_spacing)
    )
    shell_low = INNER_RADIUS * math.exp(radial_spacing * (n_radial - n_shells + 0.5))
    inv_r = 1.0 / (shell_low * radial_spacing)
    inv_t = 1.0 / (shell_low * colatitude_spacing)
    inv_p = 1.0 / (shell_low * sine_lower * azimuth_spacing)
    cosmic_ray_rate = (
        2.0 * KAPPA_HIGH * (inv_r**2 + inv_t**2 + inv_p**2)
        + V_BOUND * (inv_r + inv_t + inv_p)
        + V_BOUND * (inv_r + inv_t + inv_p + 4.0 / shell_low) / (3.0 * step_m)
    )
    return (fluid_rate, cosmic_ray_rate)


def shell_radii(start_index, cell_count, n_radial):
    cell_index = jnp.arange(cell_count, dtype=jnp.float32) + (start_index + 0.5)
    return INNER_RADIUS * jnp.exp(math.log(R_RATIO) / n_radial * cell_index)


def colatitudes(start_index, cell_count, n_colat):
    cell_index = jnp.arange(cell_count, dtype=jnp.float32) + 0.5
    return COLAT_LOW + COLAT_SPAN * (cell_index + start_index) / n_colat


def edge_fix(values, along_axis, depth, band_pos, axis_count):
    extent = values.shape[along_axis]
    low_ghost = lax.slice_in_dim(values, 0, depth, axis=along_axis)
    high_ghost = lax.slice_in_dim(values, extent - depth, extent, axis=along_axis)
    first_own = lax.slice_in_dim(values, depth, depth + 1, axis=along_axis)
    last_own = lax.slice_in_dim(values, extent - depth - 1, extent - depth, axis=along_axis)
    low_rim = jnp.where(band_pos == 0, first_own, low_ghost)
    high_rim = jnp.where(band_pos == axis_count - 1, last_own, high_ghost)
    middle = lax.slice_in_dim(values, depth, extent - depth, axis=along_axis)
    return jnp.concatenate([low_rim, middle, high_rim], axis=along_axis)


def conserved(primitive):
    density = primitive[0]
    velocity = primitive[1:4]
    magnetic_vector = primitive[4:7]
    pressure = primitive[7]
    energy = (
        pressure / (ADIABATIC - 1.0)
        + 0.5 * density * jnp.sum(velocity * velocity, axis=0)
        + 0.5 * jnp.sum(magnetic_vector * magnetic_vector, axis=0)
    )
    return jnp.concatenate(
        [density[None], density[None] * velocity, magnetic_vector, energy[None]], axis=0
    )


def face_terms(primitive, cell_state, normal):
    density = primitive[0]
    velocity = primitive[1:4]
    magnetic_vector = primitive[4:7]
    pressure = primitive[7]
    v_normal = velocity[normal]
    b_normal = magnetic_vector[normal]
    magnetic = 0.5 * jnp.sum(magnetic_vector * magnetic_vector, axis=0)
    total_p = pressure + magnetic
    momentum = [density * velocity[k] * v_normal - magnetic_vector[k] * b_normal for k in range(3)]
    momentum[normal] = momentum[normal] + total_p
    induction = [v_normal * magnetic_vector[k] - b_normal * velocity[k] for k in range(3)]
    energy_flux = (cell_state[7] + total_p) * v_normal - b_normal * jnp.sum(
        velocity * magnetic_vector, axis=0
    )
    fluxes = jnp.stack([density * v_normal] + momentum + induction + [energy_flux], axis=0)
    speeds = jnp.abs(v_normal) + jnp.sqrt((ADIABATIC * pressure + 2.0 * magnetic) / density)
    return (fluxes, speeds)


def rusanov(primitive, cell_state, normal, along_axis, spacing):
    fluxes, speeds = face_terms(primitive, cell_state, normal)
    length = speeds.shape[along_axis]
    wave_speed = jnp.maximum(
        lax.slice_in_dim(speeds, 0, length - 1, axis=along_axis),
        lax.slice_in_dim(speeds, 1, length, axis=along_axis),
    )
    flux_low = lax.slice_in_dim(fluxes, 0, length - 1, axis=along_axis + 1)
    flux_high = lax.slice_in_dim(fluxes, 1, length, axis=along_axis + 1)
    state_low = lax.slice_in_dim(cell_state, 0, length - 1, axis=along_axis + 1)
    state_high = lax.slice_in_dim(cell_state, 1, length, axis=along_axis + 1)
    face_flux = 0.5 * (flux_low + flux_high) - 0.5 * wave_speed[None] * (state_high - state_low)
    upper = lax.slice_in_dim(face_flux, 1, length - 1, axis=along_axis + 1)
    lower = lax.slice_in_dim(face_flux, 0, length - 2, axis=along_axis + 1)
    return (upper - lower) / spacing


def fluid_update(padded_array, radius_values, colatitude_mesh, timestep_length, mesh_spacing):
    ghosted = jnp.pad(padded_array, ((0, 0), (0, 0), (0, 0), (1, 1)), mode="edge")
    cell_state = conserved(ghosted)
    width_r = radius_values * mesh_spacing[0]
    width_t = radius_values * mesh_spacing[1]
    width_p = jnp.sin(colatitude_mesh)[:, None] * radius_values * mesh_spacing[2]
    radial = rusanov(ghosted[:, 1:-1, 1:-1, :], cell_state[:, 1:-1, 1:-1, :], 0, 2, width_r)
    polar = rusanov(ghosted[:, 1:-1, :, 1:-1], cell_state[:, 1:-1, :, 1:-1], 1, 1, width_t)
    azimuthal = rusanov(ghosted[:, :, 1:-1, 1:-1], cell_state[:, :, 1:-1, 1:-1], 2, 0, width_p)
    return cell_state[:, 1:-1, 1:-1, 1:-1] - timestep_length * (radial + polar + azimuthal)


def divergence(radial_pad, polar_pad, azim_pad, radius_values, colatitude_mesh, mesh_spacing):
    sin_colat = jnp.sin(colatitude_mesh)[:, None]
    cotangent = (jnp.cos(colatitude_mesh) / jnp.sin(colatitude_mesh))[:, None]
    radial_mid = radial_pad[:, :, 1:-1]
    polar_mid = polar_pad[:, 1:-1, :]
    d_radial = (radial_pad[:, :, 2:] - radial_pad[:, :, :-2]) / (
        2.0 * radius_values * mesh_spacing[0]
    )
    d_polar = (polar_pad[:, 2:, :] - polar_pad[:, :-2, :]) / (2.0 * radius_values * mesh_spacing[1])
    d_azim = (azim_pad[2:] - azim_pad[:-2]) / (2.0 * radius_values * sin_colat * mesh_spacing[2])
    return (
        d_radial
        + 2.0 * radial_mid / radius_values
        + d_polar
        + cotangent * polar_mid / radius_values
        + d_azim
    )


def transport_coefficients(
    wind_vel, mag_wind, spread, radius_values, colatitude_mesh, mesh_spacing
):
    width_r = radius_values * mesh_spacing[0]
    width_t = radius_values * mesh_spacing[1]
    width_p = jnp.sin(colatitude_mesh)[:, None] * radius_values * mesh_spacing[2]
    widths = (width_r, width_t, width_p)
    mag_sq = jnp.sum(mag_wind * mag_wind, axis=0) + B_FLOOR
    b_share = K_RATIO + (1.0 - K_RATIO) * mag_wind * mag_wind / mag_sq
    coef_list = [b_share[k] / (widths[k] * widths[k]) for k in range(3)]
    up_list = [jnp.maximum(wind_vel[k], 0.0) / widths[k] for k in range(3)]
    down_list = [jnp.minimum(wind_vel[k], 0.0) / widths[k] for k in range(3)]
    drift_rate = spread / 3.0
    return (
        coef_list,
        up_list,
        down_list,
        jnp.maximum(drift_rate, 0.0),
        jnp.minimum(drift_rate, 0.0),
    )


def transport_rate(extended, coef_set, kappa_col, step_m):
    coef_list, up_list, down_list, drift_up, drift_down = coef_set
    center = extended[1:-1, 1:-1, 1:-1, 1:-1]
    low_cells = (
        extended[1:-1, 1:-1, 1:-1, :-2],
        extended[1:-1, 1:-1, :-2, 1:-1],
        extended[1:-1, :-2, 1:-1, 1:-1],
    )
    high_cells = (
        extended[1:-1, 1:-1, 1:-1, 2:],
        extended[1:-1, 1:-1, 2:, 1:-1],
        extended[1:-1, 2:, 1:-1, 1:-1],
    )
    curvature = coef_list[0] * (high_cells[0] - 2.0 * center + low_cells[0])
    curvature = curvature + coef_list[1] * (high_cells[1] - 2.0 * center + low_cells[1])
    curvature = curvature + coef_list[2] * (high_cells[2] - 2.0 * center + low_cells[2])
    diffusion = kappa_col[:, None, None, None] * curvature
    advection = up_list[0] * (center - low_cells[0]) + down_list[0] * (high_cells[0] - center)
    advection = (
        advection + up_list[1] * (center - low_cells[1]) + down_list[1] * (high_cells[1] - center)
    )
    advection = (
        advection + up_list[2] * (center - low_cells[2]) + down_list[2] * (high_cells[2] - center)
    )
    bin_low = extended[:-2, 1:-1, 1:-1, 1:-1]
    bin_high = extended[2:, 1:-1, 1:-1, 1:-1]
    momentum = (drift_up * (bin_high - center) + drift_down * (center - bin_low)) / step_m
    return diffusion - advection + momentum


ROWS = 16


def _vec(shape, scalar):
    return jnp.full(shape, scalar, jnp.int32)


def section_kernel(scal_ref, flag_ref, kappa_ref, g_ref, gp_ref, gn_ref, azlo_ref, azhi_ref,
                   binlo_ref, binhi_ref, coef_ref, *rest, second):
    if second:
        f0_ref, out_ref = rest
    else:
        out_ref, az_first_ref, az_last_ref, bin_first_ref, bin_last_ref = rest
    step = pl.program_id(0)
    last_step = pl.num_programs(0) - 1
    bins, planes, colat, shells = g_ref.shape
    shape = (ROWS, shells)
    row = lax.broadcasted_iota(jnp.int32, shape, 0)
    lane = lax.broadcasted_iota(jnp.int32, shape, 1)
    first_az = _vec(shape, step) == 0
    last_az = _vec(shape, step) == last_step
    band_first = _vec(shape, flag_ref[0]) == 1
    band_last = _vec(shape, flag_ref[1]) == 1
    scale = scal_ref[0]

    def chunk(k, i, r0, kap, edge):
        rows = slice(r0, r0 + ROWS)
        center = g_ref[k, i, rows, :]
        if r0 == 0:
            low_t = jnp.where(row == 0, center, pltpu.roll(center, 1, 0))
        else:
            low_t = g_ref[k, i, r0 - 1:r0 - 1 + ROWS, :]
        if r0 + ROWS == colat:
            high_t = jnp.where(row == ROWS - 1, center, pltpu.roll(center, ROWS - 1, 0))
        else:
            high_t = g_ref[k, i, r0 + 1:r0 + 1 + ROWS, :]
        low_r = jnp.where(lane == 0, center, pltpu.roll(center, 1, 1))
        high_r = jnp.where(lane == shells - 1, center, pltpu.roll(center, shells - 1, 1))
        if i == 0:
            low_p = jnp.where(first_az, azlo_ref[k, 0, rows, :].astype(jnp.float32), gp_ref[k, 0, rows, :])
        else:
            low_p = g_ref[k, i - 1, rows, :]
        if i == planes - 1:
            high_p = jnp.where(last_az, azhi_ref[k, 0, rows, :].astype(jnp.float32), gn_ref[k, 0, rows, :])
        else:
            high_p = g_ref[k, i + 1, rows, :]
        if edge == "low":
            low_b = jnp.where(band_first, center, binlo_ref[0, i, rows, :].astype(jnp.float32))
        else:
            low_b = g_ref[k - 1, i, rows, :]
        if edge == "high":
            high_b = jnp.where(band_last, center, binhi_ref[0, i, rows, :].astype(jnp.float32))
        else:
            high_b = g_ref[k + 1, i, rows, :]
        d_lo = (center - low_r, center - low_t, center - low_p)
        d_hi = (high_r - center, high_t - center, high_p - center)
        curvature = coef_ref[0, i, rows, :] * (d_hi[0] - d_lo[0])
        curvature = curvature + coef_ref[1, i, rows, :] * (d_hi[1] - d_lo[1])
        curvature = curvature + coef_ref[2, i, rows, :] * (d_hi[2] - d_lo[2])
        advection = coef_ref[3, i, rows, :] * d_lo[0] + coef_ref[6, i, rows, :] * d_hi[0]
        advection = advection + coef_ref[4, i, rows, :] * d_lo[1] + coef_ref[7, i, rows, :] * d_hi[1]
        advection = advection + coef_ref[5, i, rows, :] * d_lo[2] + coef_ref[8, i, rows, :] * d_hi[2]
        momentum = coef_ref[9, i, rows, :] * (high_b - center) + coef_ref[10, i, rows, :] * (center - low_b)
        rate = kap * curvature - advection + momentum
        if second:
            value = 1.5 * center - 0.5 * f0_ref[k, i, rows, :] + scale * rate
        else:
            value = center + scale * rate
        out_ref[k, i, rows, :] = value
        if not second:
            half = value.astype(jnp.bfloat16)
            if i == 0:
                az_first_ref[k, 0, rows, :] = half
            if i == planes - 1:
                az_last_ref[k, 0, rows, :] = half
            if edge == "low":
                bin_first_ref[0, i, rows, :] = half
            if edge == "high":
                bin_last_ref[0, i, rows, :] = half

    def all_rows(k, edge):
        kap = kappa_ref[k]
        for i in range(planes):
            for r0 in range(0, colat, ROWS):
                chunk(k, i, r0, kap, edge)

    all_rows(0, "low")

    def middle(k, carry):
        all_rows(k, None)
        return carry

    lax.fori_loop(1, bins - 1, middle, 0)
    all_rows(bins - 1, "high")


PLANES = 2


def section_call(scal, flags, kappa, g, az_low, az_high, bin_low, bin_high, coefs, f0=None):
    bins, azim, colat, shells = g.shape
    block = (bins, PLANES, colat, shells)
    plane = (bins, 1, colat, shells)
    bin_block = (1, PLANES, colat, shells)
    smem = pl.BlockSpec(memory_space=pltpu.SMEM)
    in_specs = [
        smem,
        smem,
        smem,
        pl.BlockSpec(block, lambda a: (0, a, 0, 0)),
        pl.BlockSpec(plane, lambda a: (0, jnp.maximum(a * PLANES - 1, 0), 0, 0)),
        pl.BlockSpec(plane, lambda a: (0, jnp.minimum(a * PLANES + PLANES, azim - 1), 0, 0)),
        pl.BlockSpec(plane, lambda a: (0, 0, 0, 0)),
        pl.BlockSpec(plane, lambda a: (0, 0, 0, 0)),
        pl.BlockSpec(bin_block, lambda a: (0, a, 0, 0)),
        pl.BlockSpec(bin_block, lambda a: (0, a, 0, 0)),
        pl.BlockSpec((coefs.shape[0], PLANES, colat, shells), lambda a: (0, a, 0, 0)),
    ]
    args = [scal, flags, kappa, g, g, g, az_low, az_high, bin_low, bin_high, coefs]
    out_specs = pl.BlockSpec(block, lambda a: (0, a, 0, 0))
    out_shape = jax.ShapeDtypeStruct(g.shape, jnp.float32)
    if f0 is not None:
        in_specs.append(pl.BlockSpec(block, lambda a: (0, a, 0, 0)))
        args.append(f0)
    else:
        out_specs = [
            out_specs,
            pl.BlockSpec(plane, lambda a: (0, a, 0, 0)),
            pl.BlockSpec(plane, lambda a: (0, a, 0, 0)),
            pl.BlockSpec(bin_block, lambda a: (0, a, 0, 0)),
            pl.BlockSpec(bin_block, lambda a: (0, a, 0, 0)),
        ]
        half_plane = jax.ShapeDtypeStruct((bins, azim // PLANES, colat, shells), jnp.bfloat16)
        half_bin = jax.ShapeDtypeStruct((1, azim, colat, shells), jnp.bfloat16)
        out_shape = [out_shape, half_plane, half_plane, half_bin, half_bin]
    return pl.pallas_call(
        functools.partial(section_kernel, second=f0 is not None),
        grid=(azim // PLANES,),
        in_specs=in_specs,
        out_specs=out_specs,
        out_shape=out_shape,
        compiler_params=pltpu.CompilerParams(dimension_semantics=("arbitrary",)),
    )(*args)


def coef_kernel(wind_ref, prev_ref, next_ref, halo_ref, wr_ref, wt_ref, wp_ref, dr_ref, dt_ref,
                dp_ref, radius_ref, cot_ref, out_ref, *, step_m):
    step = pl.program_id(0)
    last_step = pl.num_programs(0) - 1
    u_r = wind_ref[0, 0].astype(jnp.float32)
    u_t = wind_ref[1, 0].astype(jnp.float32)
    shape = u_r.shape
    row = lax.broadcasted_iota(jnp.int32, shape, 0)
    lane = lax.broadcasted_iota(jnp.int32, shape, 1)
    nrow, nlane = shape
    low_p = jnp.where(_vec(shape, step) == 0, halo_ref[0].astype(jnp.float32),
                      prev_ref[0, 0].astype(jnp.float32))
    high_p = jnp.where(_vec(shape, step) == last_step, halo_ref[1].astype(jnp.float32),
                       next_ref[0, 0].astype(jnp.float32))
    high_r = jnp.where(lane == nlane - 1, u_r, pltpu.roll(u_r, nlane - 1, 1))
    low_r = jnp.where(lane == 0, u_r, pltpu.roll(u_r, 1, 1))
    high_t = jnp.where(row == nrow - 1, u_t, pltpu.roll(u_t, nrow - 1, 0))
    low_t = jnp.where(row == 0, u_t, pltpu.roll(u_t, 1, 0))
    radius = radius_ref[...]
    spread = (
        (high_r - low_r) / dr_ref[...]
        + 2.0 * u_r / radius
        + (high_t - low_t) / dt_ref[...]
        + cot_ref[...] * u_t / radius
        + (high_p - low_p) / dp_ref[...]
    )
    spread = spread.astype(jnp.bfloat16).astype(jnp.float32)
    b = [wind_ref[3 + n, 0].astype(jnp.float32) for n in range(3)]
    mag_sq = b[0] * b[0] + b[1] * b[1] + b[2] * b[2] + B_FLOOR
    widths = (wr_ref[...], wt_ref[...], wp_ref[...])
    for n in range(3):
        share = K_RATIO + (1.0 - K_RATIO) * b[n] * b[n] / mag_sq
        out_ref[n, 0] = share / (widths[n] * widths[n])
    for n in range(3):
        u = wind_ref[n, 0].astype(jnp.float32)
        out_ref[3 + n, 0] = jnp.maximum(u, 0.0) / widths[n]
        out_ref[6 + n, 0] = jnp.minimum(u, 0.0) / widths[n]
    drift = spread / 3.0
    out_ref[9, 0] = jnp.maximum(drift, 0.0) / step_m
    out_ref[10, 0] = jnp.minimum(drift, 0.0) / step_m


def coef_call(wind, halo, tables, step_m):
    fields, azim, colat, shells = wind.shape
    plane = (1, 1, colat, shells)
    in_specs = [
        pl.BlockSpec((fields, 1, colat, shells), lambda a: (0, a, 0, 0)),
        pl.BlockSpec(plane, lambda a: (2, jnp.maximum(a - 1, 0), 0, 0)),
        pl.BlockSpec(plane, lambda a: (2, jnp.minimum(a + 1, azim - 1), 0, 0)),
        pl.BlockSpec(halo.shape, lambda a: (0, 0, 0)),
    ] + [pl.BlockSpec(t.shape, lambda a: (0, 0)) for t in tables]
    return pl.pallas_call(
        functools.partial(coef_kernel, step_m=step_m),
        grid=(azim,),
        in_specs=in_specs,
        out_specs=pl.BlockSpec((11, 1, colat, shells), lambda a: (0, a, 0, 0)),
        out_shape=jax.ShapeDtypeStruct((11, azim, colat, shells), jnp.float32),
        compiler_params=pltpu.CompilerParams(dimension_semantics=("arbitrary",)),
    )(wind, wind, wind, halo, *tables)


def exchange(first, last, axis):
    size = lax.axis_size(axis)
    up = [(i, (i + 1) % size) for i in range(size)]
    down = [(j, i) for i, j in up]
    return lax.ppermute(last, axis, up), lax.ppermute(first, axis, down)


def cell_state(q):
    rho, v, b, p = q[0], q[1:4], q[4:7], q[7]
    vv = v[0] * v[0] + v[1] * v[1] + v[2] * v[2]
    bb = b[0] * b[0] + b[1] * b[1] + b[2] * b[2]
    energy = p / (ADIABATIC - 1.0) + 0.5 * rho * vv + 0.5 * bb
    return [rho, rho * v[0], rho * v[1], rho * v[2], b[0], b[1], b[2], energy]


def cell_flux(q, u, normal):
    rho, v, b, p = q[0], q[1:4], q[4:7], q[7]
    vn, bn = v[normal], b[normal]
    magnetic = 0.5 * (b[0] * b[0] + b[1] * b[1] + b[2] * b[2])
    total_p = p + magnetic
    momentum = [rho * v[k] * vn - b[k] * bn for k in range(3)]
    momentum[normal] = momentum[normal] + total_p
    induction = [vn * b[k] - bn * v[k] for k in range(3)]
    energy = (u[7] + total_p) * vn - bn * (v[0] * b[0] + v[1] * b[1] + v[2] * b[2])
    speed = jnp.abs(vn) + jnp.sqrt((ADIABATIC * p + 2.0 * magnetic) / rho)
    return [rho * vn] + momentum + induction + [energy], speed


def face_flux(f_low, s_low, u_low, f_high, s_high, u_high):
    wave = jnp.maximum(s_low, s_high)
    return [0.5 * (f_low[c] + f_high[c]) - 0.5 * wave * (u_high[c] - u_low[c]) for c in range(8)]


def mhd_kernel(dt_ref, rho_c, v_c, b_c, p_c, rho_m, v_m, b_m, p_m, rho_p, v_p, b_p, p_p,
               azlo_ref, azhi_ref, clo_ref, chi_ref, wr_ref, wt_ref, wp_ref, *rest, offset, last_step):
    out_ref = rest[-1]
    step = pl.program_id(0) + offset

    def prim(rho_ref, v_ref, b_ref, p_ref):
        return [rho_ref[0], v_ref[0, 0], v_ref[1, 0], v_ref[2, 0],
                b_ref[0, 0], b_ref[1, 0], b_ref[2, 0], p_ref[0]]

    q = prim(rho_c, v_c, b_c, p_c)
    shape = q[0].shape
    nrow, nlane = shape
    row = lax.broadcasted_iota(jnp.int32, shape, 0)
    lane = lax.broadcasted_iota(jnp.int32, shape, 1)
    first_az = _vec(shape, step) == 0
    last_az = _vec(shape, step) == last_step
    q_m = prim(rho_m, v_m, b_m, p_m)
    q_p = prim(rho_p, v_p, b_p, p_p)
    q_m = [jnp.where(first_az, azlo_ref[c, 0], q_m[c]) for c in range(8)]
    q_p = [jnp.where(last_az, azhi_ref[c, 0], q_p[c]) for c in range(8)]
    u = cell_state(q)
    dt = dt_ref[0]

    def lane_next(x):
        return jnp.where(lane == nlane - 1, x, pltpu.roll(x, nlane - 1, 1))

    f, s = cell_flux(q, u, 0)
    high = face_flux(f, s, u, [lane_next(x) for x in f], lane_next(s), [lane_next(x) for x in u])
    low = [jnp.where(lane == 0, f[c], pltpu.roll(high[c], 1, 1)) for c in range(8)]
    width_r = wr_ref[...]
    radial = [(high[c] - low[c]) / width_r for c in range(8)]

    q_l = [clo_ref[c, 0] for c in range(8)]
    q_h = [chi_ref[c, 0] for c in range(8)]
    u_l = cell_state(q_l)
    u_h = cell_state(q_h)
    f, s = cell_flux(q, u, 1)
    f_l, s_l = cell_flux(q_l, u_l, 1)
    f_h, s_h = cell_flux(q_h, u_h, 1)

    def row_next(x, h):
        return jnp.where(row == nrow - 1, jnp.broadcast_to(h, shape), pltpu.roll(x, nrow - 1, 0))

    high = face_flux(f, s, u, [row_next(f[c], f_h[c]) for c in range(8)], row_next(s, s_h),
                     [row_next(u[c], u_h[c]) for c in range(8)])
    first = face_flux(f_l, s_l, u_l, f, s, u)
    low = [jnp.where(row == 0, first[c], pltpu.roll(high[c], 1, 0)) for c in range(8)]
    width_t = wt_ref[...]
    polar = [(high[c] - low[c]) / width_t for c in range(8)]

    u_m = cell_state(q_m)
    u_p = cell_state(q_p)
    f, s = cell_flux(q, u, 2)
    f_m, s_m = cell_flux(q_m, u_m, 2)
    f_p, s_p = cell_flux(q_p, u_p, 2)
    high = face_flux(f, s, u, f_p, s_p, u_p)
    low = face_flux(f_m, s_m, u_m, f, s, u)
    width_p = wp_ref[...]
    for c in range(8):
        azimuthal = (high[c] - low[c]) / width_p
        out_ref[c, 0] = u[c] - dt * (radial[c] + polar[c] + azimuthal)


def mhd_call(dt, density, velocity, magnetic_vector, pressure, az_low, az_high,
             colat_low, colat_high, width_r, width_t, width_p, offset, count, previous=None):
    azim, colat, radial = density.shape
    scalar_block = (1, colat, radial)
    vector_block = (3, 1, colat, radial)

    def own(a):
        return a + offset

    def clamp_low(a):
        return jnp.maximum(a + offset - 1, 0)

    def clamp_high(a):
        return jnp.minimum(a + offset + 1, azim - 1)

    in_specs = [pl.BlockSpec(memory_space=pltpu.SMEM)]
    for pick in (own, clamp_low, clamp_high):
        in_specs += [
            pl.BlockSpec(scalar_block, lambda a, pick=pick: (pick(a), 0, 0)),
            pl.BlockSpec(vector_block, lambda a, pick=pick: (0, pick(a), 0, 0)),
            pl.BlockSpec(vector_block, lambda a, pick=pick: (0, pick(a), 0, 0)),
            pl.BlockSpec(scalar_block, lambda a, pick=pick: (pick(a), 0, 0)),
        ]
    in_specs += [
        pl.BlockSpec((8, 1, colat, radial), lambda a: (0, 0, 0, 0)),
        pl.BlockSpec((8, 1, colat, radial), lambda a: (0, 0, 0, 0)),
        pl.BlockSpec((8, 1, 1, radial), lambda a: (0, a + offset, 0, 0)),
        pl.BlockSpec((8, 1, 1, radial), lambda a: (0, a + offset, 0, 0)),
        pl.BlockSpec((1, radial), lambda a: (0, 0)),
        pl.BlockSpec((1, radial), lambda a: (0, 0)),
        pl.BlockSpec((colat, radial), lambda a: (0, 0)),
    ]
    fields = (density, velocity, magnetic_vector, pressure)
    args = [dt, *fields, *fields, *fields, az_low, az_high, colat_low, colat_high,
            width_r, width_t, width_p]
    aliases = {}
    if previous is not None:
        in_specs.append(pl.BlockSpec(memory_space=pl.ANY))
        aliases = {len(args): 0}
        args.append(previous)
    return pl.pallas_call(
        functools.partial(mhd_kernel, offset=offset, last_step=azim - 1),
        grid=(count,),
        in_specs=in_specs,
        out_specs=pl.BlockSpec((8, 1, colat, radial), lambda a: (0, a + offset, 0, 0)),
        out_shape=jax.ShapeDtypeStruct((8, azim, colat, radial), jnp.float32),
        input_output_aliases=aliases,
        compiler_params=pltpu.CompilerParams(dimension_semantics=("arbitrary",)),
    )(*args)


def mhd_halos(density, velocity, magnetic_vector, pressure, band_pos, band_count):
    fields = [density, velocity[0], velocity[1], velocity[2],
              magnetic_vector[0], magnetic_vector[1], magnetic_vector[2], pressure]
    azim, colat = density.shape[0], density.shape[1]
    az_first = jnp.stack([x[0:1] for x in fields])
    az_last = jnp.stack([x[azim - 1:azim] for x in fields])
    c_first = jnp.stack([x[:, 0:1] for x in fields])
    c_last = jnp.stack([x[:, colat - 1:colat] for x in fields])
    phi_size = lax.axis_size("phi")
    up = [(i, (i + 1) % phi_size) for i in range(phi_size)]
    down = [(j, i) for i, j in up]
    az_low = lax.ppermute(az_last, "phi", up)
    az_high = lax.ppermute(az_first, "phi", down)
    up = [(i, (i + 1) % band_count) for i in range(band_count)]
    down = [(j, i) for i, j in up]
    c_low = lax.ppermute(c_last, "band", up)
    c_high = lax.ppermute(c_first, "band", down)
    c_low = jnp.where(band_pos == 0, c_first, c_low)
    c_high = jnp.where(band_pos == band_count - 1, c_last, c_high)
    return az_low, az_high, c_low, c_high


def body(
    density,
    velocity,
    magnetic_vector,
    pressure,
    fluid_courant_number,
    cosmic_ray_density,
    diffusion_per_bin,
    super_step_scale,
):
    azim_dev = density.shape[0]
    colat_dev = density.shape[1]
    radial_cell_count = density.shape[2]
    band_count = lax.axis_size("band")
    phi_count = lax.axis_size("phi")
    colatitude_count = colat_dev * band_count
    azimuth_cell_count = azim_dev * phi_count
    bin_dev = cosmic_ray_density.shape[0]
    momentum_bin_count = bin_dev * band_count
    outer_shell_count = cosmic_ray_density.shape[3]
    band_pos = lax.axis_index("band")
    mesh_spacing = grid_steps(
        radial_cell_count, colatitude_count, azimuth_cell_count, momentum_bin_count
    )
    fluid_rate, cosmic_ray_rate = rate_limits(
        radial_cell_count,
        outer_shell_count,
        colatitude_count,
        azimuth_cell_count,
        momentum_bin_count,
    )
    radius_full = shell_radii(0, radial_cell_count, radial_cell_count)
    colatitude_local = colatitudes(band_pos * colat_dev, colat_dev, colatitude_count)
    dt = jnp.reshape(fluid_courant_number / fluid_rate, (1,)).astype(jnp.float32)
    mhd_args = (
        dt, density, velocity, magnetic_vector, pressure,
        *mhd_halos(density, velocity, magnetic_vector, pressure, band_pos, band_count),
        (radius_full * mesh_spacing[0])[None],
        (radius_full * mesh_spacing[1])[None],
        jnp.sin(colatitude_local)[:, None] * radius_full * mesh_spacing[2],
    )
    first_planes = azim_dev // 2
    fluid_state = mhd_call(*mhd_args, 0, first_planes)
    first_shell = radial_cell_count - outer_shell_count
    radius_sh = shell_radii(first_shell, outer_shell_count, radial_cell_count)
    colatitude_full = colatitudes(0, colatitude_count, colatitude_count)
    own_fields = jnp.concatenate(
        [velocity[:, :, :, first_shell:], magnetic_vector[:, :, :, first_shell:]], axis=0
    ).astype(jnp.bfloat16)
    wind_half = lax.all_gather(own_fields, "band", axis=2, tiled=True)
    fluid_state, wind_half = lax.optimization_barrier((fluid_state, wind_half))
    u_phi = own_fields[2]
    halo_low, halo_high = exchange(u_phi[0:1], u_phi[azim_dev - 1:azim_dev], "phi")
    halo = lax.all_gather(jnp.concatenate([halo_low, halo_high], axis=0), "band", axis=1, tiled=True)
    kappa_here = lax.dynamic_slice_in_dim(diffusion_per_bin, band_pos * bin_dev, bin_dev)
    sts_step = super_step_scale / cosmic_ray_rate
    sin_colat = jnp.sin(colatitude_full)[:, None]
    cot_colat = (jnp.cos(colatitude_full) / jnp.sin(colatitude_full))[:, None]
    shells = outer_shell_count
    tables = (
        (radius_sh * mesh_spacing[0])[None],
        (radius_sh * mesh_spacing[1])[None],
        sin_colat * radius_sh * mesh_spacing[2],
        (2.0 * radius_sh * mesh_spacing[0])[None],
        (2.0 * radius_sh * mesh_spacing[1])[None],
        2.0 * radius_sh * sin_colat * mesh_spacing[2],
        radius_sh[None],
        jnp.broadcast_to(cot_colat, (colatitude_count, shells)),
    )
    coefs = coef_call(wind_half, halo, tables, mesh_spacing[3])
    scal1 = jnp.reshape(sts_step / 3.0, (1,)).astype(jnp.float32)
    scal2 = jnp.reshape(sts_step / 2.0, (1,)).astype(jnp.float32)
    flags = jnp.stack([band_pos == 0, band_pos == band_count - 1]).astype(jnp.int32)
    bins = cosmic_ray_density.shape[0]
    edges = (
        cosmic_ray_density[:, 0:1],
        cosmic_ray_density[:, azim_dev - 1:azim_dev],
        cosmic_ray_density[0:1],
        cosmic_ray_density[bins - 1:bins],
    )
    edges = [x.astype(jnp.bfloat16) for x in lax.optimization_barrier(edges)]
    az_low, az_high = exchange(edges[0], edges[1], "phi")
    bin_low, bin_high = exchange(edges[2], edges[3], "band")
    first_section, *edges = section_call(
        scal1, flags, kappa_here, cosmic_ray_density, az_low, az_high, bin_low, bin_high, coefs
    )
    steps = edges[0].shape[1]
    az_low, az_high = exchange(edges[0][:, 0:1], edges[1][:, steps - 1:steps], "phi")
    bin_low, bin_high = exchange(edges[2], edges[3], "band")
    fluid_state, first_section = lax.optimization_barrier((fluid_state, first_section))
    fluid_state = mhd_call(
        *mhd_args, first_planes, azim_dev - first_planes, previous=fluid_state
    )
    fluid_state, az_low, az_high, bin_low, bin_high = lax.optimization_barrier(
        (fluid_state, az_low, az_high, bin_low, bin_high)
    )
    cosmic_ray_next = section_call(
        scal2, flags, kappa_here, first_section, az_low, az_high, bin_low, bin_high, coefs,
        cosmic_ray_density,
    )
    return (fluid_state, cosmic_ray_next)


def solution(mesh):
    placed = (
        P("phi", "band", None),
        P(None, "phi", "band", None),
        P(None, "phi", "band", None),
        P("phi", "band", None),
        P(),
        P("band", "phi", None, None),
        P(),
        P(),
    )
    return jax.shard_map(
        body,
        mesh=mesh,
        in_specs=placed,
        out_specs=(P(None, "phi", "band", None), P("band", "phi", None, None)),
        check_vma=False,
    )
```

```python
import functools
import math

import jax
import jax.numpy as jnp
from jax import lax
from jax.experimental import pallas as pl
from jax.experimental.pallas import tpu as pltpu
from jax.sharding import PartitionSpec as P

ADIABATIC = 5.0 / 3.0
INNER_RADIUS = 0.1
R_RATIO = 30.0
COLAT_LOW = math.pi / 6.0
COLAT_SPAN = 2.0 * math.pi / 3.0
P_RATIO = 1000.0
K_RATIO = 0.1
B_FLOOR = 0.1
V_BOUND = 3.0
B_BOUND = 3.0
P_HIGH = 2.0
RHO_LOW = 0.5
KAPPA_HIGH = 0.5


def padded(value, sides, width):
    for axis, dim in sides:
        size, length = (lax.axis_size(axis), value.shape[dim])
        up = [(i, (i + 1) % size) for i in range(size)]
        down = [(j, i) for i, j in up]
        last = lax.slice_in_dim(value, length - width, length, axis=dim)
        leading = lax.slice_in_dim(value, 0, width, axis=dim)
        before = lax.ppermute(last, axis, up)
        after = lax.ppermute(leading, axis, down)
        value = jnp.concatenate([before, value, after], axis=dim)
    return value


def grid_steps(n_radial, n_colat, n_azim, n_bins):
    return (
        math.log(R_RATIO) / n_radial,
        COLAT_SPAN / n_colat,
        2.0 * math.pi / n_azim,
        math.log(P_RATIO) / n_bins,
    )


def rate_limits(n_radial, n_shells, n_colat, n_azim, n_bins):
    radial_spacing, colatitude_spacing, azimuth_spacing, step_m = grid_steps(
        n_radial, n_colat, n_azim, n_bins
    )
    sine_lower = math.sin(COLAT_LOW + 0.5 * colatitude_spacing)
    fluid_radius = INNER_RADIUS * math.exp(0.5 * radial_spacing)
    fastest_limit = V_BOUND + math.sqrt((ADIABATIC * P_HIGH + 3.0 * B_BOUND**2) / RHO_LOW)
    fluid_rate = fastest_limit * (
        1.0 / (fluid_radius * radial_spacing)
        + 1.0 / (fluid_radius * colatitude_spacing)
        + 1.0 / (fluid_radius * sine_lower * azimuth_spacing)
    )
    shell_low = INNER_RADIUS * math.exp(radial_spacing * (n_radial - n_shells + 0.5))
    inv_r = 1.0 / (shell_low * radial_spacing)
    inv_t = 1.0 / (shell_low * colatitude_spacing)
    inv_p = 1.0 / (shell_low * sine_lower * azimuth_spacing)
    cosmic_ray_rate = (
        2.0 * KAPPA_HIGH * (inv_r**2 + inv_t**2 + inv_p**2)
        + V_BOUND * (inv_r + inv_t + inv_p)
        + V_BOUND * (inv_r + inv_t + inv_p + 4.0 / shell_low) / (3.0 * step_m)
    )
    return (fluid_rate, cosmic_ray_rate)


def shell_radii(start_index, cell_count, n_radial):
    cell_index = jnp.arange(cell_count, dtype=jnp.float32) + (start_index + 0.5)
    return INNER_RADIUS * jnp.exp(math.log(R_RATIO) / n_radial * cell_index)


def colatitudes(start_index, cell_count, n_colat):
    cell_index = jnp.arange(cell_count, dtype=jnp.float32) + 0.5
    return COLAT_LOW + COLAT_SPAN * (cell_index + start_index) / n_colat


def edge_fix(values, along_axis, depth, band_pos, axis_count):
    extent = values.shape[along_axis]
    low_ghost = lax.slice_in_dim(values, 0, depth, axis=along_axis)
    high_ghost = lax.slice_in_dim(values, extent - depth, extent, axis=along_axis)
    first_own = lax.slice_in_dim(values, depth, depth + 1, axis=along_axis)
    last_own = lax.slice_in_dim(values, extent - depth - 1, extent - depth, axis=along_axis)
    low_rim = jnp.where(band_pos == 0, first_own, low_ghost)
    high_rim = jnp.where(band_pos == axis_count - 1, last_own, high_ghost)
    middle = lax.slice_in_dim(values, depth, extent - depth, axis=along_axis)
    return jnp.concatenate([low_rim, middle, high_rim], axis=along_axis)


def conserved(primitive):
    density = primitive[0]
    velocity = primitive[1:4]
    magnetic_vector = primitive[4:7]
    pressure = primitive[7]
    energy = (
        pressure / (ADIABATIC - 1.0)
        + 0.5 * density * jnp.sum(velocity * velocity, axis=0)
        + 0.5 * jnp.sum(magnetic_vector * magnetic_vector, axis=0)
    )
    return jnp.concatenate(
        [density[None], density[None] * velocity, magnetic_vector, energy[None]], axis=0
    )


def face_terms(primitive, cell_state, normal):
    density = primitive[0]
    velocity = primitive[1:4]
    magnetic_vector = primitive[4:7]
    pressure = primitive[7]
    v_normal = velocity[normal]
    b_normal = magnetic_vector[normal]
    magnetic = 0.5 * jnp.sum(magnetic_vector * magnetic_vector, axis=0)
    total_p = pressure + magnetic
    momentum = [density * velocity[k] * v_normal - magnetic_vector[k] * b_normal for k in range(3)]
    momentum[normal] = momentum[normal] + total_p
    induction = [v_normal * magnetic_vector[k] - b_normal * velocity[k] for k in range(3)]
    energy_flux = (cell_state[7] + total_p) * v_normal - b_normal * jnp.sum(
        velocity * magnetic_vector, axis=0
    )
    fluxes = jnp.stack([density * v_normal] + momentum + induction + [energy_flux], axis=0)
    speeds = jnp.abs(v_normal) + jnp.sqrt((ADIABATIC * pressure + 2.0 * magnetic) / density)
    return (fluxes, speeds)


def rusanov(primitive, cell_state, normal, along_axis, spacing):
    fluxes, speeds = face_terms(primitive, cell_state, normal)
    length = speeds.shape[along_axis]
    wave_speed = jnp.maximum(
        lax.slice_in_dim(speeds, 0, length - 1, axis=along_axis),
        lax.slice_in_dim(speeds, 1, length, axis=along_axis),
    )
    flux_low = lax.slice_in_dim(fluxes, 0, length - 1, axis=along_axis + 1)
    flux_high = lax.slice_in_dim(fluxes, 1, length, axis=along_axis + 1)
    state_low = lax.slice_in_dim(cell_state, 0, length - 1, axis=along_axis + 1)
    state_high = lax.slice_in_dim(cell_state, 1, length, axis=along_axis + 1)
    face_flux = 0.5 * (flux_low + flux_high) - 0.5 * wave_speed[None] * (state_high - state_low)
    upper = lax.slice_in_dim(face_flux, 1, length - 1, axis=along_axis + 1)
    lower = lax.slice_in_dim(face_flux, 0, length - 2, axis=along_axis + 1)
    return (upper - lower) / spacing


def fluid_update(padded_array, radius_values, colatitude_mesh, timestep_length, mesh_spacing):
    ghosted = jnp.pad(padded_array, ((0, 0), (0, 0), (0, 0), (1, 1)), mode="edge")
    cell_state = conserved(ghosted)
    width_r = radius_values * mesh_spacing[0]
    width_t = radius_values * mesh_spacing[1]
    width_p = jnp.sin(colatitude_mesh)[:, None] * radius_values * mesh_spacing[2]
    radial = rusanov(ghosted[:, 1:-1, 1:-1, :], cell_state[:, 1:-1, 1:-1, :], 0, 2, width_r)
    polar = rusanov(ghosted[:, 1:-1, :, 1:-1], cell_state[:, 1:-1, :, 1:-1], 1, 1, width_t)
    azimuthal = rusanov(ghosted[:, :, 1:-1, 1:-1], cell_state[:, :, 1:-1, 1:-1], 2, 0, width_p)
    return cell_state[:, 1:-1, 1:-1, 1:-1] - timestep_length * (radial + polar + azimuthal)


def divergence(radial_pad, polar_pad, azim_pad, radius_values, colatitude_mesh, mesh_spacing):
    sin_colat = jnp.sin(colatitude_mesh)[:, None]
    cotangent = (jnp.cos(colatitude_mesh) / jnp.sin(colatitude_mesh))[:, None]
    radial_mid = radial_pad[:, :, 1:-1]
    polar_mid = polar_pad[:, 1:-1, :]
    d_radial = (radial_pad[:, :, 2:] - radial_pad[:, :, :-2]) / (
        2.0 * radius_values * mesh_spacing[0]
    )
    d_polar = (polar_pad[:, 2:, :] - polar_pad[:, :-2, :]) / (2.0 * radius_values * mesh_spacing[1])
    d_azim = (azim_pad[2:] - azim_pad[:-2]) / (2.0 * radius_values * sin_colat * mesh_spacing[2])
    return (
        d_radial
        + 2.0 * radial_mid / radius_values
        + d_polar
        + cotangent * polar_mid / radius_values
        + d_azim
    )


def transport_coefficients(
    wind_vel, mag_wind, spread, radius_values, colatitude_mesh, mesh_spacing
):
    width_r = radius_values * mesh_spacing[0]
    width_t = radius_values * mesh_spacing[1]
    width_p = jnp.sin(colatitude_mesh)[:, None] * radius_values * mesh_spacing[2]
    widths = (width_r, width_t, width_p)
    mag_sq = jnp.sum(mag_wind * mag_wind, axis=0) + B_FLOOR
    b_share = K_RATIO + (1.0 - K_RATIO) * mag_wind * mag_wind / mag_sq
    coef_list = [b_share[k] / (widths[k] * widths[k]) for k in range(3)]
    up_list = [jnp.maximum(wind_vel[k], 0.0) / widths[k] for k in range(3)]
    down_list = [jnp.minimum(wind_vel[k], 0.0) / widths[k] for k in range(3)]
    drift_rate = spread / 3.0
    return (
        coef_list,
        up_list,
        down_list,
        jnp.maximum(drift_rate, 0.0),
        jnp.minimum(drift_rate, 0.0),
    )


def transport_rate(extended, coef_set, kappa_col, step_m):
    coef_list, up_list, down_list, drift_up, drift_down = coef_set
    center = extended[1:-1, 1:-1, 1:-1, 1:-1]
    low_cells = (
        extended[1:-1, 1:-1, 1:-1, :-2],
        extended[1:-1, 1:-1, :-2, 1:-1],
        extended[1:-1, :-2, 1:-1, 1:-1],
    )
    high_cells = (
        extended[1:-1, 1:-1, 1:-1, 2:],
        extended[1:-1, 1:-1, 2:, 1:-1],
        extended[1:-1, 2:, 1:-1, 1:-1],
    )
    curvature = coef_list[0] * (high_cells[0] - 2.0 * center + low_cells[0])
    curvature = curvature + coef_list[1] * (high_cells[1] - 2.0 * center + low_cells[1])
    curvature = curvature + coef_list[2] * (high_cells[2] - 2.0 * center + low_cells[2])
    diffusion = kappa_col[:, None, None, None] * curvature
    advection = up_list[0] * (center - low_cells[0]) + down_list[0] * (high_cells[0] - center)
    advection = (
        advection + up_list[1] * (center - low_cells[1]) + down_list[1] * (high_cells[1] - center)
    )
    advection = (
        advection + up_list[2] * (center - low_cells[2]) + down_list[2] * (high_cells[2] - center)
    )
    bin_low = extended[:-2, 1:-1, 1:-1, 1:-1]
    bin_high = extended[2:, 1:-1, 1:-1, 1:-1]
    momentum = (drift_up * (bin_high - center) + drift_down * (center - bin_low)) / step_m
    return diffusion - advection + momentum


ROWS = 16


def _vec(shape, scalar):
    return jnp.full(shape, scalar, jnp.int32)


def section_kernel(scal_ref, flag_ref, kappa_ref, g_ref, gp_ref, gn_ref, azlo_ref, azhi_ref,
                   binlo_ref, binhi_ref, coef_ref, *rest, second):
    if second:
        f0_ref, out_ref = rest
    else:
        out_ref, az_first_ref, az_last_ref, bin_first_ref, bin_last_ref = rest
    step = pl.program_id(0)
    last_step = pl.num_programs(0) - 1
    bins, planes, colat, shells = g_ref.shape
    shape = (ROWS, shells)
    row = lax.broadcasted_iota(jnp.int32, shape, 0)
    lane = lax.broadcasted_iota(jnp.int32, shape, 1)
    first_az = _vec(shape, step) == 0
    last_az = _vec(shape, step) == last_step
    band_first = _vec(shape, flag_ref[0]) == 1
    band_last = _vec(shape, flag_ref[1]) == 1
    scale = scal_ref[0]

    def chunk(k, i, r0, kap, edge):
        rows = slice(r0, r0 + ROWS)
        center = g_ref[k, i, rows, :]
        if r0 == 0:
            low_t = jnp.where(row == 0, center, pltpu.roll(center, 1, 0))
        else:
            low_t = g_ref[k, i, r0 - 1:r0 - 1 + ROWS, :]
        if r0 + ROWS == colat:
            high_t = jnp.where(row == ROWS - 1, center, pltpu.roll(center, ROWS - 1, 0))
        else:
            high_t = g_ref[k, i, r0 + 1:r0 + 1 + ROWS, :]
        low_r = jnp.where(lane == 0, center, pltpu.roll(center, 1, 1))
        high_r = jnp.where(lane == shells - 1, center, pltpu.roll(center, shells - 1, 1))
        if i == 0:
            low_p = jnp.where(first_az, azlo_ref[k, 0, rows, :].astype(jnp.float32), gp_ref[k, 0, rows, :])
        else:
            low_p = g_ref[k, i - 1, rows, :]
        if i == planes - 1:
            high_p = jnp.where(last_az, azhi_ref[k, 0, rows, :].astype(jnp.float32), gn_ref[k, 0, rows, :])
        else:
            high_p = g_ref[k, i + 1, rows, :]
        if edge == "low":
            low_b = jnp.where(band_first, center, binlo_ref[0, i, rows, :].astype(jnp.float32))
        else:
            low_b = g_ref[k - 1, i, rows, :]
        if edge == "high":
            high_b = jnp.where(band_last, center, binhi_ref[0, i, rows, :].astype(jnp.float32))
        else:
            high_b = g_ref[k + 1, i, rows, :]
        d_lo = (center - low_r, center - low_t, center - low_p)
        d_hi = (high_r - center, high_t - center, high_p - center)
        curvature = coef_ref[0, i, rows, :] * (d_hi[0] - d_lo[0])
        curvature = curvature + coef_ref[1, i, rows, :] * (d_hi[1] - d_lo[1])
        curvature = curvature + coef_ref[2, i, rows, :] * (d_hi[2] - d_lo[2])
        advection = coef_ref[3, i, rows, :] * d_lo[0] + coef_ref[6, i, rows, :] * d_hi[0]
        advection = advection + coef_ref[4, i, rows, :] * d_lo[1] + coef_ref[7, i, rows, :] * d_hi[1]
        advection = advection + coef_ref[5, i, rows, :] * d_lo[2] + coef_ref[8, i, rows, :] * d_hi[2]
        momentum = coef_ref[9, i, rows, :] * (high_b - center) + coef_ref[10, i, rows, :] * (center - low_b)
        rate = kap * curvature - advection + momentum
        if second:
            value = 1.5 * center - 0.5 * f0_ref[k, i, rows, :] + scale * rate
        else:
            value = center + scale * rate
        out_ref[k, i, rows, :] = value
        if not second:
            half = value.astype(jnp.bfloat16)
            if i == 0:
                az_first_ref[k, 0, rows, :] = half
            if i == planes - 1:
                az_last_ref[k, 0, rows, :] = half
            if edge == "low":
                bin_first_ref[0, i, rows, :] = half
            if edge == "high":
                bin_last_ref[0, i, rows, :] = half

    def all_rows(k, edge):
        kap = kappa_ref[k]
        for i in range(planes):
            for r0 in range(0, colat, ROWS):
                chunk(k, i, r0, kap, edge)

    all_rows(0, "low")

    def middle(k, carry):
        all_rows(k, None)
        return carry

    lax.fori_loop(1, bins - 1, middle, 0)
    all_rows(bins - 1, "high")


PLANES = 2


def section_call(scal, flags, kappa, g, az_low, az_high, bin_low, bin_high, coefs, f0=None):
    bins, azim, colat, shells = g.shape
    block = (bins, PLANES, colat, shells)
    plane = (bins, 1, colat, shells)
    bin_block = (1, PLANES, colat, shells)
    smem = pl.BlockSpec(memory_space=pltpu.SMEM)
    in_specs = [
        smem,
        smem,
        smem,
        pl.BlockSpec(block, lambda a: (0, a, 0, 0)),
        pl.BlockSpec(plane, lambda a: (0, jnp.maximum(a * PLANES - 1, 0), 0, 0)),
        pl.BlockSpec(plane, lambda a: (0, jnp.minimum(a * PLANES + PLANES, azim - 1), 0, 0)),
        pl.BlockSpec(plane, lambda a: (0, 0, 0, 0)),
        pl.BlockSpec(plane, lambda a: (0, 0, 0, 0)),
        pl.BlockSpec(bin_block, lambda a: (0, a, 0, 0)),
        pl.BlockSpec(bin_block, lambda a: (0, a, 0, 0)),
        pl.BlockSpec((coefs.shape[0], PLANES, colat, shells), lambda a: (0, a, 0, 0)),
    ]
    args = [scal, flags, kappa, g, g, g, az_low, az_high, bin_low, bin_high, coefs]
    out_specs = pl.BlockSpec(block, lambda a: (0, a, 0, 0))
    out_shape = jax.ShapeDtypeStruct(g.shape, jnp.float32)
    if f0 is not None:
        in_specs.append(pl.BlockSpec(block, lambda a: (0, a, 0, 0)))
        args.append(f0)
    else:
        out_specs = [
            out_specs,
            pl.BlockSpec(plane, lambda a: (0, a, 0, 0)),
            pl.BlockSpec(plane, lambda a: (0, a, 0, 0)),
            pl.BlockSpec(bin_block, lambda a: (0, a, 0, 0)),
            pl.BlockSpec(bin_block, lambda a: (0, a, 0, 0)),
        ]
        half_plane = jax.ShapeDtypeStruct((bins, azim // PLANES, colat, shells), jnp.bfloat16)
        half_bin = jax.ShapeDtypeStruct((1, azim, colat, shells), jnp.bfloat16)
        out_shape = [out_shape, half_plane, half_plane, half_bin, half_bin]
    return pl.pallas_call(
        functools.partial(section_kernel, second=f0 is not None),
        grid=(azim // PLANES,),
        in_specs=in_specs,
        out_specs=out_specs,
        out_shape=out_shape,
        compiler_params=pltpu.CompilerParams(dimension_semantics=("arbitrary",)),
    )(*args)


def coef_kernel(wind_ref, prev_ref, next_ref, halo_ref, wr_ref, wt_ref, wp_ref, dr_ref, dt_ref,
                dp_ref, radius_ref, cot_ref, out_ref, *, step_m):
    step = pl.program_id(0)
    last_step = pl.num_programs(0) - 1
    u_r = wind_ref[0, 0].astype(jnp.float32)
    u_t = wind_ref[1, 0].astype(jnp.float32)
    shape = u_r.shape
    row = lax.broadcasted_iota(jnp.int32, shape, 0)
    lane = lax.broadcasted_iota(jnp.int32, shape, 1)
    nrow, nlane = shape
    low_p = jnp.where(_vec(shape, step) == 0, halo_ref[0].astype(jnp.float32),
                      prev_ref[0, 0].astype(jnp.float32))
    high_p = jnp.where(_vec(shape, step) == last_step, halo_ref[1].astype(jnp.float32),
                       next_ref[0, 0].astype(jnp.float32))
    high_r = jnp.where(lane == nlane - 1, u_r, pltpu.roll(u_r, nlane - 1, 1))
    low_r = jnp.where(lane == 0, u_r, pltpu.roll(u_r, 1, 1))
    high_t = jnp.where(row == nrow - 1, u_t, pltpu.roll(u_t, nrow - 1, 0))
    low_t = jnp.where(row == 0, u_t, pltpu.roll(u_t, 1, 0))
    radius = radius_ref[...]
    spread = (
        (high_r - low_r) / dr_ref[...]
        + 2.0 * u_r / radius
        + (high_t - low_t) / dt_ref[...]
        + cot_ref[...] * u_t / radius
        + (high_p - low_p) / dp_ref[...]
    )
    spread = spread.astype(jnp.bfloat16).astype(jnp.float32)
    b = [wind_ref[3 + n, 0].astype(jnp.float32) for n in range(3)]
    mag_sq = b[0] * b[0] + b[1] * b[1] + b[2] * b[2] + B_FLOOR
    inv_mag = 1.0 / mag_sq
    inv_widths = (wr_ref[...], wt_ref[...], wp_ref[...])
    for n in range(3):
        share = K_RATIO + (1.0 - K_RATIO) * b[n] * b[n] * inv_mag
        out_ref[n, 0] = share * (inv_widths[n] * inv_widths[n])
    for n in range(3):
        u = wind_ref[n, 0].astype(jnp.float32)
        out_ref[3 + n, 0] = jnp.maximum(u, 0.0) * inv_widths[n]
        out_ref[6 + n, 0] = jnp.minimum(u, 0.0) * inv_widths[n]
    drift = spread * (1.0 / (3.0 * step_m))
    out_ref[9, 0] = jnp.maximum(drift, 0.0)
    out_ref[10, 0] = jnp.minimum(drift, 0.0)


def coef_call(wind, halo, tables, step_m):
    fields, azim, colat, shells = wind.shape
    plane = (1, 1, colat, shells)
    in_specs = [
        pl.BlockSpec((fields, 1, colat, shells), lambda a: (0, a, 0, 0)),
        pl.BlockSpec(plane, lambda a: (2, jnp.maximum(a - 1, 0), 0, 0)),
        pl.BlockSpec(plane, lambda a: (2, jnp.minimum(a + 1, azim - 1), 0, 0)),
        pl.BlockSpec(halo.shape, lambda a: (0, 0, 0)),
    ] + [pl.BlockSpec(t.shape, lambda a: (0, 0)) for t in tables]
    return pl.pallas_call(
        functools.partial(coef_kernel, step_m=step_m),
        grid=(azim,),
        in_specs=in_specs,
        out_specs=pl.BlockSpec((11, 1, colat, shells), lambda a: (0, a, 0, 0)),
        out_shape=jax.ShapeDtypeStruct((11, azim, colat, shells), jnp.float32),
        compiler_params=pltpu.CompilerParams(dimension_semantics=("arbitrary",)),
    )(wind, wind, wind, halo, *tables)


def exchange(first, last, axis):
    size = lax.axis_size(axis)
    up = [(i, (i + 1) % size) for i in range(size)]
    down = [(j, i) for i, j in up]
    return lax.ppermute(last, axis, up), lax.ppermute(first, axis, down)


def cell_state(q):
    rho, v, b, p = q[0], q[1:4], q[4:7], q[7]
    vv = v[0] * v[0] + v[1] * v[1] + v[2] * v[2]
    bb = b[0] * b[0] + b[1] * b[1] + b[2] * b[2]
    energy = p / (ADIABATIC - 1.0) + 0.5 * rho * vv + 0.5 * bb
    return [rho, rho * v[0], rho * v[1], rho * v[2], b[0], b[1], b[2], energy]


def cell_flux(q, u, normal):
    rho, v, b, p = q[0], q[1:4], q[4:7], q[7]
    vn, bn = v[normal], b[normal]
    magnetic = 0.5 * (b[0] * b[0] + b[1] * b[1] + b[2] * b[2])
    total_p = p + magnetic
    momentum = [rho * v[k] * vn - b[k] * bn for k in range(3)]
    momentum[normal] = momentum[normal] + total_p
    induction = [vn * b[k] - bn * v[k] for k in range(3)]
    energy = (u[7] + total_p) * vn - bn * (v[0] * b[0] + v[1] * b[1] + v[2] * b[2])
    speed = jnp.abs(vn) + jnp.sqrt((ADIABATIC * p + 2.0 * magnetic) / rho)
    return [rho * vn] + momentum + induction + [energy], speed


def face_flux(f_low, s_low, u_low, f_high, s_high, u_high):
    wave = jnp.maximum(s_low, s_high)
    return [0.5 * (f_low[c] + f_high[c]) - 0.5 * wave * (u_high[c] - u_low[c]) for c in range(8)]


def mhd_kernel(dt_ref, rho_c, v_c, b_c, p_c, rho_m, v_m, b_m, p_m, rho_p, v_p, b_p, p_p,
               azlo_ref, azhi_ref, clo_ref, chi_ref, wr_ref, wt_ref, wp_ref, *rest, offset, last_step):
    out_ref = rest[-1]
    step = pl.program_id(0) + offset

    def prim(rho_ref, v_ref, b_ref, p_ref):
        return [rho_ref[0], v_ref[0, 0], v_ref[1, 0], v_ref[2, 0],
                b_ref[0, 0], b_ref[1, 0], b_ref[2, 0], p_ref[0]]

    q = prim(rho_c, v_c, b_c, p_c)
    shape = q[0].shape
    nrow, nlane = shape
    row = lax.broadcasted_iota(jnp.int32, shape, 0)
    lane = lax.broadcasted_iota(jnp.int32, shape, 1)
    first_az = _vec(shape, step) == 0
    last_az = _vec(shape, step) == last_step
    q_m = prim(rho_m, v_m, b_m, p_m)
    q_p = prim(rho_p, v_p, b_p, p_p)
    q_m = [jnp.where(first_az, azlo_ref[c, 0], q_m[c]) for c in range(8)]
    q_p = [jnp.where(last_az, azhi_ref[c, 0], q_p[c]) for c in range(8)]
    u = cell_state(q)
    dt = dt_ref[0]

    def lane_next(x):
        return jnp.where(lane == nlane - 1, x, pltpu.roll(x, nlane - 1, 1))

    f, s = cell_flux(q, u, 0)
    high = face_flux(f, s, u, [lane_next(x) for x in f], lane_next(s), [lane_next(x) for x in u])
    low = [jnp.where(lane == 0, f[c], pltpu.roll(high[c], 1, 1)) for c in range(8)]
    width_r = wr_ref[...]
    radial = [(high[c] - low[c]) / width_r for c in range(8)]

    q_l = [clo_ref[c, 0] for c in range(8)]
    q_h = [chi_ref[c, 0] for c in range(8)]
    u_l = cell_state(q_l)
    u_h = cell_state(q_h)
    f, s = cell_flux(q, u, 1)
    f_l, s_l = cell_flux(q_l, u_l, 1)
    f_h, s_h = cell_flux(q_h, u_h, 1)

    def row_next(x, h):
        return jnp.where(row == nrow - 1, jnp.broadcast_to(h, shape), pltpu.roll(x, nrow - 1, 0))

    high = face_flux(f, s, u, [row_next(f[c], f_h[c]) for c in range(8)], row_next(s, s_h),
                     [row_next(u[c], u_h[c]) for c in range(8)])
    first = face_flux(f_l, s_l, u_l, f, s, u)
    low = [jnp.where(row == 0, first[c], pltpu.roll(high[c], 1, 0)) for c in range(8)]
    width_t = wt_ref[...]
    polar = [(high[c] - low[c]) / width_t for c in range(8)]

    u_m = cell_state(q_m)
    u_p = cell_state(q_p)
    f, s = cell_flux(q, u, 2)
    f_m, s_m = cell_flux(q_m, u_m, 2)
    f_p, s_p = cell_flux(q_p, u_p, 2)
    high = face_flux(f, s, u, f_p, s_p, u_p)
    low = face_flux(f_m, s_m, u_m, f, s, u)
    width_p = wp_ref[...]
    for c in range(8):
        azimuthal = (high[c] - low[c]) / width_p
        out_ref[c, 0] = u[c] - dt * (radial[c] + polar[c] + azimuthal)


def mhd_call(dt, density, velocity, magnetic_vector, pressure, az_low, az_high,
             colat_low, colat_high, width_r, width_t, width_p, offset, count, previous=None):
    azim, colat, radial = density.shape
    scalar_block = (1, colat, radial)
    vector_block = (3, 1, colat, radial)

    def own(a):
        return a + offset

    def clamp_low(a):
        return jnp.maximum(a + offset - 1, 0)

    def clamp_high(a):
        return jnp.minimum(a + offset + 1, azim - 1)

    in_specs = [pl.BlockSpec(memory_space=pltpu.SMEM)]
    for pick in (own, clamp_low, clamp_high):
        in_specs += [
            pl.BlockSpec(scalar_block, lambda a, pick=pick: (pick(a), 0, 0)),
            pl.BlockSpec(vector_block, lambda a, pick=pick: (0, pick(a), 0, 0)),
            pl.BlockSpec(vector_block, lambda a, pick=pick: (0, pick(a), 0, 0)),
            pl.BlockSpec(scalar_block, lambda a, pick=pick: (pick(a), 0, 0)),
        ]
    in_specs += [
        pl.BlockSpec((8, 1, colat, radial), lambda a: (0, 0, 0, 0)),
        pl.BlockSpec((8, 1, colat, radial), lambda a: (0, 0, 0, 0)),
        pl.BlockSpec((8, 1, 1, radial), lambda a: (0, a + offset, 0, 0)),
        pl.BlockSpec((8, 1, 1, radial), lambda a: (0, a + offset, 0, 0)),
        pl.BlockSpec((1, radial), lambda a: (0, 0)),
        pl.BlockSpec((1, radial), lambda a: (0, 0)),
        pl.BlockSpec((colat, radial), lambda a: (0, 0)),
    ]
    fields = (density, velocity, magnetic_vector, pressure)
    args = [dt, *fields, *fields, *fields, az_low, az_high, colat_low, colat_high,
            width_r, width_t, width_p]
    aliases = {}
    if previous is not None:
        in_specs.append(pl.BlockSpec(memory_space=pl.ANY))
        aliases = {len(args): 0}
        args.append(previous)
    return pl.pallas_call(
        functools.partial(mhd_kernel, offset=offset, last_step=azim - 1),
        grid=(count,),
        in_specs=in_specs,
        out_specs=pl.BlockSpec((8, 1, colat, radial), lambda a: (0, a + offset, 0, 0)),
        out_shape=jax.ShapeDtypeStruct((8, azim, colat, radial), jnp.float32),
        input_output_aliases=aliases,
        compiler_params=pltpu.CompilerParams(dimension_semantics=("arbitrary",)),
    )(*args)


def mhd_halos(density, velocity, magnetic_vector, pressure, band_pos, band_count):
    fields = [density, velocity[0], velocity[1], velocity[2],
              magnetic_vector[0], magnetic_vector[1], magnetic_vector[2], pressure]
    azim, colat = density.shape[0], density.shape[1]
    az_first = jnp.stack([x[0:1] for x in fields])
    az_last = jnp.stack([x[azim - 1:azim] for x in fields])
    c_first = jnp.stack([x[:, 0:1] for x in fields])
    c_last = jnp.stack([x[:, colat - 1:colat] for x in fields])
    phi_size = lax.axis_size("phi")
    up = [(i, (i + 1) % phi_size) for i in range(phi_size)]
    down = [(j, i) for i, j in up]
    az_low = lax.ppermute(az_last, "phi", up)
    az_high = lax.ppermute(az_first, "phi", down)
    up = [(i, (i + 1) % band_count) for i in range(band_count)]
    down = [(j, i) for i, j in up]
    c_low = lax.ppermute(c_last, "band", up)
    c_high = lax.ppermute(c_first, "band", down)
    c_low = jnp.where(band_pos == 0, c_first, c_low)
    c_high = jnp.where(band_pos == band_count - 1, c_last, c_high)
    return az_low, az_high, c_low, c_high


def body(
    density,
    velocity,
    magnetic_vector,
    pressure,
    fluid_courant_number,
    cosmic_ray_density,
    diffusion_per_bin,
    super_step_scale,
):
    azim_dev = density.shape[0]
    colat_dev = density.shape[1]
    radial_cell_count = density.shape[2]
    band_count = lax.axis_size("band")
    phi_count = lax.axis_size("phi")
    colatitude_count = colat_dev * band_count
    azimuth_cell_count = azim_dev * phi_count
    bin_dev = cosmic_ray_density.shape[0]
    momentum_bin_count = bin_dev * band_count
    outer_shell_count = cosmic_ray_density.shape[3]
    band_pos = lax.axis_index("band")
    mesh_spacing = grid_steps(
        radial_cell_count, colatitude_count, azimuth_cell_count, momentum_bin_count
    )
    fluid_rate, cosmic_ray_rate = rate_limits(
        radial_cell_count,
        outer_shell_count,
        colatitude_count,
        azimuth_cell_count,
        momentum_bin_count,
    )
    radius_full = shell_radii(0, radial_cell_count, radial_cell_count)
    colatitude_local = colatitudes(band_pos * colat_dev, colat_dev, colatitude_count)
    dt = jnp.reshape(fluid_courant_number / fluid_rate, (1,)).astype(jnp.float32)
    mhd_args = (
        dt, density, velocity, magnetic_vector, pressure,
        *mhd_halos(density, velocity, magnetic_vector, pressure, band_pos, band_count),
        (radius_full * mesh_spacing[0])[None],
        (radius_full * mesh_spacing[1])[None],
        jnp.sin(colatitude_local)[:, None] * radius_full * mesh_spacing[2],
    )
    first_planes = azim_dev // 2
    fluid_state = mhd_call(*mhd_args, 0, first_planes)
    first_shell = radial_cell_count - outer_shell_count
    radius_sh = shell_radii(first_shell, outer_shell_count, radial_cell_count)
    colatitude_full = colatitudes(0, colatitude_count, colatitude_count)
    own_fields = jnp.concatenate(
        [velocity[:, :, :, first_shell:], magnetic_vector[:, :, :, first_shell:]], axis=0
    ).astype(jnp.bfloat16)
    wind_half = lax.all_gather(own_fields, "band", axis=2, tiled=True)
    fluid_state, wind_half = lax.optimization_barrier((fluid_state, wind_half))
    halo_low, halo_high = exchange(
        wind_half[2, 0:1], wind_half[2, azim_dev - 1:azim_dev], "phi"
    )
    halo = jnp.concatenate([halo_low, halo_high], axis=0)
    kappa_here = lax.dynamic_slice_in_dim(diffusion_per_bin, band_pos * bin_dev, bin_dev)
    sts_step = super_step_scale / cosmic_ray_rate
    sin_colat = jnp.sin(colatitude_full)[:, None]
    cot_colat = (jnp.cos(colatitude_full) / jnp.sin(colatitude_full))[:, None]
    shells = outer_shell_count
    tables = (
        1.0 / (radius_sh * mesh_spacing[0])[None],
        1.0 / (radius_sh * mesh_spacing[1])[None],
        1.0 / (sin_colat * radius_sh * mesh_spacing[2]),
        (2.0 * radius_sh * mesh_spacing[0])[None],
        (2.0 * radius_sh * mesh_spacing[1])[None],
        2.0 * radius_sh * sin_colat * mesh_spacing[2],
        radius_sh[None],
        jnp.broadcast_to(cot_colat, (colatitude_count, shells)),
    )
    coefs = coef_call(wind_half, halo, tables, mesh_spacing[3])
    scal1 = jnp.reshape(sts_step / 3.0, (1,)).astype(jnp.float32)
    scal2 = jnp.reshape(sts_step / 2.0, (1,)).astype(jnp.float32)
    flags = jnp.stack([band_pos == 0, band_pos == band_count - 1]).astype(jnp.int32)
    bins = cosmic_ray_density.shape[0]
    edges = (
        cosmic_ray_density[:, 0:1],
        cosmic_ray_density[:, azim_dev - 1:azim_dev],
        cosmic_ray_density[0:1],
        cosmic_ray_density[bins - 1:bins],
    )
    edges = [x.astype(jnp.bfloat16) for x in lax.optimization_barrier(edges)]
    az_low, az_high = exchange(edges[0], edges[1], "phi")
    bin_low, bin_high = exchange(edges[2], edges[3], "band")
    first_section, *edges = section_call(
        scal1, flags, kappa_here, cosmic_ray_density, az_low, az_high, bin_low, bin_high, coefs
    )
    steps = edges[0].shape[1]
    az_low, az_high = exchange(edges[0][:, 0:1], edges[1][:, steps - 1:steps], "phi")
    bin_low, bin_high = exchange(edges[2], edges[3], "band")
    fluid_state, first_section = lax.optimization_barrier((fluid_state, first_section))
    fluid_state = mhd_call(
        *mhd_args, first_planes, azim_dev - first_planes, previous=fluid_state
    )
    fluid_state, az_low, az_high, bin_low, bin_high = lax.optimization_barrier(
        (fluid_state, az_low, az_high, bin_low, bin_high)
    )
    cosmic_ray_next = section_call(
        scal2, flags, kappa_here, first_section, az_low, az_high, bin_low, bin_high, coefs,
        cosmic_ray_density,
    )
    return (fluid_state, cosmic_ray_next)


def solution(mesh):
    placed = (
        P("phi", "band", None),
        P(None, "phi", "band", None),
        P(None, "phi", "band", None),
        P("phi", "band", None),
        P(),
        P("band", "phi", None, None),
        P(),
        P(),
    )
    return jax.shard_map(
        body,
        mesh=mesh,
        in_specs=placed,
        out_specs=(P(None, "phi", "band", None), P("band", "phi", None, None)),
        check_vma=False,
    )
```

```python
import functools
import math

import jax
import jax.numpy as jnp
from jax import lax
from jax.experimental import pallas as pl
from jax.experimental.pallas import tpu as pltpu
from jax.sharding import PartitionSpec as P

ADIABATIC = 5.0 / 3.0
INNER_RADIUS = 0.1
R_RATIO = 30.0
COLAT_LOW = math.pi / 6.0
COLAT_SPAN = 2.0 * math.pi / 3.0
P_RATIO = 1000.0
K_RATIO = 0.1
B_FLOOR = 0.1
V_BOUND = 3.0
B_BOUND = 3.0
P_HIGH = 2.0
RHO_LOW = 0.5
KAPPA_HIGH = 0.5


def padded(value, sides, width):
    for axis, dim in sides:
        size, length = (lax.axis_size(axis), value.shape[dim])
        up = [(i, (i + 1) % size) for i in range(size)]
        down = [(j, i) for i, j in up]
        last = lax.slice_in_dim(value, length - width, length, axis=dim)
        leading = lax.slice_in_dim(value, 0, width, axis=dim)
        before = lax.ppermute(last, axis, up)
        after = lax.ppermute(leading, axis, down)
        value = jnp.concatenate([before, value, after], axis=dim)
    return value


def grid_steps(n_radial, n_colat, n_azim, n_bins):
    return (
        math.log(R_RATIO) / n_radial,
        COLAT_SPAN / n_colat,
        2.0 * math.pi / n_azim,
        math.log(P_RATIO) / n_bins,
    )


def rate_limits(n_radial, n_shells, n_colat, n_azim, n_bins):
    radial_spacing, colatitude_spacing, azimuth_spacing, step_m = grid_steps(
        n_radial, n_colat, n_azim, n_bins
    )
    sine_lower = math.sin(COLAT_LOW + 0.5 * colatitude_spacing)
    fluid_radius = INNER_RADIUS * math.exp(0.5 * radial_spacing)
    fastest_limit = V_BOUND + math.sqrt((ADIABATIC * P_HIGH + 3.0 * B_BOUND**2) / RHO_LOW)
    fluid_rate = fastest_limit * (
        1.0 / (fluid_radius * radial_spacing)
        + 1.0 / (fluid_radius * colatitude_spacing)
        + 1.0 / (fluid_radius * sine_lower * azimuth_spacing)
    )
    shell_low = INNER_RADIUS * math.exp(radial_spacing * (n_radial - n_shells + 0.5))
    inv_r = 1.0 / (shell_low * radial_spacing)
    inv_t = 1.0 / (shell_low * colatitude_spacing)
    inv_p = 1.0 / (shell_low * sine_lower * azimuth_spacing)
    cosmic_ray_rate = (
        2.0 * KAPPA_HIGH * (inv_r**2 + inv_t**2 + inv_p**2)
        + V_BOUND * (inv_r + inv_t + inv_p)
        + V_BOUND * (inv_r + inv_t + inv_p + 4.0 / shell_low) / (3.0 * step_m)
    )
    return (fluid_rate, cosmic_ray_rate)


def shell_radii(start_index, cell_count, n_radial):
    cell_index = jnp.arange(cell_count, dtype=jnp.float32) + (start_index + 0.5)
    return INNER_RADIUS * jnp.exp(math.log(R_RATIO) / n_radial * cell_index)


def colatitudes(start_index, cell_count, n_colat):
    cell_index = jnp.arange(cell_count, dtype=jnp.float32) + 0.5
    return COLAT_LOW + COLAT_SPAN * (cell_index + start_index) / n_colat


def edge_fix(values, along_axis, depth, band_pos, axis_count):
    extent = values.shape[along_axis]
    low_ghost = lax.slice_in_dim(values, 0, depth, axis=along_axis)
    high_ghost = lax.slice_in_dim(values, extent - depth, extent, axis=along_axis)
    first_own = lax.slice_in_dim(values, depth, depth + 1, axis=along_axis)
    last_own = lax.slice_in_dim(values, extent - depth - 1, extent - depth, axis=along_axis)
    low_rim = jnp.where(band_pos == 0, first_own, low_ghost)
    high_rim = jnp.where(band_pos == axis_count - 1, last_own, high_ghost)
    middle = lax.slice_in_dim(values, depth, extent - depth, axis=along_axis)
    return jnp.concatenate([low_rim, middle, high_rim], axis=along_axis)


def conserved(primitive):
    density = primitive[0]
    velocity = primitive[1:4]
    magnetic_vector = primitive[4:7]
    pressure = primitive[7]
    energy = (
        pressure / (ADIABATIC - 1.0)
        + 0.5 * density * jnp.sum(velocity * velocity, axis=0)
        + 0.5 * jnp.sum(magnetic_vector * magnetic_vector, axis=0)
    )
    return jnp.concatenate(
        [density[None], density[None] * velocity, magnetic_vector, energy[None]], axis=0
    )


def face_terms(primitive, cell_state, normal):
    density = primitive[0]
    velocity = primitive[1:4]
    magnetic_vector = primitive[4:7]
    pressure = primitive[7]
    v_normal = velocity[normal]
    b_normal = magnetic_vector[normal]
    magnetic = 0.5 * jnp.sum(magnetic_vector * magnetic_vector, axis=0)
    total_p = pressure + magnetic
    momentum = [density * velocity[k] * v_normal - magnetic_vector[k] * b_normal for k in range(3)]
    momentum[normal] = momentum[normal] + total_p
    induction = [v_normal * magnetic_vector[k] - b_normal * velocity[k] for k in range(3)]
    energy_flux = (cell_state[7] + total_p) * v_normal - b_normal * jnp.sum(
        velocity * magnetic_vector, axis=0
    )
    fluxes = jnp.stack([density * v_normal] + momentum + induction + [energy_flux], axis=0)
    speeds = jnp.abs(v_normal) + jnp.sqrt((ADIABATIC * pressure + 2.0 * magnetic) / density)
    return (fluxes, speeds)


def rusanov(primitive, cell_state, normal, along_axis, spacing):
    fluxes, speeds = face_terms(primitive, cell_state, normal)
    length = speeds.shape[along_axis]
    wave_speed = jnp.maximum(
        lax.slice_in_dim(speeds, 0, length - 1, axis=along_axis),
        lax.slice_in_dim(speeds, 1, length, axis=along_axis),
    )
    flux_low = lax.slice_in_dim(fluxes, 0, length - 1, axis=along_axis + 1)
    flux_high = lax.slice_in_dim(fluxes, 1, length, axis=along_axis + 1)
    state_low = lax.slice_in_dim(cell_state, 0, length - 1, axis=along_axis + 1)
    state_high = lax.slice_in_dim(cell_state, 1, length, axis=along_axis + 1)
    face_flux = 0.5 * (flux_low + flux_high) - 0.5 * wave_speed[None] * (state_high - state_low)
    upper = lax.slice_in_dim(face_flux, 1, length - 1, axis=along_axis + 1)
    lower = lax.slice_in_dim(face_flux, 0, length - 2, axis=along_axis + 1)
    return (upper - lower) / spacing


def fluid_update(padded_array, radius_values, colatitude_mesh, timestep_length, mesh_spacing):
    ghosted = jnp.pad(padded_array, ((0, 0), (0, 0), (0, 0), (1, 1)), mode="edge")
    cell_state = conserved(ghosted)
    width_r = radius_values * mesh_spacing[0]
    width_t = radius_values * mesh_spacing[1]
    width_p = jnp.sin(colatitude_mesh)[:, None] * radius_values * mesh_spacing[2]
    radial = rusanov(ghosted[:, 1:-1, 1:-1, :], cell_state[:, 1:-1, 1:-1, :], 0, 2, width_r)
    polar = rusanov(ghosted[:, 1:-1, :, 1:-1], cell_state[:, 1:-1, :, 1:-1], 1, 1, width_t)
    azimuthal = rusanov(ghosted[:, :, 1:-1, 1:-1], cell_state[:, :, 1:-1, 1:-1], 2, 0, width_p)
    return cell_state[:, 1:-1, 1:-1, 1:-1] - timestep_length * (radial + polar + azimuthal)


def divergence(radial_pad, polar_pad, azim_pad, radius_values, colatitude_mesh, mesh_spacing):
    sin_colat = jnp.sin(colatitude_mesh)[:, None]
    cotangent = (jnp.cos(colatitude_mesh) / jnp.sin(colatitude_mesh))[:, None]
    radial_mid = radial_pad[:, :, 1:-1]
    polar_mid = polar_pad[:, 1:-1, :]
    d_radial = (radial_pad[:, :, 2:] - radial_pad[:, :, :-2]) / (
        2.0 * radius_values * mesh_spacing[0]
    )
    d_polar = (polar_pad[:, 2:, :] - polar_pad[:, :-2, :]) / (2.0 * radius_values * mesh_spacing[1])
    d_azim = (azim_pad[2:] - azim_pad[:-2]) / (2.0 * radius_values * sin_colat * mesh_spacing[2])
    return (
        d_radial
        + 2.0 * radial_mid / radius_values
        + d_polar
        + cotangent * polar_mid / radius_values
        + d_azim
    )


def transport_coefficients(
    wind_vel, mag_wind, spread, radius_values, colatitude_mesh, mesh_spacing
):
    width_r = radius_values * mesh_spacing[0]
    width_t = radius_values * mesh_spacing[1]
    width_p = jnp.sin(colatitude_mesh)[:, None] * radius_values * mesh_spacing[2]
    widths = (width_r, width_t, width_p)
    mag_sq = jnp.sum(mag_wind * mag_wind, axis=0) + B_FLOOR
    b_share = K_RATIO + (1.0 - K_RATIO) * mag_wind * mag_wind / mag_sq
    coef_list = [b_share[k] / (widths[k] * widths[k]) for k in range(3)]
    up_list = [jnp.maximum(wind_vel[k], 0.0) / widths[k] for k in range(3)]
    down_list = [jnp.minimum(wind_vel[k], 0.0) / widths[k] for k in range(3)]
    drift_rate = spread / 3.0
    return (
        coef_list,
        up_list,
        down_list,
        jnp.maximum(drift_rate, 0.0),
        jnp.minimum(drift_rate, 0.0),
    )


def transport_rate(extended, coef_set, kappa_col, step_m):
    coef_list, up_list, down_list, drift_up, drift_down = coef_set
    center = extended[1:-1, 1:-1, 1:-1, 1:-1]
    low_cells = (
        extended[1:-1, 1:-1, 1:-1, :-2],
        extended[1:-1, 1:-1, :-2, 1:-1],
        extended[1:-1, :-2, 1:-1, 1:-1],
    )
    high_cells = (
        extended[1:-1, 1:-1, 1:-1, 2:],
        extended[1:-1, 1:-1, 2:, 1:-1],
        extended[1:-1, 2:, 1:-1, 1:-1],
    )
    curvature = coef_list[0] * (high_cells[0] - 2.0 * center + low_cells[0])
    curvature = curvature + coef_list[1] * (high_cells[1] - 2.0 * center + low_cells[1])
    curvature = curvature + coef_list[2] * (high_cells[2] - 2.0 * center + low_cells[2])
    diffusion = kappa_col[:, None, None, None] * curvature
    advection = up_list[0] * (center - low_cells[0]) + down_list[0] * (high_cells[0] - center)
    advection = (
        advection + up_list[1] * (center - low_cells[1]) + down_list[1] * (high_cells[1] - center)
    )
    advection = (
        advection + up_list[2] * (center - low_cells[2]) + down_list[2] * (high_cells[2] - center)
    )
    bin_low = extended[:-2, 1:-1, 1:-1, 1:-1]
    bin_high = extended[2:, 1:-1, 1:-1, 1:-1]
    momentum = (drift_up * (bin_high - center) + drift_down * (center - bin_low)) / step_m
    return diffusion - advection + momentum


ROWS = 16


def _vec(shape, scalar):
    return jnp.full(shape, scalar, jnp.int32)


def section_kernel(scal_ref, flag_ref, kappa_ref, g_ref, gp_ref, gn_ref, azlo_ref, azhi_ref,
                   binlo_ref, binhi_ref, coef_ref, *rest, second):
    if second:
        f0_ref, out_ref = rest
    else:
        out_ref, az_first_ref, az_last_ref, bin_first_ref, bin_last_ref = rest
    step = pl.program_id(0)
    last_step = pl.num_programs(0) - 1
    bins, planes, colat, shells = g_ref.shape
    shape = (ROWS, shells)
    row = lax.broadcasted_iota(jnp.int32, shape, 0)
    lane = lax.broadcasted_iota(jnp.int32, shape, 1)
    first_az = _vec(shape, step) == 0
    last_az = _vec(shape, step) == last_step
    band_first = _vec(shape, flag_ref[0]) == 1
    band_last = _vec(shape, flag_ref[1]) == 1
    scale = scal_ref[0]

    def chunk(k, i, r0, kap, edge):
        rows = slice(r0, r0 + ROWS)
        center = g_ref[k, i, rows, :]
        if r0 == 0:
            low_t = jnp.where(row == 0, center, pltpu.roll(center, 1, 0))
        else:
            low_t = g_ref[k, i, r0 - 1:r0 - 1 + ROWS, :]
        if r0 + ROWS == colat:
            high_t = jnp.where(row == ROWS - 1, center, pltpu.roll(center, ROWS - 1, 0))
        else:
            high_t = g_ref[k, i, r0 + 1:r0 + 1 + ROWS, :]
        low_r = jnp.where(lane == 0, center, pltpu.roll(center, 1, 1))
        high_r = jnp.where(lane == shells - 1, center, pltpu.roll(center, shells - 1, 1))
        if i == 0:
            low_p = jnp.where(first_az, azlo_ref[k, 0, rows, :].astype(jnp.float32), gp_ref[k, 0, rows, :])
        else:
            low_p = g_ref[k, i - 1, rows, :]
        if i == planes - 1:
            high_p = jnp.where(last_az, azhi_ref[k, 0, rows, :].astype(jnp.float32), gn_ref[k, 0, rows, :])
        else:
            high_p = g_ref[k, i + 1, rows, :]
        if edge == "low":
            low_b = jnp.where(band_first, center, binlo_ref[0, i, rows, :].astype(jnp.float32))
        else:
            low_b = g_ref[k - 1, i, rows, :]
        if edge == "high":
            high_b = jnp.where(band_last, center, binhi_ref[0, i, rows, :].astype(jnp.float32))
        else:
            high_b = g_ref[k + 1, i, rows, :]
        d_lo = (center - low_r, center - low_t, center - low_p)
        d_hi = (high_r - center, high_t - center, high_p - center)
        curvature = coef_ref[0, i, rows, :] * (d_hi[0] - d_lo[0])
        curvature = curvature + coef_ref[1, i, rows, :] * (d_hi[1] - d_lo[1])
        curvature = curvature + coef_ref[2, i, rows, :] * (d_hi[2] - d_lo[2])
        advection = coef_ref[3, i, rows, :] * d_lo[0] + coef_ref[6, i, rows, :] * d_hi[0]
        advection = advection + coef_ref[4, i, rows, :] * d_lo[1] + coef_ref[7, i, rows, :] * d_hi[1]
        advection = advection + coef_ref[5, i, rows, :] * d_lo[2] + coef_ref[8, i, rows, :] * d_hi[2]
        momentum = coef_ref[9, i, rows, :] * (high_b - center) + coef_ref[10, i, rows, :] * (center - low_b)
        rate = kap * curvature - advection + momentum
        if second:
            value = 1.5 * center - 0.5 * f0_ref[k, i, rows, :] + scale * rate
        else:
            value = center + scale * rate
        out_ref[k, i, rows, :] = value
        if not second:
            half = value.astype(jnp.bfloat16)
            if i == 0:
                az_first_ref[k, 0, rows, :] = half
            if i == planes - 1:
                az_last_ref[k, 0, rows, :] = half
            if edge == "low":
                bin_first_ref[0, i, rows, :] = half
            if edge == "high":
                bin_last_ref[0, i, rows, :] = half

    def all_rows(k, edge):
        kap = kappa_ref[k]
        for i in range(planes):
            for r0 in range(0, colat, ROWS):
                chunk(k, i, r0, kap, edge)

    all_rows(0, "low")

    def middle(k, carry):
        all_rows(k, None)
        return carry

    lax.fori_loop(1, bins - 1, middle, 0)
    all_rows(bins - 1, "high")


PLANES = 2


def section_call(scal, flags, kappa, g, az_low, az_high, bin_low, bin_high, coefs, f0=None):
    bins, azim, colat, shells = g.shape
    block = (bins, PLANES, colat, shells)
    plane = (bins, 1, colat, shells)
    bin_block = (1, PLANES, colat, shells)
    smem = pl.BlockSpec(memory_space=pltpu.SMEM)
    in_specs = [
        smem,
        smem,
        smem,
        pl.BlockSpec(block, lambda a: (0, a, 0, 0)),
        pl.BlockSpec(plane, lambda a: (0, jnp.maximum(a * PLANES - 1, 0), 0, 0)),
        pl.BlockSpec(plane, lambda a: (0, jnp.minimum(a * PLANES + PLANES, azim - 1), 0, 0)),
        pl.BlockSpec(plane, lambda a: (0, 0, 0, 0)),
        pl.BlockSpec(plane, lambda a: (0, 0, 0, 0)),
        pl.BlockSpec(bin_block, lambda a: (0, a, 0, 0)),
        pl.BlockSpec(bin_block, lambda a: (0, a, 0, 0)),
        pl.BlockSpec((coefs.shape[0], PLANES, colat, shells), lambda a: (0, a, 0, 0)),
    ]
    args = [scal, flags, kappa, g, g, g, az_low, az_high, bin_low, bin_high, coefs]
    out_specs = pl.BlockSpec(block, lambda a: (0, a, 0, 0))
    out_shape = jax.ShapeDtypeStruct(g.shape, jnp.float32)
    if f0 is not None:
        in_specs.append(pl.BlockSpec(block, lambda a: (0, a, 0, 0)))
        args.append(f0)
    else:
        out_specs = [
            out_specs,
            pl.BlockSpec(plane, lambda a: (0, a, 0, 0)),
            pl.BlockSpec(plane, lambda a: (0, a, 0, 0)),
            pl.BlockSpec(bin_block, lambda a: (0, a, 0, 0)),
            pl.BlockSpec(bin_block, lambda a: (0, a, 0, 0)),
        ]
        half_plane = jax.ShapeDtypeStruct((bins, azim // PLANES, colat, shells), jnp.bfloat16)
        half_bin = jax.ShapeDtypeStruct((1, azim, colat, shells), jnp.bfloat16)
        out_shape = [out_shape, half_plane, half_plane, half_bin, half_bin]
    return pl.pallas_call(
        functools.partial(section_kernel, second=f0 is not None),
        grid=(azim // PLANES,),
        in_specs=in_specs,
        out_specs=out_specs,
        out_shape=out_shape,
        compiler_params=pltpu.CompilerParams(dimension_semantics=("arbitrary",)),
    )(*args)


def exchange(first, last, axis):
    size = lax.axis_size(axis)
    up = [(i, (i + 1) % size) for i in range(size)]
    down = [(j, i) for i, j in up]
    return lax.ppermute(last, axis, up), lax.ppermute(first, axis, down)


def cell_state(q):
    rho, v, b, p = q[0], q[1:4], q[4:7], q[7]
    vv = v[0] * v[0] + v[1] * v[1] + v[2] * v[2]
    bb = b[0] * b[0] + b[1] * b[1] + b[2] * b[2]
    energy = p / (ADIABATIC - 1.0) + 0.5 * rho * vv + 0.5 * bb
    return [rho, rho * v[0], rho * v[1], rho * v[2], b[0], b[1], b[2], energy]


def cell_flux(q, u, normal):
    rho, v, b, p = q[0], q[1:4], q[4:7], q[7]
    vn, bn = v[normal], b[normal]
    magnetic = 0.5 * (b[0] * b[0] + b[1] * b[1] + b[2] * b[2])
    total_p = p + magnetic
    momentum = [rho * v[k] * vn - b[k] * bn for k in range(3)]
    momentum[normal] = momentum[normal] + total_p
    induction = [vn * b[k] - bn * v[k] for k in range(3)]
    energy = (u[7] + total_p) * vn - bn * (v[0] * b[0] + v[1] * b[1] + v[2] * b[2])
    speed = jnp.abs(vn) + jnp.sqrt((ADIABATIC * p + 2.0 * magnetic) / rho)
    return [rho * vn] + momentum + induction + [energy], speed


def face_flux(f_low, s_low, u_low, f_high, s_high, u_high):
    wave = jnp.maximum(s_low, s_high)
    return [0.5 * (f_low[c] + f_high[c]) - 0.5 * wave * (u_high[c] - u_low[c]) for c in range(8)]


def mhd_kernel(dt_ref, rho_c, v_c, b_c, p_c, rho_m, v_m, b_m, p_m, rho_p, v_p, b_p, p_p,
               azlo_ref, azhi_ref, clo_ref, chi_ref, wr_ref, wt_ref, wp_ref, *rest, offset, last_step):
    out_ref = rest[-1]
    step = pl.program_id(0) + offset

    def prim(rho_ref, v_ref, b_ref, p_ref):
        return [rho_ref[0], v_ref[0, 0], v_ref[1, 0], v_ref[2, 0],
                b_ref[0, 0], b_ref[1, 0], b_ref[2, 0], p_ref[0]]

    q = prim(rho_c, v_c, b_c, p_c)
    shape = q[0].shape
    nrow, nlane = shape
    row = lax.broadcasted_iota(jnp.int32, shape, 0)
    lane = lax.broadcasted_iota(jnp.int32, shape, 1)
    first_az = _vec(shape, step) == 0
    last_az = _vec(shape, step) == last_step
    q_m = prim(rho_m, v_m, b_m, p_m)
    q_p = prim(rho_p, v_p, b_p, p_p)
    q_m = [jnp.where(first_az, azlo_ref[c, 0], q_m[c]) for c in range(8)]
    q_p = [jnp.where(last_az, azhi_ref[c, 0], q_p[c]) for c in range(8)]
    u = cell_state(q)
    dt = dt_ref[0]

    def lane_next(x):
        return jnp.where(lane == nlane - 1, x, pltpu.roll(x, nlane - 1, 1))

    f, s = cell_flux(q, u, 0)
    high = face_flux(f, s, u, [lane_next(x) for x in f], lane_next(s), [lane_next(x) for x in u])
    low = [jnp.where(lane == 0, f[c], pltpu.roll(high[c], 1, 1)) for c in range(8)]
    width_r = wr_ref[...]
    radial = [(high[c] - low[c]) / width_r for c in range(8)]

    q_l = [clo_ref[c, 0] for c in range(8)]
    q_h = [chi_ref[c, 0] for c in range(8)]
    u_l = cell_state(q_l)
    u_h = cell_state(q_h)
    f, s = cell_flux(q, u, 1)
    f_l, s_l = cell_flux(q_l, u_l, 1)
    f_h, s_h = cell_flux(q_h, u_h, 1)

    def row_next(x, h):
        return jnp.where(row == nrow - 1, jnp.broadcast_to(h, shape), pltpu.roll(x, nrow - 1, 0))

    high = face_flux(f, s, u, [row_next(f[c], f_h[c]) for c in range(8)], row_next(s, s_h),
                     [row_next(u[c], u_h[c]) for c in range(8)])
    first = face_flux(f_l, s_l, u_l, f, s, u)
    low = [jnp.where(row == 0, first[c], pltpu.roll(high[c], 1, 0)) for c in range(8)]
    width_t = wt_ref[...]
    polar = [(high[c] - low[c]) / width_t for c in range(8)]

    u_m = cell_state(q_m)
    u_p = cell_state(q_p)
    f, s = cell_flux(q, u, 2)
    f_m, s_m = cell_flux(q_m, u_m, 2)
    f_p, s_p = cell_flux(q_p, u_p, 2)
    high = face_flux(f, s, u, f_p, s_p, u_p)
    low = face_flux(f_m, s_m, u_m, f, s, u)
    width_p = wp_ref[...]
    for c in range(8):
        azimuthal = (high[c] - low[c]) / width_p
        out_ref[c, 0] = u[c] - dt * (radial[c] + polar[c] + azimuthal)


def mhd_call(dt, density, velocity, magnetic_vector, pressure, az_low, az_high,
             colat_low, colat_high, width_r, width_t, width_p, offset, count, previous=None):
    azim, colat, radial = density.shape
    scalar_block = (1, colat, radial)
    vector_block = (3, 1, colat, radial)

    def own(a):
        return a + offset

    def clamp_low(a):
        return jnp.maximum(a + offset - 1, 0)

    def clamp_high(a):
        return jnp.minimum(a + offset + 1, azim - 1)

    in_specs = [pl.BlockSpec(memory_space=pltpu.SMEM)]
    for pick in (own, clamp_low, clamp_high):
        in_specs += [
            pl.BlockSpec(scalar_block, lambda a, pick=pick: (pick(a), 0, 0)),
            pl.BlockSpec(vector_block, lambda a, pick=pick: (0, pick(a), 0, 0)),
            pl.BlockSpec(vector_block, lambda a, pick=pick: (0, pick(a), 0, 0)),
            pl.BlockSpec(scalar_block, lambda a, pick=pick: (pick(a), 0, 0)),
        ]
    in_specs += [
        pl.BlockSpec((8, 1, colat, radial), lambda a: (0, 0, 0, 0)),
        pl.BlockSpec((8, 1, colat, radial), lambda a: (0, 0, 0, 0)),
        pl.BlockSpec((8, 1, 1, radial), lambda a: (0, a + offset, 0, 0)),
        pl.BlockSpec((8, 1, 1, radial), lambda a: (0, a + offset, 0, 0)),
        pl.BlockSpec((1, radial), lambda a: (0, 0)),
        pl.BlockSpec((1, radial), lambda a: (0, 0)),
        pl.BlockSpec((colat, radial), lambda a: (0, 0)),
    ]
    fields = (density, velocity, magnetic_vector, pressure)
    args = [dt, *fields, *fields, *fields, az_low, az_high, colat_low, colat_high,
            width_r, width_t, width_p]
    aliases = {}
    if previous is not None:
        in_specs.append(pl.BlockSpec(memory_space=pl.ANY))
        aliases = {len(args): 0}
        args.append(previous)
    return pl.pallas_call(
        functools.partial(mhd_kernel, offset=offset, last_step=azim - 1),
        grid=(count,),
        in_specs=in_specs,
        out_specs=pl.BlockSpec((8, 1, colat, radial), lambda a: (0, a + offset, 0, 0)),
        out_shape=jax.ShapeDtypeStruct((8, azim, colat, radial), jnp.float32),
        input_output_aliases=aliases,
        compiler_params=pltpu.CompilerParams(dimension_semantics=("arbitrary",)),
    )(*args)


def mhd_halos(density, velocity, magnetic_vector, pressure, band_pos, band_count):
    fields = [density, velocity[0], velocity[1], velocity[2],
              magnetic_vector[0], magnetic_vector[1], magnetic_vector[2], pressure]
    azim, colat = density.shape[0], density.shape[1]
    az_first = jnp.stack([x[0:1] for x in fields])
    az_last = jnp.stack([x[azim - 1:azim] for x in fields])
    c_first = jnp.stack([x[:, 0:1] for x in fields])
    c_last = jnp.stack([x[:, colat - 1:colat] for x in fields])
    phi_size = lax.axis_size("phi")
    up = [(i, (i + 1) % phi_size) for i in range(phi_size)]
    down = [(j, i) for i, j in up]
    az_low = lax.ppermute(az_last, "phi", up)
    az_high = lax.ppermute(az_first, "phi", down)
    up = [(i, (i + 1) % band_count) for i in range(band_count)]
    down = [(j, i) for i, j in up]
    c_low = lax.ppermute(c_last, "band", up)
    c_high = lax.ppermute(c_first, "band", down)
    c_low = jnp.where(band_pos == 0, c_first, c_low)
    c_high = jnp.where(band_pos == band_count - 1, c_last, c_high)
    return az_low, az_high, c_low, c_high


def body(
    density,
    velocity,
    magnetic_vector,
    pressure,
    fluid_courant_number,
    cosmic_ray_density,
    diffusion_per_bin,
    super_step_scale,
):
    azim_dev = density.shape[0]
    colat_dev = density.shape[1]
    radial_cell_count = density.shape[2]
    band_count = lax.axis_size("band")
    phi_count = lax.axis_size("phi")
    colatitude_count = colat_dev * band_count
    azimuth_cell_count = azim_dev * phi_count
    bin_dev = cosmic_ray_density.shape[0]
    momentum_bin_count = bin_dev * band_count
    outer_shell_count = cosmic_ray_density.shape[3]
    band_pos = lax.axis_index("band")
    mesh_spacing = grid_steps(
        radial_cell_count, colatitude_count, azimuth_cell_count, momentum_bin_count
    )
    fluid_rate, cosmic_ray_rate = rate_limits(
        radial_cell_count,
        outer_shell_count,
        colatitude_count,
        azimuth_cell_count,
        momentum_bin_count,
    )
    radius_full = shell_radii(0, radial_cell_count, radial_cell_count)
    colatitude_local = colatitudes(band_pos * colat_dev, colat_dev, colatitude_count)
    dt = jnp.reshape(fluid_courant_number / fluid_rate, (1,)).astype(jnp.float32)
    mhd_args = (
        dt, density, velocity, magnetic_vector, pressure,
        *mhd_halos(density, velocity, magnetic_vector, pressure, band_pos, band_count),
        (radius_full * mesh_spacing[0])[None],
        (radius_full * mesh_spacing[1])[None],
        jnp.sin(colatitude_local)[:, None] * radius_full * mesh_spacing[2],
    )
    first_planes = azim_dev // 2
    fluid_state = mhd_call(*mhd_args, 0, first_planes)
    first_shell = radial_cell_count - outer_shell_count
    radius_sh = shell_radii(first_shell, outer_shell_count, radial_cell_count)
    colatitude_full = colatitudes(0, colatitude_count, colatitude_count)
    own_fields = jnp.concatenate(
        [velocity[:, :, :, first_shell:], magnetic_vector[:, :, :, first_shell:]], axis=0
    ).astype(jnp.bfloat16)
    wind_half = lax.all_gather(own_fields, "band", axis=2, tiled=True)
    fluid_state, wind_half = lax.optimization_barrier((fluid_state, wind_half))
    wind_vel = wind_half[0:3].astype(jnp.float32)
    azim_pad = padded(wind_half[2], (("phi", 0),), 1).astype(jnp.float32)
    radial_pad = jnp.pad(wind_vel[0], ((0, 0), (0, 0), (1, 1)), mode="edge")
    polar_pad = jnp.pad(wind_vel[1], ((0, 0), (1, 1), (0, 0)), mode="edge")
    spread_half = divergence(
        radial_pad, polar_pad, azim_pad, radius_sh, colatitude_full, mesh_spacing
    ).astype(jnp.bfloat16)
    kappa_here = lax.dynamic_slice_in_dim(diffusion_per_bin, band_pos * bin_dev, bin_dev)
    sts_step = super_step_scale / cosmic_ray_rate
    coef_set = transport_coefficients(
        wind_half[0:3].astype(jnp.float32),
        wind_half[3:6].astype(jnp.float32),
        spread_half.astype(jnp.float32),
        radius_sh,
        colatitude_full,
        mesh_spacing,
    )

    coef_list, up_list, down_list, drift_up, drift_down = coef_set
    coefs = jnp.stack(
        list(coef_list) + list(up_list) + list(down_list)
        + [drift_up / mesh_spacing[3], drift_down / mesh_spacing[3]],
        axis=0,
    )
    scal1 = jnp.reshape(sts_step / 3.0, (1,)).astype(jnp.float32)
    scal2 = jnp.reshape(sts_step / 2.0, (1,)).astype(jnp.float32)
    flags = jnp.stack([band_pos == 0, band_pos == band_count - 1]).astype(jnp.int32)
    bins = cosmic_ray_density.shape[0]
    edges = (
        cosmic_ray_density[:, 0:1],
        cosmic_ray_density[:, azim_dev - 1:azim_dev],
        cosmic_ray_density[0:1],
        cosmic_ray_density[bins - 1:bins],
    )
    edges = [x.astype(jnp.bfloat16) for x in lax.optimization_barrier(edges)]
    az_low, az_high = exchange(edges[0], edges[1], "phi")
    bin_low, bin_high = exchange(edges[2], edges[3], "band")
    first_section, *edges = section_call(
        scal1, flags, kappa_here, cosmic_ray_density, az_low, az_high, bin_low, bin_high, coefs
    )
    steps = edges[0].shape[1]
    az_low, az_high = exchange(edges[0][:, 0:1], edges[1][:, steps - 1:steps], "phi")
    bin_low, bin_high = exchange(edges[2], edges[3], "band")
    fluid_state, first_section = lax.optimization_barrier((fluid_state, first_section))
    fluid_state = mhd_call(
        *mhd_args, first_planes, azim_dev - first_planes, previous=fluid_state
    )
    fluid_state, az_low, az_high, bin_low, bin_high = lax.optimization_barrier(
        (fluid_state, az_low, az_high, bin_low, bin_high)
    )
    cosmic_ray_next = section_call(
        scal2, flags, kappa_here, first_section, az_low, az_high, bin_low, bin_high, coefs,
        cosmic_ray_density,
    )
    return (fluid_state, cosmic_ray_next)


def solution(mesh):
    placed = (
        P("phi", "band", None),
        P(None, "phi", "band", None),
        P(None, "phi", "band", None),
        P("phi", "band", None),
        P(),
        P("band", "phi", None, None),
        P(),
        P(),
    )
    return jax.shard_map(
        body,
        mesh=mesh,
        in_specs=placed,
        out_specs=(P(None, "phi", "band", None), P("band", "phi", None, None)),
        check_vma=False,
    )
```

```python
import functools
import math

import jax
import jax.numpy as jnp
from jax import lax
from jax.experimental import pallas as pl
from jax.experimental.pallas import tpu as pltpu
from jax.sharding import PartitionSpec as P

ADIABATIC = 5.0 / 3.0
INNER_RADIUS = 0.1
R_RATIO = 30.0
COLAT_LOW = math.pi / 6.0
COLAT_SPAN = 2.0 * math.pi / 3.0
P_RATIO = 1000.0
K_RATIO = 0.1
B_FLOOR = 0.1
V_BOUND = 3.0
B_BOUND = 3.0
P_HIGH = 2.0
RHO_LOW = 0.5
KAPPA_HIGH = 0.5


def padded(value, sides, width):
    for axis, dim in sides:
        size, length = (lax.axis_size(axis), value.shape[dim])
        up = [(i, (i + 1) % size) for i in range(size)]
        down = [(j, i) for i, j in up]
        last = lax.slice_in_dim(value, length - width, length, axis=dim)
        leading = lax.slice_in_dim(value, 0, width, axis=dim)
        before = lax.ppermute(last, axis, up)
        after = lax.ppermute(leading, axis, down)
        value = jnp.concatenate([before, value, after], axis=dim)
    return value


def grid_steps(n_radial, n_colat, n_azim, n_bins):
    return (
        math.log(R_RATIO) / n_radial,
        COLAT_SPAN / n_colat,
        2.0 * math.pi / n_azim,
        math.log(P_RATIO) / n_bins,
    )


def rate_limits(n_radial, n_shells, n_colat, n_azim, n_bins):
    radial_spacing, colatitude_spacing, azimuth_spacing, step_m = grid_steps(
        n_radial, n_colat, n_azim, n_bins
    )
    sine_lower = math.sin(COLAT_LOW + 0.5 * colatitude_spacing)
    fluid_radius = INNER_RADIUS * math.exp(0.5 * radial_spacing)
    fastest_limit = V_BOUND + math.sqrt((ADIABATIC * P_HIGH + 3.0 * B_BOUND**2) / RHO_LOW)
    fluid_rate = fastest_limit * (
        1.0 / (fluid_radius * radial_spacing)
        + 1.0 / (fluid_radius * colatitude_spacing)
        + 1.0 / (fluid_radius * sine_lower * azimuth_spacing)
    )
    shell_low = INNER_RADIUS * math.exp(radial_spacing * (n_radial - n_shells + 0.5))
    inv_r = 1.0 / (shell_low * radial_spacing)
    inv_t = 1.0 / (shell_low * colatitude_spacing)
    inv_p = 1.0 / (shell_low * sine_lower * azimuth_spacing)
    cosmic_ray_rate = (
        2.0 * KAPPA_HIGH * (inv_r**2 + inv_t**2 + inv_p**2)
        + V_BOUND * (inv_r + inv_t + inv_p)
        + V_BOUND * (inv_r + inv_t + inv_p + 4.0 / shell_low) / (3.0 * step_m)
    )
    return (fluid_rate, cosmic_ray_rate)


def shell_radii(start_index, cell_count, n_radial):
    cell_index = jnp.arange(cell_count, dtype=jnp.float32) + (start_index + 0.5)
    return INNER_RADIUS * jnp.exp(math.log(R_RATIO) / n_radial * cell_index)


def colatitudes(start_index, cell_count, n_colat):
    cell_index = jnp.arange(cell_count, dtype=jnp.float32) + 0.5
    return COLAT_LOW + COLAT_SPAN * (cell_index + start_index) / n_colat


def edge_fix(values, along_axis, depth, band_pos, axis_count):
    extent = values.shape[along_axis]
    low_ghost = lax.slice_in_dim(values, 0, depth, axis=along_axis)
    high_ghost = lax.slice_in_dim(values, extent - depth, extent, axis=along_axis)
    first_own = lax.slice_in_dim(values, depth, depth + 1, axis=along_axis)
    last_own = lax.slice_in_dim(values, extent - depth - 1, extent - depth, axis=along_axis)
    low_rim = jnp.where(band_pos == 0, first_own, low_ghost)
    high_rim = jnp.where(band_pos == axis_count - 1, last_own, high_ghost)
    middle = lax.slice_in_dim(values, depth, extent - depth, axis=along_axis)
    return jnp.concatenate([low_rim, middle, high_rim], axis=along_axis)


def conserved(primitive):
    density = primitive[0]
    velocity = primitive[1:4]
    magnetic_vector = primitive[4:7]
    pressure = primitive[7]
    energy = (
        pressure / (ADIABATIC - 1.0)
        + 0.5 * density * jnp.sum(velocity * velocity, axis=0)
        + 0.5 * jnp.sum(magnetic_vector * magnetic_vector, axis=0)
    )
    return jnp.concatenate(
        [density[None], density[None] * velocity, magnetic_vector, energy[None]], axis=0
    )


def face_terms(primitive, cell_state, normal):
    density = primitive[0]
    velocity = primitive[1:4]
    magnetic_vector = primitive[4:7]
    pressure = primitive[7]
    v_normal = velocity[normal]
    b_normal = magnetic_vector[normal]
    magnetic = 0.5 * jnp.sum(magnetic_vector * magnetic_vector, axis=0)
    total_p = pressure + magnetic
    momentum = [density * velocity[k] * v_normal - magnetic_vector[k] * b_normal for k in range(3)]
    momentum[normal] = momentum[normal] + total_p
    induction = [v_normal * magnetic_vector[k] - b_normal * velocity[k] for k in range(3)]
    energy_flux = (cell_state[7] + total_p) * v_normal - b_normal * jnp.sum(
        velocity * magnetic_vector, axis=0
    )
    fluxes = jnp.stack([density * v_normal] + momentum + induction + [energy_flux], axis=0)
    speeds = jnp.abs(v_normal) + jnp.sqrt((ADIABATIC * pressure + 2.0 * magnetic) / density)
    return (fluxes, speeds)


def rusanov(primitive, cell_state, normal, along_axis, spacing):
    fluxes, speeds = face_terms(primitive, cell_state, normal)
    length = speeds.shape[along_axis]
    wave_speed = jnp.maximum(
        lax.slice_in_dim(speeds, 0, length - 1, axis=along_axis),
        lax.slice_in_dim(speeds, 1, length, axis=along_axis),
    )
    flux_low = lax.slice_in_dim(fluxes, 0, length - 1, axis=along_axis + 1)
    flux_high = lax.slice_in_dim(fluxes, 1, length, axis=along_axis + 1)
    state_low = lax.slice_in_dim(cell_state, 0, length - 1, axis=along_axis + 1)
    state_high = lax.slice_in_dim(cell_state, 1, length, axis=along_axis + 1)
    face_flux = 0.5 * (flux_low + flux_high) - 0.5 * wave_speed[None] * (state_high - state_low)
    upper = lax.slice_in_dim(face_flux, 1, length - 1, axis=along_axis + 1)
    lower = lax.slice_in_dim(face_flux, 0, length - 2, axis=along_axis + 1)
    return (upper - lower) / spacing


def fluid_update(padded_array, radius_values, colatitude_mesh, timestep_length, mesh_spacing):
    ghosted = jnp.pad(padded_array, ((0, 0), (0, 0), (0, 0), (1, 1)), mode="edge")
    cell_state = conserved(ghosted)
    width_r = radius_values * mesh_spacing[0]
    width_t = radius_values * mesh_spacing[1]
    width_p = jnp.sin(colatitude_mesh)[:, None] * radius_values * mesh_spacing[2]
    radial = rusanov(ghosted[:, 1:-1, 1:-1, :], cell_state[:, 1:-1, 1:-1, :], 0, 2, width_r)
    polar = rusanov(ghosted[:, 1:-1, :, 1:-1], cell_state[:, 1:-1, :, 1:-1], 1, 1, width_t)
    azimuthal = rusanov(ghosted[:, :, 1:-1, 1:-1], cell_state[:, :, 1:-1, 1:-1], 2, 0, width_p)
    return cell_state[:, 1:-1, 1:-1, 1:-1] - timestep_length * (radial + polar + azimuthal)


def divergence(radial_pad, polar_pad, azim_pad, radius_values, colatitude_mesh, mesh_spacing):
    sin_colat = jnp.sin(colatitude_mesh)[:, None]
    cotangent = (jnp.cos(colatitude_mesh) / jnp.sin(colatitude_mesh))[:, None]
    radial_mid = radial_pad[:, :, 1:-1]
    polar_mid = polar_pad[:, 1:-1, :]
    d_radial = (radial_pad[:, :, 2:] - radial_pad[:, :, :-2]) / (
        2.0 * radius_values * mesh_spacing[0]
    )
    d_polar = (polar_pad[:, 2:, :] - polar_pad[:, :-2, :]) / (2.0 * radius_values * mesh_spacing[1])
    d_azim = (azim_pad[2:] - azim_pad[:-2]) / (2.0 * radius_values * sin_colat * mesh_spacing[2])
    return (
        d_radial
        + 2.0 * radial_mid / radius_values
        + d_polar
        + cotangent * polar_mid / radius_values
        + d_azim
    )


def transport_coefficients(
    wind_vel, mag_wind, spread, radius_values, colatitude_mesh, mesh_spacing
):
    width_r = radius_values * mesh_spacing[0]
    width_t = radius_values * mesh_spacing[1]
    width_p = jnp.sin(colatitude_mesh)[:, None] * radius_values * mesh_spacing[2]
    widths = (width_r, width_t, width_p)
    mag_sq = jnp.sum(mag_wind * mag_wind, axis=0) + B_FLOOR
    b_share = K_RATIO + (1.0 - K_RATIO) * mag_wind * mag_wind / mag_sq
    coef_list = [b_share[k] / (widths[k] * widths[k]) for k in range(3)]
    up_list = [jnp.maximum(wind_vel[k], 0.0) / widths[k] for k in range(3)]
    down_list = [jnp.minimum(wind_vel[k], 0.0) / widths[k] for k in range(3)]
    drift_rate = spread / 3.0
    return (
        coef_list,
        up_list,
        down_list,
        jnp.maximum(drift_rate, 0.0),
        jnp.minimum(drift_rate, 0.0),
    )


def transport_rate(extended, coef_set, kappa_col, step_m):
    coef_list, up_list, down_list, drift_up, drift_down = coef_set
    center = extended[1:-1, 1:-1, 1:-1, 1:-1]
    low_cells = (
        extended[1:-1, 1:-1, 1:-1, :-2],
        extended[1:-1, 1:-1, :-2, 1:-1],
        extended[1:-1, :-2, 1:-1, 1:-1],
    )
    high_cells = (
        extended[1:-1, 1:-1, 1:-1, 2:],
        extended[1:-1, 1:-1, 2:, 1:-1],
        extended[1:-1, 2:, 1:-1, 1:-1],
    )
    curvature = coef_list[0] * (high_cells[0] - 2.0 * center + low_cells[0])
    curvature = curvature + coef_list[1] * (high_cells[1] - 2.0 * center + low_cells[1])
    curvature = curvature + coef_list[2] * (high_cells[2] - 2.0 * center + low_cells[2])
    diffusion = kappa_col[:, None, None, None] * curvature
    advection = up_list[0] * (center - low_cells[0]) + down_list[0] * (high_cells[0] - center)
    advection = (
        advection + up_list[1] * (center - low_cells[1]) + down_list[1] * (high_cells[1] - center)
    )
    advection = (
        advection + up_list[2] * (center - low_cells[2]) + down_list[2] * (high_cells[2] - center)
    )
    bin_low = extended[:-2, 1:-1, 1:-1, 1:-1]
    bin_high = extended[2:, 1:-1, 1:-1, 1:-1]
    momentum = (drift_up * (bin_high - center) + drift_down * (center - bin_low)) / step_m
    return diffusion - advection + momentum


ROWS = 16


def _vec(shape, scalar):
    return jnp.full(shape, scalar, jnp.int32)


def section_kernel(scal_ref, flag_ref, kappa_ref, g_ref, gp_ref, gn_ref, azlo_ref, azhi_ref,
                   binlo_ref, binhi_ref, coef_ref, *rest, second):
    if second:
        f0_ref, out_ref = rest
    else:
        out_ref, az_first_ref, az_last_ref, bin_first_ref, bin_last_ref = rest
    step = pl.program_id(0)
    last_step = pl.num_programs(0) - 1
    bins, planes, colat, shells = g_ref.shape
    shape = (ROWS, shells)
    row = lax.broadcasted_iota(jnp.int32, shape, 0)
    lane = lax.broadcasted_iota(jnp.int32, shape, 1)
    first_az = _vec(shape, step) == 0
    last_az = _vec(shape, step) == last_step
    band_first = _vec(shape, flag_ref[0]) == 1
    band_last = _vec(shape, flag_ref[1]) == 1
    scale = scal_ref[0]

    def chunk(k, i, r0, kap, edge):
        rows = slice(r0, r0 + ROWS)
        center = g_ref[k, i, rows, :]
        if r0 == 0:
            low_t = jnp.where(row == 0, center, pltpu.roll(center, 1, 0))
        else:
            low_t = g_ref[k, i, r0 - 1:r0 - 1 + ROWS, :]
        if r0 + ROWS == colat:
            high_t = jnp.where(row == ROWS - 1, center, pltpu.roll(center, ROWS - 1, 0))
        else:
            high_t = g_ref[k, i, r0 + 1:r0 + 1 + ROWS, :]
        low_r = jnp.where(lane == 0, center, pltpu.roll(center, 1, 1))
        high_r = jnp.where(lane == shells - 1, center, pltpu.roll(center, shells - 1, 1))
        if i == 0:
            low_p = jnp.where(first_az, azlo_ref[k, 0, rows, :].astype(jnp.float32), gp_ref[k, 0, rows, :])
        else:
            low_p = g_ref[k, i - 1, rows, :]
        if i == planes - 1:
            high_p = jnp.where(last_az, azhi_ref[k, 0, rows, :].astype(jnp.float32), gn_ref[k, 0, rows, :])
        else:
            high_p = g_ref[k, i + 1, rows, :]
        if edge == "low":
            low_b = jnp.where(band_first, center, binlo_ref[0, i, rows, :].astype(jnp.float32))
        else:
            low_b = g_ref[k - 1, i, rows, :]
        if edge == "high":
            high_b = jnp.where(band_last, center, binhi_ref[0, i, rows, :].astype(jnp.float32))
        else:
            high_b = g_ref[k + 1, i, rows, :]
        d_lo = (center - low_r, center - low_t, center - low_p)
        d_hi = (high_r - center, high_t - center, high_p - center)
        curvature = coef_ref[0, i, rows, :] * (d_hi[0] - d_lo[0])
        curvature = curvature + coef_ref[1, i, rows, :] * (d_hi[1] - d_lo[1])
        curvature = curvature + coef_ref[2, i, rows, :] * (d_hi[2] - d_lo[2])
        advection = coef_ref[3, i, rows, :] * d_lo[0] + coef_ref[6, i, rows, :] * d_hi[0]
        advection = advection + coef_ref[4, i, rows, :] * d_lo[1] + coef_ref[7, i, rows, :] * d_hi[1]
        advection = advection + coef_ref[5, i, rows, :] * d_lo[2] + coef_ref[8, i, rows, :] * d_hi[2]
        momentum = coef_ref[9, i, rows, :] * (high_b - center) + coef_ref[10, i, rows, :] * (center - low_b)
        rate = kap * curvature - advection + momentum
        if second:
            value = 1.5 * center - 0.5 * f0_ref[k, i, rows, :] + scale * rate
        else:
            value = center + scale * rate
        out_ref[k, i, rows, :] = value
        if not second:
            half = value.astype(jnp.bfloat16)
            if i == 0:
                az_first_ref[k, 0, rows, :] = half
            if i == planes - 1:
                az_last_ref[k, 0, rows, :] = half
            if edge == "low":
                bin_first_ref[0, i, rows, :] = half
            if edge == "high":
                bin_last_ref[0, i, rows, :] = half

    def all_rows(k, edge):
        kap = kappa_ref[k]
        for i in range(planes):
            for r0 in range(0, colat, ROWS):
                chunk(k, i, r0, kap, edge)

    all_rows(0, "low")

    def middle(k, carry):
        all_rows(k, None)
        return carry

    lax.fori_loop(1, bins - 1, middle, 0)
    all_rows(bins - 1, "high")


PLANES = 4


def section_call(scal, flags, kappa, g, az_low, az_high, bin_low, bin_high, coefs, f0=None):
    bins, azim, colat, shells = g.shape
    block = (bins, PLANES, colat, shells)
    plane = (bins, 1, colat, shells)
    bin_block = (1, PLANES, colat, shells)
    smem = pl.BlockSpec(memory_space=pltpu.SMEM)
    in_specs = [
        smem,
        smem,
        smem,
        pl.BlockSpec(block, lambda a: (0, a, 0, 0)),
        pl.BlockSpec(plane, lambda a: (0, jnp.maximum(a * PLANES - 1, 0), 0, 0)),
        pl.BlockSpec(plane, lambda a: (0, jnp.minimum(a * PLANES + PLANES, azim - 1), 0, 0)),
        pl.BlockSpec(plane, lambda a: (0, 0, 0, 0)),
        pl.BlockSpec(plane, lambda a: (0, 0, 0, 0)),
        pl.BlockSpec(bin_block, lambda a: (0, a, 0, 0)),
        pl.BlockSpec(bin_block, lambda a: (0, a, 0, 0)),
        pl.BlockSpec((coefs.shape[0], PLANES, colat, shells), lambda a: (0, a, 0, 0)),
    ]
    args = [scal, flags, kappa, g, g, g, az_low, az_high, bin_low, bin_high, coefs]
    out_specs = pl.BlockSpec(block, lambda a: (0, a, 0, 0))
    out_shape = jax.ShapeDtypeStruct(g.shape, jnp.float32)
    if f0 is not None:
        in_specs.append(pl.BlockSpec(block, lambda a: (0, a, 0, 0)))
        args.append(f0)
    else:
        out_specs = [
            out_specs,
            pl.BlockSpec(plane, lambda a: (0, a, 0, 0)),
            pl.BlockSpec(plane, lambda a: (0, a, 0, 0)),
            pl.BlockSpec(bin_block, lambda a: (0, a, 0, 0)),
            pl.BlockSpec(bin_block, lambda a: (0, a, 0, 0)),
        ]
        half_plane = jax.ShapeDtypeStruct((bins, azim // PLANES, colat, shells), jnp.bfloat16)
        half_bin = jax.ShapeDtypeStruct((1, azim, colat, shells), jnp.bfloat16)
        out_shape = [out_shape, half_plane, half_plane, half_bin, half_bin]
    return pl.pallas_call(
        functools.partial(section_kernel, second=f0 is not None),
        grid=(azim // PLANES,),
        in_specs=in_specs,
        out_specs=out_specs,
        out_shape=out_shape,
        compiler_params=pltpu.CompilerParams(dimension_semantics=("arbitrary",)),
    )(*args)


def exchange(first, last, axis):
    size = lax.axis_size(axis)
    up = [(i, (i + 1) % size) for i in range(size)]
    down = [(j, i) for i, j in up]
    return lax.ppermute(last, axis, up), lax.ppermute(first, axis, down)


def cell_state(q):
    rho, v, b, p = q[0], q[1:4], q[4:7], q[7]
    vv = v[0] * v[0] + v[1] * v[1] + v[2] * v[2]
    bb = b[0] * b[0] + b[1] * b[1] + b[2] * b[2]
    energy = p / (ADIABATIC - 1.0) + 0.5 * rho * vv + 0.5 * bb
    return [rho, rho * v[0], rho * v[1], rho * v[2], b[0], b[1], b[2], energy]


def cell_flux(q, u, normal):
    rho, v, b, p = q[0], q[1:4], q[4:7], q[7]
    vn, bn = v[normal], b[normal]
    magnetic = 0.5 * (b[0] * b[0] + b[1] * b[1] + b[2] * b[2])
    total_p = p + magnetic
    momentum = [rho * v[k] * vn - b[k] * bn for k in range(3)]
    momentum[normal] = momentum[normal] + total_p
    induction = [vn * b[k] - bn * v[k] for k in range(3)]
    energy = (u[7] + total_p) * vn - bn * (v[0] * b[0] + v[1] * b[1] + v[2] * b[2])
    speed = jnp.abs(vn) + jnp.sqrt((ADIABATIC * p + 2.0 * magnetic) / rho)
    return [rho * vn] + momentum + induction + [energy], speed


def face_flux(f_low, s_low, u_low, f_high, s_high, u_high):
    wave = jnp.maximum(s_low, s_high)
    return [0.5 * (f_low[c] + f_high[c]) - 0.5 * wave * (u_high[c] - u_low[c]) for c in range(8)]


def mhd_kernel(dt_ref, rho_c, v_c, b_c, p_c, rho_m, v_m, b_m, p_m, rho_p, v_p, b_p, p_p,
               azlo_ref, azhi_ref, clo_ref, chi_ref, wr_ref, wt_ref, wp_ref, *rest, offset, last_step):
    out_ref = rest[-1]
    step = pl.program_id(0) + offset

    def prim(rho_ref, v_ref, b_ref, p_ref):
        return [rho_ref[0], v_ref[0, 0], v_ref[1, 0], v_ref[2, 0],
                b_ref[0, 0], b_ref[1, 0], b_ref[2, 0], p_ref[0]]

    q = prim(rho_c, v_c, b_c, p_c)
    shape = q[0].shape
    nrow, nlane = shape
    row = lax.broadcasted_iota(jnp.int32, shape, 0)
    lane = lax.broadcasted_iota(jnp.int32, shape, 1)
    first_az = _vec(shape, step) == 0
    last_az = _vec(shape, step) == last_step
    q_m = prim(rho_m, v_m, b_m, p_m)
    q_p = prim(rho_p, v_p, b_p, p_p)
    q_m = [jnp.where(first_az, azlo_ref[c, 0], q_m[c]) for c in range(8)]
    q_p = [jnp.where(last_az, azhi_ref[c, 0], q_p[c]) for c in range(8)]
    u = cell_state(q)
    dt = dt_ref[0]

    def lane_next(x):
        return jnp.where(lane == nlane - 1, x, pltpu.roll(x, nlane - 1, 1))

    f, s = cell_flux(q, u, 0)
    high = face_flux(f, s, u, [lane_next(x) for x in f], lane_next(s), [lane_next(x) for x in u])
    low = [jnp.where(lane == 0, f[c], pltpu.roll(high[c], 1, 1)) for c in range(8)]
    width_r = wr_ref[...]
    radial = [(high[c] - low[c]) / width_r for c in range(8)]

    q_l = [clo_ref[c, 0] for c in range(8)]
    q_h = [chi_ref[c, 0] for c in range(8)]
    u_l = cell_state(q_l)
    u_h = cell_state(q_h)
    f, s = cell_flux(q, u, 1)
    f_l, s_l = cell_flux(q_l, u_l, 1)
    f_h, s_h = cell_flux(q_h, u_h, 1)

    def row_next(x, h):
        return jnp.where(row == nrow - 1, jnp.broadcast_to(h, shape), pltpu.roll(x, nrow - 1, 0))

    high = face_flux(f, s, u, [row_next(f[c], f_h[c]) for c in range(8)], row_next(s, s_h),
                     [row_next(u[c], u_h[c]) for c in range(8)])
    first = face_flux(f_l, s_l, u_l, f, s, u)
    low = [jnp.where(row == 0, first[c], pltpu.roll(high[c], 1, 0)) for c in range(8)]
    width_t = wt_ref[...]
    polar = [(high[c] - low[c]) / width_t for c in range(8)]

    u_m = cell_state(q_m)
    u_p = cell_state(q_p)
    f, s = cell_flux(q, u, 2)
    f_m, s_m = cell_flux(q_m, u_m, 2)
    f_p, s_p = cell_flux(q_p, u_p, 2)
    high = face_flux(f, s, u, f_p, s_p, u_p)
    low = face_flux(f_m, s_m, u_m, f, s, u)
    width_p = wp_ref[...]
    for c in range(8):
        azimuthal = (high[c] - low[c]) / width_p
        out_ref[c, 0] = u[c] - dt * (radial[c] + polar[c] + azimuthal)


def mhd_call(dt, density, velocity, magnetic_vector, pressure, az_low, az_high,
             colat_low, colat_high, width_r, width_t, width_p, offset, count, previous=None):
    azim, colat, radial = density.shape
    scalar_block = (1, colat, radial)
    vector_block = (3, 1, colat, radial)

    def own(a):
        return a + offset

    def clamp_low(a):
        return jnp.maximum(a + offset - 1, 0)

    def clamp_high(a):
        return jnp.minimum(a + offset + 1, azim - 1)

    in_specs = [pl.BlockSpec(memory_space=pltpu.SMEM)]
    for pick in (own, clamp_low, clamp_high):
        in_specs += [
            pl.BlockSpec(scalar_block, lambda a, pick=pick: (pick(a), 0, 0)),
            pl.BlockSpec(vector_block, lambda a, pick=pick: (0, pick(a), 0, 0)),
            pl.BlockSpec(vector_block, lambda a, pick=pick: (0, pick(a), 0, 0)),
            pl.BlockSpec(scalar_block, lambda a, pick=pick: (pick(a), 0, 0)),
        ]
    in_specs += [
        pl.BlockSpec((8, 1, colat, radial), lambda a: (0, 0, 0, 0)),
        pl.BlockSpec((8, 1, colat, radial), lambda a: (0, 0, 0, 0)),
        pl.BlockSpec((8, 1, 1, radial), lambda a: (0, a + offset, 0, 0)),
        pl.BlockSpec((8, 1, 1, radial), lambda a: (0, a + offset, 0, 0)),
        pl.BlockSpec((1, radial), lambda a: (0, 0)),
        pl.BlockSpec((1, radial), lambda a: (0, 0)),
        pl.BlockSpec((colat, radial), lambda a: (0, 0)),
    ]
    fields = (density, velocity, magnetic_vector, pressure)
    args = [dt, *fields, *fields, *fields, az_low, az_high, colat_low, colat_high,
            width_r, width_t, width_p]
    aliases = {}
    if previous is not None:
        in_specs.append(pl.BlockSpec(memory_space=pl.ANY))
        aliases = {len(args): 0}
        args.append(previous)
    return pl.pallas_call(
        functools.partial(mhd_kernel, offset=offset, last_step=azim - 1),
        grid=(count,),
        in_specs=in_specs,
        out_specs=pl.BlockSpec((8, 1, colat, radial), lambda a: (0, a + offset, 0, 0)),
        out_shape=jax.ShapeDtypeStruct((8, azim, colat, radial), jnp.float32),
        input_output_aliases=aliases,
        compiler_params=pltpu.CompilerParams(dimension_semantics=("arbitrary",)),
    )(*args)


def mhd_halos(density, velocity, magnetic_vector, pressure, band_pos, band_count):
    fields = [density, velocity[0], velocity[1], velocity[2],
              magnetic_vector[0], magnetic_vector[1], magnetic_vector[2], pressure]
    azim, colat = density.shape[0], density.shape[1]
    az_first = jnp.stack([x[0:1] for x in fields])
    az_last = jnp.stack([x[azim - 1:azim] for x in fields])
    c_first = jnp.stack([x[:, 0:1] for x in fields])
    c_last = jnp.stack([x[:, colat - 1:colat] for x in fields])
    phi_size = lax.axis_size("phi")
    up = [(i, (i + 1) % phi_size) for i in range(phi_size)]
    down = [(j, i) for i, j in up]
    az_low = lax.ppermute(az_last, "phi", up)
    az_high = lax.ppermute(az_first, "phi", down)
    up = [(i, (i + 1) % band_count) for i in range(band_count)]
    down = [(j, i) for i, j in up]
    c_low = lax.ppermute(c_last, "band", up)
    c_high = lax.ppermute(c_first, "band", down)
    c_low = jnp.where(band_pos == 0, c_first, c_low)
    c_high = jnp.where(band_pos == band_count - 1, c_last, c_high)
    return az_low, az_high, c_low, c_high


def body(
    density,
    velocity,
    magnetic_vector,
    pressure,
    fluid_courant_number,
    cosmic_ray_density,
    diffusion_per_bin,
    super_step_scale,
):
    azim_dev = density.shape[0]
    colat_dev = density.shape[1]
    radial_cell_count = density.shape[2]
    band_count = lax.axis_size("band")
    phi_count = lax.axis_size("phi")
    colatitude_count = colat_dev * band_count
    azimuth_cell_count = azim_dev * phi_count
    bin_dev = cosmic_ray_density.shape[0]
    momentum_bin_count = bin_dev * band_count
    outer_shell_count = cosmic_ray_density.shape[3]
    band_pos = lax.axis_index("band")
    mesh_spacing = grid_steps(
        radial_cell_count, colatitude_count, azimuth_cell_count, momentum_bin_count
    )
    fluid_rate, cosmic_ray_rate = rate_limits(
        radial_cell_count,
        outer_shell_count,
        colatitude_count,
        azimuth_cell_count,
        momentum_bin_count,
    )
    radius_full = shell_radii(0, radial_cell_count, radial_cell_count)
    colatitude_local = colatitudes(band_pos * colat_dev, colat_dev, colatitude_count)
    dt = jnp.reshape(fluid_courant_number / fluid_rate, (1,)).astype(jnp.float32)
    mhd_args = (
        dt, density, velocity, magnetic_vector, pressure,
        *mhd_halos(density, velocity, magnetic_vector, pressure, band_pos, band_count),
        (radius_full * mesh_spacing[0])[None],
        (radius_full * mesh_spacing[1])[None],
        jnp.sin(colatitude_local)[:, None] * radius_full * mesh_spacing[2],
    )
    first_planes = azim_dev // 2
    fluid_state = mhd_call(*mhd_args, 0, first_planes)
    first_shell = radial_cell_count - outer_shell_count
    radius_sh = shell_radii(first_shell, outer_shell_count, radial_cell_count)
    colatitude_full = colatitudes(0, colatitude_count, colatitude_count)
    own_fields = jnp.concatenate(
        [velocity[:, :, :, first_shell:], magnetic_vector[:, :, :, first_shell:]], axis=0
    ).astype(jnp.bfloat16)
    wind_half = lax.all_gather(own_fields, "band", axis=0)
    wind_half = jnp.transpose(wind_half, (1, 2, 0, 3, 4)).reshape(
        own_fields.shape[0], azim_dev, colatitude_count, outer_shell_count
    )
    fluid_state, wind_half = lax.optimization_barrier((fluid_state, wind_half))
    wind_vel = wind_half[0:3].astype(jnp.float32)
    azim_pad = padded(wind_half[2], (("phi", 0),), 1).astype(jnp.float32)
    radial_pad = jnp.pad(wind_vel[0], ((0, 0), (0, 0), (1, 1)), mode="edge")
    polar_pad = jnp.pad(wind_vel[1], ((0, 0), (1, 1), (0, 0)), mode="edge")
    spread_half = divergence(
        radial_pad, polar_pad, azim_pad, radius_sh, colatitude_full, mesh_spacing
    ).astype(jnp.bfloat16)
    kappa_here = lax.dynamic_slice_in_dim(diffusion_per_bin, band_pos * bin_dev, bin_dev)
    sts_step = super_step_scale / cosmic_ray_rate
    coef_set = transport_coefficients(
        wind_half[0:3].astype(jnp.float32),
        wind_half[3:6].astype(jnp.float32),
        spread_half.astype(jnp.float32),
        radius_sh,
        colatitude_full,
        mesh_spacing,
    )

    coef_list, up_list, down_list, drift_up, drift_down = coef_set
    coefs = jnp.stack(
        list(coef_list) + list(up_list) + list(down_list)
        + [drift_up / mesh_spacing[3], drift_down / mesh_spacing[3]],
        axis=0,
    )
    scal1 = jnp.reshape(sts_step / 3.0, (1,)).astype(jnp.float32)
    scal2 = jnp.reshape(sts_step / 2.0, (1,)).astype(jnp.float32)
    flags = jnp.stack([band_pos == 0, band_pos == band_count - 1]).astype(jnp.int32)
    bins = cosmic_ray_density.shape[0]
    edges = (
        cosmic_ray_density[:, 0:1],
        cosmic_ray_density[:, azim_dev - 1:azim_dev],
        cosmic_ray_density[0:1],
        cosmic_ray_density[bins - 1:bins],
    )
    edges = [x.astype(jnp.bfloat16) for x in lax.optimization_barrier(edges)]
    az_low, az_high = exchange(edges[0], edges[1], "phi")
    bin_low, bin_high = exchange(edges[2], edges[3], "band")
    first_section, *edges = section_call(
        scal1, flags, kappa_here, cosmic_ray_density, az_low, az_high, bin_low, bin_high, coefs
    )
    steps = edges[0].shape[1]
    az_low, az_high = exchange(edges[0][:, 0:1], edges[1][:, steps - 1:steps], "phi")
    bin_low, bin_high = exchange(edges[2], edges[3], "band")
    fluid_state, first_section = lax.optimization_barrier((fluid_state, first_section))
    fluid_state = mhd_call(
        *mhd_args, first_planes, azim_dev - first_planes, previous=fluid_state
    )
    fluid_state, az_low, az_high, bin_low, bin_high = lax.optimization_barrier(
        (fluid_state, az_low, az_high, bin_low, bin_high)
    )
    cosmic_ray_next = section_call(
        scal2, flags, kappa_here, first_section, az_low, az_high, bin_low, bin_high, coefs,
        cosmic_ray_density,
    )
    return (fluid_state, cosmic_ray_next)


def solution(mesh):
    placed = (
        P("phi", "band", None),
        P(None, "phi", "band", None),
        P(None, "phi", "band", None),
        P("phi", "band", None),
        P(),
        P("band", "phi", None, None),
        P(),
        P(),
    )
    return jax.shard_map(
        body,
        mesh=mesh,
        in_specs=placed,
        out_specs=(P(None, "phi", "band", None), P("band", "phi", None, None)),
        check_vma=False,
    )
```

```python
import functools
import math

import jax
import jax.numpy as jnp
from jax import lax
from jax.experimental import pallas as pl
from jax.experimental.pallas import tpu as pltpu
from jax.sharding import PartitionSpec as P

ADIABATIC = 5.0 / 3.0
INNER_RADIUS = 0.1
R_RATIO = 30.0
COLAT_LOW = math.pi / 6.0
COLAT_SPAN = 2.0 * math.pi / 3.0
P_RATIO = 1000.0
K_RATIO = 0.1
B_FLOOR = 0.1
V_BOUND = 3.0
B_BOUND = 3.0
P_HIGH = 2.0
RHO_LOW = 0.5
KAPPA_HIGH = 0.5


def padded(value, sides, width):
    for axis, dim in sides:
        size, length = (lax.axis_size(axis), value.shape[dim])
        up = [(i, (i + 1) % size) for i in range(size)]
        down = [(j, i) for i, j in up]
        last = lax.slice_in_dim(value, length - width, length, axis=dim)
        leading = lax.slice_in_dim(value, 0, width, axis=dim)
        before = lax.ppermute(last, axis, up)
        after = lax.ppermute(leading, axis, down)
        value = jnp.concatenate([before, value, after], axis=dim)
    return value


def grid_steps(n_radial, n_colat, n_azim, n_bins):
    return (
        math.log(R_RATIO) / n_radial,
        COLAT_SPAN / n_colat,
        2.0 * math.pi / n_azim,
        math.log(P_RATIO) / n_bins,
    )


def rate_limits(n_radial, n_shells, n_colat, n_azim, n_bins):
    radial_spacing, colatitude_spacing, azimuth_spacing, step_m = grid_steps(
        n_radial, n_colat, n_azim, n_bins
    )
    sine_lower = math.sin(COLAT_LOW + 0.5 * colatitude_spacing)
    fluid_radius = INNER_RADIUS * math.exp(0.5 * radial_spacing)
    fastest_limit = V_BOUND + math.sqrt((ADIABATIC * P_HIGH + 3.0 * B_BOUND**2) / RHO_LOW)
    fluid_rate = fastest_limit * (
        1.0 / (fluid_radius * radial_spacing)
        + 1.0 / (fluid_radius * colatitude_spacing)
        + 1.0 / (fluid_radius * sine_lower * azimuth_spacing)
    )
    shell_low = INNER_RADIUS * math.exp(radial_spacing * (n_radial - n_shells + 0.5))
    inv_r = 1.0 / (shell_low * radial_spacing)
    inv_t = 1.0 / (shell_low * colatitude_spacing)
    inv_p = 1.0 / (shell_low * sine_lower * azimuth_spacing)
    cosmic_ray_rate = (
        2.0 * KAPPA_HIGH * (inv_r**2 + inv_t**2 + inv_p**2)
        + V_BOUND * (inv_r + inv_t + inv_p)
        + V_BOUND * (inv_r + inv_t + inv_p + 4.0 / shell_low) / (3.0 * step_m)
    )
    return (fluid_rate, cosmic_ray_rate)


def shell_radii(start_index, cell_count, n_radial):
    cell_index = jnp.arange(cell_count, dtype=jnp.float32) + (start_index + 0.5)
    return INNER_RADIUS * jnp.exp(math.log(R_RATIO) / n_radial * cell_index)


def colatitudes(start_index, cell_count, n_colat):
    cell_index = jnp.arange(cell_count, dtype=jnp.float32) + 0.5
    return COLAT_LOW + COLAT_SPAN * (cell_index + start_index) / n_colat


def edge_fix(values, along_axis, depth, band_pos, axis_count):
    extent = values.shape[along_axis]
    low_ghost = lax.slice_in_dim(values, 0, depth, axis=along_axis)
    high_ghost = lax.slice_in_dim(values, extent - depth, extent, axis=along_axis)
    first_own = lax.slice_in_dim(values, depth, depth + 1, axis=along_axis)
    last_own = lax.slice_in_dim(values, extent - depth - 1, extent - depth, axis=along_axis)
    low_rim = jnp.where(band_pos == 0, first_own, low_ghost)
    high_rim = jnp.where(band_pos == axis_count - 1, last_own, high_ghost)
    middle = lax.slice_in_dim(values, depth, extent - depth, axis=along_axis)
    return jnp.concatenate([low_rim, middle, high_rim], axis=along_axis)


def conserved(primitive):
    density = primitive[0]
    velocity = primitive[1:4]
    magnetic_vector = primitive[4:7]
    pressure = primitive[7]
    energy = (
        pressure / (ADIABATIC - 1.0)
        + 0.5 * density * jnp.sum(velocity * velocity, axis=0)
        + 0.5 * jnp.sum(magnetic_vector * magnetic_vector, axis=0)
    )
    return jnp.concatenate(
        [density[None], density[None] * velocity, magnetic_vector, energy[None]], axis=0
    )


def face_terms(primitive, cell_state, normal):
    density = primitive[0]
    velocity = primitive[1:4]
    magnetic_vector = primitive[4:7]
    pressure = primitive[7]
    v_normal = velocity[normal]
    b_normal = magnetic_vector[normal]
    magnetic = 0.5 * jnp.sum(magnetic_vector * magnetic_vector, axis=0)
    total_p = pressure + magnetic
    momentum = [density * velocity[k] * v_normal - magnetic_vector[k] * b_normal for k in range(3)]
    momentum[normal] = momentum[normal] + total_p
    induction = [v_normal * magnetic_vector[k] - b_normal * velocity[k] for k in range(3)]
    energy_flux = (cell_state[7] + total_p) * v_normal - b_normal * jnp.sum(
        velocity * magnetic_vector, axis=0
    )
    fluxes = jnp.stack([density * v_normal] + momentum + induction + [energy_flux], axis=0)
    speeds = jnp.abs(v_normal) + jnp.sqrt((ADIABATIC * pressure + 2.0 * magnetic) / density)
    return (fluxes, speeds)


def rusanov(primitive, cell_state, normal, along_axis, spacing):
    fluxes, speeds = face_terms(primitive, cell_state, normal)
    length = speeds.shape[along_axis]
    wave_speed = jnp.maximum(
        lax.slice_in_dim(speeds, 0, length - 1, axis=along_axis),
        lax.slice_in_dim(speeds, 1, length, axis=along_axis),
    )
    flux_low = lax.slice_in_dim(fluxes, 0, length - 1, axis=along_axis + 1)
    flux_high = lax.slice_in_dim(fluxes, 1, length, axis=along_axis + 1)
    state_low = lax.slice_in_dim(cell_state, 0, length - 1, axis=along_axis + 1)
    state_high = lax.slice_in_dim(cell_state, 1, length, axis=along_axis + 1)
    face_flux = 0.5 * (flux_low + flux_high) - 0.5 * wave_speed[None] * (state_high - state_low)
    upper = lax.slice_in_dim(face_flux, 1, length - 1, axis=along_axis + 1)
    lower = lax.slice_in_dim(face_flux, 0, length - 2, axis=along_axis + 1)
    return (upper - lower) / spacing


def fluid_update(padded_array, radius_values, colatitude_mesh, timestep_length, mesh_spacing):
    ghosted = jnp.pad(padded_array, ((0, 0), (0, 0), (0, 0), (1, 1)), mode="edge")
    cell_state = conserved(ghosted)
    width_r = radius_values * mesh_spacing[0]
    width_t = radius_values * mesh_spacing[1]
    width_p = jnp.sin(colatitude_mesh)[:, None] * radius_values * mesh_spacing[2]
    radial = rusanov(ghosted[:, 1:-1, 1:-1, :], cell_state[:, 1:-1, 1:-1, :], 0, 2, width_r)
    polar = rusanov(ghosted[:, 1:-1, :, 1:-1], cell_state[:, 1:-1, :, 1:-1], 1, 1, width_t)
    azimuthal = rusanov(ghosted[:, :, 1:-1, 1:-1], cell_state[:, :, 1:-1, 1:-1], 2, 0, width_p)
    return cell_state[:, 1:-1, 1:-1, 1:-1] - timestep_length * (radial + polar + azimuthal)


def divergence(radial_pad, polar_pad, azim_pad, radius_values, colatitude_mesh, mesh_spacing):
    sin_colat = jnp.sin(colatitude_mesh)[:, None]
    cotangent = (jnp.cos(colatitude_mesh) / jnp.sin(colatitude_mesh))[:, None]
    radial_mid = radial_pad[:, :, 1:-1]
    polar_mid = polar_pad[:, 1:-1, :]
    d_radial = (radial_pad[:, :, 2:] - radial_pad[:, :, :-2]) / (
        2.0 * radius_values * mesh_spacing[0]
    )
    d_polar = (polar_pad[:, 2:, :] - polar_pad[:, :-2, :]) / (2.0 * radius_values * mesh_spacing[1])
    d_azim = (azim_pad[2:] - azim_pad[:-2]) / (2.0 * radius_values * sin_colat * mesh_spacing[2])
    return (
        d_radial
        + 2.0 * radial_mid / radius_values
        + d_polar
        + cotangent * polar_mid / radius_values
        + d_azim
    )


def transport_coefficients(
    wind_vel, mag_wind, spread, radius_values, colatitude_mesh, mesh_spacing
):
    width_r = radius_values * mesh_spacing[0]
    width_t = radius_values * mesh_spacing[1]
    width_p = jnp.sin(colatitude_mesh)[:, None] * radius_values * mesh_spacing[2]
    widths = (width_r, width_t, width_p)
    mag_sq = jnp.sum(mag_wind * mag_wind, axis=0) + B_FLOOR
    b_share = K_RATIO + (1.0 - K_RATIO) * mag_wind * mag_wind / mag_sq
    coef_list = [b_share[k] / (widths[k] * widths[k]) for k in range(3)]
    up_list = [jnp.maximum(wind_vel[k], 0.0) / widths[k] for k in range(3)]
    down_list = [jnp.minimum(wind_vel[k], 0.0) / widths[k] for k in range(3)]
    drift_rate = spread / 3.0
    return (
        coef_list,
        up_list,
        down_list,
        jnp.maximum(drift_rate, 0.0),
        jnp.minimum(drift_rate, 0.0),
    )


def transport_rate(extended, coef_set, kappa_col, step_m):
    coef_list, up_list, down_list, drift_up, drift_down = coef_set
    center = extended[1:-1, 1:-1, 1:-1, 1:-1]
    low_cells = (
        extended[1:-1, 1:-1, 1:-1, :-2],
        extended[1:-1, 1:-1, :-2, 1:-1],
        extended[1:-1, :-2, 1:-1, 1:-1],
    )
    high_cells = (
        extended[1:-1, 1:-1, 1:-1, 2:],
        extended[1:-1, 1:-1, 2:, 1:-1],
        extended[1:-1, 2:, 1:-1, 1:-1],
    )
    curvature = coef_list[0] * (high_cells[0] - 2.0 * center + low_cells[0])
    curvature = curvature + coef_list[1] * (high_cells[1] - 2.0 * center + low_cells[1])
    curvature = curvature + coef_list[2] * (high_cells[2] - 2.0 * center + low_cells[2])
    diffusion = kappa_col[:, None, None, None] * curvature
    advection = up_list[0] * (center - low_cells[0]) + down_list[0] * (high_cells[0] - center)
    advection = (
        advection + up_list[1] * (center - low_cells[1]) + down_list[1] * (high_cells[1] - center)
    )
    advection = (
        advection + up_list[2] * (center - low_cells[2]) + down_list[2] * (high_cells[2] - center)
    )
    bin_low = extended[:-2, 1:-1, 1:-1, 1:-1]
    bin_high = extended[2:, 1:-1, 1:-1, 1:-1]
    momentum = (drift_up * (bin_high - center) + drift_down * (center - bin_low)) / step_m
    return diffusion - advection + momentum


ROWS = 16


def _vec(shape, scalar):
    return jnp.full(shape, scalar, jnp.int32)


def section_kernel(scal_ref, flag_ref, kappa_ref, g_ref, gp_ref, gn_ref, azlo_ref, azhi_ref,
                   binlo_ref, binhi_ref, coef_ref, drift_ref, *rest, second):
    if second:
        f0_ref, out_ref = rest
    else:
        out_ref, az_first_ref, az_last_ref, bin_first_ref, bin_last_ref = rest
    step = pl.program_id(0)
    last_step = pl.num_programs(0) - 1
    bins, planes, colat, shells = g_ref.shape
    shape = (ROWS, shells)
    row = lax.broadcasted_iota(jnp.int32, shape, 0)
    lane = lax.broadcasted_iota(jnp.int32, shape, 1)
    first_az = _vec(shape, step) == 0
    last_az = _vec(shape, step) == last_step
    band_first = _vec(shape, flag_ref[0]) == 1
    band_last = _vec(shape, flag_ref[1]) == 1
    scale = scal_ref[0]

    def chunk(k, i, r0, kap, edge):
        rows = slice(r0, r0 + ROWS)
        center = g_ref[k, i, rows, :]
        if r0 == 0:
            low_t = jnp.where(row == 0, center, pltpu.roll(center, 1, 0))
        else:
            low_t = g_ref[k, i, r0 - 1:r0 - 1 + ROWS, :]
        if r0 + ROWS == colat:
            high_t = jnp.where(row == ROWS - 1, center, pltpu.roll(center, ROWS - 1, 0))
        else:
            high_t = g_ref[k, i, r0 + 1:r0 + 1 + ROWS, :]
        low_r = jnp.where(lane == 0, center, pltpu.roll(center, 1, 1))
        high_r = jnp.where(lane == shells - 1, center, pltpu.roll(center, shells - 1, 1))
        if i == 0:
            low_p = jnp.where(first_az, azlo_ref[k, 0, rows, :].astype(jnp.float32), gp_ref[k, 0, rows, :])
        else:
            low_p = g_ref[k, i - 1, rows, :]
        if i == planes - 1:
            high_p = jnp.where(last_az, azhi_ref[k, 0, rows, :].astype(jnp.float32), gn_ref[k, 0, rows, :])
        else:
            high_p = g_ref[k, i + 1, rows, :]
        if edge == "low":
            low_b = jnp.where(band_first, center, binlo_ref[0, i, rows, :].astype(jnp.float32))
        else:
            low_b = g_ref[k - 1, i, rows, :]
        if edge == "high":
            high_b = jnp.where(band_last, center, binhi_ref[0, i, rows, :].astype(jnp.float32))
        else:
            high_b = g_ref[k + 1, i, rows, :]
        d_lo = (center - low_r, center - low_t, center - low_p)
        d_hi = (high_r - center, high_t - center, high_p - center)
        curvature = coef_ref[0, i, rows, :] * (d_hi[0] - d_lo[0])
        curvature = curvature + coef_ref[1, i, rows, :] * (d_hi[1] - d_lo[1])
        curvature = curvature + coef_ref[2, i, rows, :] * (d_hi[2] - d_lo[2])
        advection = coef_ref[3, i, rows, :] * d_lo[0] + coef_ref[6, i, rows, :] * d_hi[0]
        advection = advection + coef_ref[4, i, rows, :] * d_lo[1] + coef_ref[7, i, rows, :] * d_hi[1]
        advection = advection + coef_ref[5, i, rows, :] * d_lo[2] + coef_ref[8, i, rows, :] * d_hi[2]
        momentum = drift_ref[0, i, rows, :] * (high_b - center) + drift_ref[1, i, rows, :] * (center - low_b)
        rate = kap * curvature - advection + momentum
        if second:
            value = 1.5 * center - 0.5 * f0_ref[k, i, rows, :] + scale * rate
        else:
            value = center + scale * rate
        out_ref[k, i, rows, :] = value
        if not second:
            half = value.astype(jnp.bfloat16)
            if i == 0:
                az_first_ref[k, 0, rows, :] = half
            if i == planes - 1:
                az_last_ref[k, 0, rows, :] = half
            if edge == "low":
                bin_first_ref[0, i, rows, :] = half
            if edge == "high":
                bin_last_ref[0, i, rows, :] = half

    def all_rows(k, edge):
        kap = kappa_ref[k]
        for i in range(planes):
            for r0 in range(0, colat, ROWS):
                chunk(k, i, r0, kap, edge)

    all_rows(0, "low")

    def middle(k, carry):
        all_rows(k, None)
        return carry

    lax.fori_loop(1, bins - 1, middle, 0)
    all_rows(bins - 1, "high")


PLANES = 4


def section_call(scal, flags, kappa, g, az_low, az_high, bin_low, bin_high, coefs, drift, f0=None):
    bins, azim, colat, shells = g.shape
    block = (bins, PLANES, colat, shells)
    plane = (bins, 1, colat, shells)
    bin_block = (1, PLANES, colat, shells)
    smem = pl.BlockSpec(memory_space=pltpu.SMEM)
    in_specs = [
        smem,
        smem,
        smem,
        pl.BlockSpec(block, lambda a: (0, a, 0, 0)),
        pl.BlockSpec(plane, lambda a: (0, jnp.maximum(a * PLANES - 1, 0), 0, 0)),
        pl.BlockSpec(plane, lambda a: (0, jnp.minimum(a * PLANES + PLANES, azim - 1), 0, 0)),
        pl.BlockSpec(plane, lambda a: (0, 0, 0, 0)),
        pl.BlockSpec(plane, lambda a: (0, 0, 0, 0)),
        pl.BlockSpec(bin_block, lambda a: (0, a, 0, 0)),
        pl.BlockSpec(bin_block, lambda a: (0, a, 0, 0)),
        pl.BlockSpec((coefs.shape[0], PLANES, colat, shells), lambda a: (0, a, 0, 0)),
        pl.BlockSpec((drift.shape[0], PLANES, colat, shells), lambda a: (0, a, 0, 0)),
    ]
    args = [scal, flags, kappa, g, g, g, az_low, az_high, bin_low, bin_high, coefs, drift]
    out_specs = pl.BlockSpec(block, lambda a: (0, a, 0, 0))
    out_shape = jax.ShapeDtypeStruct(g.shape, jnp.float32)
    if f0 is not None:
        in_specs.append(pl.BlockSpec(block, lambda a: (0, a, 0, 0)))
        args.append(f0)
    else:
        out_specs = [
            out_specs,
            pl.BlockSpec(plane, lambda a: (0, a, 0, 0)),
            pl.BlockSpec(plane, lambda a: (0, a, 0, 0)),
            pl.BlockSpec(bin_block, lambda a: (0, a, 0, 0)),
            pl.BlockSpec(bin_block, lambda a: (0, a, 0, 0)),
        ]
        half_plane = jax.ShapeDtypeStruct((bins, azim // PLANES, colat, shells), jnp.bfloat16)
        half_bin = jax.ShapeDtypeStruct((1, azim, colat, shells), jnp.bfloat16)
        out_shape = [out_shape, half_plane, half_plane, half_bin, half_bin]
    return pl.pallas_call(
        functools.partial(section_kernel, second=f0 is not None),
        grid=(azim // PLANES,),
        in_specs=in_specs,
        out_specs=out_specs,
        out_shape=out_shape,
        compiler_params=pltpu.CompilerParams(dimension_semantics=("arbitrary",)),
    )(*args)


def exchange(first, last, axis):
    size = lax.axis_size(axis)
    up = [(i, (i + 1) % size) for i in range(size)]
    down = [(j, i) for i, j in up]
    return lax.ppermute(last, axis, up), lax.ppermute(first, axis, down)


def cell_state(q):
    rho, v, b, p = q[0], q[1:4], q[4:7], q[7]
    vv = v[0] * v[0] + v[1] * v[1] + v[2] * v[2]
    bb = b[0] * b[0] + b[1] * b[1] + b[2] * b[2]
    energy = p / (ADIABATIC - 1.0) + 0.5 * rho * vv + 0.5 * bb
    return [rho, rho * v[0], rho * v[1], rho * v[2], b[0], b[1], b[2], energy]


def cell_flux(q, u, normal):
    rho, v, b, p = q[0], q[1:4], q[4:7], q[7]
    vn, bn = v[normal], b[normal]
    magnetic = 0.5 * (b[0] * b[0] + b[1] * b[1] + b[2] * b[2])
    total_p = p + magnetic
    momentum = [rho * v[k] * vn - b[k] * bn for k in range(3)]
    momentum[normal] = momentum[normal] + total_p
    induction = [vn * b[k] - bn * v[k] for k in range(3)]
    energy = (u[7] + total_p) * vn - bn * (v[0] * b[0] + v[1] * b[1] + v[2] * b[2])
    speed = jnp.abs(vn) + jnp.sqrt((ADIABATIC * p + 2.0 * magnetic) / rho)
    return [rho * vn] + momentum + induction + [energy], speed


def face_flux(f_low, s_low, u_low, f_high, s_high, u_high):
    wave = jnp.maximum(s_low, s_high)
    return [0.5 * (f_low[c] + f_high[c]) - 0.5 * wave * (u_high[c] - u_low[c]) for c in range(8)]


def mhd_kernel(dt_ref, rho_c, v_c, b_c, p_c, rho_m, v_m, b_m, p_m, rho_p, v_p, b_p, p_p,
               azlo_ref, azhi_ref, clo_ref, chi_ref, wr_ref, wt_ref, wp_ref, *rest, offset, last_step):
    out_ref = rest[-1]
    step = pl.program_id(0) + offset

    def prim(rho_ref, v_ref, b_ref, p_ref):
        return [rho_ref[0], v_ref[0, 0], v_ref[1, 0], v_ref[2, 0],
                b_ref[0, 0], b_ref[1, 0], b_ref[2, 0], p_ref[0]]

    q = prim(rho_c, v_c, b_c, p_c)
    shape = q[0].shape
    nrow, nlane = shape
    row = lax.broadcasted_iota(jnp.int32, shape, 0)
    lane = lax.broadcasted_iota(jnp.int32, shape, 1)
    first_az = _vec(shape, step) == 0
    last_az = _vec(shape, step) == last_step
    q_m = prim(rho_m, v_m, b_m, p_m)
    q_p = prim(rho_p, v_p, b_p, p_p)
    q_m = [jnp.where(first_az, azlo_ref[c, 0], q_m[c]) for c in range(8)]
    q_p = [jnp.where(last_az, azhi_ref[c, 0], q_p[c]) for c in range(8)]
    u = cell_state(q)
    dt = dt_ref[0]

    def lane_next(x):
        return jnp.where(lane == nlane - 1, x, pltpu.roll(x, nlane - 1, 1))

    f, s = cell_flux(q, u, 0)
    high = face_flux(f, s, u, [lane_next(x) for x in f], lane_next(s), [lane_next(x) for x in u])
    low = [jnp.where(lane == 0, f[c], pltpu.roll(high[c], 1, 1)) for c in range(8)]
    width_r = wr_ref[...]
    radial = [(high[c] - low[c]) / width_r for c in range(8)]

    q_l = [clo_ref[c, 0] for c in range(8)]
    q_h = [chi_ref[c, 0] for c in range(8)]
    u_l = cell_state(q_l)
    u_h = cell_state(q_h)
    f, s = cell_flux(q, u, 1)
    f_l, s_l = cell_flux(q_l, u_l, 1)
    f_h, s_h = cell_flux(q_h, u_h, 1)

    def row_next(x, h):
        return jnp.where(row == nrow - 1, jnp.broadcast_to(h, shape), pltpu.roll(x, nrow - 1, 0))

    high = face_flux(f, s, u, [row_next(f[c], f_h[c]) for c in range(8)], row_next(s, s_h),
                     [row_next(u[c], u_h[c]) for c in range(8)])
    first = face_flux(f_l, s_l, u_l, f, s, u)
    low = [jnp.where(row == 0, first[c], pltpu.roll(high[c], 1, 0)) for c in range(8)]
    width_t = wt_ref[...]
    polar = [(high[c] - low[c]) / width_t for c in range(8)]

    u_m = cell_state(q_m)
    u_p = cell_state(q_p)
    f, s = cell_flux(q, u, 2)
    f_m, s_m = cell_flux(q_m, u_m, 2)
    f_p, s_p = cell_flux(q_p, u_p, 2)
    high = face_flux(f, s, u, f_p, s_p, u_p)
    low = face_flux(f_m, s_m, u_m, f, s, u)
    width_p = wp_ref[...]
    for c in range(8):
        azimuthal = (high[c] - low[c]) / width_p
        out_ref[c, 0] = u[c] - dt * (radial[c] + polar[c] + azimuthal)


def mhd_call(dt, density, velocity, magnetic_vector, pressure, az_low, az_high,
             colat_low, colat_high, width_r, width_t, width_p, offset, count, previous=None):
    azim, colat, radial = density.shape
    scalar_block = (1, colat, radial)
    vector_block = (3, 1, colat, radial)

    def own(a):
        return a + offset

    def clamp_low(a):
        return jnp.maximum(a + offset - 1, 0)

    def clamp_high(a):
        return jnp.minimum(a + offset + 1, azim - 1)

    in_specs = [pl.BlockSpec(memory_space=pltpu.SMEM)]
    for pick in (own, clamp_low, clamp_high):
        in_specs += [
            pl.BlockSpec(scalar_block, lambda a, pick=pick: (pick(a), 0, 0)),
            pl.BlockSpec(vector_block, lambda a, pick=pick: (0, pick(a), 0, 0)),
            pl.BlockSpec(vector_block, lambda a, pick=pick: (0, pick(a), 0, 0)),
            pl.BlockSpec(scalar_block, lambda a, pick=pick: (pick(a), 0, 0)),
        ]
    in_specs += [
        pl.BlockSpec((8, 1, colat, radial), lambda a: (0, 0, 0, 0)),
        pl.BlockSpec((8, 1, colat, radial), lambda a: (0, 0, 0, 0)),
        pl.BlockSpec((8, 1, 1, radial), lambda a: (0, a + offset, 0, 0)),
        pl.BlockSpec((8, 1, 1, radial), lambda a: (0, a + offset, 0, 0)),
        pl.BlockSpec((1, radial), lambda a: (0, 0)),
        pl.BlockSpec((1, radial), lambda a: (0, 0)),
        pl.BlockSpec((colat, radial), lambda a: (0, 0)),
    ]
    fields = (density, velocity, magnetic_vector, pressure)
    args = [dt, *fields, *fields, *fields, az_low, az_high, colat_low, colat_high,
            width_r, width_t, width_p]
    aliases = {}
    if previous is not None:
        in_specs.append(pl.BlockSpec(memory_space=pl.ANY))
        aliases = {len(args): 0}
        args.append(previous)
    return pl.pallas_call(
        functools.partial(mhd_kernel, offset=offset, last_step=azim - 1),
        grid=(count,),
        in_specs=in_specs,
        out_specs=pl.BlockSpec((8, 1, colat, radial), lambda a: (0, a + offset, 0, 0)),
        out_shape=jax.ShapeDtypeStruct((8, azim, colat, radial), jnp.float32),
        input_output_aliases=aliases,
        compiler_params=pltpu.CompilerParams(dimension_semantics=("arbitrary",)),
    )(*args)


def mhd_halos(density, velocity, magnetic_vector, pressure, band_pos, band_count):
    fields = [density, velocity[0], velocity[1], velocity[2],
              magnetic_vector[0], magnetic_vector[1], magnetic_vector[2], pressure]
    azim, colat = density.shape[0], density.shape[1]
    az_first = jnp.stack([x[0:1] for x in fields])
    az_last = jnp.stack([x[azim - 1:azim] for x in fields])
    c_first = jnp.stack([x[:, 0:1] for x in fields])
    c_last = jnp.stack([x[:, colat - 1:colat] for x in fields])
    phi_size = lax.axis_size("phi")
    up = [(i, (i + 1) % phi_size) for i in range(phi_size)]
    down = [(j, i) for i, j in up]
    az_low = lax.ppermute(az_last, "phi", up)
    az_high = lax.ppermute(az_first, "phi", down)
    up = [(i, (i + 1) % band_count) for i in range(band_count)]
    down = [(j, i) for i, j in up]
    c_low = lax.ppermute(c_last, "band", up)
    c_high = lax.ppermute(c_first, "band", down)
    c_low = jnp.where(band_pos == 0, c_first, c_low)
    c_high = jnp.where(band_pos == band_count - 1, c_last, c_high)
    return az_low, az_high, c_low, c_high


def body(
    density,
    velocity,
    magnetic_vector,
    pressure,
    fluid_courant_number,
    cosmic_ray_density,
    diffusion_per_bin,
    super_step_scale,
):
    azim_dev = density.shape[0]
    colat_dev = density.shape[1]
    radial_cell_count = density.shape[2]
    band_count = lax.axis_size("band")
    phi_count = lax.axis_size("phi")
    colatitude_count = colat_dev * band_count
    azimuth_cell_count = azim_dev * phi_count
    bin_dev = cosmic_ray_density.shape[0]
    momentum_bin_count = bin_dev * band_count
    outer_shell_count = cosmic_ray_density.shape[3]
    band_pos = lax.axis_index("band")
    mesh_spacing = grid_steps(
        radial_cell_count, colatitude_count, azimuth_cell_count, momentum_bin_count
    )
    fluid_rate, cosmic_ray_rate = rate_limits(
        radial_cell_count,
        outer_shell_count,
        colatitude_count,
        azimuth_cell_count,
        momentum_bin_count,
    )
    radius_full = shell_radii(0, radial_cell_count, radial_cell_count)
    colatitude_local = colatitudes(band_pos * colat_dev, colat_dev, colatitude_count)
    dt = jnp.reshape(fluid_courant_number / fluid_rate, (1,)).astype(jnp.float32)
    mhd_args = (
        dt, density, velocity, magnetic_vector, pressure,
        *mhd_halos(density, velocity, magnetic_vector, pressure, band_pos, band_count),
        (radius_full * mesh_spacing[0])[None],
        (radius_full * mesh_spacing[1])[None],
        jnp.sin(colatitude_local)[:, None] * radius_full * mesh_spacing[2],
    )
    first_planes = azim_dev // 2
    fluid_state = mhd_call(*mhd_args, 0, first_planes)
    first_shell = radial_cell_count - outer_shell_count
    radius_sh = shell_radii(first_shell, outer_shell_count, radial_cell_count)
    colatitude_full = colatitudes(0, colatitude_count, colatitude_count)
    own_fields = jnp.concatenate(
        [velocity[:, :, :, first_shell:], magnetic_vector[:, :, :, first_shell:]], axis=0
    ).astype(jnp.bfloat16)
    wind_half = lax.all_gather(own_fields, "band", axis=0)
    wind_half = jnp.transpose(wind_half, (1, 2, 0, 3, 4)).reshape(
        own_fields.shape[0], azim_dev, colatitude_count, outer_shell_count
    )
    fluid_state, wind_half = lax.optimization_barrier((fluid_state, wind_half))
    wind_vel = wind_half[0:3].astype(jnp.float32)
    azim_pad = padded(wind_half[2], (("phi", 0),), 1).astype(jnp.float32)
    radial_pad = jnp.pad(wind_vel[0], ((0, 0), (0, 0), (1, 1)), mode="edge")
    polar_pad = jnp.pad(wind_vel[1], ((0, 0), (1, 1), (0, 0)), mode="edge")
    spread_half = divergence(
        radial_pad, polar_pad, azim_pad, radius_sh, colatitude_full, mesh_spacing
    ).astype(jnp.bfloat16)
    kappa_here = lax.dynamic_slice_in_dim(diffusion_per_bin, band_pos * bin_dev, bin_dev)
    sts_step = super_step_scale / cosmic_ray_rate
    coef_set = transport_coefficients(
        wind_half[0:3].astype(jnp.float32),
        wind_half[3:6].astype(jnp.float32),
        spread_half.astype(jnp.float32),
        radius_sh,
        colatitude_full,
        mesh_spacing,
    )

    coef_list, up_list, down_list, drift_up, drift_down = coef_set
    coefs = jnp.stack(list(coef_list) + list(up_list) + list(down_list), axis=0)
    drift = jnp.stack([drift_up / mesh_spacing[3], drift_down / mesh_spacing[3]], axis=0)
    scal1 = jnp.reshape(sts_step / 3.0, (1,)).astype(jnp.float32)
    scal2 = jnp.reshape(sts_step / 2.0, (1,)).astype(jnp.float32)
    flags = jnp.stack([band_pos == 0, band_pos == band_count - 1]).astype(jnp.int32)
    bins = cosmic_ray_density.shape[0]
    edges = (
        cosmic_ray_density[:, 0:1],
        cosmic_ray_density[:, azim_dev - 1:azim_dev],
        cosmic_ray_density[0:1],
        cosmic_ray_density[bins - 1:bins],
    )
    edges = [x.astype(jnp.bfloat16) for x in lax.optimization_barrier(edges)]
    az_low, az_high = exchange(edges[0], edges[1], "phi")
    bin_low, bin_high = exchange(edges[2], edges[3], "band")
    first_section, *edges = section_call(
        scal1, flags, kappa_here, cosmic_ray_density, az_low, az_high, bin_low, bin_high, coefs,
        drift,
    )
    steps = edges[0].shape[1]
    az_low, az_high = exchange(edges[0][:, 0:1], edges[1][:, steps - 1:steps], "phi")
    bin_low, bin_high = exchange(edges[2], edges[3], "band")
    fluid_state, first_section = lax.optimization_barrier((fluid_state, first_section))
    fluid_state = mhd_call(
        *mhd_args, first_planes, azim_dev - first_planes, previous=fluid_state
    )
    fluid_state, az_low, az_high, bin_low, bin_high = lax.optimization_barrier(
        (fluid_state, az_low, az_high, bin_low, bin_high)
    )
    cosmic_ray_next = section_call(
        scal2, flags, kappa_here, first_section, az_low, az_high, bin_low, bin_high, coefs,
        drift, cosmic_ray_density,
    )
    return (fluid_state, cosmic_ray_next)


def solution(mesh):
    placed = (
        P("phi", "band", None),
        P(None, "phi", "band", None),
        P(None, "phi", "band", None),
        P("phi", "band", None),
        P(),
        P("band", "phi", None, None),
        P(),
        P(),
    )
    return jax.shard_map(
        body,
        mesh=mesh,
        in_specs=placed,
        out_specs=(P(None, "phi", "band", None), P("band", "phi", None, None)),
        check_vma=False,
    )
```

```python
import functools
import math

import jax
import jax.numpy as jnp
from jax import lax
from jax.experimental import pallas as pl
from jax.experimental.pallas import tpu as pltpu
from jax.sharding import PartitionSpec as P

ADIABATIC = 5.0 / 3.0
INNER_RADIUS = 0.1
R_RATIO = 30.0
COLAT_LOW = math.pi / 6.0
COLAT_SPAN = 2.0 * math.pi / 3.0
P_RATIO = 1000.0
K_RATIO = 0.1
B_FLOOR = 0.1
V_BOUND = 3.0
B_BOUND = 3.0
P_HIGH = 2.0
RHO_LOW = 0.5
KAPPA_HIGH = 0.5


def padded(value, sides, width):
    for axis, dim in sides:
        size, length = (lax.axis_size(axis), value.shape[dim])
        up = [(i, (i + 1) % size) for i in range(size)]
        down = [(j, i) for i, j in up]
        last = lax.slice_in_dim(value, length - width, length, axis=dim)
        leading = lax.slice_in_dim(value, 0, width, axis=dim)
        before = lax.ppermute(last, axis, up)
        after = lax.ppermute(leading, axis, down)
        value = jnp.concatenate([before, value, after], axis=dim)
    return value


def grid_steps(n_radial, n_colat, n_azim, n_bins):
    return (
        math.log(R_RATIO) / n_radial,
        COLAT_SPAN / n_colat,
        2.0 * math.pi / n_azim,
        math.log(P_RATIO) / n_bins,
    )


def rate_limits(n_radial, n_shells, n_colat, n_azim, n_bins):
    radial_spacing, colatitude_spacing, azimuth_spacing, step_m = grid_steps(
        n_radial, n_colat, n_azim, n_bins
    )
    sine_lower = math.sin(COLAT_LOW + 0.5 * colatitude_spacing)
    fluid_radius = INNER_RADIUS * math.exp(0.5 * radial_spacing)
    fastest_limit = V_BOUND + math.sqrt((ADIABATIC * P_HIGH + 3.0 * B_BOUND**2) / RHO_LOW)
    fluid_rate = fastest_limit * (
        1.0 / (fluid_radius * radial_spacing)
        + 1.0 / (fluid_radius * colatitude_spacing)
        + 1.0 / (fluid_radius * sine_lower * azimuth_spacing)
    )
    shell_low = INNER_RADIUS * math.exp(radial_spacing * (n_radial - n_shells + 0.5))
    inv_r = 1.0 / (shell_low * radial_spacing)
    inv_t = 1.0 / (shell_low * colatitude_spacing)
    inv_p = 1.0 / (shell_low * sine_lower * azimuth_spacing)
    cosmic_ray_rate = (
        2.0 * KAPPA_HIGH * (inv_r**2 + inv_t**2 + inv_p**2)
        + V_BOUND * (inv_r + inv_t + inv_p)
        + V_BOUND * (inv_r + inv_t + inv_p + 4.0 / shell_low) / (3.0 * step_m)
    )
    return (fluid_rate, cosmic_ray_rate)


def shell_radii(start_index, cell_count, n_radial):
    cell_index = jnp.arange(cell_count, dtype=jnp.float32) + (start_index + 0.5)
    return INNER_RADIUS * jnp.exp(math.log(R_RATIO) / n_radial * cell_index)


def colatitudes(start_index, cell_count, n_colat):
    cell_index = jnp.arange(cell_count, dtype=jnp.float32) + 0.5
    return COLAT_LOW + COLAT_SPAN * (cell_index + start_index) / n_colat


def edge_fix(values, along_axis, depth, band_pos, axis_count):
    extent = values.shape[along_axis]
    low_ghost = lax.slice_in_dim(values, 0, depth, axis=along_axis)
    high_ghost = lax.slice_in_dim(values, extent - depth, extent, axis=along_axis)
    first_own = lax.slice_in_dim(values, depth, depth + 1, axis=along_axis)
    last_own = lax.slice_in_dim(values, extent - depth - 1, extent - depth, axis=along_axis)
    low_rim = jnp.where(band_pos == 0, first_own, low_ghost)
    high_rim = jnp.where(band_pos == axis_count - 1, last_own, high_ghost)
    middle = lax.slice_in_dim(values, depth, extent - depth, axis=along_axis)
    return jnp.concatenate([low_rim, middle, high_rim], axis=along_axis)


def conserved(primitive):
    density = primitive[0]
    velocity = primitive[1:4]
    magnetic_vector = primitive[4:7]
    pressure = primitive[7]
    energy = (
        pressure / (ADIABATIC - 1.0)
        + 0.5 * density * jnp.sum(velocity * velocity, axis=0)
        + 0.5 * jnp.sum(magnetic_vector * magnetic_vector, axis=0)
    )
    return jnp.concatenate(
        [density[None], density[None] * velocity, magnetic_vector, energy[None]], axis=0
    )


def face_terms(primitive, cell_state, normal):
    density = primitive[0]
    velocity = primitive[1:4]
    magnetic_vector = primitive[4:7]
    pressure = primitive[7]
    v_normal = velocity[normal]
    b_normal = magnetic_vector[normal]
    magnetic = 0.5 * jnp.sum(magnetic_vector * magnetic_vector, axis=0)
    total_p = pressure + magnetic
    momentum = [density * velocity[k] * v_normal - magnetic_vector[k] * b_normal for k in range(3)]
    momentum[normal] = momentum[normal] + total_p
    induction = [v_normal * magnetic_vector[k] - b_normal * velocity[k] for k in range(3)]
    energy_flux = (cell_state[7] + total_p) * v_normal - b_normal * jnp.sum(
        velocity * magnetic_vector, axis=0
    )
    fluxes = jnp.stack([density * v_normal] + momentum + induction + [energy_flux], axis=0)
    speeds = jnp.abs(v_normal) + jnp.sqrt((ADIABATIC * pressure + 2.0 * magnetic) / density)
    return (fluxes, speeds)


def rusanov(primitive, cell_state, normal, along_axis, spacing):
    fluxes, speeds = face_terms(primitive, cell_state, normal)
    length = speeds.shape[along_axis]
    wave_speed = jnp.maximum(
        lax.slice_in_dim(speeds, 0, length - 1, axis=along_axis),
        lax.slice_in_dim(speeds, 1, length, axis=along_axis),
    )
    flux_low = lax.slice_in_dim(fluxes, 0, length - 1, axis=along_axis + 1)
    flux_high = lax.slice_in_dim(fluxes, 1, length, axis=along_axis + 1)
    state_low = lax.slice_in_dim(cell_state, 0, length - 1, axis=along_axis + 1)
    state_high = lax.slice_in_dim(cell_state, 1, length, axis=along_axis + 1)
    face_flux = 0.5 * (flux_low + flux_high) - 0.5 * wave_speed[None] * (state_high - state_low)
    upper = lax.slice_in_dim(face_flux, 1, length - 1, axis=along_axis + 1)
    lower = lax.slice_in_dim(face_flux, 0, length - 2, axis=along_axis + 1)
    return (upper - lower) / spacing


def fluid_update(padded_array, radius_values, colatitude_mesh, timestep_length, mesh_spacing):
    ghosted = jnp.pad(padded_array, ((0, 0), (0, 0), (0, 0), (1, 1)), mode="edge")
    cell_state = conserved(ghosted)
    width_r = radius_values * mesh_spacing[0]
    width_t = radius_values * mesh_spacing[1]
    width_p = jnp.sin(colatitude_mesh)[:, None] * radius_values * mesh_spacing[2]
    radial = rusanov(ghosted[:, 1:-1, 1:-1, :], cell_state[:, 1:-1, 1:-1, :], 0, 2, width_r)
    polar = rusanov(ghosted[:, 1:-1, :, 1:-1], cell_state[:, 1:-1, :, 1:-1], 1, 1, width_t)
    azimuthal = rusanov(ghosted[:, :, 1:-1, 1:-1], cell_state[:, :, 1:-1, 1:-1], 2, 0, width_p)
    return cell_state[:, 1:-1, 1:-1, 1:-1] - timestep_length * (radial + polar + azimuthal)


def divergence(radial_pad, polar_pad, azim_pad, radius_values, colatitude_mesh, mesh_spacing):
    sin_colat = jnp.sin(colatitude_mesh)[:, None]
    cotangent = (jnp.cos(colatitude_mesh) / jnp.sin(colatitude_mesh))[:, None]
    radial_mid = radial_pad[:, :, 1:-1]
    polar_mid = polar_pad[:, 1:-1, :]
    d_radial = (radial_pad[:, :, 2:] - radial_pad[:, :, :-2]) / (
        2.0 * radius_values * mesh_spacing[0]
    )
    d_polar = (polar_pad[:, 2:, :] - polar_pad[:, :-2, :]) / (2.0 * radius_values * mesh_spacing[1])
    d_azim = (azim_pad[2:] - azim_pad[:-2]) / (2.0 * radius_values * sin_colat * mesh_spacing[2])
    return (
        d_radial
        + 2.0 * radial_mid / radius_values
        + d_polar
        + cotangent * polar_mid / radius_values
        + d_azim
    )


def transport_coefficients(
    wind_vel, mag_wind, spread, radius_values, colatitude_mesh, mesh_spacing
):
    width_r = radius_values * mesh_spacing[0]
    width_t = radius_values * mesh_spacing[1]
    width_p = jnp.sin(colatitude_mesh)[:, None] * radius_values * mesh_spacing[2]
    widths = (width_r, width_t, width_p)
    mag_sq = jnp.sum(mag_wind * mag_wind, axis=0) + B_FLOOR
    b_share = K_RATIO + (1.0 - K_RATIO) * mag_wind * mag_wind / mag_sq
    coef_list = [b_share[k] / (widths[k] * widths[k]) for k in range(3)]
    up_list = [jnp.maximum(wind_vel[k], 0.0) / widths[k] for k in range(3)]
    down_list = [jnp.minimum(wind_vel[k], 0.0) / widths[k] for k in range(3)]
    drift_rate = spread / 3.0
    return (
        coef_list,
        up_list,
        down_list,
        jnp.maximum(drift_rate, 0.0),
        jnp.minimum(drift_rate, 0.0),
    )


def transport_rate(extended, coef_set, kappa_col, step_m):
    coef_list, up_list, down_list, drift_up, drift_down = coef_set
    center = extended[1:-1, 1:-1, 1:-1, 1:-1]
    low_cells = (
        extended[1:-1, 1:-1, 1:-1, :-2],
        extended[1:-1, 1:-1, :-2, 1:-1],
        extended[1:-1, :-2, 1:-1, 1:-1],
    )
    high_cells = (
        extended[1:-1, 1:-1, 1:-1, 2:],
        extended[1:-1, 1:-1, 2:, 1:-1],
        extended[1:-1, 2:, 1:-1, 1:-1],
    )
    curvature = coef_list[0] * (high_cells[0] - 2.0 * center + low_cells[0])
    curvature = curvature + coef_list[1] * (high_cells[1] - 2.0 * center + low_cells[1])
    curvature = curvature + coef_list[2] * (high_cells[2] - 2.0 * center + low_cells[2])
    diffusion = kappa_col[:, None, None, None] * curvature
    advection = up_list[0] * (center - low_cells[0]) + down_list[0] * (high_cells[0] - center)
    advection = (
        advection + up_list[1] * (center - low_cells[1]) + down_list[1] * (high_cells[1] - center)
    )
    advection = (
        advection + up_list[2] * (center - low_cells[2]) + down_list[2] * (high_cells[2] - center)
    )
    bin_low = extended[:-2, 1:-1, 1:-1, 1:-1]
    bin_high = extended[2:, 1:-1, 1:-1, 1:-1]
    momentum = (drift_up * (bin_high - center) + drift_down * (center - bin_low)) / step_m
    return diffusion - advection + momentum


ROWS = 16


def _vec(shape, scalar):
    return jnp.full(shape, scalar, jnp.int32)


def section_kernel(scal_ref, flag_ref, kappa_ref, g_ref, gp_ref, gn_ref, azlo_ref, azhi_ref,
                   binlo_ref, binhi_ref, coef_ref, *rest, second):
    if second:
        f0_ref, out_ref = rest
    else:
        out_ref, az_first_ref, az_last_ref, bin_first_ref, bin_last_ref = rest
    step = pl.program_id(0)
    last_step = pl.num_programs(0) - 1
    bins, planes, colat, shells = g_ref.shape
    shape = (ROWS, shells)
    row = lax.broadcasted_iota(jnp.int32, shape, 0)
    lane = lax.broadcasted_iota(jnp.int32, shape, 1)
    first_az = _vec(shape, step) == 0
    last_az = _vec(shape, step) == last_step
    band_first = _vec(shape, flag_ref[0]) == 1
    band_last = _vec(shape, flag_ref[1]) == 1
    scale = scal_ref[0]

    def chunk(k, i, r0, kap, edge):
        rows = slice(r0, r0 + ROWS)
        center = g_ref[k, i, rows, :]
        if r0 == 0:
            low_t = jnp.where(row == 0, center, pltpu.roll(center, 1, 0))
        else:
            low_t = g_ref[k, i, r0 - 1:r0 - 1 + ROWS, :]
        if r0 + ROWS == colat:
            high_t = jnp.where(row == ROWS - 1, center, pltpu.roll(center, ROWS - 1, 0))
        else:
            high_t = g_ref[k, i, r0 + 1:r0 + 1 + ROWS, :]
        low_r = jnp.where(lane == 0, center, pltpu.roll(center, 1, 1))
        high_r = jnp.where(lane == shells - 1, center, pltpu.roll(center, shells - 1, 1))
        if i == 0:
            low_p = jnp.where(first_az, azlo_ref[k, 0, rows, :].astype(jnp.float32), gp_ref[k, 0, rows, :])
        else:
            low_p = g_ref[k, i - 1, rows, :]
        if i == planes - 1:
            high_p = jnp.where(last_az, azhi_ref[k, 0, rows, :].astype(jnp.float32), gn_ref[k, 0, rows, :])
        else:
            high_p = g_ref[k, i + 1, rows, :]
        if edge == "low":
            low_b = jnp.where(band_first, center, binlo_ref[0, i, rows, :].astype(jnp.float32))
        else:
            low_b = g_ref[k - 1, i, rows, :]
        if edge == "high":
            high_b = jnp.where(band_last, center, binhi_ref[0, i, rows, :].astype(jnp.float32))
        else:
            high_b = g_ref[k + 1, i, rows, :]
        d_lo = (center - low_r, center - low_t, center - low_p)
        d_hi = (high_r - center, high_t - center, high_p - center)
        curvature = coef_ref[0, i, rows, :] * (d_hi[0] - d_lo[0])
        curvature = curvature + coef_ref[1, i, rows, :] * (d_hi[1] - d_lo[1])
        curvature = curvature + coef_ref[2, i, rows, :] * (d_hi[2] - d_lo[2])
        advection = coef_ref[3, i, rows, :] * d_lo[0] + coef_ref[6, i, rows, :] * d_hi[0]
        advection = advection + coef_ref[4, i, rows, :] * d_lo[1] + coef_ref[7, i, rows, :] * d_hi[1]
        advection = advection + coef_ref[5, i, rows, :] * d_lo[2] + coef_ref[8, i, rows, :] * d_hi[2]
        momentum = coef_ref[9, i, rows, :] * (high_b - center) + coef_ref[10, i, rows, :] * (center - low_b)
        rate = kap * curvature - advection + momentum
        if second:
            value = 1.5 * center - 0.5 * f0_ref[k, i, rows, :] + scale * rate
        else:
            value = center + scale * rate
        out_ref[k, i, rows, :] = value
        if not second:
            half = value.astype(jnp.bfloat16)
            if i == 0:
                az_first_ref[k, 0, rows, :] = half
            if i == planes - 1:
                az_last_ref[k, 0, rows, :] = half
            if edge == "low":
                bin_first_ref[0, i, rows, :] = half
            if edge == "high":
                bin_last_ref[0, i, rows, :] = half

    def all_rows(k, edge):
        kap = kappa_ref[k]
        for i in range(planes):
            for r0 in range(0, colat, ROWS):
                chunk(k, i, r0, kap, edge)

    all_rows(0, "low")

    def middle(k, carry):
        all_rows(k, None)
        return carry

    lax.fori_loop(1, bins - 1, middle, 0)
    all_rows(bins - 1, "high")


PLANES = 4


def section_call(scal, flags, kappa, g, az_low, az_high, bin_low, bin_high, coefs, f0=None):
    bins, azim, colat, shells = g.shape
    block = (bins, PLANES, colat, shells)
    plane = (bins, 1, colat, shells)
    bin_block = (1, PLANES, colat, shells)
    smem = pl.BlockSpec(memory_space=pltpu.SMEM)
    in_specs = [
        smem,
        smem,
        smem,
        pl.BlockSpec(block, lambda a: (0, a, 0, 0)),
        pl.BlockSpec(plane, lambda a: (0, jnp.maximum(a * PLANES - 1, 0), 0, 0)),
        pl.BlockSpec(plane, lambda a: (0, jnp.minimum(a * PLANES + PLANES, azim - 1), 0, 0)),
        pl.BlockSpec(plane, lambda a: (0, 0, 0, 0)),
        pl.BlockSpec(plane, lambda a: (0, 0, 0, 0)),
        pl.BlockSpec(bin_block, lambda a: (0, a, 0, 0)),
        pl.BlockSpec(bin_block, lambda a: (0, a, 0, 0)),
        pl.BlockSpec((coefs.shape[0], PLANES, colat, shells), lambda a: (0, a, 0, 0)),
    ]
    args = [scal, flags, kappa, g, g, g, az_low, az_high, bin_low, bin_high, coefs]
    out_specs = pl.BlockSpec(block, lambda a: (0, a, 0, 0))
    out_shape = jax.ShapeDtypeStruct(g.shape, jnp.float32)
    if f0 is not None:
        in_specs.append(pl.BlockSpec(block, lambda a: (0, a, 0, 0)))
        args.append(f0)
    else:
        out_specs = [
            out_specs,
            pl.BlockSpec(plane, lambda a: (0, a, 0, 0)),
            pl.BlockSpec(plane, lambda a: (0, a, 0, 0)),
            pl.BlockSpec(bin_block, lambda a: (0, a, 0, 0)),
            pl.BlockSpec(bin_block, lambda a: (0, a, 0, 0)),
        ]
        half_plane = jax.ShapeDtypeStruct((bins, azim // PLANES, colat, shells), jnp.bfloat16)
        half_bin = jax.ShapeDtypeStruct((1, azim, colat, shells), jnp.bfloat16)
        out_shape = [out_shape, half_plane, half_plane, half_bin, half_bin]
    return pl.pallas_call(
        functools.partial(section_kernel, second=f0 is not None),
        grid=(azim // PLANES,),
        in_specs=in_specs,
        out_specs=out_specs,
        out_shape=out_shape,
        compiler_params=pltpu.CompilerParams(dimension_semantics=("arbitrary",)),
    )(*args)


def exchange(first, last, axis):
    size = lax.axis_size(axis)
    up = [(i, (i + 1) % size) for i in range(size)]
    down = [(j, i) for i, j in up]
    return lax.ppermute(last, axis, up), lax.ppermute(first, axis, down)


def cell_state(q):
    rho, v, b, p = q[0], q[1:4], q[4:7], q[7]
    vv = v[0] * v[0] + v[1] * v[1] + v[2] * v[2]
    bb = b[0] * b[0] + b[1] * b[1] + b[2] * b[2]
    energy = p / (ADIABATIC - 1.0) + 0.5 * rho * vv + 0.5 * bb
    return [rho, rho * v[0], rho * v[1], rho * v[2], b[0], b[1], b[2], energy]


def cell_flux(q, u, normal):
    rho, v, b, p = q[0], q[1:4], q[4:7], q[7]
    vn, bn = v[normal], b[normal]
    magnetic = 0.5 * (b[0] * b[0] + b[1] * b[1] + b[2] * b[2])
    total_p = p + magnetic
    momentum = [rho * v[k] * vn - b[k] * bn for k in range(3)]
    momentum[normal] = momentum[normal] + total_p
    induction = [vn * b[k] - bn * v[k] for k in range(3)]
    energy = (u[7] + total_p) * vn - bn * (v[0] * b[0] + v[1] * b[1] + v[2] * b[2])
    speed = jnp.abs(vn) + jnp.sqrt((ADIABATIC * p + 2.0 * magnetic) / rho)
    return [rho * vn] + momentum + induction + [energy], speed


def face_flux(f_low, s_low, u_low, f_high, s_high, u_high):
    wave = jnp.maximum(s_low, s_high)
    return [0.5 * (f_low[c] + f_high[c]) - 0.5 * wave * (u_high[c] - u_low[c]) for c in range(8)]


def mhd_kernel(dt_ref, rho_c, v_c, b_c, p_c, rho_m, v_m, b_m, p_m, rho_p, v_p, b_p, p_p,
               azlo_ref, azhi_ref, clo_ref, chi_ref, wr_ref, wt_ref, wp_ref, *rest, offset, last_step):
    out_ref = rest[-1]
    step = pl.program_id(0) + offset

    def prim(rho_ref, v_ref, b_ref, p_ref):
        return [rho_ref[0], v_ref[0, 0], v_ref[1, 0], v_ref[2, 0],
                b_ref[0, 0], b_ref[1, 0], b_ref[2, 0], p_ref[0]]

    q = prim(rho_c, v_c, b_c, p_c)
    shape = q[0].shape
    nrow, nlane = shape
    row = lax.broadcasted_iota(jnp.int32, shape, 0)
    lane = lax.broadcasted_iota(jnp.int32, shape, 1)
    first_az = _vec(shape, step) == 0
    last_az = _vec(shape, step) == last_step
    q_m = prim(rho_m, v_m, b_m, p_m)
    q_p = prim(rho_p, v_p, b_p, p_p)
    q_m = [jnp.where(first_az, azlo_ref[c, 0], q_m[c]) for c in range(8)]
    q_p = [jnp.where(last_az, azhi_ref[c, 0], q_p[c]) for c in range(8)]
    u = cell_state(q)
    dt = dt_ref[0]

    def lane_next(x):
        return jnp.where(lane == nlane - 1, x, pltpu.roll(x, nlane - 1, 1))

    f, s = cell_flux(q, u, 0)
    high = face_flux(f, s, u, [lane_next(x) for x in f], lane_next(s), [lane_next(x) for x in u])
    low = [jnp.where(lane == 0, f[c], pltpu.roll(high[c], 1, 1)) for c in range(8)]
    width_r = wr_ref[...]
    radial = [(high[c] - low[c]) / width_r for c in range(8)]

    q_l = [clo_ref[c, 0] for c in range(8)]
    q_h = [chi_ref[c, 0] for c in range(8)]
    u_l = cell_state(q_l)
    u_h = cell_state(q_h)
    f, s = cell_flux(q, u, 1)
    f_l, s_l = cell_flux(q_l, u_l, 1)
    f_h, s_h = cell_flux(q_h, u_h, 1)

    def row_next(x, h):
        return jnp.where(row == nrow - 1, jnp.broadcast_to(h, shape), pltpu.roll(x, nrow - 1, 0))

    high = face_flux(f, s, u, [row_next(f[c], f_h[c]) for c in range(8)], row_next(s, s_h),
                     [row_next(u[c], u_h[c]) for c in range(8)])
    first = face_flux(f_l, s_l, u_l, f, s, u)
    low = [jnp.where(row == 0, first[c], pltpu.roll(high[c], 1, 0)) for c in range(8)]
    width_t = wt_ref[...]
    polar = [(high[c] - low[c]) / width_t for c in range(8)]

    u_m = cell_state(q_m)
    u_p = cell_state(q_p)
    f, s = cell_flux(q, u, 2)
    f_m, s_m = cell_flux(q_m, u_m, 2)
    f_p, s_p = cell_flux(q_p, u_p, 2)
    high = face_flux(f, s, u, f_p, s_p, u_p)
    low = face_flux(f_m, s_m, u_m, f, s, u)
    width_p = wp_ref[...]
    for c in range(8):
        azimuthal = (high[c] - low[c]) / width_p
        out_ref[c, 0] = u[c] - dt * (radial[c] + polar[c] + azimuthal)


def mhd_call(dt, density, velocity, magnetic_vector, pressure, az_low, az_high,
             colat_low, colat_high, width_r, width_t, width_p, offset, count, previous=None):
    azim, colat, radial = density.shape
    scalar_block = (1, colat, radial)
    vector_block = (3, 1, colat, radial)

    def own(a):
        return a + offset

    def clamp_low(a):
        return jnp.maximum(a + offset - 1, 0)

    def clamp_high(a):
        return jnp.minimum(a + offset + 1, azim - 1)

    in_specs = [pl.BlockSpec(memory_space=pltpu.SMEM)]
    for pick in (own, clamp_low, clamp_high):
        in_specs += [
            pl.BlockSpec(scalar_block, lambda a, pick=pick: (pick(a), 0, 0)),
            pl.BlockSpec(vector_block, lambda a, pick=pick: (0, pick(a), 0, 0)),
            pl.BlockSpec(vector_block, lambda a, pick=pick: (0, pick(a), 0, 0)),
            pl.BlockSpec(scalar_block, lambda a, pick=pick: (pick(a), 0, 0)),
        ]
    in_specs += [
        pl.BlockSpec((8, 1, colat, radial), lambda a: (0, 0, 0, 0)),
        pl.BlockSpec((8, 1, colat, radial), lambda a: (0, 0, 0, 0)),
        pl.BlockSpec((8, 1, 1, radial), lambda a: (0, a + offset, 0, 0)),
        pl.BlockSpec((8, 1, 1, radial), lambda a: (0, a + offset, 0, 0)),
        pl.BlockSpec((1, radial), lambda a: (0, 0)),
        pl.BlockSpec((1, radial), lambda a: (0, 0)),
        pl.BlockSpec((colat, radial), lambda a: (0, 0)),
    ]
    fields = (density, velocity, magnetic_vector, pressure)
    args = [dt, *fields, *fields, *fields, az_low, az_high, colat_low, colat_high,
            width_r, width_t, width_p]
    aliases = {}
    if previous is not None:
        in_specs.append(pl.BlockSpec(memory_space=pl.ANY))
        aliases = {len(args): 0}
        args.append(previous)
    return pl.pallas_call(
        functools.partial(mhd_kernel, offset=offset, last_step=azim - 1),
        grid=(count,),
        in_specs=in_specs,
        out_specs=pl.BlockSpec((8, 1, colat, radial), lambda a: (0, a + offset, 0, 0)),
        out_shape=jax.ShapeDtypeStruct((8, azim, colat, radial), jnp.float32),
        input_output_aliases=aliases,
        compiler_params=pltpu.CompilerParams(dimension_semantics=("arbitrary",)),
    )(*args)


def mhd_halos(density, velocity, magnetic_vector, pressure, band_pos, band_count):
    fields = [density, velocity[0], velocity[1], velocity[2],
              magnetic_vector[0], magnetic_vector[1], magnetic_vector[2], pressure]
    azim, colat = density.shape[0], density.shape[1]
    az_first = jnp.stack([x[0:1] for x in fields])
    az_last = jnp.stack([x[azim - 1:azim] for x in fields])
    c_first = jnp.stack([x[:, 0:1] for x in fields])
    c_last = jnp.stack([x[:, colat - 1:colat] for x in fields])
    phi_size = lax.axis_size("phi")
    up = [(i, (i + 1) % phi_size) for i in range(phi_size)]
    down = [(j, i) for i, j in up]
    az_low = lax.ppermute(az_last, "phi", up)
    az_high = lax.ppermute(az_first, "phi", down)
    up = [(i, (i + 1) % band_count) for i in range(band_count)]
    down = [(j, i) for i, j in up]
    c_low = lax.ppermute(c_last, "band", up)
    c_high = lax.ppermute(c_first, "band", down)
    c_low = jnp.where(band_pos == 0, c_first, c_low)
    c_high = jnp.where(band_pos == band_count - 1, c_last, c_high)
    return az_low, az_high, c_low, c_high


def body(
    density,
    velocity,
    magnetic_vector,
    pressure,
    fluid_courant_number,
    cosmic_ray_density,
    diffusion_per_bin,
    super_step_scale,
):
    azim_dev = density.shape[0]
    colat_dev = density.shape[1]
    radial_cell_count = density.shape[2]
    band_count = lax.axis_size("band")
    phi_count = lax.axis_size("phi")
    colatitude_count = colat_dev * band_count
    azimuth_cell_count = azim_dev * phi_count
    bin_dev = cosmic_ray_density.shape[0]
    momentum_bin_count = bin_dev * band_count
    outer_shell_count = cosmic_ray_density.shape[3]
    band_pos = lax.axis_index("band")
    mesh_spacing = grid_steps(
        radial_cell_count, colatitude_count, azimuth_cell_count, momentum_bin_count
    )
    fluid_rate, cosmic_ray_rate = rate_limits(
        radial_cell_count,
        outer_shell_count,
        colatitude_count,
        azimuth_cell_count,
        momentum_bin_count,
    )
    radius_full = shell_radii(0, radial_cell_count, radial_cell_count)
    colatitude_local = colatitudes(band_pos * colat_dev, colat_dev, colatitude_count)
    dt = jnp.reshape(fluid_courant_number / fluid_rate, (1,)).astype(jnp.float32)
    mhd_args = (
        dt, density, velocity, magnetic_vector, pressure,
        *mhd_halos(density, velocity, magnetic_vector, pressure, band_pos, band_count),
        (radius_full * mesh_spacing[0])[None],
        (radius_full * mesh_spacing[1])[None],
        jnp.sin(colatitude_local)[:, None] * radius_full * mesh_spacing[2],
    )
    first_planes = azim_dev // 2
    fluid_state = mhd_call(*mhd_args, 0, first_planes)
    first_shell = radial_cell_count - outer_shell_count
    radius_sh = shell_radii(first_shell, outer_shell_count, radial_cell_count)
    colatitude_full = colatitudes(0, colatitude_count, colatitude_count)
    own_fields = jnp.concatenate(
        [velocity[:, :, :, first_shell:], magnetic_vector[:, :, :, first_shell:]], axis=0
    ).astype(jnp.bfloat16)
    gathered = lax.all_gather(own_fields, "band", axis=0)
    edge_low = gathered[:, 2, 0].reshape(1, colatitude_count, outer_shell_count)
    edge_high = gathered[:, 2, azim_dev - 1].reshape(1, colatitude_count, outer_shell_count)
    phi_low, phi_high = exchange(edge_low, edge_high, "phi")
    wind_half = jnp.transpose(gathered, (1, 2, 0, 3, 4)).reshape(
        own_fields.shape[0], azim_dev, colatitude_count, outer_shell_count
    )
    fluid_state, wind_half = lax.optimization_barrier((fluid_state, wind_half))
    wind_vel = wind_half[0:3].astype(jnp.float32)
    azim_pad = jnp.concatenate([phi_low, wind_half[2], phi_high], axis=0).astype(jnp.float32)
    radial_pad = jnp.pad(wind_vel[0], ((0, 0), (0, 0), (1, 1)), mode="edge")
    polar_pad = jnp.pad(wind_vel[1], ((0, 0), (1, 1), (0, 0)), mode="edge")
    spread_half = divergence(
        radial_pad, polar_pad, azim_pad, radius_sh, colatitude_full, mesh_spacing
    ).astype(jnp.bfloat16)
    kappa_here = lax.dynamic_slice_in_dim(diffusion_per_bin, band_pos * bin_dev, bin_dev)
    sts_step = super_step_scale / cosmic_ray_rate
    coef_set = transport_coefficients(
        wind_half[0:3].astype(jnp.float32),
        wind_half[3:6].astype(jnp.float32),
        spread_half.astype(jnp.float32),
        radius_sh,
        colatitude_full,
        mesh_spacing,
    )

    coef_list, up_list, down_list, drift_up, drift_down = coef_set
    coefs = jnp.stack(
        list(coef_list) + list(up_list) + list(down_list)
        + [drift_up / mesh_spacing[3], drift_down / mesh_spacing[3]],
        axis=0,
    )
    scal1 = jnp.reshape(sts_step / 3.0, (1,)).astype(jnp.float32)
    scal2 = jnp.reshape(sts_step / 2.0, (1,)).astype(jnp.float32)
    flags = jnp.stack([band_pos == 0, band_pos == band_count - 1]).astype(jnp.int32)
    bins = cosmic_ray_density.shape[0]
    edges = (
        cosmic_ray_density[:, 0:1],
        cosmic_ray_density[:, azim_dev - 1:azim_dev],
        cosmic_ray_density[0:1],
        cosmic_ray_density[bins - 1:bins],
    )
    edges = [x.astype(jnp.bfloat16) for x in lax.optimization_barrier(edges)]
    az_low, az_high = exchange(edges[0], edges[1], "phi")
    bin_low, bin_high = exchange(edges[2], edges[3], "band")
    first_section, *edges = section_call(
        scal1, flags, kappa_here, cosmic_ray_density, az_low, az_high, bin_low, bin_high, coefs
    )
    steps = edges[0].shape[1]
    az_low, az_high = exchange(edges[0][:, 0:1], edges[1][:, steps - 1:steps], "phi")
    bin_low, bin_high = exchange(edges[2], edges[3], "band")
    fluid_state, first_section = lax.optimization_barrier((fluid_state, first_section))
    fluid_state = mhd_call(
        *mhd_args, first_planes, azim_dev - first_planes, previous=fluid_state
    )
    fluid_state, az_low, az_high, bin_low, bin_high = lax.optimization_barrier(
        (fluid_state, az_low, az_high, bin_low, bin_high)
    )
    cosmic_ray_next = section_call(
        scal2, flags, kappa_here, first_section, az_low, az_high, bin_low, bin_high, coefs,
        cosmic_ray_density,
    )
    return (fluid_state, cosmic_ray_next)


def solution(mesh):
    placed = (
        P("phi", "band", None),
        P(None, "phi", "band", None),
        P(None, "phi", "band", None),
        P("phi", "band", None),
        P(),
        P("band", "phi", None, None),
        P(),
        P(),
    )
    return jax.shard_map(
        body,
        mesh=mesh,
        in_specs=placed,
        out_specs=(P(None, "phi", "band", None), P("band", "phi", None, None)),
        check_vma=False,
    )
```

```python
import functools
import math

import jax
import jax.numpy as jnp
from jax import lax
from jax.experimental import pallas as pl
from jax.experimental.pallas import tpu as pltpu
from jax.sharding import PartitionSpec as P

ADIABATIC = 5.0 / 3.0
INNER_RADIUS = 0.1
R_RATIO = 30.0
COLAT_LOW = math.pi / 6.0
COLAT_SPAN = 2.0 * math.pi / 3.0
P_RATIO = 1000.0
K_RATIO = 0.1
B_FLOOR = 0.1
V_BOUND = 3.0
B_BOUND = 3.0
P_HIGH = 2.0
RHO_LOW = 0.5
KAPPA_HIGH = 0.5


def padded(value, sides, width):
    for axis, dim in sides:
        size, length = (lax.axis_size(axis), value.shape[dim])
        up = [(i, (i + 1) % size) for i in range(size)]
        down = [(j, i) for i, j in up]
        last = lax.slice_in_dim(value, length - width, length, axis=dim)
        leading = lax.slice_in_dim(value, 0, width, axis=dim)
        before = lax.ppermute(last, axis, up)
        after = lax.ppermute(leading, axis, down)
        value = jnp.concatenate([before, value, after], axis=dim)
    return value


def grid_steps(n_radial, n_colat, n_azim, n_bins):
    return (
        math.log(R_RATIO) / n_radial,
        COLAT_SPAN / n_colat,
        2.0 * math.pi / n_azim,
        math.log(P_RATIO) / n_bins,
    )


def rate_limits(n_radial, n_shells, n_colat, n_azim, n_bins):
    radial_spacing, colatitude_spacing, azimuth_spacing, step_m = grid_steps(
        n_radial, n_colat, n_azim, n_bins
    )
    sine_lower = math.sin(COLAT_LOW + 0.5 * colatitude_spacing)
    fluid_radius = INNER_RADIUS * math.exp(0.5 * radial_spacing)
    fastest_limit = V_BOUND + math.sqrt((ADIABATIC * P_HIGH + 3.0 * B_BOUND**2) / RHO_LOW)
    fluid_rate = fastest_limit * (
        1.0 / (fluid_radius * radial_spacing)
        + 1.0 / (fluid_radius * colatitude_spacing)
        + 1.0 / (fluid_radius * sine_lower * azimuth_spacing)
    )
    shell_low = INNER_RADIUS * math.exp(radial_spacing * (n_radial - n_shells + 0.5))
    inv_r = 1.0 / (shell_low * radial_spacing)
    inv_t = 1.0 / (shell_low * colatitude_spacing)
    inv_p = 1.0 / (shell_low * sine_lower * azimuth_spacing)
    cosmic_ray_rate = (
        2.0 * KAPPA_HIGH * (inv_r**2 + inv_t**2 + inv_p**2)
        + V_BOUND * (inv_r + inv_t + inv_p)
        + V_BOUND * (inv_r + inv_t + inv_p + 4.0 / shell_low) / (3.0 * step_m)
    )
    return (fluid_rate, cosmic_ray_rate)


def shell_radii(start_index, cell_count, n_radial):
    cell_index = jnp.arange(cell_count, dtype=jnp.float32) + (start_index + 0.5)
    return INNER_RADIUS * jnp.exp(math.log(R_RATIO) / n_radial * cell_index)


def colatitudes(start_index, cell_count, n_colat):
    cell_index = jnp.arange(cell_count, dtype=jnp.float32) + 0.5
    return COLAT_LOW + COLAT_SPAN * (cell_index + start_index) / n_colat


def edge_fix(values, along_axis, depth, band_pos, axis_count):
    extent = values.shape[along_axis]
    low_ghost = lax.slice_in_dim(values, 0, depth, axis=along_axis)
    high_ghost = lax.slice_in_dim(values, extent - depth, extent, axis=along_axis)
    first_own = lax.slice_in_dim(values, depth, depth + 1, axis=along_axis)
    last_own = lax.slice_in_dim(values, extent - depth - 1, extent - depth, axis=along_axis)
    low_rim = jnp.where(band_pos == 0, first_own, low_ghost)
    high_rim = jnp.where(band_pos == axis_count - 1, last_own, high_ghost)
    middle = lax.slice_in_dim(values, depth, extent - depth, axis=along_axis)
    return jnp.concatenate([low_rim, middle, high_rim], axis=along_axis)


def conserved(primitive):
    density = primitive[0]
    velocity = primitive[1:4]
    magnetic_vector = primitive[4:7]
    pressure = primitive[7]
    energy = (
        pressure / (ADIABATIC - 1.0)
        + 0.5 * density * jnp.sum(velocity * velocity, axis=0)
        + 0.5 * jnp.sum(magnetic_vector * magnetic_vector, axis=0)
    )
    return jnp.concatenate(
        [density[None], density[None] * velocity, magnetic_vector, energy[None]], axis=0
    )


def face_terms(primitive, cell_state, normal):
    density = primitive[0]
    velocity = primitive[1:4]
    magnetic_vector = primitive[4:7]
    pressure = primitive[7]
    v_normal = velocity[normal]
    b_normal = magnetic_vector[normal]
    magnetic = 0.5 * jnp.sum(magnetic_vector * magnetic_vector, axis=0)
    total_p = pressure + magnetic
    momentum = [density * velocity[k] * v_normal - magnetic_vector[k] * b_normal for k in range(3)]
    momentum[normal] = momentum[normal] + total_p
    induction = [v_normal * magnetic_vector[k] - b_normal * velocity[k] for k in range(3)]
    energy_flux = (cell_state[7] + total_p) * v_normal - b_normal * jnp.sum(
        velocity * magnetic_vector, axis=0
    )
    fluxes = jnp.stack([density * v_normal] + momentum + induction + [energy_flux], axis=0)
    speeds = jnp.abs(v_normal) + jnp.sqrt((ADIABATIC * pressure + 2.0 * magnetic) / density)
    return (fluxes, speeds)


def rusanov(primitive, cell_state, normal, along_axis, spacing):
    fluxes, speeds = face_terms(primitive, cell_state, normal)
    length = speeds.shape[along_axis]
    wave_speed = jnp.maximum(
        lax.slice_in_dim(speeds, 0, length - 1, axis=along_axis),
        lax.slice_in_dim(speeds, 1, length, axis=along_axis),
    )
    flux_low = lax.slice_in_dim(fluxes, 0, length - 1, axis=along_axis + 1)
    flux_high = lax.slice_in_dim(fluxes, 1, length, axis=along_axis + 1)
    state_low = lax.slice_in_dim(cell_state, 0, length - 1, axis=along_axis + 1)
    state_high = lax.slice_in_dim(cell_state, 1, length, axis=along_axis + 1)
    face_flux = 0.5 * (flux_low + flux_high) - 0.5 * wave_speed[None] * (state_high - state_low)
    upper = lax.slice_in_dim(face_flux, 1, length - 1, axis=along_axis + 1)
    lower = lax.slice_in_dim(face_flux, 0, length - 2, axis=along_axis + 1)
    return (upper - lower) / spacing


def fluid_update(padded_array, radius_values, colatitude_mesh, timestep_length, mesh_spacing):
    ghosted = jnp.pad(padded_array, ((0, 0), (0, 0), (0, 0), (1, 1)), mode="edge")
    cell_state = conserved(ghosted)
    width_r = radius_values * mesh_spacing[0]
    width_t = radius_values * mesh_spacing[1]
    width_p = jnp.sin(colatitude_mesh)[:, None] * radius_values * mesh_spacing[2]
    radial = rusanov(ghosted[:, 1:-1, 1:-1, :], cell_state[:, 1:-1, 1:-1, :], 0, 2, width_r)
    polar = rusanov(ghosted[:, 1:-1, :, 1:-1], cell_state[:, 1:-1, :, 1:-1], 1, 1, width_t)
    azimuthal = rusanov(ghosted[:, :, 1:-1, 1:-1], cell_state[:, :, 1:-1, 1:-1], 2, 0, width_p)
    return cell_state[:, 1:-1, 1:-1, 1:-1] - timestep_length * (radial + polar + azimuthal)


def divergence(radial_pad, polar_pad, azim_pad, radius_values, colatitude_mesh, mesh_spacing):
    sin_colat = jnp.sin(colatitude_mesh)[:, None]
    cotangent = (jnp.cos(colatitude_mesh) / jnp.sin(colatitude_mesh))[:, None]
    radial_mid = radial_pad[:, :, 1:-1]
    polar_mid = polar_pad[:, 1:-1, :]
    d_radial = (radial_pad[:, :, 2:] - radial_pad[:, :, :-2]) / (
        2.0 * radius_values * mesh_spacing[0]
    )
    d_polar = (polar_pad[:, 2:, :] - polar_pad[:, :-2, :]) / (2.0 * radius_values * mesh_spacing[1])
    d_azim = (azim_pad[2:] - azim_pad[:-2]) / (2.0 * radius_values * sin_colat * mesh_spacing[2])
    return (
        d_radial
        + 2.0 * radial_mid / radius_values
        + d_polar
        + cotangent * polar_mid / radius_values
        + d_azim
    )


def transport_coefficients(
    wind_vel, mag_wind, spread, radius_values, colatitude_mesh, mesh_spacing
):
    width_r = radius_values * mesh_spacing[0]
    width_t = radius_values * mesh_spacing[1]
    width_p = jnp.sin(colatitude_mesh)[:, None] * radius_values * mesh_spacing[2]
    widths = (width_r, width_t, width_p)
    mag_sq = jnp.sum(mag_wind * mag_wind, axis=0) + B_FLOOR
    b_share = K_RATIO + (1.0 - K_RATIO) * mag_wind * mag_wind / mag_sq
    coef_list = [b_share[k] / (widths[k] * widths[k]) for k in range(3)]
    up_list = [jnp.maximum(wind_vel[k], 0.0) / widths[k] for k in range(3)]
    down_list = [jnp.minimum(wind_vel[k], 0.0) / widths[k] for k in range(3)]
    drift_rate = spread / 3.0
    return (
        coef_list,
        up_list,
        down_list,
        jnp.maximum(drift_rate, 0.0),
        jnp.minimum(drift_rate, 0.0),
    )


def transport_rate(extended, coef_set, kappa_col, step_m):
    coef_list, up_list, down_list, drift_up, drift_down = coef_set
    center = extended[1:-1, 1:-1, 1:-1, 1:-1]
    low_cells = (
        extended[1:-1, 1:-1, 1:-1, :-2],
        extended[1:-1, 1:-1, :-2, 1:-1],
        extended[1:-1, :-2, 1:-1, 1:-1],
    )
    high_cells = (
        extended[1:-1, 1:-1, 1:-1, 2:],
        extended[1:-1, 1:-1, 2:, 1:-1],
        extended[1:-1, 2:, 1:-1, 1:-1],
    )
    curvature = coef_list[0] * (high_cells[0] - 2.0 * center + low_cells[0])
    curvature = curvature + coef_list[1] * (high_cells[1] - 2.0 * center + low_cells[1])
    curvature = curvature + coef_list[2] * (high_cells[2] - 2.0 * center + low_cells[2])
    diffusion = kappa_col[:, None, None, None] * curvature
    advection = up_list[0] * (center - low_cells[0]) + down_list[0] * (high_cells[0] - center)
    advection = (
        advection + up_list[1] * (center - low_cells[1]) + down_list[1] * (high_cells[1] - center)
    )
    advection = (
        advection + up_list[2] * (center - low_cells[2]) + down_list[2] * (high_cells[2] - center)
    )
    bin_low = extended[:-2, 1:-1, 1:-1, 1:-1]
    bin_high = extended[2:, 1:-1, 1:-1, 1:-1]
    momentum = (drift_up * (bin_high - center) + drift_down * (center - bin_low)) / step_m
    return diffusion - advection + momentum


ROWS = 16


def _vec(shape, scalar):
    return jnp.full(shape, scalar, jnp.int32)


def section_kernel(scal_ref, flag_ref, kappa_ref, g_ref, gp_ref, gn_ref, azlo_ref, azhi_ref,
                   binlo_ref, binhi_ref, coef_ref, *rest, second):
    if second:
        f0_ref, out_ref = rest
    else:
        out_ref, az_first_ref, az_last_ref, bin_first_ref, bin_last_ref = rest
    step = pl.program_id(0)
    last_step = pl.num_programs(0) - 1
    bins, planes, colat, shells = g_ref.shape
    shape = (ROWS, shells)
    row = lax.broadcasted_iota(jnp.int32, shape, 0)
    lane = lax.broadcasted_iota(jnp.int32, shape, 1)
    first_az = _vec(shape, step) == 0
    last_az = _vec(shape, step) == last_step
    band_first = _vec(shape, flag_ref[0]) == 1
    band_last = _vec(shape, flag_ref[1]) == 1
    scale = scal_ref[0]

    def chunk(k, i, r0, kap, edge):
        rows = slice(r0, r0 + ROWS)
        center = g_ref[k, i, rows, :]
        if r0 == 0:
            low_t = jnp.where(row == 0, center, pltpu.roll(center, 1, 0))
        else:
            low_t = g_ref[k, i, r0 - 1:r0 - 1 + ROWS, :]
        if r0 + ROWS == colat:
            high_t = jnp.where(row == ROWS - 1, center, pltpu.roll(center, ROWS - 1, 0))
        else:
            high_t = g_ref[k, i, r0 + 1:r0 + 1 + ROWS, :]
        low_r = jnp.where(lane == 0, center, pltpu.roll(center, 1, 1))
        high_r = jnp.where(lane == shells - 1, center, pltpu.roll(center, shells - 1, 1))
        if i == 0:
            low_p = jnp.where(first_az, azlo_ref[k, 0, rows, :].astype(jnp.float32), gp_ref[k, 0, rows, :])
        else:
            low_p = g_ref[k, i - 1, rows, :]
        if i == planes - 1:
            high_p = jnp.where(last_az, azhi_ref[k, 0, rows, :].astype(jnp.float32), gn_ref[k, 0, rows, :])
        else:
            high_p = g_ref[k, i + 1, rows, :]
        if edge == "low":
            low_b = jnp.where(band_first, center, binlo_ref[0, i, rows, :].astype(jnp.float32))
        else:
            low_b = g_ref[k - 1, i, rows, :]
        if edge == "high":
            high_b = jnp.where(band_last, center, binhi_ref[0, i, rows, :].astype(jnp.float32))
        else:
            high_b = g_ref[k + 1, i, rows, :]
        d_lo = (center - low_r, center - low_t, center - low_p)
        d_hi = (high_r - center, high_t - center, high_p - center)
        curvature = coef_ref[0, i, rows, :] * (d_hi[0] - d_lo[0])
        curvature = curvature + coef_ref[1, i, rows, :] * (d_hi[1] - d_lo[1])
        curvature = curvature + coef_ref[2, i, rows, :] * (d_hi[2] - d_lo[2])
        advection = coef_ref[3, i, rows, :] * d_lo[0] + coef_ref[6, i, rows, :] * d_hi[0]
        advection = advection + coef_ref[4, i, rows, :] * d_lo[1] + coef_ref[7, i, rows, :] * d_hi[1]
        advection = advection + coef_ref[5, i, rows, :] * d_lo[2] + coef_ref[8, i, rows, :] * d_hi[2]
        momentum = coef_ref[9, i, rows, :] * (high_b - center) + coef_ref[10, i, rows, :] * (center - low_b)
        rate = kap * curvature - advection + momentum
        if second:
            value = 1.5 * center - 0.5 * f0_ref[k, i, rows, :] + scale * rate
        else:
            value = center + scale * rate
        out_ref[k, i, rows, :] = value
        if not second:
            half = value.astype(jnp.bfloat16)
            if i == 0:
                az_first_ref[k, 0, rows, :] = half
            if i == planes - 1:
                az_last_ref[k, 0, rows, :] = half
            if edge == "low":
                bin_first_ref[0, i, rows, :] = half
            if edge == "high":
                bin_last_ref[0, i, rows, :] = half

    def all_rows(k, edge):
        kap = kappa_ref[k]
        for i in range(planes):
            for r0 in range(0, colat, ROWS):
                chunk(k, i, r0, kap, edge)

    all_rows(0, "low")

    def middle(k, carry):
        all_rows(k, None)
        return carry

    lax.fori_loop(1, bins - 1, middle, 0)
    all_rows(bins - 1, "high")


PLANES = 4


def section_call(scal, flags, kappa, g, az_low, az_high, bin_low, bin_high, coefs, f0=None):
    bins, azim, colat, shells = g.shape
    block = (bins, PLANES, colat, shells)
    plane = (bins, 1, colat, shells)
    bin_block = (1, PLANES, colat, shells)
    smem = pl.BlockSpec(memory_space=pltpu.SMEM)
    in_specs = [
        smem,
        smem,
        smem,
        pl.BlockSpec(block, lambda a: (0, a, 0, 0)),
        pl.BlockSpec(plane, lambda a: (0, jnp.maximum(a * PLANES - 1, 0), 0, 0)),
        pl.BlockSpec(plane, lambda a: (0, jnp.minimum(a * PLANES + PLANES, azim - 1), 0, 0)),
        pl.BlockSpec(plane, lambda a: (0, 0, 0, 0)),
        pl.BlockSpec(plane, lambda a: (0, 0, 0, 0)),
        pl.BlockSpec(bin_block, lambda a: (0, a, 0, 0)),
        pl.BlockSpec(bin_block, lambda a: (0, a, 0, 0)),
        pl.BlockSpec((coefs.shape[0], PLANES, colat, shells), lambda a: (0, a, 0, 0)),
    ]
    args = [scal, flags, kappa, g, g, g, az_low, az_high, bin_low, bin_high, coefs]
    out_specs = pl.BlockSpec(block, lambda a: (0, a, 0, 0))
    out_shape = jax.ShapeDtypeStruct(g.shape, jnp.float32)
    if f0 is not None:
        in_specs.append(pl.BlockSpec(block, lambda a: (0, a, 0, 0)))
        args.append(f0)
    else:
        out_specs = [
            out_specs,
            pl.BlockSpec(plane, lambda a: (0, a, 0, 0)),
            pl.BlockSpec(plane, lambda a: (0, a, 0, 0)),
            pl.BlockSpec(bin_block, lambda a: (0, a, 0, 0)),
            pl.BlockSpec(bin_block, lambda a: (0, a, 0, 0)),
        ]
        half_plane = jax.ShapeDtypeStruct((bins, azim // PLANES, colat, shells), jnp.bfloat16)
        half_bin = jax.ShapeDtypeStruct((1, azim, colat, shells), jnp.bfloat16)
        out_shape = [out_shape, half_plane, half_plane, half_bin, half_bin]
    return pl.pallas_call(
        functools.partial(section_kernel, second=f0 is not None),
        grid=(azim // PLANES,),
        in_specs=in_specs,
        out_specs=out_specs,
        out_shape=out_shape,
        compiler_params=pltpu.CompilerParams(dimension_semantics=("arbitrary",)),
    )(*args)


def exchange(first, last, axis):
    size = lax.axis_size(axis)
    up = [(i, (i + 1) % size) for i in range(size)]
    down = [(j, i) for i, j in up]
    return lax.ppermute(last, axis, up), lax.ppermute(first, axis, down)


def cell_state(q):
    rho, v, b, p = q[0], q[1:4], q[4:7], q[7]
    vv = v[0] * v[0] + v[1] * v[1] + v[2] * v[2]
    bb = b[0] * b[0] + b[1] * b[1] + b[2] * b[2]
    energy = p / (ADIABATIC - 1.0) + 0.5 * rho * vv + 0.5 * bb
    return [rho, rho * v[0], rho * v[1], rho * v[2], b[0], b[1], b[2], energy]


def cell_flux(q, u, normal):
    rho, v, b, p = q[0], q[1:4], q[4:7], q[7]
    vn, bn = v[normal], b[normal]
    magnetic = 0.5 * (b[0] * b[0] + b[1] * b[1] + b[2] * b[2])
    total_p = p + magnetic
    momentum = [rho * v[k] * vn - b[k] * bn for k in range(3)]
    momentum[normal] = momentum[normal] + total_p
    induction = [vn * b[k] - bn * v[k] for k in range(3)]
    energy = (u[7] + total_p) * vn - bn * (v[0] * b[0] + v[1] * b[1] + v[2] * b[2])
    speed = jnp.abs(vn) + jnp.sqrt((ADIABATIC * p + 2.0 * magnetic) / rho)
    return [rho * vn] + momentum + induction + [energy], speed


def face_flux(f_low, s_low, u_low, f_high, s_high, u_high):
    wave = jnp.maximum(s_low, s_high)
    return [0.5 * (f_low[c] + f_high[c]) - 0.5 * wave * (u_high[c] - u_low[c]) for c in range(8)]


def mhd_kernel(dt_ref, rho_c, v_c, b_c, p_c, rho_m, v_m, b_m, p_m, rho_p, v_p, b_p, p_p,
               azlo_ref, azhi_ref, clo_ref, chi_ref, wr_ref, wt_ref, wp_ref, *rest, offset, last_step):
    out_ref = rest[-1]
    step = pl.program_id(0) + offset

    def prim(rho_ref, v_ref, b_ref, p_ref):
        return [rho_ref[0], v_ref[0, 0], v_ref[1, 0], v_ref[2, 0],
                b_ref[0, 0], b_ref[1, 0], b_ref[2, 0], p_ref[0]]

    q = prim(rho_c, v_c, b_c, p_c)
    shape = q[0].shape
    nrow, nlane = shape
    row = lax.broadcasted_iota(jnp.int32, shape, 0)
    lane = lax.broadcasted_iota(jnp.int32, shape, 1)
    first_az = _vec(shape, step) == 0
    last_az = _vec(shape, step) == last_step
    q_m = prim(rho_m, v_m, b_m, p_m)
    q_p = prim(rho_p, v_p, b_p, p_p)
    q_m = [jnp.where(first_az, azlo_ref[c, 0], q_m[c]) for c in range(8)]
    q_p = [jnp.where(last_az, azhi_ref[c, 0], q_p[c]) for c in range(8)]
    u = cell_state(q)
    dt = dt_ref[0]

    def lane_next(x):
        return jnp.where(lane == nlane - 1, x, pltpu.roll(x, nlane - 1, 1))

    f, s = cell_flux(q, u, 0)
    high = face_flux(f, s, u, [lane_next(x) for x in f], lane_next(s), [lane_next(x) for x in u])
    low = [jnp.where(lane == 0, f[c], pltpu.roll(high[c], 1, 1)) for c in range(8)]
    width_r = wr_ref[...]
    radial = [(high[c] - low[c]) / width_r for c in range(8)]

    q_l = [clo_ref[c, 0] for c in range(8)]
    q_h = [chi_ref[c, 0] for c in range(8)]
    u_l = cell_state(q_l)
    u_h = cell_state(q_h)
    f, s = cell_flux(q, u, 1)
    f_l, s_l = cell_flux(q_l, u_l, 1)
    f_h, s_h = cell_flux(q_h, u_h, 1)

    def row_next(x, h):
        return jnp.where(row == nrow - 1, jnp.broadcast_to(h, shape), pltpu.roll(x, nrow - 1, 0))

    high = face_flux(f, s, u, [row_next(f[c], f_h[c]) for c in range(8)], row_next(s, s_h),
                     [row_next(u[c], u_h[c]) for c in range(8)])
    first = face_flux(f_l, s_l, u_l, f, s, u)
    low = [jnp.where(row == 0, first[c], pltpu.roll(high[c], 1, 0)) for c in range(8)]
    width_t = wt_ref[...]
    polar = [(high[c] - low[c]) / width_t for c in range(8)]

    u_m = cell_state(q_m)
    u_p = cell_state(q_p)
    f, s = cell_flux(q, u, 2)
    f_m, s_m = cell_flux(q_m, u_m, 2)
    f_p, s_p = cell_flux(q_p, u_p, 2)
    high = face_flux(f, s, u, f_p, s_p, u_p)
    low = face_flux(f_m, s_m, u_m, f, s, u)
    width_p = wp_ref[...]
    for c in range(8):
        azimuthal = (high[c] - low[c]) / width_p
        out_ref[c, 0] = u[c] - dt * (radial[c] + polar[c] + azimuthal)


def mhd_call(dt, density, velocity, magnetic_vector, pressure, az_low, az_high,
             colat_low, colat_high, width_r, width_t, width_p, offset, count, previous=None):
    azim, colat, radial = density.shape
    scalar_block = (1, colat, radial)
    vector_block = (3, 1, colat, radial)

    def own(a):
        return a + offset

    def clamp_low(a):
        return jnp.maximum(a + offset - 1, 0)

    def clamp_high(a):
        return jnp.minimum(a + offset + 1, azim - 1)

    in_specs = [pl.BlockSpec(memory_space=pltpu.SMEM)]
    for pick in (own, clamp_low, clamp_high):
        in_specs += [
            pl.BlockSpec(scalar_block, lambda a, pick=pick: (pick(a), 0, 0)),
            pl.BlockSpec(vector_block, lambda a, pick=pick: (0, pick(a), 0, 0)),
            pl.BlockSpec(vector_block, lambda a, pick=pick: (0, pick(a), 0, 0)),
            pl.BlockSpec(scalar_block, lambda a, pick=pick: (pick(a), 0, 0)),
        ]
    in_specs += [
        pl.BlockSpec((8, 1, colat, radial), lambda a: (0, 0, 0, 0)),
        pl.BlockSpec((8, 1, colat, radial), lambda a: (0, 0, 0, 0)),
        pl.BlockSpec((8, 1, 1, radial), lambda a: (0, a + offset, 0, 0)),
        pl.BlockSpec((8, 1, 1, radial), lambda a: (0, a + offset, 0, 0)),
        pl.BlockSpec((1, radial), lambda a: (0, 0)),
        pl.BlockSpec((1, radial), lambda a: (0, 0)),
        pl.BlockSpec((colat, radial), lambda a: (0, 0)),
    ]
    fields = (density, velocity, magnetic_vector, pressure)
    args = [dt, *fields, *fields, *fields, az_low, az_high, colat_low, colat_high,
            width_r, width_t, width_p]
    aliases = {}
    if previous is not None:
        in_specs.append(pl.BlockSpec(memory_space=pl.ANY))
        aliases = {len(args): 0}
        args.append(previous)
    return pl.pallas_call(
        functools.partial(mhd_kernel, offset=offset, last_step=azim - 1),
        grid=(count,),
        in_specs=in_specs,
        out_specs=pl.BlockSpec((8, 1, colat, radial), lambda a: (0, a + offset, 0, 0)),
        out_shape=jax.ShapeDtypeStruct((8, azim, colat, radial), jnp.float32),
        input_output_aliases=aliases,
        compiler_params=pltpu.CompilerParams(dimension_semantics=("arbitrary",)),
    )(*args)


def mhd_halos(density, velocity, magnetic_vector, pressure, band_pos, band_count):
    fields = [density, velocity[0], velocity[1], velocity[2],
              magnetic_vector[0], magnetic_vector[1], magnetic_vector[2], pressure]
    azim, colat = density.shape[0], density.shape[1]
    az_first = jnp.stack([x[0:1] for x in fields])
    az_last = jnp.stack([x[azim - 1:azim] for x in fields])
    c_first = jnp.stack([x[:, 0:1] for x in fields])
    c_last = jnp.stack([x[:, colat - 1:colat] for x in fields])
    phi_size = lax.axis_size("phi")
    up = [(i, (i + 1) % phi_size) for i in range(phi_size)]
    down = [(j, i) for i, j in up]
    az_low = lax.ppermute(az_last, "phi", up)
    az_high = lax.ppermute(az_first, "phi", down)
    up = [(i, (i + 1) % band_count) for i in range(band_count)]
    down = [(j, i) for i, j in up]
    c_low = lax.ppermute(c_last, "band", up)
    c_high = lax.ppermute(c_first, "band", down)
    c_low = jnp.where(band_pos == 0, c_first, c_low)
    c_high = jnp.where(band_pos == band_count - 1, c_last, c_high)
    return az_low, az_high, c_low, c_high


def body(
    density,
    velocity,
    magnetic_vector,
    pressure,
    fluid_courant_number,
    cosmic_ray_density,
    diffusion_per_bin,
    super_step_scale,
):
    azim_dev = density.shape[0]
    colat_dev = density.shape[1]
    radial_cell_count = density.shape[2]
    band_count = lax.axis_size("band")
    phi_count = lax.axis_size("phi")
    colatitude_count = colat_dev * band_count
    azimuth_cell_count = azim_dev * phi_count
    bin_dev = cosmic_ray_density.shape[0]
    momentum_bin_count = bin_dev * band_count
    outer_shell_count = cosmic_ray_density.shape[3]
    band_pos = lax.axis_index("band")
    mesh_spacing = grid_steps(
        radial_cell_count, colatitude_count, azimuth_cell_count, momentum_bin_count
    )
    fluid_rate, cosmic_ray_rate = rate_limits(
        radial_cell_count,
        outer_shell_count,
        colatitude_count,
        azimuth_cell_count,
        momentum_bin_count,
    )
    radius_full = shell_radii(0, radial_cell_count, radial_cell_count)
    colatitude_local = colatitudes(band_pos * colat_dev, colat_dev, colatitude_count)
    dt = jnp.reshape(fluid_courant_number / fluid_rate, (1,)).astype(jnp.float32)
    mhd_args = (
        dt, density, velocity, magnetic_vector, pressure,
        *mhd_halos(density, velocity, magnetic_vector, pressure, band_pos, band_count),
        (radius_full * mesh_spacing[0])[None],
        (radius_full * mesh_spacing[1])[None],
        jnp.sin(colatitude_local)[:, None] * radius_full * mesh_spacing[2],
    )
    first_planes = azim_dev // 2
    fluid_state = mhd_call(*mhd_args, 0, first_planes)
    first_shell = radial_cell_count - outer_shell_count
    radius_sh = shell_radii(first_shell, outer_shell_count, radial_cell_count)
    colatitude_full = colatitudes(0, colatitude_count, colatitude_count)
    own_fields = jnp.concatenate(
        [velocity[:, :, :, first_shell:], magnetic_vector[:, :, :, first_shell:]], axis=0
    ).astype(jnp.bfloat16)
    wind_half = lax.all_gather(own_fields, "band", axis=2, tiled=True)
    fluid_state, wind_half = lax.optimization_barrier((fluid_state, wind_half))
    wind_vel = wind_half[0:3].astype(jnp.float32)
    azim_pad = padded(wind_half[2], (("phi", 0),), 1).astype(jnp.float32)
    radial_pad = jnp.pad(wind_vel[0], ((0, 0), (0, 0), (1, 1)), mode="edge")
    polar_pad = jnp.pad(wind_vel[1], ((0, 0), (1, 1), (0, 0)), mode="edge")
    spread_half = divergence(
        radial_pad, polar_pad, azim_pad, radius_sh, colatitude_full, mesh_spacing
    ).astype(jnp.bfloat16)
    kappa_here = lax.dynamic_slice_in_dim(diffusion_per_bin, band_pos * bin_dev, bin_dev)
    sts_step = super_step_scale / cosmic_ray_rate
    coef_set = transport_coefficients(
        wind_half[0:3].astype(jnp.float32),
        wind_half[3:6].astype(jnp.float32),
        spread_half.astype(jnp.float32),
        radius_sh,
        colatitude_full,
        mesh_spacing,
    )

    coef_list, up_list, down_list, drift_up, drift_down = coef_set
    coefs = jnp.stack(
        list(coef_list) + list(up_list) + list(down_list)
        + [drift_up / mesh_spacing[3], drift_down / mesh_spacing[3]],
        axis=0,
    )
    scal1 = jnp.reshape(sts_step / 3.0, (1,)).astype(jnp.float32)
    scal2 = jnp.reshape(sts_step / 2.0, (1,)).astype(jnp.float32)
    flags = jnp.stack([band_pos == 0, band_pos == band_count - 1]).astype(jnp.int32)
    bins = cosmic_ray_density.shape[0]
    edges = (
        cosmic_ray_density[:, 0:1],
        cosmic_ray_density[:, azim_dev - 1:azim_dev],
        cosmic_ray_density[0:1],
        cosmic_ray_density[bins - 1:bins],
    )
    edges = [x.astype(jnp.bfloat16) for x in lax.optimization_barrier(edges)]
    az_low, az_high = exchange(edges[0], edges[1], "phi")
    bin_low, bin_high = exchange(edges[2], edges[3], "band")
    first_section, *edges = section_call(
        scal1, flags, kappa_here, cosmic_ray_density, az_low, az_high, bin_low, bin_high, coefs
    )
    steps = edges[0].shape[1]
    az_low, az_high = exchange(edges[0][:, 0:1], edges[1][:, steps - 1:steps], "phi")
    bin_low, bin_high = exchange(edges[2], edges[3], "band")
    fluid_state, first_section = lax.optimization_barrier((fluid_state, first_section))
    fluid_state = mhd_call(
        *mhd_args, first_planes, azim_dev - first_planes, previous=fluid_state
    )
    fluid_state, az_low, az_high, bin_low, bin_high = lax.optimization_barrier(
        (fluid_state, az_low, az_high, bin_low, bin_high)
    )
    cosmic_ray_next = section_call(
        scal2, flags, kappa_here, first_section, az_low, az_high, bin_low, bin_high, coefs,
        cosmic_ray_density,
    )
    return (fluid_state, cosmic_ray_next)


def solution(mesh):
    placed = (
        P("phi", "band", None),
        P(None, "phi", "band", None),
        P(None, "phi", "band", None),
        P("phi", "band", None),
        P(),
        P("band", "phi", None, None),
        P(),
        P(),
    )
    return jax.shard_map(
        body,
        mesh=mesh,
        in_specs=placed,
        out_specs=(P(None, "phi", "band", None), P("band", "phi", None, None)),
        check_vma=False,
    )
```
